32 devices in a mesh: gx: 4 (over y, x), gy: 8 (over z, core).
Axes of the slice: x: 2, y: 2, z: 4, core: 2. Of those that a mesh axis runs over, the one named last changes fastest.
Arguments:
- atom_data: float32 [4, 16, 32, 2, 128], P(None, 'gx', 'gy'), as said below
- counts: int32 [16, 32, 2], P('gx', 'gy'), may hold values from 32 to 128, as said below
- near_flags: int32 [26, 16, 32, 2], P(None, 'gx', 'gy'), may hold values 0 or 1
- child_up: bfloat16 [8, 81, 81], replicated, may hold values from -0.25 to 0.25
- child_down: bfloat16 [8, 81, 81], replicated, may hold values from -0.5 to 0.5
- leaf_far: bfloat16 [81, 81], replicated, may hold values from -0.1875 to 0.1875
- parent_far: bfloat16 [81, 81], replicated, may hold values from -0.0625 to 0.0625
- column_up: bfloat16 [81, 81], replicated, may hold values from -0.3125 to 0.3125
- column_down: bfloat16 [81, 81], replicated, may hold values from -0.5 to 0.5
- tree_up: bfloat16 [2, 2, 81, 81], replicated, may hold values from -0.5 to 0.5
- tree_down: bfloat16 [2, 2, 81, 81], replicated, may hold values from -0.5 to 0.5
- tree_side: bfloat16 [2, 2, 81, 81], replicated, may hold values from -0.5 to 0.5
- lattice: bfloat16 [81, 81], replicated, may hold values from -0.625 to 0.625
Outputs:
- fields: float32 [4, 16, 32, 2, 128], P(None, 'gx', 'gy')
The draws below stay inside these ranges and needn't reach their ends.
Inputs may be any that keep to these rules, and one draw needn't show every extreme that they name: `atom_data`: rows 0 to 2 give an atom's position inside its leaf in leaf widths, from 0 to 1; row 3 its charge. Slots at or past a leaf's count are padding. A leaf's atoms fill its first counts slots; some leaf is full.
All inputs are finite; a program needn't handle non-finite values. No bound on the sum of `near_flags` on one device may be relied on, other than what follows from the above.
Results may differ from the reference program's by a relative error of at most 0.0003.
Values sent between devices are 32-bit elements; how exact they have to be, the bound alone decides.
No kernel may reach another device: no remote copies, remote signals or barrier semaphores. Data moves between devices by JAX's collectives and lax.ppermute only.
A program may use at most 64 MiB of HBM per device.

```python
import jax
import jax.numpy as jnp
from jax import lax

SLOTS = 128
NCOEF = 81
CX = 4
CY = 4
LZ = 2
NX = 16
NY = 32
N_GX = 4
N_GY = 8


def draw_atom_data(key, part):
    first_key, second_key = jax.random.split(key)
    grid_shape = (NX, NY, LZ, SLOTS)
    places = jax.random.uniform(first_key, (3,) + grid_shape, jnp.float32)
    charge = 0.5 * jax.random.normal(second_key, grid_shape, jnp.float32)
    return jnp.concatenate([places, charge[None]], axis=0)


def draw_counts(key, part):
    grid_shape = (NX, NY, LZ)
    drawn = jax.random.randint(key, grid_shape, SLOTS // 4, SLOTS + 1)
    first_leaf = jnp.arange(NX * NY * LZ, dtype=jnp.int32).reshape(grid_shape) == 0
    return jnp.where(first_leaf, SLOTS, drawn).astype(jnp.int32)


def place_ends(array, key, low, top_value):
    longest = array.shape.index(max(array.shape))
    spots = []
    for shift in (0, 1):
        where = [jax.random.randint(jax.random.fold_in(key, axis), (), 0, length) for axis, length in enumerate(array.shape)]
        where[longest] = (where[longest] + shift) % array.shape[longest]
        spots.append(tuple(where))
    return array.at[spots[0]].set(low).at[spots[1]].set(top_value)


def normal_values(stream_key, dims, width, bound, kind=jnp.bfloat16):
    return jnp.clip(width * jax.random.normal(stream_key, dims, jnp.float32), -bound, bound).astype(kind)


def setup_inputs(seed: int = 0) -> dict:
    streams_of = jax.random.split(jax.random.key(seed), 14)
    return {
        "atom_data": draw_atom_data(jax.random.fold_in(streams_of[13], 71), 0),
        "counts": draw_counts(jax.random.fold_in(streams_of[13], 71), 0),
        "near_flags": place_ends((jax.random.randint(streams_of[2], (26, NX, NY, LZ), 0, 2) < 1).astype(jnp.int32), jax.random.fold_in(streams_of[2], 1), 0, 1),
        "child_up": normal_values(streams_of[3], (8, NCOEF, NCOEF), (8 * NCOEF) ** -0.5, 0.25),
        "child_down": normal_values(streams_of[4], (8, NCOEF, NCOEF), (2 * NCOEF) ** -0.5, 0.5),
        "leaf_far": normal_values(streams_of[5], (NCOEF, NCOEF), (13 * NCOEF) ** -0.5, 0.1875),
        "parent_far": normal_values(streams_of[6], (NCOEF, NCOEF), (98 * NCOEF) ** -0.5, 0.0625),
        "column_up": normal_values(streams_of[7], (NCOEF, NCOEF), ((CX // 2) * (CY // 2) * (LZ // 2) * NCOEF) ** -0.5, 0.3125),
        "column_down": normal_values(streams_of[8], (NCOEF, NCOEF), (2 * NCOEF) ** -0.5, 0.5),
        "tree_up": normal_values(streams_of[9], (2, 2, NCOEF, NCOEF), (2 * NCOEF) ** -0.5, 0.5),
        "tree_down": normal_values(streams_of[10], (2, 2, NCOEF, NCOEF), (2 * NCOEF) ** -0.5, 0.5),
        "tree_side": normal_values(streams_of[11], (2, 2, NCOEF, NCOEF), (2 * NCOEF) ** -0.5, 0.5),
        "lattice": normal_values(streams_of[12], (NCOEF, NCOEF), NCOEF ** -0.5, 0.625),
    }


soften = 0.04
coulomb = 0.1
highest = lax.Precision.HIGHEST

def wave_table(coef_count, float_type):
    half_count = (coef_count - 1) // 2
    order_index = jnp.arange(1, half_count + 1, dtype=jnp.int32).astype(float_type)
    height = 1.0 - 2.0 * (order_index - 0.5) / half_count
    radius = jnp.sqrt(jnp.maximum(1.0 - height * height, 0.0))
    angle_turn = 2.399963 * order_index
    magnitude = 1.5 + jnp.mod(order_index, 3.0)
    return jnp.stack([radius * jnp.cos(angle_turn), radius * jnp.sin(angle_turn), height]) * magnitude[None]

def waves_at(atom_data, waves):
    shape_lead = (waves.shape[1],) + (1,) * (atom_data.ndim - 1)
    phases = waves[0].reshape(shape_lead) * (atom_data[0] - 0.5)[None]
    phases = phases + waves[1].reshape(shape_lead) * (atom_data[1] - 0.5)[None]
    phases = phases + waves[2].reshape(shape_lead) * (atom_data[2] - 0.5)[None]
    return (jnp.cos(phases), jnp.sin(phases))

def rotate_by(field, phase):
    half_count = phase.shape[0]
    cosine = jnp.cos(phase)
    sine_part = jnp.sin(phase)
    cos_coef = field[1:1 + half_count]
    sin_coef = field[1 + half_count:]
    return jnp.concatenate([field[0:1], cos_coef * cosine - sin_coef * sine_part, cos_coef * sine_part + sin_coef * cosine], axis=0)

def offset_phase(waves, offset):
    return waves[0] * float(offset[0]) + waves[1] * float(offset[1]) + waves[2] * float(offset[2])

def block_phase(waves, size_x, size_y, size_z, float_type):
    place_x = jnp.arange(size_x, dtype=jnp.int32).astype(float_type)
    place_y = jnp.arange(size_y, dtype=jnp.int32).astype(float_type)
    place_z = jnp.arange(size_z, dtype=jnp.int32).astype(float_type)
    phase = waves[0][:, None, None, None] * place_x[None, :, None, None]
    phase = phase + waves[1][:, None, None, None] * place_y[None, None, :, None]
    return phase + waves[2][:, None, None, None] * place_z[None, None, None, :]

def leaf_moments(atom_data, waves):
    cosine, sine_part = waves_at(atom_data, waves)
    charge = atom_data[3]
    summed = lax.optimization_barrier(jnp.sum(charge, axis=-1))[None]
    return jnp.concatenate([summed, lax.optimization_barrier(jnp.sum(cosine * charge[None], axis=-1)), lax.optimization_barrier(jnp.sum(sine_part * charge[None], axis=-1))], axis=0)

def evaluate(atom_data, local_exp, waves):
    cosine, sine_part = waves_at(atom_data, waves)
    half_count = waves.shape[1]
    cos_local = local_exp[1:1 + half_count][..., None]
    sin_local = local_exp[1 + half_count:][..., None]
    potential = local_exp[0][..., None] + lax.optimization_barrier(jnp.sum(cos_local * cosine + sin_local * sine_part, axis=0))
    mixed_term = cos_local * sine_part - sin_local * cosine
    shape_lead = (half_count,) + (1,) * (mixed_term.ndim - 1)
    field_parts = [lax.optimization_barrier(jnp.sum(waves[component].reshape(shape_lead) * mixed_term, axis=0)) for component in range(3)]
    return (potential, field_parts)

def near_row(target, source, flag_grid, shift_vec, keep_self):
    weight = source[3] * flag_grid[..., None]
    delta_x = target[0][..., :, None] - (source[0][..., None, :] + shift_vec[0])
    delta_y = target[1][..., :, None] - (source[1][..., None, :] + shift_vec[1])
    delta_z = target[2][..., :, None] - (source[2][..., None, :] + shift_vec[2])
    inverse = lax.rsqrt(delta_x * delta_x + delta_y * delta_y + delta_z * delta_z + soften)
    pair_term = weight[..., None, :] * keep_self * inverse
    cube_term = pair_term * inverse * inverse
    return jnp.stack([lax.optimization_barrier(jnp.sum(pair_term, axis=-1)), lax.optimization_barrier(jnp.sum(cube_term * delta_x, axis=-1)), lax.optimization_barrier(jnp.sum(cube_term * delta_y, axis=-1)), lax.optimization_barrier(jnp.sum(cube_term * delta_z, axis=-1))])

def full_flags(near_flags, float_type):
    flags_float = near_flags.astype(float_type)
    centre = jnp.ones((1,) + flags_float.shape[1:], float_type)
    return jnp.concatenate([flags_float[:13], centre, flags_float[13:]], axis=0)

def leaf_offsets():
    return [(shift_x, shift_y, shift_z) for shift_x in (-1, 0, 1) for shift_y in (-1, 0, 1) for shift_z in (-1, 0, 1) if (shift_x, shift_y, shift_z) != (0, 0, 0)]

def parent_offsets():
    return [(shift_x, shift_y, shift_z) for shift_x in range(-2, 3) for shift_y in range(-2, 3) for shift_z in range(-2, 3) if max(abs(shift_x), abs(shift_y), abs(shift_z)) == 2]

def moved_grid(field_grid, offset):
    rolled = jnp.roll(field_grid, (-offset[0], -offset[1]), axis=(1, 2))
    depth_z = field_grid.shape[3]
    padded = jnp.pad(rolled, ((0, 0), (0, 0), (0, 0), (2, 2)))
    return padded[:, :, :, 2 + offset[2]:2 + offset[2] + depth_z]

def climb_children(moments, matrices):
    coef_count, size_x, size_y, size_z = moments.shape
    parted = moments.reshape(coef_count, size_x // 2, 2, size_y // 2, 2, size_z // 2, 2)
    return jnp.einsum('abckj,jxaybzc->kxyz', matrices.reshape(2, 2, 2, coef_count, coef_count), parted, precision=highest)

def descend_children(parent_local, matrices):
    coef_count, size_x, size_y, size_z = parent_local.shape
    spread = jnp.einsum('abckj,jxyz->kxaybzc', matrices.reshape(2, 2, 2, coef_count, coef_count), parent_local, precision=highest)
    return spread.reshape(coef_count, 2 * size_x, 2 * size_y, 2 * size_z)

def flip_pair(column_grid, axis_num, level_bit):
    coef_count, size_x, size_y = column_grid.shape
    span_size = 2 ** level_bit
    if axis_num == 0:
        parted = column_grid.reshape(coef_count, size_x // (2 * span_size), 2, span_size, size_y)
        return parted[:, :, ::-1].reshape(column_grid.shape)
    parted = column_grid.reshape(coef_count, size_x, size_y // (2 * span_size), 2, span_size)
    return parted[:, :, :, ::-1].reshape(column_grid.shape)

def side_grid(axis_num, level_bit, size_x, size_y):
    positions = jnp.arange(size_x if axis_num == 0 else size_y, dtype=jnp.int32)
    own_side = positions // 2 ** level_bit % 2
    return own_side[:, None] if axis_num == 0 else own_side[None, :]

def choose_side(matrices, own_side, column_grid):
    first = jnp.einsum('kj,jxy->kxy', matrices[0], column_grid, precision=highest)
    second = jnp.einsum('kj,jxy->kxy', matrices[1], column_grid, precision=highest)
    return jnp.where(own_side[None] == 0, first, second)

def column_tree(column_grid, tree_up, tree_down, tree_side, lattice):
    float_type = column_grid.dtype
    coef_count, size_x, size_y = column_grid.shape
    levels = [(0, level_bit) for level_bit in range(size_x.bit_length() - 1)] + [(1, level_bit) for level_bit in range(size_y.bit_length() - 1)]
    current = column_grid
    visited = []
    for axis_num, level_bit in levels:
        partner = flip_pair(current, axis_num, level_bit)
        own_side = side_grid(axis_num, level_bit, size_x, size_y)
        climbs = tree_up[axis_num].astype(float_type)
        current = choose_side(climbs, own_side, current) + choose_side(climbs, 1 - own_side, partner)
        visited.append((axis_num, own_side, partner))
    local_exp = jnp.einsum('kj,jxy->kxy', lattice.astype(float_type), current, precision=highest)
    for axis_num, own_side, partner in reversed(visited):
        local_exp = choose_side(tree_down[axis_num].astype(float_type), own_side, local_exp) + choose_side(tree_side[axis_num].astype(float_type), own_side, partner)
    return local_exp

def assemble(near_terms, potential, field_parts, charge, live_slots):
    rows = [coulomb * (near_terms[0] + potential) * live_slots]
    for component in range(3):
        rows.append(coulomb * charge * (near_terms[1 + component] + field_parts[component]))
    return jnp.stack(rows)

def near_field(charged, flag_table):
    depth_z = charged.shape[3]
    slot_count = charged.shape[4]
    padded = jnp.pad(charged, ((0, 0), (0, 0), (0, 0), (1, 1), (0, 0)))
    target = jnp.moveaxis(charged, 1, 0)
    identity = jnp.eye(slot_count, dtype=charged.dtype)

    def offset_step(running, offset_index):
        shift_x = offset_index // 9 - 1
        shift_y = offset_index // 3 % 3 - 1
        shift_z = offset_index % 3 - 1
        source = jnp.roll(padded, (-shift_x, -shift_y), axis=(1, 2))
        source = lax.dynamic_slice_in_dim(source, 1 + shift_z, depth_z, 3)
        source = jnp.moveaxis(source, 1, 0)
        flag_grid = flag_table[offset_index]
        keep_self = 1.0 - identity * (offset_index == 13).astype(charged.dtype)
        shift_vec = jnp.stack([shift_x, shift_y, shift_z]).astype(charged.dtype)
        row_terms = lax.map(lambda packed: near_row(packed[0], packed[1], packed[2], shift_vec, keep_self), (target, source, flag_grid))
        return (running + row_terms, None)
    running, unused = lax.scan(offset_step, jnp.zeros_like(target), jnp.arange(27, dtype=jnp.int32))
    return jnp.moveaxis(running, 0, 1)

def reference(atom_data, counts, near_flags, child_up, child_down, leaf_far, parent_far, column_up, column_down, tree_up, tree_down, tree_side, lattice):
    float_type = atom_data.dtype
    coef_count = lattice.shape[0]
    slot_count = atom_data.shape[4]
    live_slots = (jnp.arange(slot_count, dtype=jnp.int32)[None, None, None, :] < counts[..., None]).astype(float_type)
    charged = jnp.concatenate([atom_data[:3], (atom_data[3] * live_slots)[None]], axis=0)
    waves = wave_table(coef_count, float_type)
    half_count = waves.shape[1]
    flag_table = full_flags(near_flags, float_type)
    near_terms = near_field(charged, flag_table)
    moments = leaf_moments(charged, waves)
    parents = climb_children(moments, child_up.astype(float_type))
    grid_x, grid_y, grid_z = (parents.shape[1], parents.shape[2], parents.shape[3])
    block_x, block_y = (grid_x // N_GX, grid_y // N_GY)
    blocks = parents.reshape(coef_count, N_GX, block_x, N_GY, block_y, grid_z)
    phase_grid = block_phase(waves, block_x, block_y, grid_z, float_type).reshape(half_count, 1, block_x, 1, block_y, grid_z)
    turned = lax.optimization_barrier(jnp.sum(rotate_by(blocks, phase_grid), axis=(2, 4, 5)))
    columns = jnp.einsum('kj,jgh->kgh', column_up.astype(float_type), turned, precision=highest)
    column_local = column_tree(columns, tree_up, tree_down, tree_side, lattice)
    lowered = jnp.einsum('kj,jgh->kgh', column_down.astype(float_type), column_local, precision=highest)
    spread = jnp.broadcast_to(lowered[:, :, None, :, None, None], blocks.shape)
    parent_local = rotate_by(spread, -phase_grid).reshape(parents.shape)
    parent_sum = jnp.zeros_like(parents)
    for offset in parent_offsets():
        parent_sum = parent_sum + rotate_by(moved_grid(parents, offset), offset_phase(waves, offset).reshape(half_count, 1, 1, 1))
    parent_local = parent_local + jnp.einsum('kj,jxyz->kxyz', parent_far.astype(float_type), parent_sum, precision=highest)
    leaf_local = descend_children(parent_local, child_down.astype(float_type))
    leaf_sum = jnp.zeros_like(moments)
    for offset_num, offset in enumerate(leaf_offsets()):
        far_weight = (1.0 - near_flags[offset_num].astype(float_type))[None]
        leaf_sum = leaf_sum + rotate_by(moved_grid(moments, offset) * far_weight, offset_phase(waves, offset).reshape(half_count, 1, 1, 1))
    leaf_local = leaf_local + jnp.einsum('kj,jxyz->kxyz', leaf_far.astype(float_type), leaf_sum, precision=highest)
    potential, field_parts = evaluate(charged, leaf_local, waves)
    return assemble(near_terms, potential, field_parts, charged[3], live_slots)
```

```python
import functools

import jax
import jax.numpy as jnp
from jax import lax
from jax.experimental import pallas as pl
from jax.experimental.pallas import tpu as pltpu
from jax.sharding import PartitionSpec as P

soften = 0.04
coulomb = 0.1
highest = lax.Precision.HIGHEST


def from_partner(value, axis, bit):
    mask = 2**bit
    pairs = [(source, source ^ mask) for source in range(lax.axis_size(axis))]
    return lax.ppermute(value, axis, pairs)


def extended_2(block, sides, width):
    for axis, dim in sides:
        count = lax.axis_size(axis)
        forward = [(i, i + 1) for i in range(count - 1)]
        forward.append((count - 1, 0))
        backward = [(target, source) for source, target in forward]
        low = lax.ppermute(
            lax.slice_in_dim(block, block.shape[dim] - width, None, axis=dim), axis, forward
        )
        high = lax.ppermute(lax.slice_in_dim(block, 0, width, axis=dim), axis, backward)
        block = jnp.concatenate([low, block, high], axis=dim)
    return block


def wave_table(coef_count, float_type):
    half_count = (coef_count - 1) // 2
    order_index = jnp.arange(1, half_count + 1, dtype=jnp.int32).astype(float_type)
    height = 1.0 - 2.0 * (order_index - 0.5) / half_count
    radius = jnp.sqrt(jnp.maximum(1.0 - height * height, 0.0))
    angle_turn = 2.399963 * order_index
    magnitude = 1.5 + jnp.mod(order_index, 3.0)
    return (
        jnp.stack([radius * jnp.cos(angle_turn), radius * jnp.sin(angle_turn), height])
        * magnitude[None]
    )


def waves_at(atom_data, waves):
    shape_lead = (waves.shape[1],) + (1,) * (atom_data.ndim - 1)
    phases = waves[0].reshape(shape_lead) * (atom_data[0] - 0.5)[None]
    phases = phases + waves[1].reshape(shape_lead) * (atom_data[1] - 0.5)[None]
    phases = phases + waves[2].reshape(shape_lead) * (atom_data[2] - 0.5)[None]
    return (jnp.cos(phases), jnp.sin(phases))


def rotate_by(field, phase):
    half_count = phase.shape[0]
    cosine = jnp.cos(phase)
    sine_part = jnp.sin(phase)
    cos_coef = field[1 : 1 + half_count]
    sin_coef = field[1 + half_count :]
    return jnp.concatenate(
        [
            field[0:1],
            cos_coef * cosine - sin_coef * sine_part,
            cos_coef * sine_part + sin_coef * cosine,
        ],
        axis=0,
    )


def offset_phases(waves, offsets):
    table = jnp.array(offsets, dtype=jnp.float32)
    return (
        table[:, 0:1] * waves[0][None]
        + table[:, 1:2] * waves[1][None]
        + table[:, 2:3] * waves[2][None]
    )


def block_phase(waves, size_x, size_y, size_z, float_type):
    place_x = jnp.arange(size_x, dtype=jnp.int32).astype(float_type)
    place_y = jnp.arange(size_y, dtype=jnp.int32).astype(float_type)
    place_z = jnp.arange(size_z, dtype=jnp.int32).astype(float_type)
    phase = waves[0][:, None, None, None] * place_x[None, :, None, None]
    phase = phase + waves[1][:, None, None, None] * place_y[None, None, :, None]
    return phase + waves[2][:, None, None, None] * place_z[None, None, None, :]


def leaf_moments(atom_data, waves):
    cosine, sine_part = waves_at(atom_data, waves)
    charge = atom_data[3]
    summed = jnp.sum(charge, axis=-1)[None]
    return jnp.concatenate(
        [
            summed,
            jnp.sum(cosine * charge[None], axis=-1),
            jnp.sum(sine_part * charge[None], axis=-1),
        ],
        axis=0,
    )


def evaluate(atom_data, local_exp, waves):
    cosine, sine_part = waves_at(atom_data, waves)
    half_count = waves.shape[1]
    cos_local = local_exp[1 : 1 + half_count][..., None]
    sin_local = local_exp[1 + half_count :][..., None]
    potential = local_exp[0][..., None] + jnp.sum(
        cos_local * cosine + sin_local * sine_part, axis=0
    )
    mixed_term = cos_local * sine_part - sin_local * cosine
    shape_lead = (half_count,) + (1,) * (mixed_term.ndim - 1)
    field_parts = [
        jnp.sum(waves[component].reshape(shape_lead) * mixed_term, axis=0) for component in range(3)
    ]
    return (potential, field_parts)


def near_row(target, source, flag_grid, shift_vec, keep_self):
    weight = source[3] * flag_grid[..., None]
    delta_x = target[0][..., :, None] - (source[0][..., None, :] + shift_vec[0])
    delta_y = target[1][..., :, None] - (source[1][..., None, :] + shift_vec[1])
    delta_z = target[2][..., :, None] - (source[2][..., None, :] + shift_vec[2])
    inverse = lax.rsqrt(delta_x * delta_x + delta_y * delta_y + delta_z * delta_z + soften)
    pair_term = weight[..., None, :] * keep_self * inverse
    cube_term = pair_term * inverse * inverse
    return jnp.stack(
        [
            jnp.sum(pair_term, axis=-1),
            jnp.sum(cube_term * delta_x, axis=-1),
            jnp.sum(cube_term * delta_y, axis=-1),
            jnp.sum(cube_term * delta_z, axis=-1),
        ]
    )


def full_flags(near_flags, float_type):
    flags_float = near_flags.astype(float_type)
    centre = jnp.ones((1,) + flags_float.shape[1:], float_type)
    return jnp.concatenate([flags_float[:13], centre, flags_float[13:]], axis=0)


def leaf_offsets():
    return [
        (shift_x, shift_y, shift_z)
        for shift_x in (-1, 0, 1)
        for shift_y in (-1, 0, 1)
        for shift_z in (-1, 0, 1)
        if (shift_x, shift_y, shift_z) != (0, 0, 0)
    ]


def parent_offsets():
    return [
        (shift_x, shift_y, shift_z)
        for shift_x in range(-2, 3)
        for shift_y in range(-2, 3)
        for shift_z in range(-2, 3)
        if max(abs(shift_x), abs(shift_y), abs(shift_z)) == 2
    ]


def climb_children(moments, matrices):
    coef_count, size_x, size_y, size_z = moments.shape
    parted = moments.reshape(coef_count, size_x // 2, 2, size_y // 2, 2, size_z // 2, 2)
    return jnp.einsum(
        "abckj,jxaybzc->kxyz",
        matrices.reshape(2, 2, 2, coef_count, coef_count),
        parted,
        precision=highest,
    )


def descend_children(parent_local, matrices):
    coef_count, size_x, size_y, size_z = parent_local.shape
    spread = jnp.einsum(
        "abckj,jxyz->kxaybzc",
        matrices.reshape(2, 2, 2, coef_count, coef_count),
        parent_local,
        precision=highest,
    )
    return spread.reshape(coef_count, 2 * size_x, 2 * size_y, 2 * size_z)


def matrix_vector(matrix, vector):
    return jnp.dot(matrix, vector, precision=highest)


def pick_side(matrices, own_side):
    return lax.dynamic_index_in_dim(matrices, own_side, 0, keepdims=False)


def pair_step(matrices, own_side, current, partner):
    return matrix_vector(pick_side(matrices, own_side), current) + matrix_vector(
        pick_side(matrices, 1 - own_side), partner
    )


def chain_tree(column, tree_up, tree_down, tree_side, lattice):
    climbs = tree_up.astype(jnp.float32)
    lowers = tree_down.astype(jnp.float32)
    sideways = tree_side.astype(jnp.float32)
    current = column
    visited = []
    for level_bit in range(lax.axis_size("gx").bit_length() - 1):
        partner = from_partner(current, "gx", level_bit)
        own_side = lax.axis_index("gx") // 2**level_bit % 2
        current = pair_step(climbs[0], own_side, current, partner)
        visited.append((0, own_side, partner))
    for level_bit in range(lax.axis_size("gy").bit_length() - 1):
        partner = from_partner(current, "gy", level_bit)
        own_side = lax.axis_index("gy") // 2**level_bit % 2
        current = pair_step(climbs[1], own_side, current, partner)
        visited.append((1, own_side, partner))
    local_exp = matrix_vector(lattice.astype(jnp.float32), current)
    for axis_num, own_side, partner in reversed(visited):
        local_exp = matrix_vector(pick_side(lowers[axis_num], own_side), local_exp) + matrix_vector(
            pick_side(sideways[axis_num], own_side), partner
        )
    return local_exp


def assemble(near_terms, potential, field_parts, charge, live_slots):
    rows = [coulomb * (near_terms[0] + potential) * live_slots]
    for component in range(3):
        rows.append(coulomb * charge * (near_terms[1 + component] + field_parts[component]))
    return jnp.stack(rows)


NEAR_ROWS = 16


def near_pairs(tx, ty, tz, srow, shift, mask):
    sx = srow[0:1, :] + shift[0]
    sy = srow[1:2, :] + shift[1]
    sz = srow[2:3, :] + shift[2]
    weight = srow[3:4, :]
    delta_x = tx - sx
    delta_y = ty - sy
    delta_z = tz - sz
    inverse = lax.rsqrt(delta_x * delta_x + delta_y * delta_y + delta_z * delta_z + soften)
    pair_term = weight * inverse
    if mask is not None:
        pair_term = jnp.where(mask, pair_term, 0.0)
    cube_term = pair_term * inverse * inverse
    return (pair_term, cube_term * delta_x, cube_term * delta_y, cube_term * delta_z)


def near_kernel(grid_shape, count_ref, active_ref, target_ref, source_ref, out_ref):
    size_x, size_y, size_z = grid_shape
    leaf_count = size_x * size_y * size_z
    ext_y, ext_z = size_y + 2, size_z
    rows = NEAR_ROWS
    lanes = out_ref.shape[2]
    out_ref[...] = jnp.zeros(out_ref.shape, out_ref.dtype)
    lane = lax.broadcasted_iota(jnp.int32, (rows, lanes), 1)
    row = lax.broadcasted_iota(jnp.int32, (rows, lanes), 0)
    offsets = leaf_offsets()

    def leaf_body(leaf, carry):
        leaf_x = leaf // (size_y * size_z)
        leaf_y = leaf // size_z % size_y
        leaf_z = leaf % size_z
        chunk_count = (count_ref[leaf] + rows - 1) // rows

        def chunk_body(chunk, carry2):
            first = pl.multiple_of(chunk * rows, rows)
            column = target_ref[leaf, pl.ds(first, rows), :]
            tx = jnp.broadcast_to(column[:, 0:1], (rows, lanes))
            ty = jnp.broadcast_to(column[:, 1:2], (rows, lanes))
            tz = jnp.broadcast_to(column[:, 2:3], (rows, lanes))
            centre = ((leaf_x + 1) * ext_y + leaf_y + 1) * ext_z + leaf_z
            acc = near_pairs(tx, ty, tz, source_ref[centre], (0.0, 0.0, 0.0), row + first != lane)
            for number, offset in enumerate(offsets):
                place = ((leaf_x + 1 + offset[0]) * ext_y + leaf_y + 1 + offset[1]) * ext_z + leaf_z + offset[2]
                place = jnp.minimum(jnp.maximum(place, 0), source_ref.shape[0] - 1)
                shift = tuple(float(v) for v in offset)

                def taken(acc, place=place, shift=shift):
                    terms = near_pairs(tx, ty, tz, source_ref[place], shift, None)
                    return tuple(a + b for a, b in zip(acc, terms))

                acc = lax.cond(active_ref[number * leaf_count + leaf] != 0, taken, lambda acc: acc, acc)
            sums = [jnp.sum(part, axis=1, keepdims=True) for part in acc]
            tile = jnp.where(
                lane == 0, sums[0], jnp.where(lane == 1, sums[1], jnp.where(lane == 2, sums[2], sums[3]))
            )
            out_ref[leaf, pl.ds(first, rows), :] = jnp.where(lane < 4, tile, 0.0)
            return carry2

        lax.fori_loop(0, chunk_count, chunk_body, 0)
        return carry

    lax.fori_loop(0, leaf_count, leaf_body, 0)


def near_local(charged, rimmed, counts, near_flags):
    size_x, size_y, size_z, slot_count = charged.shape[1:]
    leaf_count = size_x * size_y * size_z
    target = jnp.transpose(charged, (1, 2, 3, 4, 0)).reshape(leaf_count, slot_count, 4)
    source = jnp.transpose(rimmed, (1, 2, 3, 0, 4)).reshape(-1, 4, slot_count)
    source = jnp.pad(source, ((0, 0), (0, 4), (0, 0)))
    layer = jnp.arange(size_z, dtype=jnp.int32)
    valid = jnp.stack([((layer + offset[2] >= 0) & (layer + offset[2] < size_z)) for offset in leaf_offsets()])
    active = (near_flags != 0) & valid[:, None, None, :]
    active = active.astype(jnp.int32).reshape(-1)
    pairs = leaf_count * slot_count * slot_count * 27
    out = pl.pallas_call(
        functools.partial(near_kernel, (size_x, size_y, size_z)),
        out_shape=jax.ShapeDtypeStruct((leaf_count, slot_count, 128), jnp.float32),
        in_specs=[
            pl.BlockSpec(memory_space=pltpu.SMEM),
            pl.BlockSpec(memory_space=pltpu.SMEM),
            pl.BlockSpec(memory_space=pltpu.VMEM),
            pl.BlockSpec(memory_space=pltpu.VMEM),
        ],
        out_specs=pl.BlockSpec(memory_space=pltpu.VMEM),
        cost_estimate=pl.CostEstimate(
            flops=10 * pairs, transcendentals=pairs // 2, bytes_accessed=8 * leaf_count * slot_count * 128
        ),
    )(counts.reshape(-1), active, target, source)
    near = jnp.transpose(out[:, :, :4], (2, 0, 1))
    return near.reshape(4, size_x, size_y, size_z, slot_count)


def body(
    atom_data,
    counts,
    near_flags,
    child_up,
    child_down,
    leaf_far,
    parent_far,
    column_up,
    column_down,
    tree_up,
    tree_down,
    tree_side,
    lattice,
):
    coef_count = lattice.shape[0]
    slot_count = atom_data.shape[4]
    size_x, size_y, size_z = (atom_data.shape[1], atom_data.shape[2], atom_data.shape[3])
    live_slots = (
        jnp.arange(slot_count, dtype=jnp.int32)[None, None, None, :] < counts[..., None]
    ).astype(jnp.float32)
    charged = jnp.concatenate([atom_data[:3], (atom_data[3] * live_slots)[None]], axis=0)
    waves = wave_table(coef_count, jnp.float32)
    half_count = waves.shape[1]
    rimmed = extended_2(charged, (("gx", 1), ("gy", 2)), 1)
    moments = leaf_moments(charged, waves)
    parents = climb_children(moments, child_up.astype(jnp.float32))
    parent_rim = extended_2(parents, (("gx", 1), ("gy", 2)), 2)
    parent_rim = jnp.pad(parent_rim, ((0, 0), (0, 0), (0, 0), (2, 2)))
    half_x, half_y, half_z = (parents.shape[1], parents.shape[2], parents.shape[3])
    phase_grid = block_phase(waves, half_x, half_y, half_z, jnp.float32)
    turned = jnp.sum(rotate_by(parents, phase_grid), axis=(1, 2, 3))
    column = matrix_vector(column_up.astype(jnp.float32), turned)
    column_local = chain_tree(column, tree_up, tree_down, tree_side, lattice)
    leaf_rim = leaf_moments(rimmed, waves)
    leaf_rim = jnp.pad(leaf_rim, ((0, 0), (0, 0), (0, 0), (1, 1)))
    near_terms = near_local(charged, rimmed, counts, near_flags)
    lowered = matrix_vector(column_down.astype(jnp.float32), column_local)
    parent_local = rotate_by(
        jnp.broadcast_to(lowered[:, None, None, None], parents.shape), -phase_grid
    )
    far_parents = parent_offsets()
    parent_stack = jnp.stack(
        [
            parent_rim[
                :,
                2 + offset[0] : 2 + offset[0] + half_x,
                2 + offset[1] : 2 + offset[1] + half_y,
                2 + offset[2] : 2 + offset[2] + half_z,
            ]
            for offset in far_parents
        ]
    )
    parent_turns = offset_phases(waves, far_parents).reshape(len(far_parents), half_count, 1, 1, 1)
    parent_sum = jnp.sum(jax.vmap(rotate_by)(parent_stack, parent_turns), axis=0)
    parent_local = parent_local + jnp.einsum(
        "kj,jxyz->kxyz", parent_far.astype(jnp.float32), parent_sum, precision=highest
    )
    leaf_local = descend_children(parent_local, child_down.astype(jnp.float32))
    near_leaves = leaf_offsets()
    leaf_stack = jnp.stack(
        [
            leaf_rim[
                :,
                1 + offset[0] : 1 + offset[0] + size_x,
                1 + offset[1] : 1 + offset[1] + size_y,
                1 + offset[2] : 1 + offset[2] + size_z,
            ]
            for offset in near_leaves
        ]
    )
    leaf_stack = leaf_stack * (1.0 - near_flags.astype(jnp.float32))[:, None]
    leaf_turns = offset_phases(waves, near_leaves).reshape(len(near_leaves), half_count, 1, 1, 1)
    leaf_sum = jnp.sum(jax.vmap(rotate_by)(leaf_stack, leaf_turns), axis=0)
    leaf_local = leaf_local + jnp.einsum(
        "kj,jxyz->kxyz", leaf_far.astype(jnp.float32), leaf_sum, precision=highest
    )
    potential, field_parts = evaluate(charged, leaf_local, waves)
    return assemble(near_terms, potential, field_parts, charged[3], live_slots)


def solution(mesh):
    in_specs = (
        P(None, "gx", "gy", None, None),
        P("gx", "gy", None),
        P(None, "gx", "gy", None),
        P(),
        P(),
        P(),
        P(),
        P(),
        P(),
        P(),
        P(),
        P(),
        P(),
    )
    out_specs = P(None, "gx", "gy", None, None)
    return jax.shard_map(body, mesh=mesh, in_specs=in_specs, out_specs=out_specs, check_vma=False)
```

```python
import functools

import jax
import jax.numpy as jnp
from jax import lax
from jax.experimental import pallas as pl
from jax.experimental.pallas import tpu as pltpu
from jax.sharding import PartitionSpec as P

soften = 0.04
coulomb = 0.1
highest = lax.Precision.HIGHEST


def from_partner(value, axis, bit):
    mask = 2**bit
    pairs = [(source, source ^ mask) for source in range(lax.axis_size(axis))]
    return lax.ppermute(value, axis, pairs)


def extended_2(block, sides, width):
    for axis, dim in sides:
        count = lax.axis_size(axis)
        forward = [(i, i + 1) for i in range(count - 1)]
        forward.append((count - 1, 0))
        backward = [(target, source) for source, target in forward]
        low = lax.ppermute(
            lax.slice_in_dim(block, block.shape[dim] - width, None, axis=dim), axis, forward
        )
        high = lax.ppermute(lax.slice_in_dim(block, 0, width, axis=dim), axis, backward)
        block = jnp.concatenate([low, block, high], axis=dim)
    return block


def wave_table(coef_count, float_type):
    half_count = (coef_count - 1) // 2
    order_index = jnp.arange(1, half_count + 1, dtype=jnp.int32).astype(float_type)
    height = 1.0 - 2.0 * (order_index - 0.5) / half_count
    radius = jnp.sqrt(jnp.maximum(1.0 - height * height, 0.0))
    angle_turn = 2.399963 * order_index
    magnitude = 1.5 + jnp.mod(order_index, 3.0)
    return (
        jnp.stack([radius * jnp.cos(angle_turn), radius * jnp.sin(angle_turn), height])
        * magnitude[None]
    )


def waves_at(atom_data, waves):
    shape_lead = (waves.shape[1],) + (1,) * (atom_data.ndim - 1)
    phases = waves[0].reshape(shape_lead) * (atom_data[0] - 0.5)[None]
    phases = phases + waves[1].reshape(shape_lead) * (atom_data[1] - 0.5)[None]
    phases = phases + waves[2].reshape(shape_lead) * (atom_data[2] - 0.5)[None]
    return (jnp.cos(phases), jnp.sin(phases))


def rotate_by(field, phase):
    half_count = phase.shape[0]
    cosine = jnp.cos(phase)
    sine_part = jnp.sin(phase)
    cos_coef = field[1 : 1 + half_count]
    sin_coef = field[1 + half_count :]
    return jnp.concatenate(
        [
            field[0:1],
            cos_coef * cosine - sin_coef * sine_part,
            cos_coef * sine_part + sin_coef * cosine,
        ],
        axis=0,
    )


def offset_phases(waves, offsets):
    table = jnp.array(offsets, dtype=jnp.float32)
    return (
        table[:, 0:1] * waves[0][None]
        + table[:, 1:2] * waves[1][None]
        + table[:, 2:3] * waves[2][None]
    )


def block_phase(waves, size_x, size_y, size_z, float_type):
    place_x = jnp.arange(size_x, dtype=jnp.int32).astype(float_type)
    place_y = jnp.arange(size_y, dtype=jnp.int32).astype(float_type)
    place_z = jnp.arange(size_z, dtype=jnp.int32).astype(float_type)
    phase = waves[0][:, None, None, None] * place_x[None, :, None, None]
    phase = phase + waves[1][:, None, None, None] * place_y[None, None, :, None]
    return phase + waves[2][:, None, None, None] * place_z[None, None, None, :]


def leaf_moments(atom_data, waves):
    cosine, sine_part = waves_at(atom_data, waves)
    charge = atom_data[3]
    summed = jnp.sum(charge, axis=-1)[None]
    return jnp.concatenate(
        [
            summed,
            jnp.sum(cosine * charge[None], axis=-1),
            jnp.sum(sine_part * charge[None], axis=-1),
        ],
        axis=0,
    )


def evaluate(atom_data, local_exp, waves):
    cosine, sine_part = waves_at(atom_data, waves)
    half_count = waves.shape[1]
    cos_local = local_exp[1 : 1 + half_count][..., None]
    sin_local = local_exp[1 + half_count :][..., None]
    potential = local_exp[0][..., None] + jnp.sum(
        cos_local * cosine + sin_local * sine_part, axis=0
    )
    mixed_term = cos_local * sine_part - sin_local * cosine
    shape_lead = (half_count,) + (1,) * (mixed_term.ndim - 1)
    field_parts = [
        jnp.sum(waves[component].reshape(shape_lead) * mixed_term, axis=0) for component in range(3)
    ]
    return (potential, field_parts)


def near_row(target, source, flag_grid, shift_vec, keep_self):
    weight = source[3] * flag_grid[..., None]
    delta_x = target[0][..., :, None] - (source[0][..., None, :] + shift_vec[0])
    delta_y = target[1][..., :, None] - (source[1][..., None, :] + shift_vec[1])
    delta_z = target[2][..., :, None] - (source[2][..., None, :] + shift_vec[2])
    inverse = lax.rsqrt(delta_x * delta_x + delta_y * delta_y + delta_z * delta_z + soften)
    pair_term = weight[..., None, :] * keep_self * inverse
    cube_term = pair_term * inverse * inverse
    return jnp.stack(
        [
            jnp.sum(pair_term, axis=-1),
            jnp.sum(cube_term * delta_x, axis=-1),
            jnp.sum(cube_term * delta_y, axis=-1),
            jnp.sum(cube_term * delta_z, axis=-1),
        ]
    )


def full_flags(near_flags, float_type):
    flags_float = near_flags.astype(float_type)
    centre = jnp.ones((1,) + flags_float.shape[1:], float_type)
    return jnp.concatenate([flags_float[:13], centre, flags_float[13:]], axis=0)


def leaf_offsets():
    return [
        (shift_x, shift_y, shift_z)
        for shift_x in (-1, 0, 1)
        for shift_y in (-1, 0, 1)
        for shift_z in (-1, 0, 1)
        if (shift_x, shift_y, shift_z) != (0, 0, 0)
    ]


def parent_offsets():
    return [
        (shift_x, shift_y, shift_z)
        for shift_x in range(-2, 3)
        for shift_y in range(-2, 3)
        for shift_z in range(-2, 3)
        if max(abs(shift_x), abs(shift_y), abs(shift_z)) == 2
    ]


def climb_children(moments, matrices):
    coef_count, size_x, size_y, size_z = moments.shape
    parted = moments.reshape(coef_count, size_x // 2, 2, size_y // 2, 2, size_z // 2, 2)
    return jnp.einsum(
        "abckj,jxaybzc->kxyz",
        matrices.reshape(2, 2, 2, coef_count, coef_count),
        parted,
        precision=highest,
    )


def descend_children(parent_local, matrices):
    coef_count, size_x, size_y, size_z = parent_local.shape
    spread = jnp.einsum(
        "abckj,jxyz->kxaybzc",
        matrices.reshape(2, 2, 2, coef_count, coef_count),
        parent_local,
        precision=highest,
    )
    return spread.reshape(coef_count, 2 * size_x, 2 * size_y, 2 * size_z)


def matrix_vector(matrix, vector):
    return jnp.dot(matrix, vector, precision=highest)


def pick_side(matrices, own_side):
    return lax.dynamic_index_in_dim(matrices, own_side, 0, keepdims=False)


def pair_step(matrices, own_side, current, partner):
    return matrix_vector(pick_side(matrices, own_side), current) + matrix_vector(
        pick_side(matrices, 1 - own_side), partner
    )


def chain_tree(column, tree_up, tree_down, tree_side, lattice):
    climbs = tree_up.astype(jnp.float32)
    lowers = tree_down.astype(jnp.float32)
    sideways = tree_side.astype(jnp.float32)
    current = column
    visited = []
    for level_bit in range(lax.axis_size("gx").bit_length() - 1):
        partner = from_partner(current, "gx", level_bit)
        own_side = lax.axis_index("gx") // 2**level_bit % 2
        current = pair_step(climbs[0], own_side, current, partner)
        visited.append((0, own_side, partner))
    for level_bit in range(lax.axis_size("gy").bit_length() - 1):
        partner = from_partner(current, "gy", level_bit)
        own_side = lax.axis_index("gy") // 2**level_bit % 2
        current = pair_step(climbs[1], own_side, current, partner)
        visited.append((1, own_side, partner))
    local_exp = matrix_vector(lattice.astype(jnp.float32), current)
    for axis_num, own_side, partner in reversed(visited):
        local_exp = matrix_vector(pick_side(lowers[axis_num], own_side), local_exp) + matrix_vector(
            pick_side(sideways[axis_num], own_side), partner
        )
    return local_exp


def assemble(near_terms, potential, field_parts, charge, live_slots):
    rows = [coulomb * (near_terms[0] + potential) * live_slots]
    for component in range(3):
        rows.append(coulomb * charge * (near_terms[1 + component] + field_parts[component]))
    return jnp.stack(rows)


NEAR_ROWS = 32
NEAR_PIECES = 8


def near_pairs(tx, ty, tz, srow, mask):
    weight = srow[3:4, :]
    delta_x = tx - srow[0:1, :]
    delta_y = ty - srow[1:2, :]
    delta_z = tz - srow[2:3, :]
    inverse = lax.rsqrt(delta_x * delta_x + delta_y * delta_y + delta_z * delta_z + soften)
    pair_term = weight * inverse
    if mask is not None:
        pair_term = jnp.where(mask, pair_term, 0.0)
    cube_term = pair_term * inverse * inverse
    return (pair_term, cube_term * delta_x, cube_term * delta_y, cube_term * delta_z)


def near_kernel(first_leaf, count_ref, listed_ref, place_ref, kind_ref, target_ref, source_ref, shift_ref, out_ref):
    piece_leaves = out_ref.shape[0]
    listed_width = place_ref.shape[0] // count_ref.shape[0]
    rows = NEAR_ROWS
    lanes = out_ref.shape[2]
    out_ref[...] = jnp.zeros(out_ref.shape, out_ref.dtype)
    lane = lax.broadcasted_iota(jnp.int32, (rows, lanes), 1)
    row = lax.broadcasted_iota(jnp.int32, (rows, lanes), 0)

    def leaf_body(local, carry):
        leaf = first_leaf + local
        chunk_count = (count_ref[leaf] + rows - 1) // rows
        listed = listed_ref[leaf]
        base = leaf * listed_width

        def chunk_body(chunk, carry2):
            first = pl.multiple_of(chunk * rows, rows)
            column = target_ref[local, pl.ds(first, rows), :]
            tx = jnp.broadcast_to(column[:, 0:1], (rows, lanes))
            ty = jnp.broadcast_to(column[:, 1:2], (rows, lanes))
            tz = jnp.broadcast_to(column[:, 2:3], (rows, lanes))
            acc = near_pairs(tx, ty, tz, source_ref[place_ref[base]], row + first != lane)

            def offset_body(number, acc):
                srow = source_ref[place_ref[base + number]] + shift_ref[kind_ref[base + number]]
                terms = near_pairs(tx, ty, tz, srow, None)
                return tuple(a + b for a, b in zip(acc, terms))

            acc = lax.fori_loop(1, listed, offset_body, acc)
            sums = [jnp.sum(part, axis=1, keepdims=True) for part in acc]
            tile = jnp.where(
                lane == 0, sums[0], jnp.where(lane == 1, sums[1], jnp.where(lane == 2, sums[2], sums[3]))
            )
            out_ref[local, pl.ds(first, rows), :] = jnp.where(lane < 4, tile, 0.0)
            return carry2

        lax.fori_loop(0, chunk_count, chunk_body, 0)
        return carry

    lax.fori_loop(0, piece_leaves, leaf_body, 0)


def near_local(charged, rimmed, counts, near_flags):
    size_x, size_y, size_z, slot_count = charged.shape[1:]
    leaf_count = size_x * size_y * size_z
    ext_y = size_y + 2
    target = jnp.transpose(charged, (1, 2, 3, 4, 0)).reshape(leaf_count, slot_count, 4)
    source = jnp.transpose(rimmed, (1, 2, 3, 0, 4)).reshape(-1, 4, slot_count)
    source = jnp.pad(source, ((0, 0), (0, 4), (0, 0)))
    offsets = [(0, 0, 0)] + leaf_offsets()
    shift_rows = jnp.array([[float(v) for v in offset] + [0.0] * 5 for offset in offsets], jnp.float32)
    shift_table = jnp.broadcast_to(shift_rows[:, :, None], (len(offsets), 8, slot_count))
    leaf_x = jnp.arange(size_x, dtype=jnp.int32)[:, None, None]
    leaf_y = jnp.arange(size_y, dtype=jnp.int32)[None, :, None]
    leaf_z = jnp.arange(size_z, dtype=jnp.int32)[None, None, :]
    places = []
    for offset in offsets:
        place = ((leaf_x + 1 + offset[0]) * ext_y + leaf_y + 1 + offset[1]) * size_z + leaf_z + offset[2]
        places.append(jnp.broadcast_to(place, (size_x, size_y, size_z)))
    places = jnp.stack(places).reshape(len(offsets), leaf_count)
    layer = jnp.arange(size_z, dtype=jnp.int32)
    valid = jnp.stack([((layer + offset[2] >= 0) & (layer + offset[2] < size_z)) for offset in offsets[1:]])
    active = (near_flags != 0) & valid[:, None, None, :]
    active = jnp.concatenate([jnp.ones((1, leaf_count), bool), active.reshape(len(offsets) - 1, leaf_count)])
    order = jnp.argsort(jnp.logical_not(active).astype(jnp.int32), axis=0, stable=True)
    listed = jnp.sum(active.astype(jnp.int32), axis=0)
    place_list = jnp.take_along_axis(places, order, axis=0)
    place_list = jnp.where(jnp.take_along_axis(active, order, axis=0), place_list, 0)
    place_list = jnp.transpose(place_list).reshape(-1)
    kind_list = jnp.transpose(order).reshape(-1).astype(jnp.int32)
    count_list = counts.reshape(-1)
    piece = leaf_count // NEAR_PIECES if leaf_count % NEAR_PIECES == 0 else leaf_count
    outs = []
    for first_leaf in range(0, leaf_count, piece):
        pairs = piece * slot_count * slot_count * 10
        outs.append(
            pl.pallas_call(
                functools.partial(near_kernel, first_leaf),
                out_shape=jax.ShapeDtypeStruct((piece, slot_count, 128), jnp.float32),
                in_specs=[pl.BlockSpec(memory_space=pltpu.SMEM)] * 4 + [pl.BlockSpec(memory_space=pltpu.VMEM)] * 3,
                out_specs=pl.BlockSpec(memory_space=pltpu.VMEM),
                cost_estimate=pl.CostEstimate(
                    flops=20 * pairs, transcendentals=pairs, bytes_accessed=8 * piece * slot_count * 128
                ),
            )(count_list, listed, place_list, kind_list, target[first_leaf : first_leaf + piece], source, shift_table)
        )
    out = jnp.concatenate([part[:, :, :4] for part in outs], axis=0)
    near = jnp.transpose(out, (2, 0, 1))
    return near.reshape(4, size_x, size_y, size_z, slot_count)


def body(
    atom_data,
    counts,
    near_flags,
    child_up,
    child_down,
    leaf_far,
    parent_far,
    column_up,
    column_down,
    tree_up,
    tree_down,
    tree_side,
    lattice,
):
    coef_count = lattice.shape[0]
    slot_count = atom_data.shape[4]
    size_x, size_y, size_z = (atom_data.shape[1], atom_data.shape[2], atom_data.shape[3])
    live_slots = (
        jnp.arange(slot_count, dtype=jnp.int32)[None, None, None, :] < counts[..., None]
    ).astype(jnp.float32)
    charged = jnp.concatenate([atom_data[:3], (atom_data[3] * live_slots)[None]], axis=0)
    waves = wave_table(coef_count, jnp.float32)
    half_count = waves.shape[1]
    rimmed = extended_2(charged, (("gx", 1), ("gy", 2)), 1)
    moments = leaf_moments(charged, waves)
    parents = climb_children(moments, child_up.astype(jnp.float32))
    parent_rim = extended_2(parents, (("gx", 1), ("gy", 2)), 2)
    parent_rim = jnp.pad(parent_rim, ((0, 0), (0, 0), (0, 0), (2, 2)))
    half_x, half_y, half_z = (parents.shape[1], parents.shape[2], parents.shape[3])
    phase_grid = block_phase(waves, half_x, half_y, half_z, jnp.float32)
    turned = jnp.sum(rotate_by(parents, phase_grid), axis=(1, 2, 3))
    column = matrix_vector(column_up.astype(jnp.float32), turned)
    column_local = chain_tree(column, tree_up, tree_down, tree_side, lattice)
    leaf_rim = leaf_moments(rimmed, waves)
    leaf_rim = jnp.pad(leaf_rim, ((0, 0), (0, 0), (0, 0), (1, 1)))
    near_terms = near_local(charged, rimmed, counts, near_flags)
    lowered = matrix_vector(column_down.astype(jnp.float32), column_local)
    parent_local = rotate_by(
        jnp.broadcast_to(lowered[:, None, None, None], parents.shape), -phase_grid
    )
    far_parents = parent_offsets()
    parent_stack = jnp.stack(
        [
            parent_rim[
                :,
                2 + offset[0] : 2 + offset[0] + half_x,
                2 + offset[1] : 2 + offset[1] + half_y,
                2 + offset[2] : 2 + offset[2] + half_z,
            ]
            for offset in far_parents
        ]
    )
    parent_turns = offset_phases(waves, far_parents).reshape(len(far_parents), half_count, 1, 1, 1)
    parent_sum = jnp.sum(jax.vmap(rotate_by)(parent_stack, parent_turns), axis=0)
    parent_local = parent_local + jnp.einsum(
        "kj,jxyz->kxyz", parent_far.astype(jnp.float32), parent_sum, precision=highest
    )
    leaf_local = descend_children(parent_local, child_down.astype(jnp.float32))
    near_leaves = leaf_offsets()
    leaf_stack = jnp.stack(
        [
            leaf_rim[
                :,
                1 + offset[0] : 1 + offset[0] + size_x,
                1 + offset[1] : 1 + offset[1] + size_y,
                1 + offset[2] : 1 + offset[2] + size_z,
            ]
            for offset in near_leaves
        ]
    )
    leaf_stack = leaf_stack * (1.0 - near_flags.astype(jnp.float32))[:, None]
    leaf_turns = offset_phases(waves, near_leaves).reshape(len(near_leaves), half_count, 1, 1, 1)
    leaf_sum = jnp.sum(jax.vmap(rotate_by)(leaf_stack, leaf_turns), axis=0)
    leaf_local = leaf_local + jnp.einsum(
        "kj,jxyz->kxyz", leaf_far.astype(jnp.float32), leaf_sum, precision=highest
    )
    potential, field_parts = evaluate(charged, leaf_local, waves)
    return assemble(near_terms, potential, field_parts, charged[3], live_slots)


def solution(mesh):
    in_specs = (
        P(None, "gx", "gy", None, None),
        P("gx", "gy", None),
        P(None, "gx", "gy", None),
        P(),
        P(),
        P(),
        P(),
        P(),
        P(),
        P(),
        P(),
        P(),
        P(),
    )
    out_specs = P(None, "gx", "gy", None, None)
    return jax.shard_map(body, mesh=mesh, in_specs=in_specs, out_specs=out_specs, check_vma=False)
```

```python
import functools

import jax
import jax.numpy as jnp
from jax import lax
from jax.experimental import pallas as pl
from jax.experimental.pallas import tpu as pltpu
from jax.sharding import PartitionSpec as P

soften = 0.04
coulomb = 0.1
highest = lax.Precision.HIGHEST


def from_partner(value, axis, bit):
    mask = 2**bit
    pairs = [(source, source ^ mask) for source in range(lax.axis_size(axis))]
    return lax.ppermute(value, axis, pairs)


def extended_2(block, sides, width):
    return extended_joint([(block, width)], sides)[0]


def extended_joint(parts, sides):
    blocks = [block for block, width in parts]
    for axis, dim in sides:
        count = lax.axis_size(axis)
        forward = [(i, i + 1) for i in range(count - 1)]
        forward.append((count - 1, 0))
        backward = [(target, source) for source, target in forward]
        lows = [lax.slice_in_dim(b, b.shape[dim] - w, None, axis=dim) for b, (_, w) in zip(blocks, parts)]
        highs = [lax.slice_in_dim(b, 0, w, axis=dim) for b, (_, w) in zip(blocks, parts)]
        sizes = [piece.size for piece in lows]
        low_all = lax.ppermute(jnp.concatenate([piece.reshape(-1) for piece in lows]), axis, forward)
        high_all = lax.ppermute(jnp.concatenate([piece.reshape(-1) for piece in highs]), axis, backward)
        grown = []
        place = 0
        for b, piece, size in zip(blocks, lows, sizes):
            low = low_all[place : place + size].reshape(piece.shape)
            high = high_all[place : place + size].reshape(piece.shape)
            place += size
            grown.append(jnp.concatenate([low, b, high], axis=dim))
        blocks = grown
    return blocks


def wave_table(coef_count, float_type):
    half_count = (coef_count - 1) // 2
    order_index = jnp.arange(1, half_count + 1, dtype=jnp.int32).astype(float_type)
    height = 1.0 - 2.0 * (order_index - 0.5) / half_count
    radius = jnp.sqrt(jnp.maximum(1.0 - height * height, 0.0))
    angle_turn = 2.399963 * order_index
    magnitude = 1.5 + jnp.mod(order_index, 3.0)
    return (
        jnp.stack([radius * jnp.cos(angle_turn), radius * jnp.sin(angle_turn), height])
        * magnitude[None]
    )


def waves_at(atom_data, waves):
    shape_lead = (waves.shape[1],) + (1,) * (atom_data.ndim - 1)
    phases = waves[0].reshape(shape_lead) * (atom_data[0] - 0.5)[None]
    phases = phases + waves[1].reshape(shape_lead) * (atom_data[1] - 0.5)[None]
    phases = phases + waves[2].reshape(shape_lead) * (atom_data[2] - 0.5)[None]
    return (jnp.cos(phases), jnp.sin(phases))


def rotate_by(field, phase):
    half_count = phase.shape[0]
    cosine = jnp.cos(phase)
    sine_part = jnp.sin(phase)
    cos_coef = field[1 : 1 + half_count]
    sin_coef = field[1 + half_count :]
    return jnp.concatenate(
        [
            field[0:1],
            cos_coef * cosine - sin_coef * sine_part,
            cos_coef * sine_part + sin_coef * cosine,
        ],
        axis=0,
    )


def offset_phases(waves, offsets):
    table = jnp.array(offsets, dtype=jnp.float32)
    return (
        table[:, 0:1] * waves[0][None]
        + table[:, 1:2] * waves[1][None]
        + table[:, 2:3] * waves[2][None]
    )


def block_phase(waves, size_x, size_y, size_z, float_type):
    place_x = jnp.arange(size_x, dtype=jnp.int32).astype(float_type)
    place_y = jnp.arange(size_y, dtype=jnp.int32).astype(float_type)
    place_z = jnp.arange(size_z, dtype=jnp.int32).astype(float_type)
    phase = waves[0][:, None, None, None] * place_x[None, :, None, None]
    phase = phase + waves[1][:, None, None, None] * place_y[None, None, :, None]
    return phase + waves[2][:, None, None, None] * place_z[None, None, None, :]


def leaf_moments(atom_data, waves):
    cosine, sine_part = waves_at(atom_data, waves)
    charge = atom_data[3]
    summed = jnp.sum(charge, axis=-1)[None]
    return jnp.concatenate(
        [
            summed,
            jnp.sum(cosine * charge[None], axis=-1),
            jnp.sum(sine_part * charge[None], axis=-1),
        ],
        axis=0,
    )


def evaluate(atom_data, local_exp, waves):
    cosine, sine_part = waves_at(atom_data, waves)
    half_count = waves.shape[1]
    cos_local = local_exp[1 : 1 + half_count][..., None]
    sin_local = local_exp[1 + half_count :][..., None]
    potential = local_exp[0][..., None] + jnp.sum(
        cos_local * cosine + sin_local * sine_part, axis=0
    )
    mixed_term = cos_local * sine_part - sin_local * cosine
    shape_lead = (half_count,) + (1,) * (mixed_term.ndim - 1)
    field_parts = [
        jnp.sum(waves[component].reshape(shape_lead) * mixed_term, axis=0) for component in range(3)
    ]
    return (potential, field_parts)


def near_row(target, source, flag_grid, shift_vec, keep_self):
    weight = source[3] * flag_grid[..., None]
    delta_x = target[0][..., :, None] - (source[0][..., None, :] + shift_vec[0])
    delta_y = target[1][..., :, None] - (source[1][..., None, :] + shift_vec[1])
    delta_z = target[2][..., :, None] - (source[2][..., None, :] + shift_vec[2])
    inverse = lax.rsqrt(delta_x * delta_x + delta_y * delta_y + delta_z * delta_z + soften)
    pair_term = weight[..., None, :] * keep_self * inverse
    cube_term = pair_term * inverse * inverse
    return jnp.stack(
        [
            jnp.sum(pair_term, axis=-1),
            jnp.sum(cube_term * delta_x, axis=-1),
            jnp.sum(cube_term * delta_y, axis=-1),
            jnp.sum(cube_term * delta_z, axis=-1),
        ]
    )


def full_flags(near_flags, float_type):
    flags_float = near_flags.astype(float_type)
    centre = jnp.ones((1,) + flags_float.shape[1:], float_type)
    return jnp.concatenate([flags_float[:13], centre, flags_float[13:]], axis=0)


def leaf_offsets():
    return [
        (shift_x, shift_y, shift_z)
        for shift_x in (-1, 0, 1)
        for shift_y in (-1, 0, 1)
        for shift_z in (-1, 0, 1)
        if (shift_x, shift_y, shift_z) != (0, 0, 0)
    ]


def parent_offsets():
    return [
        (shift_x, shift_y, shift_z)
        for shift_x in range(-2, 3)
        for shift_y in range(-2, 3)
        for shift_z in range(-2, 3)
        if max(abs(shift_x), abs(shift_y), abs(shift_z)) == 2
    ]


def climb_children(moments, matrices):
    coef_count, size_x, size_y, size_z = moments.shape
    parted = moments.reshape(coef_count, size_x // 2, 2, size_y // 2, 2, size_z // 2, 2)
    return jnp.einsum(
        "abckj,jxaybzc->kxyz",
        matrices.reshape(2, 2, 2, coef_count, coef_count),
        parted,
        precision=highest,
    )


def descend_children(parent_local, matrices):
    coef_count, size_x, size_y, size_z = parent_local.shape
    spread = jnp.einsum(
        "abckj,jxyz->kxaybzc",
        matrices.reshape(2, 2, 2, coef_count, coef_count),
        parent_local,
        precision=highest,
    )
    return spread.reshape(coef_count, 2 * size_x, 2 * size_y, 2 * size_z)


def matrix_vector(matrix, vector):
    return jnp.dot(matrix, vector, precision=highest)


def pick_side(matrices, own_side):
    return lax.dynamic_index_in_dim(matrices, own_side, 0, keepdims=False)


def pair_step(matrices, own_side, current, partner):
    return matrix_vector(pick_side(matrices, own_side), current) + matrix_vector(
        pick_side(matrices, 1 - own_side), partner
    )


def chain_tree(column, tree_up, tree_down, tree_side, lattice):
    climbs = tree_up.astype(jnp.float32)
    lowers = tree_down.astype(jnp.float32)
    sideways = tree_side.astype(jnp.float32)
    current = column
    visited = []
    for level_bit in range(lax.axis_size("gx").bit_length() - 1):
        partner = from_partner(current, "gx", level_bit)
        own_side = lax.axis_index("gx") // 2**level_bit % 2
        current = pair_step(climbs[0], own_side, current, partner)
        visited.append((0, own_side, partner))
    for level_bit in range(lax.axis_size("gy").bit_length() - 1):
        partner = from_partner(current, "gy", level_bit)
        own_side = lax.axis_index("gy") // 2**level_bit % 2
        current = pair_step(climbs[1], own_side, current, partner)
        visited.append((1, own_side, partner))
    local_exp = matrix_vector(lattice.astype(jnp.float32), current)
    for axis_num, own_side, partner in reversed(visited):
        local_exp = matrix_vector(pick_side(lowers[axis_num], own_side), local_exp) + matrix_vector(
            pick_side(sideways[axis_num], own_side), partner
        )
    return local_exp


def flip_pair(column_grid, axis_num, level_bit):
    coef_count, size_x, size_y = column_grid.shape
    span_size = 2**level_bit
    if axis_num == 0:
        parted = column_grid.reshape(coef_count, size_x // (2 * span_size), 2, span_size, size_y)
        return parted[:, :, ::-1].reshape(column_grid.shape)
    parted = column_grid.reshape(coef_count, size_x, size_y // (2 * span_size), 2, span_size)
    return parted[:, :, :, ::-1].reshape(column_grid.shape)


def side_grid(axis_num, level_bit, size_x, size_y):
    positions = jnp.arange(size_x if axis_num == 0 else size_y, dtype=jnp.int32)
    own_side = positions // 2**level_bit % 2
    return own_side[:, None] if axis_num == 0 else own_side[None, :]


def choose_side(matrices, own_side, column_grid):
    first = jnp.einsum("kj,jxy->kxy", matrices[0], column_grid, precision=highest)
    second = jnp.einsum("kj,jxy->kxy", matrices[1], column_grid, precision=highest)
    return jnp.where(own_side[None] == 0, first, second)


def gathered_tree(column, tree_up, tree_down, tree_side, lattice):
    size_x, size_y = lax.axis_size("gx"), lax.axis_size("gy")
    gathered = lax.all_gather(column, ("gx", "gy")).reshape(size_x, size_y, -1)
    current = jnp.transpose(gathered, (2, 0, 1))
    levels = [(0, bit) for bit in range(size_x.bit_length() - 1)] + [
        (1, bit) for bit in range(size_y.bit_length() - 1)
    ]
    visited = []
    for axis_num, level_bit in levels:
        partner = flip_pair(current, axis_num, level_bit)
        own_side = side_grid(axis_num, level_bit, size_x, size_y)
        climbs = tree_up[axis_num].astype(jnp.float32)
        current = choose_side(climbs, own_side, current) + choose_side(climbs, 1 - own_side, partner)
        visited.append((axis_num, own_side, partner))
    local_exp = jnp.einsum("kj,jxy->kxy", lattice.astype(jnp.float32), current, precision=highest)
    for axis_num, own_side, partner in reversed(visited):
        local_exp = choose_side(tree_down[axis_num].astype(jnp.float32), own_side, local_exp) + choose_side(
            tree_side[axis_num].astype(jnp.float32), own_side, partner
        )
    own = lax.dynamic_slice(local_exp, (0, lax.axis_index("gx"), lax.axis_index("gy")), (local_exp.shape[0], 1, 1))
    return own.reshape(-1)


def assemble(near_terms, potential, field_parts, charge, live_slots):
    rows = [coulomb * (near_terms[0] + potential) * live_slots]
    for component in range(3):
        rows.append(coulomb * charge * (near_terms[1 + component] + field_parts[component]))
    return jnp.stack(rows)


NEAR_ROWS = 32
NEAR_PIECES = 8


def near_pairs(tx, ty, tz, srow, mask):
    weight = srow[3:4, :]
    delta_x = tx - srow[0:1, :]
    delta_y = ty - srow[1:2, :]
    delta_z = tz - srow[2:3, :]
    inverse = lax.rsqrt(delta_x * delta_x + delta_y * delta_y + delta_z * delta_z + soften)
    pair_term = weight * inverse
    if mask is not None:
        pair_term = jnp.where(mask, pair_term, 0.0)
    cube_term = pair_term * inverse * inverse
    return (pair_term, cube_term * delta_x, cube_term * delta_y, cube_term * delta_z)


def near_kernel(first_leaf, count_ref, listed_ref, place_ref, kind_ref, target_ref, source_ref, shift_ref, out_ref):
    piece_leaves = out_ref.shape[0]
    listed_width = place_ref.shape[0] // count_ref.shape[0]
    rows = NEAR_ROWS
    lanes = out_ref.shape[2]
    out_ref[...] = jnp.zeros(out_ref.shape, out_ref.dtype)
    lane = lax.broadcasted_iota(jnp.int32, (rows, lanes), 1)
    row = lax.broadcasted_iota(jnp.int32, (rows, lanes), 0)

    def leaf_body(local, carry):
        leaf = first_leaf + local
        chunk_count = (count_ref[leaf] + rows - 1) // rows
        listed = listed_ref[leaf]
        base = leaf * listed_width

        def chunk_body(chunk, carry2):
            first = pl.multiple_of(chunk * rows, rows)
            column = target_ref[local, pl.ds(first, rows), :]
            tx = jnp.broadcast_to(column[:, 0:1], (rows, lanes))
            ty = jnp.broadcast_to(column[:, 1:2], (rows, lanes))
            tz = jnp.broadcast_to(column[:, 2:3], (rows, lanes))
            acc = near_pairs(tx, ty, tz, source_ref[place_ref[base]], row + first != lane)

            def offset_body(number, acc):
                srow = source_ref[place_ref[base + number]] + shift_ref[kind_ref[base + number]]
                terms = near_pairs(tx, ty, tz, srow, None)
                return tuple(a + b for a, b in zip(acc, terms))

            acc = lax.fori_loop(1, listed, offset_body, acc)
            sums = [jnp.sum(part, axis=1, keepdims=True) for part in acc]
            tile = jnp.where(
                lane == 0, sums[0], jnp.where(lane == 1, sums[1], jnp.where(lane == 2, sums[2], sums[3]))
            )
            out_ref[local, pl.ds(first, rows), :] = jnp.where(lane < 4, tile, 0.0)
            return carry2

        lax.fori_loop(0, chunk_count, chunk_body, 0)
        return carry

    lax.fori_loop(0, piece_leaves, leaf_body, 0)


def near_local(charged, rimmed, counts, near_flags):
    size_x, size_y, size_z, slot_count = charged.shape[1:]
    leaf_count = size_x * size_y * size_z
    ext_y = size_y + 2
    target = jnp.transpose(charged, (1, 2, 3, 4, 0)).reshape(leaf_count, slot_count, 4)
    source = jnp.transpose(rimmed, (1, 2, 3, 0, 4)).reshape(-1, 4, slot_count)
    source = jnp.pad(source, ((0, 0), (0, 4), (0, 0)))
    offsets = [(0, 0, 0)] + leaf_offsets()
    shift_rows = jnp.array([[float(v) for v in offset] + [0.0] * 5 for offset in offsets], jnp.float32)
    shift_table = jnp.broadcast_to(shift_rows[:, :, None], (len(offsets), 8, slot_count))
    leaf_x = jnp.arange(size_x, dtype=jnp.int32)[:, None, None]
    leaf_y = jnp.arange(size_y, dtype=jnp.int32)[None, :, None]
    leaf_z = jnp.arange(size_z, dtype=jnp.int32)[None, None, :]
    places = []
    for offset in offsets:
        place = ((leaf_x + 1 + offset[0]) * ext_y + leaf_y + 1 + offset[1]) * size_z + leaf_z + offset[2]
        places.append(jnp.broadcast_to(place, (size_x, size_y, size_z)))
    places = jnp.stack(places).reshape(len(offsets), leaf_count)
    layer = jnp.arange(size_z, dtype=jnp.int32)
    valid = jnp.stack([((layer + offset[2] >= 0) & (layer + offset[2] < size_z)) for offset in offsets[1:]])
    active = (near_flags != 0) & valid[:, None, None, :]
    active = jnp.concatenate([jnp.ones((1, leaf_count), bool), active.reshape(len(offsets) - 1, leaf_count)])
    order = jnp.argsort(jnp.logical_not(active).astype(jnp.int32), axis=0, stable=True)
    listed = jnp.sum(active.astype(jnp.int32), axis=0)
    place_list = jnp.take_along_axis(places, order, axis=0)
    place_list = jnp.where(jnp.take_along_axis(active, order, axis=0), place_list, 0)
    place_list = jnp.transpose(place_list).reshape(-1)
    kind_list = jnp.transpose(order).reshape(-1).astype(jnp.int32)
    count_list = counts.reshape(-1)
    piece = leaf_count // NEAR_PIECES if leaf_count % NEAR_PIECES == 0 else leaf_count
    outs = []
    for first_leaf in range(0, leaf_count, piece):
        pairs = piece * slot_count * slot_count * 10
        outs.append(
            pl.pallas_call(
                functools.partial(near_kernel, first_leaf),
                out_shape=jax.ShapeDtypeStruct((piece, slot_count, 128), jnp.float32),
                in_specs=[pl.BlockSpec(memory_space=pltpu.SMEM)] * 4 + [pl.BlockSpec(memory_space=pltpu.VMEM)] * 3,
                out_specs=pl.BlockSpec(memory_space=pltpu.VMEM),
                cost_estimate=pl.CostEstimate(
                    flops=20 * pairs, transcendentals=pairs, bytes_accessed=8 * piece * slot_count * 128
                ),
            )(count_list, listed, place_list, kind_list, target[first_leaf : first_leaf + piece], source, shift_table)
        )
    out = jnp.concatenate([part[:, :, :4] for part in outs], axis=0)
    near = jnp.transpose(out, (2, 0, 1))
    return near.reshape(4, size_x, size_y, size_z, slot_count)


def body(
    atom_data,
    counts,
    near_flags,
    child_up,
    child_down,
    leaf_far,
    parent_far,
    column_up,
    column_down,
    tree_up,
    tree_down,
    tree_side,
    lattice,
):
    coef_count = lattice.shape[0]
    slot_count = atom_data.shape[4]
    size_x, size_y, size_z = (atom_data.shape[1], atom_data.shape[2], atom_data.shape[3])
    live_slots = (
        jnp.arange(slot_count, dtype=jnp.int32)[None, None, None, :] < counts[..., None]
    ).astype(jnp.float32)
    charged = jnp.concatenate([atom_data[:3], (atom_data[3] * live_slots)[None]], axis=0)
    waves = wave_table(coef_count, jnp.float32)
    half_count = waves.shape[1]
    moments = leaf_moments(charged, waves)
    parents = climb_children(moments, child_up.astype(jnp.float32))
    rimmed, parent_rim = extended_joint([(charged, 1), (parents, 2)], (("gx", 1), ("gy", 2)))
    parent_rim = jnp.pad(parent_rim, ((0, 0), (0, 0), (0, 0), (2, 2)))
    half_x, half_y, half_z = (parents.shape[1], parents.shape[2], parents.shape[3])
    phase_grid = block_phase(waves, half_x, half_y, half_z, jnp.float32)
    turned = jnp.sum(rotate_by(parents, phase_grid), axis=(1, 2, 3))
    column = matrix_vector(column_up.astype(jnp.float32), turned)
    column_local = gathered_tree(column, tree_up, tree_down, tree_side, lattice)
    leaf_rim = leaf_moments(rimmed, waves)
    leaf_rim = jnp.pad(leaf_rim, ((0, 0), (0, 0), (0, 0), (1, 1)))
    near_terms = near_local(charged, rimmed, counts, near_flags)
    lowered = matrix_vector(column_down.astype(jnp.float32), column_local)
    parent_local = rotate_by(
        jnp.broadcast_to(lowered[:, None, None, None], parents.shape), -phase_grid
    )
    far_parents = parent_offsets()
    parent_stack = jnp.stack(
        [
            parent_rim[
                :,
                2 + offset[0] : 2 + offset[0] + half_x,
                2 + offset[1] : 2 + offset[1] + half_y,
                2 + offset[2] : 2 + offset[2] + half_z,
            ]
            for offset in far_parents
        ]
    )
    parent_turns = offset_phases(waves, far_parents).reshape(len(far_parents), half_count, 1, 1, 1)
    parent_sum = jnp.sum(jax.vmap(rotate_by)(parent_stack, parent_turns), axis=0)
    parent_local = parent_local + jnp.einsum(
        "kj,jxyz->kxyz", parent_far.astype(jnp.float32), parent_sum, precision=highest
    )
    leaf_local = descend_children(parent_local, child_down.astype(jnp.float32))
    near_leaves = leaf_offsets()
    leaf_stack = jnp.stack(
        [
            leaf_rim[
                :,
                1 + offset[0] : 1 + offset[0] + size_x,
                1 + offset[1] : 1 + offset[1] + size_y,
                1 + offset[2] : 1 + offset[2] + size_z,
            ]
            for offset in near_leaves
        ]
    )
    leaf_stack = leaf_stack * (1.0 - near_flags.astype(jnp.float32))[:, None]
    leaf_turns = offset_phases(waves, near_leaves).reshape(len(near_leaves), half_count, 1, 1, 1)
    leaf_sum = jnp.sum(jax.vmap(rotate_by)(leaf_stack, leaf_turns), axis=0)
    leaf_local = leaf_local + jnp.einsum(
        "kj,jxyz->kxyz", leaf_far.astype(jnp.float32), leaf_sum, precision=highest
    )
    potential, field_parts = evaluate(charged, leaf_local, waves)
    return assemble(near_terms, potential, field_parts, charged[3], live_slots)


def solution(mesh):
    in_specs = (
        P(None, "gx", "gy", None, None),
        P("gx", "gy", None),
        P(None, "gx", "gy", None),
        P(),
        P(),
        P(),
        P(),
        P(),
        P(),
        P(),
        P(),
        P(),
        P(),
    )
    out_specs = P(None, "gx", "gy", None, None)
    return jax.shard_map(body, mesh=mesh, in_specs=in_specs, out_specs=out_specs, check_vma=False)
```

```python
import functools

import jax
import jax.numpy as jnp
from jax import lax
from jax.experimental import pallas as pl
from jax.experimental.pallas import tpu as pltpu
from jax.sharding import PartitionSpec as P

soften = 0.04
coulomb = 0.1
highest = lax.Precision.HIGHEST


def from_partner(value, axis, bit):
    mask = 2**bit
    pairs = [(source, source ^ mask) for source in range(lax.axis_size(axis))]
    return lax.ppermute(value, axis, pairs)


def extended_2(block, sides, width):
    return extended_joint([(block, width)], sides)[0]


def extended_joint(parts, sides):
    blocks = [block for block, width in parts]
    for axis, dim in sides:
        count = lax.axis_size(axis)
        forward = [(i, i + 1) for i in range(count - 1)]
        forward.append((count - 1, 0))
        backward = [(target, source) for source, target in forward]
        lows = [lax.slice_in_dim(b, b.shape[dim] - w, None, axis=dim) for b, (_, w) in zip(blocks, parts)]
        highs = [lax.slice_in_dim(b, 0, w, axis=dim) for b, (_, w) in zip(blocks, parts)]
        sizes = [piece.size for piece in lows]
        low_all = lax.ppermute(jnp.concatenate([piece.reshape(-1) for piece in lows]), axis, forward)
        high_all = lax.ppermute(jnp.concatenate([piece.reshape(-1) for piece in highs]), axis, backward)
        grown = []
        place = 0
        for b, piece, size in zip(blocks, lows, sizes):
            low = low_all[place : place + size].reshape(piece.shape)
            high = high_all[place : place + size].reshape(piece.shape)
            place += size
            grown.append(jnp.concatenate([low, b, high], axis=dim))
        blocks = grown
    return blocks


def wave_table(coef_count, float_type):
    half_count = (coef_count - 1) // 2
    order_index = jnp.arange(1, half_count + 1, dtype=jnp.int32).astype(float_type)
    height = 1.0 - 2.0 * (order_index - 0.5) / half_count
    radius = jnp.sqrt(jnp.maximum(1.0 - height * height, 0.0))
    angle_turn = 2.399963 * order_index
    magnitude = 1.5 + jnp.mod(order_index, 3.0)
    return (
        jnp.stack([radius * jnp.cos(angle_turn), radius * jnp.sin(angle_turn), height])
        * magnitude[None]
    )


def waves_at(atom_data, waves):
    shape_lead = (waves.shape[1],) + (1,) * (atom_data.ndim - 1)
    phases = waves[0].reshape(shape_lead) * (atom_data[0] - 0.5)[None]
    phases = phases + waves[1].reshape(shape_lead) * (atom_data[1] - 0.5)[None]
    phases = phases + waves[2].reshape(shape_lead) * (atom_data[2] - 0.5)[None]
    return (jnp.cos(phases), jnp.sin(phases))


def rotate_by(field, phase):
    half_count = phase.shape[0]
    cosine = jnp.cos(phase)
    sine_part = jnp.sin(phase)
    cos_coef = field[1 : 1 + half_count]
    sin_coef = field[1 + half_count :]
    return jnp.concatenate(
        [
            field[0:1],
            cos_coef * cosine - sin_coef * sine_part,
            cos_coef * sine_part + sin_coef * cosine,
        ],
        axis=0,
    )


def offset_phases(waves, offsets):
    table = jnp.array(offsets, dtype=jnp.float32)
    return (
        table[:, 0:1] * waves[0][None]
        + table[:, 1:2] * waves[1][None]
        + table[:, 2:3] * waves[2][None]
    )


def block_phase(waves, size_x, size_y, size_z, float_type):
    place_x = jnp.arange(size_x, dtype=jnp.int32).astype(float_type)
    place_y = jnp.arange(size_y, dtype=jnp.int32).astype(float_type)
    place_z = jnp.arange(size_z, dtype=jnp.int32).astype(float_type)
    phase = waves[0][:, None, None, None] * place_x[None, :, None, None]
    phase = phase + waves[1][:, None, None, None] * place_y[None, None, :, None]
    return phase + waves[2][:, None, None, None] * place_z[None, None, None, :]


def leaf_moments(atom_data, waves):
    cosine, sine_part = waves_at(atom_data, waves)
    charge = atom_data[3]
    summed = jnp.sum(charge, axis=-1)[None]
    return jnp.concatenate(
        [
            summed,
            jnp.sum(cosine * charge[None], axis=-1),
            jnp.sum(sine_part * charge[None], axis=-1),
        ],
        axis=0,
    )


def evaluate(atom_data, local_exp, waves):
    cosine, sine_part = waves_at(atom_data, waves)
    half_count = waves.shape[1]
    cos_local = local_exp[1 : 1 + half_count][..., None]
    sin_local = local_exp[1 + half_count :][..., None]
    potential = local_exp[0][..., None] + jnp.sum(
        cos_local * cosine + sin_local * sine_part, axis=0
    )
    mixed_term = cos_local * sine_part - sin_local * cosine
    shape_lead = (half_count,) + (1,) * (mixed_term.ndim - 1)
    field_parts = [
        jnp.sum(waves[component].reshape(shape_lead) * mixed_term, axis=0) for component in range(3)
    ]
    return (potential, field_parts)


def near_row(target, source, flag_grid, shift_vec, keep_self):
    weight = source[3] * flag_grid[..., None]
    delta_x = target[0][..., :, None] - (source[0][..., None, :] + shift_vec[0])
    delta_y = target[1][..., :, None] - (source[1][..., None, :] + shift_vec[1])
    delta_z = target[2][..., :, None] - (source[2][..., None, :] + shift_vec[2])
    inverse = lax.rsqrt(delta_x * delta_x + delta_y * delta_y + delta_z * delta_z + soften)
    pair_term = weight[..., None, :] * keep_self * inverse
    cube_term = pair_term * inverse * inverse
    return jnp.stack(
        [
            jnp.sum(pair_term, axis=-1),
            jnp.sum(cube_term * delta_x, axis=-1),
            jnp.sum(cube_term * delta_y, axis=-1),
            jnp.sum(cube_term * delta_z, axis=-1),
        ]
    )


def full_flags(near_flags, float_type):
    flags_float = near_flags.astype(float_type)
    centre = jnp.ones((1,) + flags_float.shape[1:], float_type)
    return jnp.concatenate([flags_float[:13], centre, flags_float[13:]], axis=0)


def leaf_offsets():
    return [
        (shift_x, shift_y, shift_z)
        for shift_x in (-1, 0, 1)
        for shift_y in (-1, 0, 1)
        for shift_z in (-1, 0, 1)
        if (shift_x, shift_y, shift_z) != (0, 0, 0)
    ]


def parent_offsets():
    return [
        (shift_x, shift_y, shift_z)
        for shift_x in range(-2, 3)
        for shift_y in range(-2, 3)
        for shift_z in range(-2, 3)
        if max(abs(shift_x), abs(shift_y), abs(shift_z)) == 2
    ]


def climb_children(moments, matrices):
    coef_count, size_x, size_y, size_z = moments.shape
    parted = moments.reshape(coef_count, size_x // 2, 2, size_y // 2, 2, size_z // 2, 2)
    return jnp.einsum(
        "abckj,jxaybzc->kxyz",
        matrices.reshape(2, 2, 2, coef_count, coef_count),
        parted,
        precision=highest,
    )


def descend_children(parent_local, matrices):
    coef_count, size_x, size_y, size_z = parent_local.shape
    spread = jnp.einsum(
        "abckj,jxyz->kxaybzc",
        matrices.reshape(2, 2, 2, coef_count, coef_count),
        parent_local,
        precision=highest,
    )
    return spread.reshape(coef_count, 2 * size_x, 2 * size_y, 2 * size_z)


def matrix_vector(matrix, vector):
    return jnp.dot(matrix, vector, precision=highest)


def pick_side(matrices, own_side):
    return lax.dynamic_index_in_dim(matrices, own_side, 0, keepdims=False)


def pair_step(matrices, own_side, current, partner):
    return matrix_vector(pick_side(matrices, own_side), current) + matrix_vector(
        pick_side(matrices, 1 - own_side), partner
    )


def chain_tree(column, tree_up, tree_down, tree_side, lattice, hook):
    climbs = tree_up.astype(jnp.float32)
    lowers = tree_down.astype(jnp.float32)
    sideways = tree_side.astype(jnp.float32)
    current = column
    visited = []
    partner = None
    for level_bit in range(lax.axis_size("gx").bit_length() - 1):
        current = hook(current, partner)
        partner = from_partner(current, "gx", level_bit)
        own_side = lax.axis_index("gx") // 2**level_bit % 2
        current = pair_step(climbs[0], own_side, current, partner)
        visited.append((0, own_side, partner))
    for level_bit in range(lax.axis_size("gy").bit_length() - 1):
        current = hook(current, partner)
        partner = from_partner(current, "gy", level_bit)
        own_side = lax.axis_index("gy") // 2**level_bit % 2
        current = pair_step(climbs[1], own_side, current, partner)
        visited.append((1, own_side, partner))
    local_exp = matrix_vector(lattice.astype(jnp.float32), current)
    for axis_num, own_side, partner in reversed(visited):
        local_exp = matrix_vector(pick_side(lowers[axis_num], own_side), local_exp) + matrix_vector(
            pick_side(sideways[axis_num], own_side), partner
        )
    return local_exp


def flip_pair(column_grid, axis_num, level_bit):
    coef_count, size_x, size_y = column_grid.shape
    span_size = 2**level_bit
    if axis_num == 0:
        parted = column_grid.reshape(coef_count, size_x // (2 * span_size), 2, span_size, size_y)
        return parted[:, :, ::-1].reshape(column_grid.shape)
    parted = column_grid.reshape(coef_count, size_x, size_y // (2 * span_size), 2, span_size)
    return parted[:, :, :, ::-1].reshape(column_grid.shape)


def side_grid(axis_num, level_bit, size_x, size_y):
    positions = jnp.arange(size_x if axis_num == 0 else size_y, dtype=jnp.int32)
    own_side = positions // 2**level_bit % 2
    return own_side[:, None] if axis_num == 0 else own_side[None, :]


def choose_side(matrices, own_side, column_grid):
    first = jnp.einsum("kj,jxy->kxy", matrices[0], column_grid, precision=highest)
    second = jnp.einsum("kj,jxy->kxy", matrices[1], column_grid, precision=highest)
    return jnp.where(own_side[None] == 0, first, second)


def gathered_tree(column, tree_up, tree_down, tree_side, lattice):
    size_x, size_y = lax.axis_size("gx"), lax.axis_size("gy")
    gathered = lax.all_gather(column, ("gx", "gy")).reshape(size_x, size_y, -1)
    current = jnp.transpose(gathered, (2, 0, 1))
    levels = [(0, bit) for bit in range(size_x.bit_length() - 1)] + [
        (1, bit) for bit in range(size_y.bit_length() - 1)
    ]
    visited = []
    for axis_num, level_bit in levels:
        partner = flip_pair(current, axis_num, level_bit)
        own_side = side_grid(axis_num, level_bit, size_x, size_y)
        climbs = tree_up[axis_num].astype(jnp.float32)
        current = choose_side(climbs, own_side, current) + choose_side(climbs, 1 - own_side, partner)
        visited.append((axis_num, own_side, partner))
    local_exp = jnp.einsum("kj,jxy->kxy", lattice.astype(jnp.float32), current, precision=highest)
    for axis_num, own_side, partner in reversed(visited):
        local_exp = choose_side(tree_down[axis_num].astype(jnp.float32), own_side, local_exp) + choose_side(
            tree_side[axis_num].astype(jnp.float32), own_side, partner
        )
    own = lax.dynamic_slice(local_exp, (0, lax.axis_index("gx"), lax.axis_index("gy")), (local_exp.shape[0], 1, 1))
    return own.reshape(-1)


def assemble(near_terms, potential, field_parts, charge, live_slots):
    rows = [coulomb * (near_terms[0] + potential) * live_slots]
    for component in range(3):
        rows.append(coulomb * charge * (near_terms[1 + component] + field_parts[component]))
    return jnp.stack(rows)


NEAR_ROWS = 32
NEAR_PIECES = 8


def near_pairs(tx, ty, tz, srow, mask):
    weight = srow[3:4, :]
    delta_x = tx - srow[0:1, :]
    delta_y = ty - srow[1:2, :]
    delta_z = tz - srow[2:3, :]
    inverse = lax.rsqrt(delta_x * delta_x + delta_y * delta_y + delta_z * delta_z + soften)
    pair_term = weight * inverse
    if mask is not None:
        pair_term = jnp.where(mask, pair_term, 0.0)
    cube_term = pair_term * inverse * inverse
    return (pair_term, cube_term * delta_x, cube_term * delta_y, cube_term * delta_z)


def near_kernel(first_leaf, count_ref, listed_ref, place_ref, kind_ref, target_ref, source_ref, shift_ref, out_ref):
    piece_leaves = out_ref.shape[0]
    listed_width = place_ref.shape[0] // count_ref.shape[0]
    rows = NEAR_ROWS
    lanes = out_ref.shape[2]
    out_ref[...] = jnp.zeros(out_ref.shape, out_ref.dtype)
    lane = lax.broadcasted_iota(jnp.int32, (rows, lanes), 1)
    row = lax.broadcasted_iota(jnp.int32, (rows, lanes), 0)

    def leaf_body(local, carry):
        leaf = first_leaf + local
        chunk_count = (count_ref[leaf] + rows - 1) // rows
        listed = listed_ref[leaf]
        base = leaf * listed_width

        def chunk_body(chunk, carry2):
            first = pl.multiple_of(chunk * rows, rows)
            column = target_ref[local, pl.ds(first, rows), :]
            tx = jnp.broadcast_to(column[:, 0:1], (rows, lanes))
            ty = jnp.broadcast_to(column[:, 1:2], (rows, lanes))
            tz = jnp.broadcast_to(column[:, 2:3], (rows, lanes))
            acc = near_pairs(tx, ty, tz, source_ref[place_ref[base]], row + first != lane)

            def offset_body(number, acc):
                srow = source_ref[place_ref[base + number]] + shift_ref[kind_ref[base + number]]
                terms = near_pairs(tx, ty, tz, srow, None)
                return tuple(a + b for a, b in zip(acc, terms))

            acc = lax.fori_loop(1, listed, offset_body, acc)
            sums = [jnp.sum(part, axis=1, keepdims=True) for part in acc]
            tile = jnp.where(
                lane == 0, sums[0], jnp.where(lane == 1, sums[1], jnp.where(lane == 2, sums[2], sums[3]))
            )
            out_ref[local, pl.ds(first, rows), :] = jnp.where(lane < 4, tile, 0.0)
            return carry2

        lax.fori_loop(0, chunk_count, chunk_body, 0)
        return carry

    lax.fori_loop(0, piece_leaves, leaf_body, 0)


def near_local(charged, rimmed, counts, near_flags):
    size_x, size_y, size_z, slot_count = charged.shape[1:]
    leaf_count = size_x * size_y * size_z
    ext_y = size_y + 2
    target = jnp.transpose(charged, (1, 2, 3, 4, 0)).reshape(leaf_count, slot_count, 4)
    source = jnp.transpose(rimmed, (1, 2, 3, 0, 4)).reshape(-1, 4, slot_count)
    source = jnp.pad(source, ((0, 0), (0, 4), (0, 0)))
    offsets = [(0, 0, 0)] + leaf_offsets()
    shift_rows = jnp.array([[float(v) for v in offset] + [0.0] * 5 for offset in offsets], jnp.float32)
    shift_table = jnp.broadcast_to(shift_rows[:, :, None], (len(offsets), 8, slot_count))
    leaf_x = jnp.arange(size_x, dtype=jnp.int32)[:, None, None]
    leaf_y = jnp.arange(size_y, dtype=jnp.int32)[None, :, None]
    leaf_z = jnp.arange(size_z, dtype=jnp.int32)[None, None, :]
    places = []
    for offset in offsets:
        place = ((leaf_x + 1 + offset[0]) * ext_y + leaf_y + 1 + offset[1]) * size_z + leaf_z + offset[2]
        places.append(jnp.broadcast_to(place, (size_x, size_y, size_z)))
    places = jnp.stack(places).reshape(len(offsets), leaf_count)
    layer = jnp.arange(size_z, dtype=jnp.int32)
    valid = jnp.stack([((layer + offset[2] >= 0) & (layer + offset[2] < size_z)) for offset in offsets[1:]])
    active = (near_flags != 0) & valid[:, None, None, :]
    active = jnp.concatenate([jnp.ones((1, leaf_count), bool), active.reshape(len(offsets) - 1, leaf_count)])
    order = jnp.argsort(jnp.logical_not(active).astype(jnp.int32), axis=0, stable=True)
    listed = jnp.sum(active.astype(jnp.int32), axis=0)
    place_list = jnp.take_along_axis(places, order, axis=0)
    place_list = jnp.where(jnp.take_along_axis(active, order, axis=0), place_list, 0)
    place_list = jnp.transpose(place_list).reshape(-1)
    kind_list = jnp.transpose(order).reshape(-1).astype(jnp.int32)
    count_list = counts.reshape(-1)
    piece = leaf_count // NEAR_PIECES if leaf_count % NEAR_PIECES == 0 else leaf_count
    pairs = piece * slot_count * slot_count * 10

    def run_piece(number, gate):
        first_leaf = number * piece
        own = target[first_leaf : first_leaf + piece]
        if gate is not None:
            own, unused = lax.optimization_barrier((own, gate))
        return pl.pallas_call(
            functools.partial(near_kernel, first_leaf),
            out_shape=jax.ShapeDtypeStruct((piece, slot_count, 128), jnp.float32),
            in_specs=[pl.BlockSpec(memory_space=pltpu.SMEM)] * 4 + [pl.BlockSpec(memory_space=pltpu.VMEM)] * 3,
            out_specs=pl.BlockSpec(memory_space=pltpu.VMEM),
            cost_estimate=pl.CostEstimate(
                flops=20 * pairs, transcendentals=pairs, bytes_accessed=8 * piece * slot_count * 128
            ),
        )(count_list, listed, place_list, kind_list, own, source, shift_table)

    def finish_near(outs):
        out = jnp.concatenate([part[:, :, :4] for part in outs], axis=0)
        near = jnp.transpose(out, (2, 0, 1))
        return near.reshape(4, size_x, size_y, size_z, slot_count)

    return leaf_count // piece, run_piece, finish_near


def body(
    atom_data,
    counts,
    near_flags,
    child_up,
    child_down,
    leaf_far,
    parent_far,
    column_up,
    column_down,
    tree_up,
    tree_down,
    tree_side,
    lattice,
):
    coef_count = lattice.shape[0]
    slot_count = atom_data.shape[4]
    size_x, size_y, size_z = (atom_data.shape[1], atom_data.shape[2], atom_data.shape[3])
    live_slots = (
        jnp.arange(slot_count, dtype=jnp.int32)[None, None, None, :] < counts[..., None]
    ).astype(jnp.float32)
    charged = jnp.concatenate([atom_data[:3], (atom_data[3] * live_slots)[None]], axis=0)
    waves = wave_table(coef_count, jnp.float32)
    half_count = waves.shape[1]
    moments = leaf_moments(charged, waves)
    parents = climb_children(moments, child_up.astype(jnp.float32))
    rimmed, parent_rim = extended_joint([(charged, 1), (parents, 2)], (("gx", 1), ("gy", 2)))
    parent_rim = jnp.pad(parent_rim, ((0, 0), (0, 0), (0, 0), (2, 2)))
    half_x, half_y, half_z = (parents.shape[1], parents.shape[2], parents.shape[3])
    phase_grid = block_phase(waves, half_x, half_y, half_z, jnp.float32)
    turned = jnp.sum(rotate_by(parents, phase_grid), axis=(1, 2, 3))
    column = matrix_vector(column_up.astype(jnp.float32), turned)
    piece_count, run_piece, finish_near = near_local(charged, rimmed, counts, near_flags)
    pieces = []

    def hook(value, prior):
        number = len(pieces)
        if number < piece_count:
            if number > 0:
                value, unused = lax.optimization_barrier((value, pieces[-1]))
            pieces.append(run_piece(number, prior))
        return value

    column_local = chain_tree(column, tree_up, tree_down, tree_side, lattice, hook)
    while len(pieces) < piece_count:
        pieces.append(run_piece(len(pieces), None))
    near_terms = finish_near(pieces)
    leaf_rim = leaf_moments(rimmed, waves)
    leaf_rim = jnp.pad(leaf_rim, ((0, 0), (0, 0), (0, 0), (1, 1)))
    lowered = matrix_vector(column_down.astype(jnp.float32), column_local)
    parent_local = rotate_by(
        jnp.broadcast_to(lowered[:, None, None, None], parents.shape), -phase_grid
    )
    far_parents = parent_offsets()
    parent_stack = jnp.stack(
        [
            parent_rim[
                :,
                2 + offset[0] : 2 + offset[0] + half_x,
                2 + offset[1] : 2 + offset[1] + half_y,
                2 + offset[2] : 2 + offset[2] + half_z,
            ]
            for offset in far_parents
        ]
    )
    parent_turns = offset_phases(waves, far_parents).reshape(len(far_parents), half_count, 1, 1, 1)
    parent_sum = jnp.sum(jax.vmap(rotate_by)(parent_stack, parent_turns), axis=0)
    parent_local = parent_local + jnp.einsum(
        "kj,jxyz->kxyz", parent_far.astype(jnp.float32), parent_sum, precision=highest
    )
    leaf_local = descend_children(parent_local, child_down.astype(jnp.float32))
    near_leaves = leaf_offsets()
    leaf_stack = jnp.stack(
        [
            leaf_rim[
                :,
                1 + offset[0] : 1 + offset[0] + size_x,
                1 + offset[1] : 1 + offset[1] + size_y,
                1 + offset[2] : 1 + offset[2] + size_z,
            ]
            for offset in near_leaves
        ]
    )
    leaf_stack = leaf_stack * (1.0 - near_flags.astype(jnp.float32))[:, None]
    leaf_turns = offset_phases(waves, near_leaves).reshape(len(near_leaves), half_count, 1, 1, 1)
    leaf_sum = jnp.sum(jax.vmap(rotate_by)(leaf_stack, leaf_turns), axis=0)
    leaf_local = leaf_local + jnp.einsum(
        "kj,jxyz->kxyz", leaf_far.astype(jnp.float32), leaf_sum, precision=highest
    )
    potential, field_parts = evaluate(charged, leaf_local, waves)
    return assemble(near_terms, potential, field_parts, charged[3], live_slots)


def solution(mesh):
    in_specs = (
        P(None, "gx", "gy", None, None),
        P("gx", "gy", None),
        P(None, "gx", "gy", None),
        P(),
        P(),
        P(),
        P(),
        P(),
        P(),
        P(),
        P(),
        P(),
        P(),
    )
    out_specs = P(None, "gx", "gy", None, None)
    return jax.shard_map(body, mesh=mesh, in_specs=in_specs, out_specs=out_specs, check_vma=False)
```

```python
import functools

import jax
import jax.numpy as jnp
from jax import lax
from jax.experimental import pallas as pl
from jax.experimental.pallas import tpu as pltpu
from jax.sharding import PartitionSpec as P

soften = 0.04
coulomb = 0.1
highest = lax.Precision.HIGHEST


def from_partner(value, axis, bit):
    mask = 2**bit
    pairs = [(source, source ^ mask) for source in range(lax.axis_size(axis))]
    return lax.ppermute(value, axis, pairs)


def extended_2(block, sides, width):
    return extended_joint([(block, width)], sides)[0]


def extended_joint(parts, sides):
    blocks = [block for block, width in parts]
    for axis, dim in sides:
        count = lax.axis_size(axis)
        forward = [(i, i + 1) for i in range(count - 1)]
        forward.append((count - 1, 0))
        backward = [(target, source) for source, target in forward]
        lows = [lax.slice_in_dim(b, b.shape[dim] - w, None, axis=dim) for b, (_, w) in zip(blocks, parts)]
        highs = [lax.slice_in_dim(b, 0, w, axis=dim) for b, (_, w) in zip(blocks, parts)]
        sizes = [piece.size for piece in lows]
        low_all = lax.ppermute(jnp.concatenate([piece.reshape(-1) for piece in lows]), axis, forward)
        high_all = lax.ppermute(jnp.concatenate([piece.reshape(-1) for piece in highs]), axis, backward)
        grown = []
        place = 0
        for b, piece, size in zip(blocks, lows, sizes):
            low = low_all[place : place + size].reshape(piece.shape)
            high = high_all[place : place + size].reshape(piece.shape)
            place += size
            grown.append(jnp.concatenate([low, b, high], axis=dim))
        blocks = grown
    return blocks


def wave_table(coef_count, float_type):
    half_count = (coef_count - 1) // 2
    order_index = jnp.arange(1, half_count + 1, dtype=jnp.int32).astype(float_type)
    height = 1.0 - 2.0 * (order_index - 0.5) / half_count
    radius = jnp.sqrt(jnp.maximum(1.0 - height * height, 0.0))
    angle_turn = 2.399963 * order_index
    magnitude = 1.5 + jnp.mod(order_index, 3.0)
    return (
        jnp.stack([radius * jnp.cos(angle_turn), radius * jnp.sin(angle_turn), height])
        * magnitude[None]
    )


def waves_at(atom_data, waves):
    shape_lead = (waves.shape[1],) + (1,) * (atom_data.ndim - 1)
    phases = waves[0].reshape(shape_lead) * (atom_data[0] - 0.5)[None]
    phases = phases + waves[1].reshape(shape_lead) * (atom_data[1] - 0.5)[None]
    phases = phases + waves[2].reshape(shape_lead) * (atom_data[2] - 0.5)[None]
    return (jnp.cos(phases), jnp.sin(phases))


def rotate_by(field, phase):
    half_count = phase.shape[0]
    cosine = jnp.cos(phase)
    sine_part = jnp.sin(phase)
    cos_coef = field[1 : 1 + half_count]
    sin_coef = field[1 + half_count :]
    return jnp.concatenate(
        [
            field[0:1],
            cos_coef * cosine - sin_coef * sine_part,
            cos_coef * sine_part + sin_coef * cosine,
        ],
        axis=0,
    )


def offset_phases(waves, offsets):
    table = jnp.array(offsets, dtype=jnp.float32)
    return (
        table[:, 0:1] * waves[0][None]
        + table[:, 1:2] * waves[1][None]
        + table[:, 2:3] * waves[2][None]
    )


def block_phase(waves, size_x, size_y, size_z, float_type):
    place_x = jnp.arange(size_x, dtype=jnp.int32).astype(float_type)
    place_y = jnp.arange(size_y, dtype=jnp.int32).astype(float_type)
    place_z = jnp.arange(size_z, dtype=jnp.int32).astype(float_type)
    phase = waves[0][:, None, None, None] * place_x[None, :, None, None]
    phase = phase + waves[1][:, None, None, None] * place_y[None, None, :, None]
    return phase + waves[2][:, None, None, None] * place_z[None, None, None, :]


def leaf_moments(atom_data, waves):
    cosine, sine_part = waves_at(atom_data, waves)
    charge = atom_data[3]
    summed = jnp.sum(charge, axis=-1)[None]
    return jnp.concatenate(
        [
            summed,
            jnp.sum(cosine * charge[None], axis=-1),
            jnp.sum(sine_part * charge[None], axis=-1),
        ],
        axis=0,
    )


def evaluate(atom_data, local_exp, waves):
    cosine, sine_part = waves_at(atom_data, waves)
    half_count = waves.shape[1]
    cos_local = local_exp[1 : 1 + half_count][..., None]
    sin_local = local_exp[1 + half_count :][..., None]
    potential = local_exp[0][..., None] + jnp.sum(
        cos_local * cosine + sin_local * sine_part, axis=0
    )
    mixed_term = cos_local * sine_part - sin_local * cosine
    shape_lead = (half_count,) + (1,) * (mixed_term.ndim - 1)
    field_parts = [
        jnp.sum(waves[component].reshape(shape_lead) * mixed_term, axis=0) for component in range(3)
    ]
    return (potential, field_parts)


def near_row(target, source, flag_grid, shift_vec, keep_self):
    weight = source[3] * flag_grid[..., None]
    delta_x = target[0][..., :, None] - (source[0][..., None, :] + shift_vec[0])
    delta_y = target[1][..., :, None] - (source[1][..., None, :] + shift_vec[1])
    delta_z = target[2][..., :, None] - (source[2][..., None, :] + shift_vec[2])
    inverse = lax.rsqrt(delta_x * delta_x + delta_y * delta_y + delta_z * delta_z + soften)
    pair_term = weight[..., None, :] * keep_self * inverse
    cube_term = pair_term * inverse * inverse
    return jnp.stack(
        [
            jnp.sum(pair_term, axis=-1),
            jnp.sum(cube_term * delta_x, axis=-1),
            jnp.sum(cube_term * delta_y, axis=-1),
            jnp.sum(cube_term * delta_z, axis=-1),
        ]
    )


def full_flags(near_flags, float_type):
    flags_float = near_flags.astype(float_type)
    centre = jnp.ones((1,) + flags_float.shape[1:], float_type)
    return jnp.concatenate([flags_float[:13], centre, flags_float[13:]], axis=0)


def leaf_offsets():
    return [
        (shift_x, shift_y, shift_z)
        for shift_x in (-1, 0, 1)
        for shift_y in (-1, 0, 1)
        for shift_z in (-1, 0, 1)
        if (shift_x, shift_y, shift_z) != (0, 0, 0)
    ]


def parent_offsets():
    return [
        (shift_x, shift_y, shift_z)
        for shift_x in range(-2, 3)
        for shift_y in range(-2, 3)
        for shift_z in range(-2, 3)
        if max(abs(shift_x), abs(shift_y), abs(shift_z)) == 2
    ]


def climb_children(moments, matrices):
    coef_count, size_x, size_y, size_z = moments.shape
    parted = moments.reshape(coef_count, size_x // 2, 2, size_y // 2, 2, size_z // 2, 2)
    return jnp.einsum(
        "abckj,jxaybzc->kxyz",
        matrices.reshape(2, 2, 2, coef_count, coef_count),
        parted,
        precision=highest,
    )


def descend_children(parent_local, matrices):
    coef_count, size_x, size_y, size_z = parent_local.shape
    spread = jnp.einsum(
        "abckj,jxyz->kxaybzc",
        matrices.reshape(2, 2, 2, coef_count, coef_count),
        parent_local,
        precision=highest,
    )
    return spread.reshape(coef_count, 2 * size_x, 2 * size_y, 2 * size_z)


def matrix_vector(matrix, vector):
    return jnp.dot(matrix, vector, precision=highest)


def pick_side(matrices, own_side):
    return lax.dynamic_index_in_dim(matrices, own_side, 0, keepdims=False)


def pair_step(matrices, own_side, current, partner):
    return matrix_vector(pick_side(matrices, own_side), current) + matrix_vector(
        pick_side(matrices, 1 - own_side), partner
    )


def chain_tree(column, tree_up, tree_down, tree_side, lattice, hook):
    climbs = tree_up.astype(jnp.float32)
    lowers = tree_down.astype(jnp.float32)
    sideways = tree_side.astype(jnp.float32)
    current = column
    visited = []
    partner = None
    for level_bit in range(lax.axis_size("gx").bit_length() - 1):
        current = hook(current, partner)
        partner = from_partner(current, "gx", level_bit)
        own_side = lax.axis_index("gx") // 2**level_bit % 2
        current = pair_step(climbs[0], own_side, current, partner)
        visited.append((0, own_side, partner))
    for level_bit in range(lax.axis_size("gy").bit_length() - 1):
        current = hook(current, partner)
        partner = from_partner(current, "gy", level_bit)
        own_side = lax.axis_index("gy") // 2**level_bit % 2
        current = pair_step(climbs[1], own_side, current, partner)
        visited.append((1, own_side, partner))
    local_exp = matrix_vector(lattice.astype(jnp.float32), current)
    for axis_num, own_side, partner in reversed(visited):
        local_exp = matrix_vector(pick_side(lowers[axis_num], own_side), local_exp) + matrix_vector(
            pick_side(sideways[axis_num], own_side), partner
        )
    return local_exp


def flip_pair(column_grid, axis_num, level_bit):
    coef_count, size_x, size_y = column_grid.shape
    span_size = 2**level_bit
    if axis_num == 0:
        parted = column_grid.reshape(coef_count, size_x // (2 * span_size), 2, span_size, size_y)
        return parted[:, :, ::-1].reshape(column_grid.shape)
    parted = column_grid.reshape(coef_count, size_x, size_y // (2 * span_size), 2, span_size)
    return parted[:, :, :, ::-1].reshape(column_grid.shape)


def side_grid(axis_num, level_bit, size_x, size_y):
    positions = jnp.arange(size_x if axis_num == 0 else size_y, dtype=jnp.int32)
    own_side = positions // 2**level_bit % 2
    return own_side[:, None] if axis_num == 0 else own_side[None, :]


def choose_side(matrices, own_side, column_grid):
    first = jnp.einsum("kj,jxy->kxy", matrices[0], column_grid, precision=highest)
    second = jnp.einsum("kj,jxy->kxy", matrices[1], column_grid, precision=highest)
    return jnp.where(own_side[None] == 0, first, second)


def gathered_tree(column, tree_up, tree_down, tree_side, lattice):
    size_x, size_y = lax.axis_size("gx"), lax.axis_size("gy")
    gathered = lax.all_gather(column, ("gx", "gy")).reshape(size_x, size_y, -1)
    current = jnp.transpose(gathered, (2, 0, 1))
    levels = [(0, bit) for bit in range(size_x.bit_length() - 1)] + [
        (1, bit) for bit in range(size_y.bit_length() - 1)
    ]
    visited = []
    for axis_num, level_bit in levels:
        partner = flip_pair(current, axis_num, level_bit)
        own_side = side_grid(axis_num, level_bit, size_x, size_y)
        climbs = tree_up[axis_num].astype(jnp.float32)
        current = choose_side(climbs, own_side, current) + choose_side(climbs, 1 - own_side, partner)
        visited.append((axis_num, own_side, partner))
    local_exp = jnp.einsum("kj,jxy->kxy", lattice.astype(jnp.float32), current, precision=highest)
    for axis_num, own_side, partner in reversed(visited):
        local_exp = choose_side(tree_down[axis_num].astype(jnp.float32), own_side, local_exp) + choose_side(
            tree_side[axis_num].astype(jnp.float32), own_side, partner
        )
    own = lax.dynamic_slice(local_exp, (0, lax.axis_index("gx"), lax.axis_index("gy")), (local_exp.shape[0], 1, 1))
    return own.reshape(-1)


def assemble(near_terms, potential, field_parts, charge, live_slots):
    rows = [coulomb * (near_terms[0] + potential) * live_slots]
    for component in range(3):
        rows.append(coulomb * charge * (near_terms[1 + component] + field_parts[component]))
    return jnp.stack(rows)


NEAR_ROWS = 32
NEAR_PIECES = 8


def near_pairs(tx, ty, tz, srow, mask):
    weight = srow[3:4, :]
    delta_x = tx - srow[0:1, :]
    delta_y = ty - srow[1:2, :]
    delta_z = tz - srow[2:3, :]
    inverse = lax.rsqrt(delta_x * delta_x + delta_y * delta_y + delta_z * delta_z + soften)
    pair_term = weight * inverse
    if mask is not None:
        pair_term = jnp.where(mask, pair_term, 0.0)
    cube_term = pair_term * inverse * inverse
    return (pair_term, cube_term * delta_x, cube_term * delta_y, cube_term * delta_z)


def near_kernel(first_leaf, leaf_count, listed_width, table_ref, target_ref, source_ref, shift_ref, out_ref):
    piece_leaves = out_ref.shape[0]
    place_start = 2 * leaf_count
    kind_start = place_start + leaf_count * listed_width
    rows = NEAR_ROWS
    lanes = out_ref.shape[2]
    out_ref[...] = jnp.zeros(out_ref.shape, out_ref.dtype)
    lane = lax.broadcasted_iota(jnp.int32, (rows, lanes), 1)
    row = lax.broadcasted_iota(jnp.int32, (rows, lanes), 0)

    def leaf_body(local, carry):
        leaf = first_leaf + local
        chunk_count = (table_ref[leaf] + rows - 1) // rows
        listed = table_ref[leaf_count + leaf]
        base = leaf * listed_width

        def chunk_body(chunk, carry2):
            first = pl.multiple_of(chunk * rows, rows)
            column = target_ref[local, pl.ds(first, rows), :]
            tx = jnp.broadcast_to(column[:, 0:1], (rows, lanes))
            ty = jnp.broadcast_to(column[:, 1:2], (rows, lanes))
            tz = jnp.broadcast_to(column[:, 2:3], (rows, lanes))
            acc = near_pairs(tx, ty, tz, source_ref[table_ref[place_start + base]], row + first != lane)

            def offset_body(number, acc):
                srow = source_ref[table_ref[place_start + base + number]] + shift_ref[table_ref[kind_start + base + number]]
                terms = near_pairs(tx, ty, tz, srow, None)
                return tuple(a + b for a, b in zip(acc, terms))

            acc = lax.fori_loop(1, listed, offset_body, acc)
            sums = [jnp.sum(part, axis=1, keepdims=True) for part in acc]
            tile = jnp.where(
                lane == 0, sums[0], jnp.where(lane == 1, sums[1], jnp.where(lane == 2, sums[2], sums[3]))
            )
            out_ref[local, pl.ds(first, rows), :] = jnp.where(lane < 4, tile, 0.0)
            return carry2

        lax.fori_loop(0, chunk_count, chunk_body, 0)
        return carry

    lax.fori_loop(0, piece_leaves, leaf_body, 0)


def near_local(charged, rimmed, counts, near_flags):
    size_x, size_y, size_z, slot_count = charged.shape[1:]
    leaf_count = size_x * size_y * size_z
    ext_y = size_y + 2
    target = jnp.transpose(charged, (1, 2, 3, 4, 0)).reshape(leaf_count, slot_count, 4)
    source = jnp.transpose(rimmed, (1, 2, 3, 0, 4)).reshape(-1, 4, slot_count)
    source = jnp.pad(source, ((0, 0), (0, 4), (0, 0)))
    offsets = [(0, 0, 0)] + leaf_offsets()
    shift_rows = jnp.array([[float(v) for v in offset] + [0.0] * 5 for offset in offsets], jnp.float32)
    shift_table = jnp.broadcast_to(shift_rows[:, :, None], (len(offsets), 8, slot_count))
    leaf_x = jnp.arange(size_x, dtype=jnp.int32)[:, None, None]
    leaf_y = jnp.arange(size_y, dtype=jnp.int32)[None, :, None]
    leaf_z = jnp.arange(size_z, dtype=jnp.int32)[None, None, :]
    places = []
    for offset in offsets:
        place = ((leaf_x + 1 + offset[0]) * ext_y + leaf_y + 1 + offset[1]) * size_z + leaf_z + offset[2]
        places.append(jnp.broadcast_to(place, (size_x, size_y, size_z)))
    places = jnp.stack(places).reshape(len(offsets), leaf_count)
    layer = jnp.arange(size_z, dtype=jnp.int32)
    valid = jnp.stack([((layer + offset[2] >= 0) & (layer + offset[2] < size_z)) for offset in offsets[1:]])
    active = (near_flags != 0) & valid[:, None, None, :]
    active = jnp.concatenate([jnp.ones((1, leaf_count), bool), active.reshape(len(offsets) - 1, leaf_count)])
    listed = jnp.sum(active.astype(jnp.int32), axis=0)
    position = jnp.cumsum(active.astype(jnp.int32), axis=0) - 1
    slots = jnp.arange(len(offsets), dtype=jnp.int32)
    chosen = active[None] & (position[None] == slots[:, None, None])
    kind_list = jnp.sum(jnp.where(chosen, slots[None, :, None], 0), axis=1)
    place_list = jnp.sum(jnp.where(chosen, places[None], 0), axis=1)
    table = jnp.concatenate(
        [counts.reshape(-1), listed, jnp.transpose(place_list).reshape(-1), jnp.transpose(kind_list).reshape(-1)]
    ).astype(jnp.int32)
    piece = leaf_count // NEAR_PIECES if leaf_count % NEAR_PIECES == 0 else leaf_count
    pairs = piece * slot_count * slot_count * 10

    def run_piece(number, gate):
        first_leaf = number * piece
        own = target[first_leaf : first_leaf + piece]
        if gate is not None:
            own, unused = lax.optimization_barrier((own, gate))
        return pl.pallas_call(
            functools.partial(near_kernel, first_leaf, leaf_count, len(offsets)),
            out_shape=jax.ShapeDtypeStruct((piece, slot_count, 128), jnp.float32),
            in_specs=[pl.BlockSpec(memory_space=pltpu.SMEM)] + [pl.BlockSpec(memory_space=pltpu.VMEM)] * 3,
            out_specs=pl.BlockSpec(memory_space=pltpu.VMEM),
            cost_estimate=pl.CostEstimate(
                flops=20 * pairs, transcendentals=pairs, bytes_accessed=8 * piece * slot_count * 128
            ),
        )(table, own, source, shift_table)

    def finish_near(outs):
        out = jnp.concatenate([part[:, :, :4] for part in outs], axis=0)
        near = jnp.transpose(out, (2, 0, 1))
        return near.reshape(4, size_x, size_y, size_z, slot_count)

    return leaf_count // piece, run_piece, finish_near


def body(
    atom_data,
    counts,
    near_flags,
    child_up,
    child_down,
    leaf_far,
    parent_far,
    column_up,
    column_down,
    tree_up,
    tree_down,
    tree_side,
    lattice,
):
    coef_count = lattice.shape[0]
    slot_count = atom_data.shape[4]
    size_x, size_y, size_z = (atom_data.shape[1], atom_data.shape[2], atom_data.shape[3])
    live_slots = (
        jnp.arange(slot_count, dtype=jnp.int32)[None, None, None, :] < counts[..., None]
    ).astype(jnp.float32)
    charged = jnp.concatenate([atom_data[:3], (atom_data[3] * live_slots)[None]], axis=0)
    waves = wave_table(coef_count, jnp.float32)
    half_count = waves.shape[1]
    moments = leaf_moments(charged, waves)
    parents = climb_children(moments, child_up.astype(jnp.float32))
    rimmed, parent_rim, leaf_rim = extended_joint([(charged, 1), (parents, 2), (moments, 1)], (("gx", 1), ("gy", 2)))
    parent_rim = jnp.pad(parent_rim, ((0, 0), (0, 0), (0, 0), (2, 2)))
    half_x, half_y, half_z = (parents.shape[1], parents.shape[2], parents.shape[3])
    phase_grid = block_phase(waves, half_x, half_y, half_z, jnp.float32)
    turned = jnp.sum(rotate_by(parents, phase_grid), axis=(1, 2, 3))
    column = matrix_vector(column_up.astype(jnp.float32), turned)
    piece_count, run_piece, finish_near = near_local(charged, rimmed, counts, near_flags)
    pieces = []

    def hook(value, prior):
        number = len(pieces)
        if number < piece_count:
            if number > 0:
                value, unused = lax.optimization_barrier((value, pieces[-1]))
            pieces.append(run_piece(number, prior))
        return value

    column_local = chain_tree(column, tree_up, tree_down, tree_side, lattice, hook)
    while len(pieces) < piece_count:
        pieces.append(run_piece(len(pieces), None))
    near_terms = finish_near(pieces)
    leaf_rim = jnp.pad(leaf_rim, ((0, 0), (0, 0), (0, 0), (1, 1)))
    lowered = matrix_vector(column_down.astype(jnp.float32), column_local)
    parent_local = rotate_by(
        jnp.broadcast_to(lowered[:, None, None, None], parents.shape), -phase_grid
    )
    far_parents = parent_offsets()
    parent_stack = jnp.stack(
        [
            parent_rim[
                :,
                2 + offset[0] : 2 + offset[0] + half_x,
                2 + offset[1] : 2 + offset[1] + half_y,
                2 + offset[2] : 2 + offset[2] + half_z,
            ]
            for offset in far_parents
        ]
    )
    parent_turns = offset_phases(waves, far_parents).reshape(len(far_parents), half_count, 1, 1, 1)
    parent_sum = jnp.sum(jax.vmap(rotate_by)(parent_stack, parent_turns), axis=0)
    parent_local = parent_local + jnp.einsum(
        "kj,jxyz->kxyz", parent_far.astype(jnp.float32), parent_sum, precision=highest
    )
    leaf_local = descend_children(parent_local, child_down.astype(jnp.float32))
    near_leaves = leaf_offsets()
    leaf_stack = jnp.stack(
        [
            leaf_rim[
                :,
                1 + offset[0] : 1 + offset[0] + size_x,
                1 + offset[1] : 1 + offset[1] + size_y,
                1 + offset[2] : 1 + offset[2] + size_z,
            ]
            for offset in near_leaves
        ]
    )
    leaf_stack = leaf_stack * (1.0 - near_flags.astype(jnp.float32))[:, None]
    leaf_turns = offset_phases(waves, near_leaves).reshape(len(near_leaves), half_count, 1, 1, 1)
    leaf_sum = jnp.sum(jax.vmap(rotate_by)(leaf_stack, leaf_turns), axis=0)
    leaf_local = leaf_local + jnp.einsum(
        "kj,jxyz->kxyz", leaf_far.astype(jnp.float32), leaf_sum, precision=highest
    )
    potential, field_parts = evaluate(charged, leaf_local, waves)
    return assemble(near_terms, potential, field_parts, charged[3], live_slots)


def solution(mesh):
    in_specs = (
        P(None, "gx", "gy", None, None),
        P("gx", "gy", None),
        P(None, "gx", "gy", None),
        P(),
        P(),
        P(),
        P(),
        P(),
        P(),
        P(),
        P(),
        P(),
        P(),
    )
    out_specs = P(None, "gx", "gy", None, None)
    return jax.shard_map(body, mesh=mesh, in_specs=in_specs, out_specs=out_specs, check_vma=False)
```

```python
import functools

import jax
import jax.numpy as jnp
from jax import lax
from jax.experimental import pallas as pl
from jax.experimental.pallas import tpu as pltpu
from jax.sharding import PartitionSpec as P

soften = 0.04
coulomb = 0.1
highest = lax.Precision.HIGHEST


def from_partner(value, axis, bit):
    mask = 2**bit
    pairs = [(source, source ^ mask) for source in range(lax.axis_size(axis))]
    return lax.ppermute(value, axis, pairs)


def extended_2(block, sides, width):
    return extended_joint([(block, width)], sides)[0]


def extended_joint(parts, sides):
    blocks = [block for block, width in parts]
    for axis, dim in sides:
        count = lax.axis_size(axis)
        forward = [(i, i + 1) for i in range(count - 1)]
        forward.append((count - 1, 0))
        backward = [(target, source) for source, target in forward]
        lows = [lax.slice_in_dim(b, b.shape[dim] - w, None, axis=dim) for b, (_, w) in zip(blocks, parts)]
        highs = [lax.slice_in_dim(b, 0, w, axis=dim) for b, (_, w) in zip(blocks, parts)]
        sizes = [piece.size for piece in lows]
        low_all = lax.ppermute(jnp.concatenate([piece.reshape(-1) for piece in lows]), axis, forward)
        high_all = lax.ppermute(jnp.concatenate([piece.reshape(-1) for piece in highs]), axis, backward)
        grown = []
        place = 0
        for b, piece, size in zip(blocks, lows, sizes):
            low = low_all[place : place + size].reshape(piece.shape)
            high = high_all[place : place + size].reshape(piece.shape)
            place += size
            grown.append(jnp.concatenate([low, b, high], axis=dim))
        blocks = grown
    return blocks


def wave_table(coef_count, float_type):
    half_count = (coef_count - 1) // 2
    order_index = jnp.arange(1, half_count + 1, dtype=jnp.int32).astype(float_type)
    height = 1.0 - 2.0 * (order_index - 0.5) / half_count
    radius = jnp.sqrt(jnp.maximum(1.0 - height * height, 0.0))
    angle_turn = 2.399963 * order_index
    magnitude = 1.5 + jnp.mod(order_index, 3.0)
    return (
        jnp.stack([radius * jnp.cos(angle_turn), radius * jnp.sin(angle_turn), height])
        * magnitude[None]
    )


def waves_at(atom_data, waves):
    shape_lead = (waves.shape[1],) + (1,) * (atom_data.ndim - 1)
    phases = waves[0].reshape(shape_lead) * (atom_data[0] - 0.5)[None]
    phases = phases + waves[1].reshape(shape_lead) * (atom_data[1] - 0.5)[None]
    phases = phases + waves[2].reshape(shape_lead) * (atom_data[2] - 0.5)[None]
    return (jnp.cos(phases), jnp.sin(phases))


def rotate_by(field, phase):
    half_count = phase.shape[0]
    cosine = jnp.cos(phase)
    sine_part = jnp.sin(phase)
    cos_coef = field[1 : 1 + half_count]
    sin_coef = field[1 + half_count :]
    return jnp.concatenate(
        [
            field[0:1],
            cos_coef * cosine - sin_coef * sine_part,
            cos_coef * sine_part + sin_coef * cosine,
        ],
        axis=0,
    )


def offset_phases(waves, offsets):
    table = jnp.array(offsets, dtype=jnp.float32)
    return (
        table[:, 0:1] * waves[0][None]
        + table[:, 1:2] * waves[1][None]
        + table[:, 2:3] * waves[2][None]
    )


def block_phase(waves, size_x, size_y, size_z, float_type):
    place_x = jnp.arange(size_x, dtype=jnp.int32).astype(float_type)
    place_y = jnp.arange(size_y, dtype=jnp.int32).astype(float_type)
    place_z = jnp.arange(size_z, dtype=jnp.int32).astype(float_type)
    phase = waves[0][:, None, None, None] * place_x[None, :, None, None]
    phase = phase + waves[1][:, None, None, None] * place_y[None, None, :, None]
    return phase + waves[2][:, None, None, None] * place_z[None, None, None, :]


def leaf_moments(atom_data, waves):
    cosine, sine_part = waves_at(atom_data, waves)
    charge = atom_data[3]
    summed = jnp.sum(charge, axis=-1)[None]
    return jnp.concatenate(
        [
            summed,
            jnp.sum(cosine * charge[None], axis=-1),
            jnp.sum(sine_part * charge[None], axis=-1),
        ],
        axis=0,
    )


def evaluate(atom_data, local_exp, waves):
    cosine, sine_part = waves_at(atom_data, waves)
    half_count = waves.shape[1]
    cos_local = local_exp[1 : 1 + half_count][..., None]
    sin_local = local_exp[1 + half_count :][..., None]
    potential = local_exp[0][..., None] + jnp.sum(
        cos_local * cosine + sin_local * sine_part, axis=0
    )
    mixed_term = cos_local * sine_part - sin_local * cosine
    shape_lead = (half_count,) + (1,) * (mixed_term.ndim - 1)
    field_parts = [
        jnp.sum(waves[component].reshape(shape_lead) * mixed_term, axis=0) for component in range(3)
    ]
    return (potential, field_parts)


def near_row(target, source, flag_grid, shift_vec, keep_self):
    weight = source[3] * flag_grid[..., None]
    delta_x = target[0][..., :, None] - (source[0][..., None, :] + shift_vec[0])
    delta_y = target[1][..., :, None] - (source[1][..., None, :] + shift_vec[1])
    delta_z = target[2][..., :, None] - (source[2][..., None, :] + shift_vec[2])
    inverse = lax.rsqrt(delta_x * delta_x + delta_y * delta_y + delta_z * delta_z + soften)
    pair_term = weight[..., None, :] * keep_self * inverse
    cube_term = pair_term * inverse * inverse
    return jnp.stack(
        [
            jnp.sum(pair_term, axis=-1),
            jnp.sum(cube_term * delta_x, axis=-1),
            jnp.sum(cube_term * delta_y, axis=-1),
            jnp.sum(cube_term * delta_z, axis=-1),
        ]
    )


def full_flags(near_flags, float_type):
    flags_float = near_flags.astype(float_type)
    centre = jnp.ones((1,) + flags_float.shape[1:], float_type)
    return jnp.concatenate([flags_float[:13], centre, flags_float[13:]], axis=0)


def leaf_offsets():
    return [
        (shift_x, shift_y, shift_z)
        for shift_x in (-1, 0, 1)
        for shift_y in (-1, 0, 1)
        for shift_z in (-1, 0, 1)
        if (shift_x, shift_y, shift_z) != (0, 0, 0)
    ]


def parent_offsets():
    return [
        (shift_x, shift_y, shift_z)
        for shift_x in range(-2, 3)
        for shift_y in range(-2, 3)
        for shift_z in range(-2, 3)
        if max(abs(shift_x), abs(shift_y), abs(shift_z)) == 2
    ]


def climb_children(moments, matrices):
    coef_count, size_x, size_y, size_z = moments.shape
    parted = moments.reshape(coef_count, size_x // 2, 2, size_y // 2, 2, size_z // 2, 2)
    return jnp.einsum(
        "abckj,jxaybzc->kxyz",
        matrices.reshape(2, 2, 2, coef_count, coef_count),
        parted,
        precision=highest,
    )


def descend_children(parent_local, matrices):
    coef_count, size_x, size_y, size_z = parent_local.shape
    spread = jnp.einsum(
        "abckj,jxyz->kxaybzc",
        matrices.reshape(2, 2, 2, coef_count, coef_count),
        parent_local,
        precision=highest,
    )
    return spread.reshape(coef_count, 2 * size_x, 2 * size_y, 2 * size_z)


def matrix_vector(matrix, vector):
    return jnp.dot(matrix, vector, precision=highest)


def pick_side(matrices, own_side):
    return lax.dynamic_index_in_dim(matrices, own_side, 0, keepdims=False)


def pair_step(matrices, own_side, current, partner):
    return matrix_vector(pick_side(matrices, own_side), current) + matrix_vector(
        pick_side(matrices, 1 - own_side), partner
    )


def chain_tree(column, tree_up, tree_down, tree_side, lattice, hook):
    climbs = tree_up.astype(jnp.float32)
    lowers = tree_down.astype(jnp.float32)
    sideways = tree_side.astype(jnp.float32)
    current = column
    visited = []
    partner = None
    for level_bit in range(lax.axis_size("gx").bit_length() - 1):
        current = hook(current, partner)
        partner = from_partner(current, "gx", level_bit)
        own_side = lax.axis_index("gx") // 2**level_bit % 2
        current = pair_step(climbs[0], own_side, current, partner)
        visited.append((0, own_side, partner))
    for level_bit in range(lax.axis_size("gy").bit_length() - 1):
        current = hook(current, partner)
        partner = from_partner(current, "gy", level_bit)
        own_side = lax.axis_index("gy") // 2**level_bit % 2
        current = pair_step(climbs[1], own_side, current, partner)
        visited.append((1, own_side, partner))
    local_exp = matrix_vector(lattice.astype(jnp.float32), current)
    for axis_num, own_side, partner in reversed(visited):
        local_exp = matrix_vector(pick_side(lowers[axis_num], own_side), local_exp) + matrix_vector(
            pick_side(sideways[axis_num], own_side), partner
        )
    return local_exp


def flip_pair(column_grid, axis_num, level_bit):
    coef_count, size_x, size_y = column_grid.shape
    span_size = 2**level_bit
    if axis_num == 0:
        parted = column_grid.reshape(coef_count, size_x // (2 * span_size), 2, span_size, size_y)
        return parted[:, :, ::-1].reshape(column_grid.shape)
    parted = column_grid.reshape(coef_count, size_x, size_y // (2 * span_size), 2, span_size)
    return parted[:, :, :, ::-1].reshape(column_grid.shape)


def side_grid(axis_num, level_bit, size_x, size_y):
    positions = jnp.arange(size_x if axis_num == 0 else size_y, dtype=jnp.int32)
    own_side = positions // 2**level_bit % 2
    return own_side[:, None] if axis_num == 0 else own_side[None, :]


def choose_side(matrices, own_side, column_grid):
    first = jnp.einsum("kj,jxy->kxy", matrices[0], column_grid, precision=highest)
    second = jnp.einsum("kj,jxy->kxy", matrices[1], column_grid, precision=highest)
    return jnp.where(own_side[None] == 0, first, second)


def gathered_tree(column, tree_up, tree_down, tree_side, lattice):
    size_x, size_y = lax.axis_size("gx"), lax.axis_size("gy")
    gathered = lax.all_gather(column, ("gx", "gy")).reshape(size_x, size_y, -1)
    current = jnp.transpose(gathered, (2, 0, 1))
    levels = [(0, bit) for bit in range(size_x.bit_length() - 1)] + [
        (1, bit) for bit in range(size_y.bit_length() - 1)
    ]
    visited = []
    for axis_num, level_bit in levels:
        partner = flip_pair(current, axis_num, level_bit)
        own_side = side_grid(axis_num, level_bit, size_x, size_y)
        climbs = tree_up[axis_num].astype(jnp.float32)
        current = choose_side(climbs, own_side, current) + choose_side(climbs, 1 - own_side, partner)
        visited.append((axis_num, own_side, partner))
    local_exp = jnp.einsum("kj,jxy->kxy", lattice.astype(jnp.float32), current, precision=highest)
    for axis_num, own_side, partner in reversed(visited):
        local_exp = choose_side(tree_down[axis_num].astype(jnp.float32), own_side, local_exp) + choose_side(
            tree_side[axis_num].astype(jnp.float32), own_side, partner
        )
    own = lax.dynamic_slice(local_exp, (0, lax.axis_index("gx"), lax.axis_index("gy")), (local_exp.shape[0], 1, 1))
    return own.reshape(-1)


def assemble(near_terms, potential, field_parts, charge, live_slots):
    rows = [coulomb * (near_terms[0] + potential) * live_slots]
    for component in range(3):
        rows.append(coulomb * charge * (near_terms[1 + component] + field_parts[component]))
    return jnp.stack(rows)


NEAR_ROWS = 32
NEAR_PIECES = 8


def near_pairs(tx, ty, tz, srow, mask):
    weight = srow[3:4, :]
    delta_x = tx - srow[0:1, :]
    delta_y = ty - srow[1:2, :]
    delta_z = tz - srow[2:3, :]
    inverse = lax.rsqrt(delta_x * delta_x + delta_y * delta_y + delta_z * delta_z + soften)
    pair_term = weight * inverse
    if mask is not None:
        pair_term = jnp.where(mask, pair_term, 0.0)
    cube_term = pair_term * inverse * inverse
    return (pair_term, cube_term * delta_x, cube_term * delta_y, cube_term * delta_z)


def near_kernel(first_leaf, leaf_count, listed_width, table_ref, target_ref, source_ref, shift_ref, out_ref, tile_ref):
    piece_leaves = out_ref.shape[0]
    place_start = 2 * leaf_count
    kind_start = place_start + leaf_count * listed_width
    rows = NEAR_ROWS
    lanes = out_ref.shape[2]
    lane = lax.broadcasted_iota(jnp.int32, (rows, lanes), 1)
    row = lax.broadcasted_iota(jnp.int32, (rows, lanes), 0)

    def leaf_body(local, carry):
        leaf = first_leaf + local
        chunk_count = (table_ref[leaf] + rows - 1) // rows
        listed = table_ref[leaf_count + leaf]
        base = leaf * listed_width
        tile_ref[...] = jnp.zeros(tile_ref.shape, tile_ref.dtype)

        def chunk_body(chunk, carry2):
            first = pl.multiple_of(chunk * rows, rows)
            column = target_ref[local, pl.ds(first, rows), :]
            tx = jnp.broadcast_to(column[:, 0:1], (rows, lanes))
            ty = jnp.broadcast_to(column[:, 1:2], (rows, lanes))
            tz = jnp.broadcast_to(column[:, 2:3], (rows, lanes))
            acc = near_pairs(tx, ty, tz, source_ref[table_ref[place_start + base]], row + first != lane)

            def offset_body(pair_number, acc):
                number = base + 1 + 2 * pair_number
                first_row = source_ref[table_ref[place_start + number]] + shift_ref[table_ref[kind_start + number]]
                second_row = source_ref[table_ref[place_start + number + 1]] + shift_ref[table_ref[kind_start + number + 1]]
                first_terms = near_pairs(tx, ty, tz, first_row, None)
                second_terms = near_pairs(tx, ty, tz, second_row, None)
                return tuple(a + b + c for a, b, c in zip(acc, first_terms, second_terms))

            acc = lax.fori_loop(0, listed // 2, offset_body, acc)
            sums = [jnp.sum(part, axis=1, keepdims=True) for part in acc]
            tile = jnp.where(
                lane == 0, sums[0], jnp.where(lane == 1, sums[1], jnp.where(lane == 2, sums[2], sums[3]))
            )
            tile_ref[pl.ds(first, rows), :] = jnp.where(lane < 4, tile, 0.0)
            return carry2

        lax.fori_loop(0, chunk_count, chunk_body, 0)
        out_ref[local] = jnp.transpose(tile_ref[...])[0 : out_ref.shape[1], :]
        return carry

    lax.fori_loop(0, piece_leaves, leaf_body, 0)


def near_local(charged, rimmed, counts, near_flags):
    size_x, size_y, size_z, slot_count = charged.shape[1:]
    leaf_count = size_x * size_y * size_z
    ext_y = size_y + 2
    target = jnp.transpose(charged, (1, 2, 3, 4, 0)).reshape(leaf_count, slot_count, 4)
    source = jnp.transpose(rimmed, (1, 2, 3, 0, 4)).reshape(-1, 4, slot_count)
    source = jnp.pad(source, ((0, 1), (0, 4), (0, 0)))
    empty_leaf = source.shape[0] - 1
    offsets = [(0, 0, 0)] + leaf_offsets()
    shift_rows = jnp.array([[float(v) for v in offset] + [0.0] * 5 for offset in offsets], jnp.float32)
    shift_table = jnp.broadcast_to(shift_rows[:, :, None], (len(offsets), 8, slot_count))
    leaf_x = jnp.arange(size_x, dtype=jnp.int32)[:, None, None]
    leaf_y = jnp.arange(size_y, dtype=jnp.int32)[None, :, None]
    leaf_z = jnp.arange(size_z, dtype=jnp.int32)[None, None, :]
    places = []
    for offset in offsets:
        place = ((leaf_x + 1 + offset[0]) * ext_y + leaf_y + 1 + offset[1]) * size_z + leaf_z + offset[2]
        places.append(jnp.broadcast_to(place, (size_x, size_y, size_z)))
    places = jnp.stack(places).reshape(len(offsets), leaf_count)
    layer = jnp.arange(size_z, dtype=jnp.int32)
    valid = jnp.stack([((layer + offset[2] >= 0) & (layer + offset[2] < size_z)) for offset in offsets[1:]])
    active = (near_flags != 0) & valid[:, None, None, :]
    active = jnp.concatenate([jnp.ones((1, leaf_count), bool), active.reshape(len(offsets) - 1, leaf_count)])
    listed = jnp.sum(active.astype(jnp.int32), axis=0)
    listed = listed + (listed + 1) % 2
    position = jnp.cumsum(active.astype(jnp.int32), axis=0) - 1
    slots = jnp.arange(len(offsets), dtype=jnp.int32)
    chosen = active[None] & (position[None] == slots[:, None, None])
    kind_list = jnp.sum(jnp.where(chosen, slots[None, :, None], 0), axis=1)
    place_list = jnp.sum(jnp.where(chosen, places[None], 0), axis=1)
    place_list = jnp.where(slots[:, None] < jnp.sum(active.astype(jnp.int32), axis=0)[None], place_list, empty_leaf)
    table = jnp.concatenate(
        [counts.reshape(-1), listed, jnp.transpose(place_list).reshape(-1), jnp.transpose(kind_list).reshape(-1)]
    ).astype(jnp.int32)
    piece = leaf_count // NEAR_PIECES if leaf_count % NEAR_PIECES == 0 else leaf_count
    pairs = piece * slot_count * slot_count * 10

    def run_piece(number, gate):
        first_leaf = number * piece
        own = target[first_leaf : first_leaf + piece]
        if gate is not None:
            own, unused = lax.optimization_barrier((own, gate))
        return pl.pallas_call(
            functools.partial(near_kernel, first_leaf, leaf_count, len(offsets)),
            out_shape=jax.ShapeDtypeStruct((piece, 8, slot_count), jnp.float32),
            in_specs=[pl.BlockSpec(memory_space=pltpu.SMEM)] + [pl.BlockSpec(memory_space=pltpu.VMEM)] * 3,
            out_specs=pl.BlockSpec(memory_space=pltpu.VMEM),
            scratch_shapes=[pltpu.VMEM((slot_count, 128), jnp.float32)],
            cost_estimate=pl.CostEstimate(
                flops=20 * pairs, transcendentals=pairs, bytes_accessed=8 * piece * slot_count * 128
            ),
        )(table, own, source, shift_table)

    def finish_near(outs):
        out = jnp.concatenate(outs, axis=0)
        near = jnp.transpose(out[:, :4, :], (1, 0, 2))
        return near.reshape(4, size_x, size_y, size_z, slot_count)

    return leaf_count // piece, run_piece, finish_near


def body(
    atom_data,
    counts,
    near_flags,
    child_up,
    child_down,
    leaf_far,
    parent_far,
    column_up,
    column_down,
    tree_up,
    tree_down,
    tree_side,
    lattice,
):
    coef_count = lattice.shape[0]
    slot_count = atom_data.shape[4]
    size_x, size_y, size_z = (atom_data.shape[1], atom_data.shape[2], atom_data.shape[3])
    live_slots = (
        jnp.arange(slot_count, dtype=jnp.int32)[None, None, None, :] < counts[..., None]
    ).astype(jnp.float32)
    charged = jnp.concatenate([atom_data[:3], (atom_data[3] * live_slots)[None]], axis=0)
    waves = wave_table(coef_count, jnp.float32)
    half_count = waves.shape[1]
    moments = leaf_moments(charged, waves)
    parents = climb_children(moments, child_up.astype(jnp.float32))
    rimmed, parent_rim, leaf_rim = extended_joint([(charged, 1), (parents, 2), (moments, 1)], (("gx", 1), ("gy", 2)))
    parent_rim = jnp.pad(parent_rim, ((0, 0), (0, 0), (0, 0), (2, 2)))
    half_x, half_y, half_z = (parents.shape[1], parents.shape[2], parents.shape[3])
    phase_grid = block_phase(waves, half_x, half_y, half_z, jnp.float32)
    turned = jnp.sum(rotate_by(parents, phase_grid), axis=(1, 2, 3))
    column = matrix_vector(column_up.astype(jnp.float32), turned)
    piece_count, run_piece, finish_near = near_local(charged, rimmed, counts, near_flags)
    pieces = []

    def hook(value, prior):
        number = len(pieces)
        if number < piece_count:
            if number > 0:
                value, unused = lax.optimization_barrier((value, pieces[-1]))
            pieces.append(run_piece(number, prior))
        return value

    column_local = chain_tree(column, tree_up, tree_down, tree_side, lattice, hook)
    while len(pieces) < piece_count:
        pieces.append(run_piece(len(pieces), None))
    near_terms = finish_near(pieces)
    leaf_rim = jnp.pad(leaf_rim, ((0, 0), (0, 0), (0, 0), (1, 1)))
    lowered = matrix_vector(column_down.astype(jnp.float32), column_local)
    parent_local = rotate_by(
        jnp.broadcast_to(lowered[:, None, None, None], parents.shape), -phase_grid
    )
    far_parents = parent_offsets()
    parent_stack = jnp.stack(
        [
            parent_rim[
                :,
                2 + offset[0] : 2 + offset[0] + half_x,
                2 + offset[1] : 2 + offset[1] + half_y,
                2 + offset[2] : 2 + offset[2] + half_z,
            ]
            for offset in far_parents
        ]
    )
    parent_turns = offset_phases(waves, far_parents).reshape(len(far_parents), half_count, 1, 1, 1)
    parent_sum = jnp.sum(jax.vmap(rotate_by)(parent_stack, parent_turns), axis=0)
    parent_local = parent_local + jnp.einsum(
        "kj,jxyz->kxyz", parent_far.astype(jnp.float32), parent_sum, precision=highest
    )
    leaf_local = descend_children(parent_local, child_down.astype(jnp.float32))
    near_leaves = leaf_offsets()
    leaf_stack = jnp.stack(
        [
            leaf_rim[
                :,
                1 + offset[0] : 1 + offset[0] + size_x,
                1 + offset[1] : 1 + offset[1] + size_y,
                1 + offset[2] : 1 + offset[2] + size_z,
            ]
            for offset in near_leaves
        ]
    )
    leaf_stack = leaf_stack * (1.0 - near_flags.astype(jnp.float32))[:, None]
    leaf_turns = offset_phases(waves, near_leaves).reshape(len(near_leaves), half_count, 1, 1, 1)
    leaf_sum = jnp.sum(jax.vmap(rotate_by)(leaf_stack, leaf_turns), axis=0)
    leaf_local = leaf_local + jnp.einsum(
        "kj,jxyz->kxyz", leaf_far.astype(jnp.float32), leaf_sum, precision=highest
    )
    potential, field_parts = evaluate(charged, leaf_local, waves)
    return assemble(near_terms, potential, field_parts, charged[3], live_slots)


def solution(mesh):
    in_specs = (
        P(None, "gx", "gy", None, None),
        P("gx", "gy", None),
        P(None, "gx", "gy", None),
        P(),
        P(),
        P(),
        P(),
        P(),
        P(),
        P(),
        P(),
        P(),
        P(),
    )
    out_specs = P(None, "gx", "gy", None, None)
    return jax.shard_map(body, mesh=mesh, in_specs=in_specs, out_specs=out_specs, check_vma=False)
```

```python
import functools

import jax
import jax.numpy as jnp
from jax import lax
from jax.experimental import pallas as pl
from jax.experimental.pallas import tpu as pltpu
from jax.sharding import PartitionSpec as P

soften = 0.04
coulomb = 0.1
highest = lax.Precision.HIGHEST


def from_partner(value, axis, bit):
    mask = 2**bit
    pairs = [(source, source ^ mask) for source in range(lax.axis_size(axis))]
    return lax.ppermute(value, axis, pairs)


def extended_2(block, sides, width):
    return extended_joint([(block, width)], sides)[0]


def extended_joint(parts, sides):
    blocks = [block for block, width in parts]
    for axis, dim in sides:
        count = lax.axis_size(axis)
        forward = [(i, i + 1) for i in range(count - 1)]
        forward.append((count - 1, 0))
        backward = [(target, source) for source, target in forward]
        lows = [lax.slice_in_dim(b, b.shape[dim] - w, None, axis=dim) for b, (_, w) in zip(blocks, parts)]
        highs = [lax.slice_in_dim(b, 0, w, axis=dim) for b, (_, w) in zip(blocks, parts)]
        sizes = [piece.size for piece in lows]
        low_all = lax.ppermute(jnp.concatenate([piece.reshape(-1) for piece in lows]), axis, forward)
        high_all = lax.ppermute(jnp.concatenate([piece.reshape(-1) for piece in highs]), axis, backward)
        grown = []
        place = 0
        for b, piece, size in zip(blocks, lows, sizes):
            low = low_all[place : place + size].reshape(piece.shape)
            high = high_all[place : place + size].reshape(piece.shape)
            place += size
            grown.append(jnp.concatenate([low, b, high], axis=dim))
        blocks = grown
    return blocks


def wave_table(coef_count, float_type):
    half_count = (coef_count - 1) // 2
    order_index = jnp.arange(1, half_count + 1, dtype=jnp.int32).astype(float_type)
    height = 1.0 - 2.0 * (order_index - 0.5) / half_count
    radius = jnp.sqrt(jnp.maximum(1.0 - height * height, 0.0))
    angle_turn = 2.399963 * order_index
    magnitude = 1.5 + jnp.mod(order_index, 3.0)
    return (
        jnp.stack([radius * jnp.cos(angle_turn), radius * jnp.sin(angle_turn), height])
        * magnitude[None]
    )


def waves_at(atom_data, waves):
    shape_lead = (waves.shape[1],) + (1,) * (atom_data.ndim - 1)
    phases = waves[0].reshape(shape_lead) * (atom_data[0] - 0.5)[None]
    phases = phases + waves[1].reshape(shape_lead) * (atom_data[1] - 0.5)[None]
    phases = phases + waves[2].reshape(shape_lead) * (atom_data[2] - 0.5)[None]
    return (jnp.cos(phases), jnp.sin(phases))


def rotate_by(field, phase):
    half_count = phase.shape[0]
    cosine = jnp.cos(phase)
    sine_part = jnp.sin(phase)
    cos_coef = field[1 : 1 + half_count]
    sin_coef = field[1 + half_count :]
    return jnp.concatenate(
        [
            field[0:1],
            cos_coef * cosine - sin_coef * sine_part,
            cos_coef * sine_part + sin_coef * cosine,
        ],
        axis=0,
    )


def offset_phases(waves, offsets):
    table = jnp.array(offsets, dtype=jnp.float32)
    return (
        table[:, 0:1] * waves[0][None]
        + table[:, 1:2] * waves[1][None]
        + table[:, 2:3] * waves[2][None]
    )


def block_phase(waves, size_x, size_y, size_z, float_type):
    place_x = jnp.arange(size_x, dtype=jnp.int32).astype(float_type)
    place_y = jnp.arange(size_y, dtype=jnp.int32).astype(float_type)
    place_z = jnp.arange(size_z, dtype=jnp.int32).astype(float_type)
    phase = waves[0][:, None, None, None] * place_x[None, :, None, None]
    phase = phase + waves[1][:, None, None, None] * place_y[None, None, :, None]
    return phase + waves[2][:, None, None, None] * place_z[None, None, None, :]


def leaf_moments(atom_data, waves):
    cosine, sine_part = waves_at(atom_data, waves)
    charge = atom_data[3]
    summed = jnp.sum(charge, axis=-1)[None]
    return jnp.concatenate(
        [
            summed,
            jnp.sum(cosine * charge[None], axis=-1),
            jnp.sum(sine_part * charge[None], axis=-1),
        ],
        axis=0,
    )


def evaluate(atom_data, local_exp, waves):
    cosine, sine_part = waves_at(atom_data, waves)
    half_count = waves.shape[1]
    cos_local = local_exp[1 : 1 + half_count][..., None]
    sin_local = local_exp[1 + half_count :][..., None]
    potential = local_exp[0][..., None] + jnp.sum(
        cos_local * cosine + sin_local * sine_part, axis=0
    )
    mixed_term = cos_local * sine_part - sin_local * cosine
    shape_lead = (half_count,) + (1,) * (mixed_term.ndim - 1)
    field_parts = [
        jnp.sum(waves[component].reshape(shape_lead) * mixed_term, axis=0) for component in range(3)
    ]
    return (potential, field_parts)


def near_row(target, source, flag_grid, shift_vec, keep_self):
    weight = source[3] * flag_grid[..., None]
    delta_x = target[0][..., :, None] - (source[0][..., None, :] + shift_vec[0])
    delta_y = target[1][..., :, None] - (source[1][..., None, :] + shift_vec[1])
    delta_z = target[2][..., :, None] - (source[2][..., None, :] + shift_vec[2])
    inverse = lax.rsqrt(delta_x * delta_x + delta_y * delta_y + delta_z * delta_z + soften)
    pair_term = weight[..., None, :] * keep_self * inverse
    cube_term = pair_term * inverse * inverse
    return jnp.stack(
        [
            jnp.sum(pair_term, axis=-1),
            jnp.sum(cube_term * delta_x, axis=-1),
            jnp.sum(cube_term * delta_y, axis=-1),
            jnp.sum(cube_term * delta_z, axis=-1),
        ]
    )


def full_flags(near_flags, float_type):
    flags_float = near_flags.astype(float_type)
    centre = jnp.ones((1,) + flags_float.shape[1:], float_type)
    return jnp.concatenate([flags_float[:13], centre, flags_float[13:]], axis=0)


def leaf_offsets():
    return [
        (shift_x, shift_y, shift_z)
        for shift_x in (-1, 0, 1)
        for shift_y in (-1, 0, 1)
        for shift_z in (-1, 0, 1)
        if (shift_x, shift_y, shift_z) != (0, 0, 0)
    ]


def parent_offsets():
    return [
        (shift_x, shift_y, shift_z)
        for shift_x in range(-2, 3)
        for shift_y in range(-2, 3)
        for shift_z in range(-2, 3)
        if max(abs(shift_x), abs(shift_y), abs(shift_z)) == 2
    ]


def climb_children(moments, matrices):
    coef_count, size_x, size_y, size_z = moments.shape
    parted = moments.reshape(coef_count, size_x // 2, 2, size_y // 2, 2, size_z // 2, 2)
    return jnp.einsum(
        "abckj,jxaybzc->kxyz",
        matrices.reshape(2, 2, 2, coef_count, coef_count),
        parted,
        precision=highest,
    )


def descend_children(parent_local, matrices):
    coef_count, size_x, size_y, size_z = parent_local.shape
    spread = jnp.einsum(
        "abckj,jxyz->kxaybzc",
        matrices.reshape(2, 2, 2, coef_count, coef_count),
        parent_local,
        precision=highest,
    )
    return spread.reshape(coef_count, 2 * size_x, 2 * size_y, 2 * size_z)


def matrix_vector(matrix, vector):
    return jnp.dot(matrix, vector, precision=highest)


def pick_side(matrices, own_side):
    return lax.dynamic_index_in_dim(matrices, own_side, 0, keepdims=False)


def pair_step(matrices, own_side, current, partner):
    return matrix_vector(pick_side(matrices, own_side), current) + matrix_vector(
        pick_side(matrices, 1 - own_side), partner
    )


def chain_tree(column, tree_up, tree_down, tree_side, lattice, hook):
    climbs = tree_up.astype(jnp.float32)
    lowers = tree_down.astype(jnp.float32)
    sideways = tree_side.astype(jnp.float32)
    current = column
    visited = []
    partner = None
    for level_bit in range(lax.axis_size("gx").bit_length() - 1):
        current = hook(current, partner)
        partner = from_partner(current, "gx", level_bit)
        own_side = lax.axis_index("gx") // 2**level_bit % 2
        current = pair_step(climbs[0], own_side, current, partner)
        visited.append((0, own_side, partner))
    for level_bit in range(lax.axis_size("gy").bit_length() - 1):
        current = hook(current, partner)
        partner = from_partner(current, "gy", level_bit)
        own_side = lax.axis_index("gy") // 2**level_bit % 2
        current = pair_step(climbs[1], own_side, current, partner)
        visited.append((1, own_side, partner))
    local_exp = matrix_vector(lattice.astype(jnp.float32), current)
    for axis_num, own_side, partner in reversed(visited):
        local_exp = matrix_vector(pick_side(lowers[axis_num], own_side), local_exp) + matrix_vector(
            pick_side(sideways[axis_num], own_side), partner
        )
    return local_exp


def flip_pair(column_grid, axis_num, level_bit):
    coef_count, size_x, size_y = column_grid.shape
    span_size = 2**level_bit
    if axis_num == 0:
        parted = column_grid.reshape(coef_count, size_x // (2 * span_size), 2, span_size, size_y)
        return parted[:, :, ::-1].reshape(column_grid.shape)
    parted = column_grid.reshape(coef_count, size_x, size_y // (2 * span_size), 2, span_size)
    return parted[:, :, :, ::-1].reshape(column_grid.shape)


def side_grid(axis_num, level_bit, size_x, size_y):
    positions = jnp.arange(size_x if axis_num == 0 else size_y, dtype=jnp.int32)
    own_side = positions // 2**level_bit % 2
    return own_side[:, None] if axis_num == 0 else own_side[None, :]


def choose_side(matrices, own_side, column_grid):
    first = jnp.einsum("kj,jxy->kxy", matrices[0], column_grid, precision=highest)
    second = jnp.einsum("kj,jxy->kxy", matrices[1], column_grid, precision=highest)
    return jnp.where(own_side[None] == 0, first, second)


def gathered_tree(column, tree_up, tree_down, tree_side, lattice):
    size_x, size_y = lax.axis_size("gx"), lax.axis_size("gy")
    gathered = lax.all_gather(column, ("gx", "gy")).reshape(size_x, size_y, -1)
    current = jnp.transpose(gathered, (2, 0, 1))
    levels = [(0, bit) for bit in range(size_x.bit_length() - 1)] + [
        (1, bit) for bit in range(size_y.bit_length() - 1)
    ]
    visited = []
    for axis_num, level_bit in levels:
        partner = flip_pair(current, axis_num, level_bit)
        own_side = side_grid(axis_num, level_bit, size_x, size_y)
        climbs = tree_up[axis_num].astype(jnp.float32)
        current = choose_side(climbs, own_side, current) + choose_side(climbs, 1 - own_side, partner)
        visited.append((axis_num, own_side, partner))
    local_exp = jnp.einsum("kj,jxy->kxy", lattice.astype(jnp.float32), current, precision=highest)
    for axis_num, own_side, partner in reversed(visited):
        local_exp = choose_side(tree_down[axis_num].astype(jnp.float32), own_side, local_exp) + choose_side(
            tree_side[axis_num].astype(jnp.float32), own_side, partner
        )
    own = lax.dynamic_slice(local_exp, (0, lax.axis_index("gx"), lax.axis_index("gy")), (local_exp.shape[0], 1, 1))
    return own.reshape(-1)


def assemble(near_terms, potential, field_parts, charge, live_slots):
    rows = [coulomb * (near_terms[0] + potential) * live_slots]
    for component in range(3):
        rows.append(coulomb * charge * (near_terms[1 + component] + field_parts[component]))
    return jnp.stack(rows)


NEAR_ROWS = 32
NEAR_PIECES = 8


def near_pairs(tx, ty, tz, srow, mask):
    weight = srow[3:4, :]
    delta_x = tx - srow[0:1, :]
    delta_y = ty - srow[1:2, :]
    delta_z = tz - srow[2:3, :]
    inverse = lax.rsqrt(delta_x * delta_x + delta_y * delta_y + delta_z * delta_z + soften)
    pair_term = weight * inverse
    if mask is not None:
        pair_term = jnp.where(mask, pair_term, 0.0)
    cube_term = pair_term * inverse * inverse
    return (pair_term, cube_term * delta_x, cube_term * delta_y, cube_term * delta_z)


def near_kernel(first_leaf, leaf_count, listed_width, table_ref, target_ref, source_ref, shift_ref, out_ref, tile_ref):
    piece_leaves = out_ref.shape[0]
    place_start = 2 * leaf_count
    kind_start = place_start + leaf_count * listed_width
    order_start = kind_start + leaf_count * listed_width
    rows = NEAR_ROWS
    lanes = out_ref.shape[2]
    lane = lax.broadcasted_iota(jnp.int32, (rows, lanes), 1)
    row = lax.broadcasted_iota(jnp.int32, (rows, lanes), 0)

    def leaf_body(local, carry):
        leaf = table_ref[order_start + first_leaf + local]
        chunk_count = (table_ref[leaf] + rows - 1) // rows
        listed = table_ref[leaf_count + leaf]
        base = leaf * listed_width
        tile_ref[...] = jnp.zeros(tile_ref.shape, tile_ref.dtype)

        def chunk_body(chunk, carry2):
            first = pl.multiple_of(chunk * rows, rows)
            column = target_ref[local, pl.ds(first, rows), :]
            tx = jnp.broadcast_to(column[:, 0:1], (rows, lanes))
            ty = jnp.broadcast_to(column[:, 1:2], (rows, lanes))
            tz = jnp.broadcast_to(column[:, 2:3], (rows, lanes))
            acc = near_pairs(tx, ty, tz, source_ref[table_ref[place_start + base]], row + first != lane)

            def offset_body(pair_number, acc):
                number = base + 1 + 2 * pair_number
                first_row = source_ref[table_ref[place_start + number]] + shift_ref[table_ref[kind_start + number]]
                second_row = source_ref[table_ref[place_start + number + 1]] + shift_ref[table_ref[kind_start + number + 1]]
                first_terms = near_pairs(tx, ty, tz, first_row, None)
                second_terms = near_pairs(tx, ty, tz, second_row, None)
                return tuple(a + b + c for a, b, c in zip(acc, first_terms, second_terms))

            acc = lax.fori_loop(0, listed // 2, offset_body, acc)
            sums = [jnp.sum(part, axis=1, keepdims=True) for part in acc]
            tile = jnp.where(
                lane == 0, sums[0], jnp.where(lane == 1, sums[1], jnp.where(lane == 2, sums[2], sums[3]))
            )
            tile_ref[pl.ds(first, rows), :] = jnp.where(lane < 4, tile, 0.0)
            return carry2

        lax.fori_loop(0, chunk_count, chunk_body, 0)
        out_ref[local] = jnp.transpose(tile_ref[...])[0 : out_ref.shape[1], :]
        return carry

    lax.fori_loop(0, piece_leaves, leaf_body, 0)


def near_local(charged, rimmed, counts, near_flags):
    size_x, size_y, size_z, slot_count = charged.shape[1:]
    leaf_count = size_x * size_y * size_z
    ext_y = size_y + 2
    target = jnp.transpose(charged, (1, 2, 3, 4, 0)).reshape(leaf_count, slot_count, 4)
    inner = [
        leaf
        for leaf in range(leaf_count)
        if 0 < leaf // (size_y * size_z) < size_x - 1 and 0 < leaf // size_z % size_y < size_y - 1
    ]
    order = inner + [leaf for leaf in range(leaf_count) if leaf not in inner]
    back = [order.index(leaf) for leaf in range(leaf_count)]
    target = jnp.concatenate([target[leaf : leaf + 1] for leaf in order], axis=0)

    def source_table(grid):
        table = jnp.transpose(grid, (1, 2, 3, 0, 4)).reshape(-1, 4, slot_count)
        return jnp.pad(table, ((0, 1), (0, 4), (0, 0)))

    source = source_table(rimmed)
    early_source = source_table(jnp.pad(charged, ((0, 0), (1, 1), (1, 1), (0, 0), (0, 0))))
    empty_leaf = source.shape[0] - 1
    offsets = [(0, 0, 0)] + leaf_offsets()
    shift_rows = jnp.array([[float(v) for v in offset] + [0.0] * 5 for offset in offsets], jnp.float32)
    shift_table = jnp.broadcast_to(shift_rows[:, :, None], (len(offsets), 8, slot_count))
    leaf_x = jnp.arange(size_x, dtype=jnp.int32)[:, None, None]
    leaf_y = jnp.arange(size_y, dtype=jnp.int32)[None, :, None]
    leaf_z = jnp.arange(size_z, dtype=jnp.int32)[None, None, :]
    places = []
    for offset in offsets:
        place = ((leaf_x + 1 + offset[0]) * ext_y + leaf_y + 1 + offset[1]) * size_z + leaf_z + offset[2]
        places.append(jnp.broadcast_to(place, (size_x, size_y, size_z)))
    places = jnp.stack(places).reshape(len(offsets), leaf_count)
    layer = jnp.arange(size_z, dtype=jnp.int32)
    valid = jnp.stack([((layer + offset[2] >= 0) & (layer + offset[2] < size_z)) for offset in offsets[1:]])
    active = (near_flags != 0) & valid[:, None, None, :]
    active = jnp.concatenate([jnp.ones((1, leaf_count), bool), active.reshape(len(offsets) - 1, leaf_count)])
    listed = jnp.sum(active.astype(jnp.int32), axis=0)
    listed = listed + (listed + 1) % 2
    position = jnp.cumsum(active.astype(jnp.int32), axis=0) - 1
    slots = jnp.arange(len(offsets), dtype=jnp.int32)
    chosen = active[None] & (position[None] == slots[:, None, None])
    kind_list = jnp.sum(jnp.where(chosen, slots[None, :, None], 0), axis=1)
    place_list = jnp.sum(jnp.where(chosen, places[None], 0), axis=1)
    place_list = jnp.where(slots[:, None] < jnp.sum(active.astype(jnp.int32), axis=0)[None], place_list, empty_leaf)
    table = jnp.concatenate(
        [
            counts.reshape(-1),
            listed,
            jnp.transpose(place_list).reshape(-1),
            jnp.transpose(kind_list).reshape(-1),
            jnp.array(order, jnp.int32),
        ]
    ).astype(jnp.int32)
    piece = leaf_count // NEAR_PIECES if leaf_count % NEAR_PIECES == 0 else leaf_count
    pairs = piece * slot_count * slot_count * 10

    def run_piece(number, gate):
        first_leaf = number * piece
        own = target[first_leaf : first_leaf + piece]
        early = all(leaf in inner for leaf in order[first_leaf : first_leaf + piece])
        if gate is not None:
            own, unused = lax.optimization_barrier((own, gate))
        return pl.pallas_call(
            functools.partial(near_kernel, first_leaf, leaf_count, len(offsets)),
            out_shape=jax.ShapeDtypeStruct((piece, 8, slot_count), jnp.float32),
            in_specs=[pl.BlockSpec(memory_space=pltpu.SMEM)] + [pl.BlockSpec(memory_space=pltpu.VMEM)] * 3,
            out_specs=pl.BlockSpec(memory_space=pltpu.VMEM),
            scratch_shapes=[pltpu.VMEM((slot_count, 128), jnp.float32)],
            cost_estimate=pl.CostEstimate(
                flops=20 * pairs, transcendentals=pairs, bytes_accessed=8 * piece * slot_count * 128
            ),
        )(table, own, early_source if early else source, shift_table)

    def finish_near(outs):
        out = jnp.concatenate(outs, axis=0)
        out = jnp.concatenate([out[place : place + 1] for place in back], axis=0)
        near = jnp.transpose(out[:, :4, :], (1, 0, 2))
        return near.reshape(4, size_x, size_y, size_z, slot_count)

    return leaf_count // piece, run_piece, finish_near


def body(
    atom_data,
    counts,
    near_flags,
    child_up,
    child_down,
    leaf_far,
    parent_far,
    column_up,
    column_down,
    tree_up,
    tree_down,
    tree_side,
    lattice,
):
    coef_count = lattice.shape[0]
    slot_count = atom_data.shape[4]
    size_x, size_y, size_z = (atom_data.shape[1], atom_data.shape[2], atom_data.shape[3])
    live_slots = (
        jnp.arange(slot_count, dtype=jnp.int32)[None, None, None, :] < counts[..., None]
    ).astype(jnp.float32)
    charged = jnp.concatenate([atom_data[:3], (atom_data[3] * live_slots)[None]], axis=0)
    waves = wave_table(coef_count, jnp.float32)
    half_count = waves.shape[1]
    moments = leaf_moments(charged, waves)
    parents = climb_children(moments, child_up.astype(jnp.float32))
    rimmed, parent_rim, leaf_rim = extended_joint([(charged, 1), (parents, 2), (moments, 1)], (("gx", 1), ("gy", 2)))
    parent_rim = jnp.pad(parent_rim, ((0, 0), (0, 0), (0, 0), (2, 2)))
    half_x, half_y, half_z = (parents.shape[1], parents.shape[2], parents.shape[3])
    phase_grid = block_phase(waves, half_x, half_y, half_z, jnp.float32)
    turned = jnp.sum(rotate_by(parents, phase_grid), axis=(1, 2, 3))
    column = matrix_vector(column_up.astype(jnp.float32), turned)
    piece_count, run_piece, finish_near = near_local(charged, rimmed, counts, near_flags)
    pieces = []

    def hook(value, prior):
        number = len(pieces)
        if number < piece_count:
            if number > 0:
                value, unused = lax.optimization_barrier((value, pieces[-1]))
            pieces.append(run_piece(number, prior))
        return value

    column_local = chain_tree(column, tree_up, tree_down, tree_side, lattice, hook)
    while len(pieces) < piece_count:
        pieces.append(run_piece(len(pieces), None))
    near_terms = finish_near(pieces)
    leaf_rim = jnp.pad(leaf_rim, ((0, 0), (0, 0), (0, 0), (1, 1)))
    lowered = matrix_vector(column_down.astype(jnp.float32), column_local)
    parent_local = rotate_by(
        jnp.broadcast_to(lowered[:, None, None, None], parents.shape), -phase_grid
    )
    far_parents = parent_offsets()
    parent_stack = jnp.stack(
        [
            parent_rim[
                :,
                2 + offset[0] : 2 + offset[0] + half_x,
                2 + offset[1] : 2 + offset[1] + half_y,
                2 + offset[2] : 2 + offset[2] + half_z,
            ]
            for offset in far_parents
        ]
    )
    parent_turns = offset_phases(waves, far_parents).reshape(len(far_parents), half_count, 1, 1, 1)
    parent_sum = jnp.sum(jax.vmap(rotate_by)(parent_stack, parent_turns), axis=0)
    parent_local = parent_local + jnp.einsum(
        "kj,jxyz->kxyz", parent_far.astype(jnp.float32), parent_sum, precision=highest
    )
    leaf_local = descend_children(parent_local, child_down.astype(jnp.float32))
    near_leaves = leaf_offsets()
    leaf_stack = jnp.stack(
        [
            leaf_rim[
                :,
                1 + offset[0] : 1 + offset[0] + size_x,
                1 + offset[1] : 1 + offset[1] + size_y,
                1 + offset[2] : 1 + offset[2] + size_z,
            ]
            for offset in near_leaves
        ]
    )
    leaf_stack = leaf_stack * (1.0 - near_flags.astype(jnp.float32))[:, None]
    leaf_turns = offset_phases(waves, near_leaves).reshape(len(near_leaves), half_count, 1, 1, 1)
    leaf_sum = jnp.sum(jax.vmap(rotate_by)(leaf_stack, leaf_turns), axis=0)
    leaf_local = leaf_local + jnp.einsum(
        "kj,jxyz->kxyz", leaf_far.astype(jnp.float32), leaf_sum, precision=highest
    )
    potential, field_parts = evaluate(charged, leaf_local, waves)
    return assemble(near_terms, potential, field_parts, charged[3], live_slots)


def solution(mesh):
    in_specs = (
        P(None, "gx", "gy", None, None),
        P("gx", "gy", None),
        P(None, "gx", "gy", None),
        P(),
        P(),
        P(),
        P(),
        P(),
        P(),
        P(),
        P(),
        P(),
        P(),
    )
    out_specs = P(None, "gx", "gy", None, None)
    return jax.shard_map(body, mesh=mesh, in_specs=in_specs, out_specs=out_specs, check_vma=False)
```

```python
import functools

import jax
import jax.numpy as jnp
from jax import lax
from jax.experimental import pallas as pl
from jax.experimental.pallas import tpu as pltpu
from jax.sharding import PartitionSpec as P

soften = 0.04
coulomb = 0.1
highest = lax.Precision.HIGHEST


def from_partner(value, axis, bit):
    mask = 2**bit
    pairs = [(source, source ^ mask) for source in range(lax.axis_size(axis))]
    return lax.ppermute(value, axis, pairs)


def extended_2(block, sides, width):
    return extended_joint([(block, width)], sides)[0]


def extended_joint(parts, sides):
    blocks = [block for block, width in parts]
    for axis, dim in sides:
        count = lax.axis_size(axis)
        forward = [(i, i + 1) for i in range(count - 1)]
        forward.append((count - 1, 0))
        backward = [(target, source) for source, target in forward]
        lows = [lax.slice_in_dim(b, b.shape[dim] - w, None, axis=dim) for b, (_, w) in zip(blocks, parts)]
        highs = [lax.slice_in_dim(b, 0, w, axis=dim) for b, (_, w) in zip(blocks, parts)]
        sizes = [piece.size for piece in lows]
        low_all = lax.ppermute(jnp.concatenate([piece.reshape(-1) for piece in lows]), axis, forward)
        high_all = lax.ppermute(jnp.concatenate([piece.reshape(-1) for piece in highs]), axis, backward)
        grown = []
        place = 0
        for b, piece, size in zip(blocks, lows, sizes):
            low = low_all[place : place + size].reshape(piece.shape)
            high = high_all[place : place + size].reshape(piece.shape)
            place += size
            grown.append(jnp.concatenate([low, b, high], axis=dim))
        blocks = grown
    return blocks


def wave_table(coef_count, float_type):
    half_count = (coef_count - 1) // 2
    order_index = jnp.arange(1, half_count + 1, dtype=jnp.int32).astype(float_type)
    height = 1.0 - 2.0 * (order_index - 0.5) / half_count
    radius = jnp.sqrt(jnp.maximum(1.0 - height * height, 0.0))
    angle_turn = 2.399963 * order_index
    magnitude = 1.5 + jnp.mod(order_index, 3.0)
    return (
        jnp.stack([radius * jnp.cos(angle_turn), radius * jnp.sin(angle_turn), height])
        * magnitude[None]
    )


def waves_at(atom_data, waves):
    shape_lead = (waves.shape[1],) + (1,) * (atom_data.ndim - 1)
    phases = waves[0].reshape(shape_lead) * (atom_data[0] - 0.5)[None]
    phases = phases + waves[1].reshape(shape_lead) * (atom_data[1] - 0.5)[None]
    phases = phases + waves[2].reshape(shape_lead) * (atom_data[2] - 0.5)[None]
    return (jnp.cos(phases), jnp.sin(phases))


def rotate_by(field, phase):
    half_count = phase.shape[0]
    cosine = jnp.cos(phase)
    sine_part = jnp.sin(phase)
    cos_coef = field[1 : 1 + half_count]
    sin_coef = field[1 + half_count :]
    return jnp.concatenate(
        [
            field[0:1],
            cos_coef * cosine - sin_coef * sine_part,
            cos_coef * sine_part + sin_coef * cosine,
        ],
        axis=0,
    )


def offset_phases(waves, offsets):
    table = jnp.array(offsets, dtype=jnp.float32)
    return (
        table[:, 0:1] * waves[0][None]
        + table[:, 1:2] * waves[1][None]
        + table[:, 2:3] * waves[2][None]
    )


def block_phase(waves, size_x, size_y, size_z, float_type):
    place_x = jnp.arange(size_x, dtype=jnp.int32).astype(float_type)
    place_y = jnp.arange(size_y, dtype=jnp.int32).astype(float_type)
    place_z = jnp.arange(size_z, dtype=jnp.int32).astype(float_type)
    phase = waves[0][:, None, None, None] * place_x[None, :, None, None]
    phase = phase + waves[1][:, None, None, None] * place_y[None, None, :, None]
    return phase + waves[2][:, None, None, None] * place_z[None, None, None, :]


def leaf_moments(atom_data, waves):
    cosine, sine_part = waves_at(atom_data, waves)
    charge = atom_data[3]
    summed = jnp.sum(charge, axis=-1)[None]
    return jnp.concatenate(
        [
            summed,
            jnp.sum(cosine * charge[None], axis=-1),
            jnp.sum(sine_part * charge[None], axis=-1),
        ],
        axis=0,
    )


def evaluate(atom_data, local_exp, waves):
    cosine, sine_part = waves_at(atom_data, waves)
    half_count = waves.shape[1]
    cos_local = local_exp[1 : 1 + half_count][..., None]
    sin_local = local_exp[1 + half_count :][..., None]
    potential = local_exp[0][..., None] + jnp.sum(
        cos_local * cosine + sin_local * sine_part, axis=0
    )
    mixed_term = cos_local * sine_part - sin_local * cosine
    shape_lead = (half_count,) + (1,) * (mixed_term.ndim - 1)
    field_parts = [
        jnp.sum(waves[component].reshape(shape_lead) * mixed_term, axis=0) for component in range(3)
    ]
    return (potential, field_parts)


def near_row(target, source, flag_grid, shift_vec, keep_self):
    weight = source[3] * flag_grid[..., None]
    delta_x = target[0][..., :, None] - (source[0][..., None, :] + shift_vec[0])
    delta_y = target[1][..., :, None] - (source[1][..., None, :] + shift_vec[1])
    delta_z = target[2][..., :, None] - (source[2][..., None, :] + shift_vec[2])
    inverse = lax.rsqrt(delta_x * delta_x + delta_y * delta_y + delta_z * delta_z + soften)
    pair_term = weight[..., None, :] * keep_self * inverse
    cube_term = pair_term * inverse * inverse
    return jnp.stack(
        [
            jnp.sum(pair_term, axis=-1),
            jnp.sum(cube_term * delta_x, axis=-1),
            jnp.sum(cube_term * delta_y, axis=-1),
            jnp.sum(cube_term * delta_z, axis=-1),
        ]
    )


def full_flags(near_flags, float_type):
    flags_float = near_flags.astype(float_type)
    centre = jnp.ones((1,) + flags_float.shape[1:], float_type)
    return jnp.concatenate([flags_float[:13], centre, flags_float[13:]], axis=0)


def leaf_offsets():
    return [
        (shift_x, shift_y, shift_z)
        for shift_x in (-1, 0, 1)
        for shift_y in (-1, 0, 1)
        for shift_z in (-1, 0, 1)
        if (shift_x, shift_y, shift_z) != (0, 0, 0)
    ]


def parent_offsets():
    return [
        (shift_x, shift_y, shift_z)
        for shift_x in range(-2, 3)
        for shift_y in range(-2, 3)
        for shift_z in range(-2, 3)
        if max(abs(shift_x), abs(shift_y), abs(shift_z)) == 2
    ]


def climb_children(moments, matrices):
    coef_count, size_x, size_y, size_z = moments.shape
    parted = moments.reshape(coef_count, size_x // 2, 2, size_y // 2, 2, size_z // 2, 2)
    return jnp.einsum(
        "abckj,jxaybzc->kxyz",
        matrices.reshape(2, 2, 2, coef_count, coef_count),
        parted,
        precision=highest,
    )


def descend_children(parent_local, matrices):
    coef_count, size_x, size_y, size_z = parent_local.shape
    spread = jnp.einsum(
        "abckj,jxyz->kxaybzc",
        matrices.reshape(2, 2, 2, coef_count, coef_count),
        parent_local,
        precision=highest,
    )
    return spread.reshape(coef_count, 2 * size_x, 2 * size_y, 2 * size_z)


def matrix_vector(matrix, vector):
    return jnp.dot(matrix, vector, precision=highest)


def pick_side(matrices, own_side):
    return lax.dynamic_index_in_dim(matrices, own_side, 0, keepdims=False)


def pair_step(matrices, own_side, current, partner):
    return matrix_vector(pick_side(matrices, own_side), current) + matrix_vector(
        pick_side(matrices, 1 - own_side), partner
    )


def chain_tree(column, tree_up, tree_down, tree_side, lattice, hook):
    climbs = tree_up.astype(jnp.float32)
    lowers = tree_down.astype(jnp.float32)
    sideways = tree_side.astype(jnp.float32)
    current = column
    visited = []
    partner = None
    for level_bit in range(lax.axis_size("gx").bit_length() - 1):
        current = hook(current, partner)
        partner = from_partner(current, "gx", level_bit)
        own_side = lax.axis_index("gx") // 2**level_bit % 2
        current = pair_step(climbs[0], own_side, current, partner)
        visited.append((0, own_side, partner))
    for level_bit in range(lax.axis_size("gy").bit_length() - 1):
        current = hook(current, partner)
        partner = from_partner(current, "gy", level_bit)
        own_side = lax.axis_index("gy") // 2**level_bit % 2
        current = pair_step(climbs[1], own_side, current, partner)
        visited.append((1, own_side, partner))
    local_exp = matrix_vector(lattice.astype(jnp.float32), current)
    for axis_num, own_side, partner in reversed(visited):
        local_exp = matrix_vector(pick_side(lowers[axis_num], own_side), local_exp) + matrix_vector(
            pick_side(sideways[axis_num], own_side), partner
        )
    return local_exp


def flip_pair(column_grid, axis_num, level_bit):
    coef_count, size_x, size_y = column_grid.shape
    span_size = 2**level_bit
    if axis_num == 0:
        parted = column_grid.reshape(coef_count, size_x // (2 * span_size), 2, span_size, size_y)
        return parted[:, :, ::-1].reshape(column_grid.shape)
    parted = column_grid.reshape(coef_count, size_x, size_y // (2 * span_size), 2, span_size)
    return parted[:, :, :, ::-1].reshape(column_grid.shape)


def side_grid(axis_num, level_bit, size_x, size_y):
    positions = jnp.arange(size_x if axis_num == 0 else size_y, dtype=jnp.int32)
    own_side = positions // 2**level_bit % 2
    return own_side[:, None] if axis_num == 0 else own_side[None, :]


def choose_side(matrices, own_side, column_grid):
    first = jnp.einsum("kj,jxy->kxy", matrices[0], column_grid, precision=highest)
    second = jnp.einsum("kj,jxy->kxy", matrices[1], column_grid, precision=highest)
    return jnp.where(own_side[None] == 0, first, second)


def gathered_tree(column, tree_up, tree_down, tree_side, lattice):
    size_x, size_y = lax.axis_size("gx"), lax.axis_size("gy")
    gathered = lax.all_gather(column, ("gx", "gy")).reshape(size_x, size_y, -1)
    current = jnp.transpose(gathered, (2, 0, 1))
    levels = [(0, bit) for bit in range(size_x.bit_length() - 1)] + [
        (1, bit) for bit in range(size_y.bit_length() - 1)
    ]
    visited = []
    for axis_num, level_bit in levels:
        partner = flip_pair(current, axis_num, level_bit)
        own_side = side_grid(axis_num, level_bit, size_x, size_y)
        climbs = tree_up[axis_num].astype(jnp.float32)
        current = choose_side(climbs, own_side, current) + choose_side(climbs, 1 - own_side, partner)
        visited.append((axis_num, own_side, partner))
    local_exp = jnp.einsum("kj,jxy->kxy", lattice.astype(jnp.float32), current, precision=highest)
    for axis_num, own_side, partner in reversed(visited):
        local_exp = choose_side(tree_down[axis_num].astype(jnp.float32), own_side, local_exp) + choose_side(
            tree_side[axis_num].astype(jnp.float32), own_side, partner
        )
    own = lax.dynamic_slice(local_exp, (0, lax.axis_index("gx"), lax.axis_index("gy")), (local_exp.shape[0], 1, 1))
    return own.reshape(-1)


def assemble(near_terms, potential, field_parts, charge, live_slots):
    rows = [coulomb * (near_terms[0] + potential) * live_slots]
    for component in range(3):
        rows.append(coulomb * charge * (near_terms[1 + component] + field_parts[component]))
    return jnp.stack(rows)


NEAR_ROWS = 64
NEAR_PIECES = 8
NEAR_UNROLL = 2


def near_pairs(tx, ty, tz, srow, mask):
    weight = srow[3:4, :]
    delta_x = tx - srow[0:1, :]
    delta_y = ty - srow[1:2, :]
    delta_z = tz - srow[2:3, :]
    inverse = lax.rsqrt(delta_x * delta_x + delta_y * delta_y + delta_z * delta_z + soften)
    pair_term = weight * inverse
    if mask is not None:
        pair_term = jnp.where(mask, pair_term, 0.0)
    cube_term = pair_term * inverse * inverse
    return (pair_term, cube_term * delta_x, cube_term * delta_y, cube_term * delta_z)


def near_kernel(first_leaf, leaf_count, listed_width, table_ref, target_ref, source_ref, shift_ref, out_ref, tile_ref):
    piece_leaves = out_ref.shape[0]
    place_start = 2 * leaf_count
    kind_start = place_start + leaf_count * listed_width
    rows = NEAR_ROWS
    lanes = out_ref.shape[2]
    lane = lax.broadcasted_iota(jnp.int32, (rows, lanes), 1)
    row = lax.broadcasted_iota(jnp.int32, (rows, lanes), 0)

    def leaf_body(local, carry):
        leaf = first_leaf + local
        chunk_count = (table_ref[leaf] + rows - 1) // rows
        listed = table_ref[leaf_count + leaf]
        base = leaf * listed_width
        tile_ref[...] = jnp.zeros(tile_ref.shape, tile_ref.dtype)

        def chunk_body(chunk, carry2):
            first = pl.multiple_of(chunk * rows, rows)
            column = target_ref[local, pl.ds(first, rows), :]
            tx = jnp.broadcast_to(column[:, 0:1], (rows, lanes))
            ty = jnp.broadcast_to(column[:, 1:2], (rows, lanes))
            tz = jnp.broadcast_to(column[:, 2:3], (rows, lanes))
            acc = near_pairs(tx, ty, tz, source_ref[table_ref[place_start + base]], row + first != lane)

            def offset_body(step, acc):
                number = base + 1 + NEAR_UNROLL * step
                for extra in range(NEAR_UNROLL):
                    srow = source_ref[table_ref[place_start + number + extra]]
                    srow = srow + shift_ref[table_ref[kind_start + number + extra]]
                    terms = near_pairs(tx, ty, tz, srow, None)
                    acc = tuple(a + b for a, b in zip(acc, terms))
                return acc

            acc = lax.fori_loop(0, (listed - 1) // NEAR_UNROLL, offset_body, acc)
            sums = [jnp.sum(part, axis=1, keepdims=True) for part in acc]
            tile = jnp.where(
                lane == 0, sums[0], jnp.where(lane == 1, sums[1], jnp.where(lane == 2, sums[2], sums[3]))
            )
            tile_ref[pl.ds(first, rows), :] = jnp.where(lane < 4, tile, 0.0)
            return carry2

        lax.fori_loop(0, chunk_count, chunk_body, 0)
        out_ref[local] = jnp.transpose(tile_ref[...])[0 : out_ref.shape[1], :]
        return carry

    lax.fori_loop(0, piece_leaves, leaf_body, 0)


def near_local(charged, rimmed, counts, near_flags):
    size_x, size_y, size_z, slot_count = charged.shape[1:]
    leaf_count = size_x * size_y * size_z
    ext_y = size_y + 2
    target = jnp.transpose(charged, (1, 2, 3, 4, 0)).reshape(leaf_count, slot_count, 4)
    source = jnp.transpose(rimmed, (1, 2, 3, 0, 4)).reshape(-1, 4, slot_count)
    source = jnp.pad(source, ((0, 1), (0, 4), (0, 0)))
    empty_leaf = source.shape[0] - 1
    offsets = [(0, 0, 0)] + leaf_offsets()
    shift_rows = jnp.array([[float(v) for v in offset] + [0.0] * 5 for offset in offsets], jnp.float32)
    shift_table = jnp.broadcast_to(shift_rows[:, :, None], (len(offsets), 8, slot_count))
    leaf_x = jnp.arange(size_x, dtype=jnp.int32)[:, None, None]
    leaf_y = jnp.arange(size_y, dtype=jnp.int32)[None, :, None]
    leaf_z = jnp.arange(size_z, dtype=jnp.int32)[None, None, :]
    places = []
    for offset in offsets:
        place = ((leaf_x + 1 + offset[0]) * ext_y + leaf_y + 1 + offset[1]) * size_z + leaf_z + offset[2]
        places.append(jnp.broadcast_to(place, (size_x, size_y, size_z)))
    places = jnp.stack(places).reshape(len(offsets), leaf_count)
    layer = jnp.arange(size_z, dtype=jnp.int32)
    valid = jnp.stack([((layer + offset[2] >= 0) & (layer + offset[2] < size_z)) for offset in offsets[1:]])
    active = (near_flags != 0) & valid[:, None, None, :]
    active = jnp.concatenate([jnp.ones((1, leaf_count), bool), active.reshape(len(offsets) - 1, leaf_count)])
    listed = jnp.sum(active.astype(jnp.int32), axis=0)
    listed = listed + (NEAR_UNROLL - (listed - 1) % NEAR_UNROLL) % NEAR_UNROLL
    position = jnp.cumsum(active.astype(jnp.int32), axis=0) - 1
    width = 1 + -(-(len(offsets) - 1) // NEAR_UNROLL) * NEAR_UNROLL
    slots = jnp.arange(width, dtype=jnp.int32)
    chosen = active[None] & (position[None] == slots[:, None, None])
    kinds = jnp.arange(len(offsets), dtype=jnp.int32)
    kind_list = jnp.sum(jnp.where(chosen, kinds[None, :, None], 0), axis=1)
    place_list = jnp.sum(jnp.where(chosen, places[None], 0), axis=1)
    place_list = jnp.where(slots[:, None] < jnp.sum(active.astype(jnp.int32), axis=0)[None], place_list, empty_leaf)
    table = jnp.concatenate(
        [counts.reshape(-1), listed, jnp.transpose(place_list).reshape(-1), jnp.transpose(kind_list).reshape(-1)]
    ).astype(jnp.int32)
    piece = leaf_count // NEAR_PIECES if leaf_count % NEAR_PIECES == 0 else leaf_count
    pairs = piece * slot_count * slot_count * 10

    def run_piece(number, gate):
        first_leaf = number * piece
        own = target[first_leaf : first_leaf + piece]
        if gate is not None:
            own, unused = lax.optimization_barrier((own, gate))
        return pl.pallas_call(
            functools.partial(near_kernel, first_leaf, leaf_count, width),
            out_shape=jax.ShapeDtypeStruct((piece, 8, slot_count), jnp.float32),
            in_specs=[pl.BlockSpec(memory_space=pltpu.SMEM)] + [pl.BlockSpec(memory_space=pltpu.VMEM)] * 3,
            out_specs=pl.BlockSpec(memory_space=pltpu.VMEM),
            scratch_shapes=[pltpu.VMEM((slot_count, 128), jnp.float32)],
            cost_estimate=pl.CostEstimate(
                flops=20 * pairs, transcendentals=pairs, bytes_accessed=8 * piece * slot_count * 128
            ),
        )(table, own, source, shift_table)

    def finish_near(outs):
        out = jnp.concatenate(outs, axis=0)
        near = jnp.transpose(out[:, :4, :], (1, 0, 2))
        return near.reshape(4, size_x, size_y, size_z, slot_count)

    return leaf_count // piece, run_piece, finish_near


def body(
    atom_data,
    counts,
    near_flags,
    child_up,
    child_down,
    leaf_far,
    parent_far,
    column_up,
    column_down,
    tree_up,
    tree_down,
    tree_side,
    lattice,
):
    coef_count = lattice.shape[0]
    slot_count = atom_data.shape[4]
    size_x, size_y, size_z = (atom_data.shape[1], atom_data.shape[2], atom_data.shape[3])
    live_slots = (
        jnp.arange(slot_count, dtype=jnp.int32)[None, None, None, :] < counts[..., None]
    ).astype(jnp.float32)
    charged = jnp.concatenate([atom_data[:3], (atom_data[3] * live_slots)[None]], axis=0)
    waves = wave_table(coef_count, jnp.float32)
    half_count = waves.shape[1]
    moments = leaf_moments(charged, waves)
    parents = climb_children(moments, child_up.astype(jnp.float32))
    rimmed, parent_rim, leaf_rim = extended_joint([(charged, 1), (parents, 2), (moments, 1)], (("gx", 1), ("gy", 2)))
    parent_rim = jnp.pad(parent_rim, ((0, 0), (0, 0), (0, 0), (2, 2)))
    half_x, half_y, half_z = (parents.shape[1], parents.shape[2], parents.shape[3])
    phase_grid = block_phase(waves, half_x, half_y, half_z, jnp.float32)
    turned = jnp.sum(rotate_by(parents, phase_grid), axis=(1, 2, 3))
    column = matrix_vector(column_up.astype(jnp.float32), turned)
    piece_count, run_piece, finish_near = near_local(charged, rimmed, counts, near_flags)
    pieces = []

    def hook(value, prior):
        number = len(pieces)
        if number < piece_count:
            if number > 0:
                value, unused = lax.optimization_barrier((value, pieces[-1]))
            pieces.append(run_piece(number, prior))
        return value

    column_local = chain_tree(column, tree_up, tree_down, tree_side, lattice, hook)
    while len(pieces) < piece_count:
        pieces.append(run_piece(len(pieces), None))
    near_terms = finish_near(pieces)
    leaf_rim = jnp.pad(leaf_rim, ((0, 0), (0, 0), (0, 0), (1, 1)))
    lowered = matrix_vector(column_down.astype(jnp.float32), column_local)
    parent_local = rotate_by(
        jnp.broadcast_to(lowered[:, None, None, None], parents.shape), -phase_grid
    )
    far_parents = parent_offsets()
    parent_stack = jnp.stack(
        [
            parent_rim[
                :,
                2 + offset[0] : 2 + offset[0] + half_x,
                2 + offset[1] : 2 + offset[1] + half_y,
                2 + offset[2] : 2 + offset[2] + half_z,
            ]
            for offset in far_parents
        ]
    )
    parent_turns = offset_phases(waves, far_parents).reshape(len(far_parents), half_count, 1, 1, 1)
    parent_sum = jnp.sum(jax.vmap(rotate_by)(parent_stack, parent_turns), axis=0)
    parent_local = parent_local + jnp.einsum(
        "kj,jxyz->kxyz", parent_far.astype(jnp.float32), parent_sum, precision=highest
    )
    leaf_local = descend_children(parent_local, child_down.astype(jnp.float32))
    near_leaves = leaf_offsets()
    leaf_stack = jnp.stack(
        [
            leaf_rim[
                :,
                1 + offset[0] : 1 + offset[0] + size_x,
                1 + offset[1] : 1 + offset[1] + size_y,
                1 + offset[2] : 1 + offset[2] + size_z,
            ]
            for offset in near_leaves
        ]
    )
    leaf_stack = leaf_stack * (1.0 - near_flags.astype(jnp.float32))[:, None]
    leaf_turns = offset_phases(waves, near_leaves).reshape(len(near_leaves), half_count, 1, 1, 1)
    leaf_sum = jnp.sum(jax.vmap(rotate_by)(leaf_stack, leaf_turns), axis=0)
    leaf_local = leaf_local + jnp.einsum(
        "kj,jxyz->kxyz", leaf_far.astype(jnp.float32), leaf_sum, precision=highest
    )
    potential, field_parts = evaluate(charged, leaf_local, waves)
    return assemble(near_terms, potential, field_parts, charged[3], live_slots)


def solution(mesh):
    in_specs = (
        P(None, "gx", "gy", None, None),
        P("gx", "gy", None),
        P(None, "gx", "gy", None),
        P(),
        P(),
        P(),
        P(),
        P(),
        P(),
        P(),
        P(),
        P(),
        P(),
    )
    out_specs = P(None, "gx", "gy", None, None)
    return jax.shard_map(body, mesh=mesh, in_specs=in_specs, out_specs=out_specs, check_vma=False)
```

```python
import functools

import jax
import jax.numpy as jnp
from jax import lax
from jax.experimental import pallas as pl
from jax.experimental.pallas import tpu as pltpu
from jax.sharding import PartitionSpec as P

soften = 0.04
coulomb = 0.1
highest = lax.Precision.HIGHEST


def from_partner(value, axis, bit):
    mask = 2**bit
    pairs = [(source, source ^ mask) for source in range(lax.axis_size(axis))]
    return lax.ppermute(value, axis, pairs)


def extended_2(block, sides, width):
    return extended_joint([(block, width)], sides)[0]


def extended_joint(parts, sides):
    blocks = [block for block, width in parts]
    for axis, dim in sides:
        count = lax.axis_size(axis)
        forward = [(i, i + 1) for i in range(count - 1)]
        forward.append((count - 1, 0))
        backward = [(target, source) for source, target in forward]
        lows = [lax.slice_in_dim(b, b.shape[dim] - w, None, axis=dim) for b, (_, w) in zip(blocks, parts)]
        highs = [lax.slice_in_dim(b, 0, w, axis=dim) for b, (_, w) in zip(blocks, parts)]
        sizes = [piece.size for piece in lows]
        low_all = lax.ppermute(jnp.concatenate([piece.reshape(-1) for piece in lows]), axis, forward)
        high_all = lax.ppermute(jnp.concatenate([piece.reshape(-1) for piece in highs]), axis, backward)
        grown = []
        place = 0
        for b, piece, size in zip(blocks, lows, sizes):
            low = low_all[place : place + size].reshape(piece.shape)
            high = high_all[place : place + size].reshape(piece.shape)
            place += size
            grown.append(jnp.concatenate([low, b, high], axis=dim))
        blocks = grown
    return blocks


def wave_table(coef_count, float_type):
    half_count = (coef_count - 1) // 2
    order_index = jnp.arange(1, half_count + 1, dtype=jnp.int32).astype(float_type)
    height = 1.0 - 2.0 * (order_index - 0.5) / half_count
    radius = jnp.sqrt(jnp.maximum(1.0 - height * height, 0.0))
    angle_turn = 2.399963 * order_index
    magnitude = 1.5 + jnp.mod(order_index, 3.0)
    return (
        jnp.stack([radius * jnp.cos(angle_turn), radius * jnp.sin(angle_turn), height])
        * magnitude[None]
    )


def waves_at(atom_data, waves):
    shape_lead = (waves.shape[1],) + (1,) * (atom_data.ndim - 1)
    phases = waves[0].reshape(shape_lead) * (atom_data[0] - 0.5)[None]
    phases = phases + waves[1].reshape(shape_lead) * (atom_data[1] - 0.5)[None]
    phases = phases + waves[2].reshape(shape_lead) * (atom_data[2] - 0.5)[None]
    return (jnp.cos(phases), jnp.sin(phases))


def rotate_by(field, phase):
    half_count = phase.shape[0]
    cosine = jnp.cos(phase)
    sine_part = jnp.sin(phase)
    cos_coef = field[1 : 1 + half_count]
    sin_coef = field[1 + half_count :]
    return jnp.concatenate(
        [
            field[0:1],
            cos_coef * cosine - sin_coef * sine_part,
            cos_coef * sine_part + sin_coef * cosine,
        ],
        axis=0,
    )


def offset_phases(waves, offsets):
    table = jnp.array(offsets, dtype=jnp.float32)
    return (
        table[:, 0:1] * waves[0][None]
        + table[:, 1:2] * waves[1][None]
        + table[:, 2:3] * waves[2][None]
    )


def block_phase(waves, size_x, size_y, size_z, float_type):
    place_x = jnp.arange(size_x, dtype=jnp.int32).astype(float_type)
    place_y = jnp.arange(size_y, dtype=jnp.int32).astype(float_type)
    place_z = jnp.arange(size_z, dtype=jnp.int32).astype(float_type)
    phase = waves[0][:, None, None, None] * place_x[None, :, None, None]
    phase = phase + waves[1][:, None, None, None] * place_y[None, None, :, None]
    return phase + waves[2][:, None, None, None] * place_z[None, None, None, :]


def leaf_moments(atom_data, waves):
    cosine, sine_part = waves_at(atom_data, waves)
    charge = atom_data[3]
    summed = jnp.sum(charge, axis=-1)[None]
    return jnp.concatenate(
        [
            summed,
            jnp.sum(cosine * charge[None], axis=-1),
            jnp.sum(sine_part * charge[None], axis=-1),
        ],
        axis=0,
    )


def evaluate(atom_data, local_exp, waves):
    cosine, sine_part = waves_at(atom_data, waves)
    half_count = waves.shape[1]
    cos_local = local_exp[1 : 1 + half_count][..., None]
    sin_local = local_exp[1 + half_count :][..., None]
    potential = local_exp[0][..., None] + jnp.sum(
        cos_local * cosine + sin_local * sine_part, axis=0
    )
    mixed_term = cos_local * sine_part - sin_local * cosine
    shape_lead = (half_count,) + (1,) * (mixed_term.ndim - 1)
    field_parts = [
        jnp.sum(waves[component].reshape(shape_lead) * mixed_term, axis=0) for component in range(3)
    ]
    return (potential, field_parts)


def near_row(target, source, flag_grid, shift_vec, keep_self):
    weight = source[3] * flag_grid[..., None]
    delta_x = target[0][..., :, None] - (source[0][..., None, :] + shift_vec[0])
    delta_y = target[1][..., :, None] - (source[1][..., None, :] + shift_vec[1])
    delta_z = target[2][..., :, None] - (source[2][..., None, :] + shift_vec[2])
    inverse = lax.rsqrt(delta_x * delta_x + delta_y * delta_y + delta_z * delta_z + soften)
    pair_term = weight[..., None, :] * keep_self * inverse
    cube_term = pair_term * inverse * inverse
    return jnp.stack(
        [
            jnp.sum(pair_term, axis=-1),
            jnp.sum(cube_term * delta_x, axis=-1),
            jnp.sum(cube_term * delta_y, axis=-1),
            jnp.sum(cube_term * delta_z, axis=-1),
        ]
    )


def full_flags(near_flags, float_type):
    flags_float = near_flags.astype(float_type)
    centre = jnp.ones((1,) + flags_float.shape[1:], float_type)
    return jnp.concatenate([flags_float[:13], centre, flags_float[13:]], axis=0)


def leaf_offsets():
    return [
        (shift_x, shift_y, shift_z)
        for shift_x in (-1, 0, 1)
        for shift_y in (-1, 0, 1)
        for shift_z in (-1, 0, 1)
        if (shift_x, shift_y, shift_z) != (0, 0, 0)
    ]


def parent_offsets():
    return [
        (shift_x, shift_y, shift_z)
        for shift_x in range(-2, 3)
        for shift_y in range(-2, 3)
        for shift_z in range(-2, 3)
        if max(abs(shift_x), abs(shift_y), abs(shift_z)) == 2
    ]


def climb_children(moments, matrices):
    coef_count, size_x, size_y, size_z = moments.shape
    parted = moments.reshape(coef_count, size_x // 2, 2, size_y // 2, 2, size_z // 2, 2)
    return jnp.einsum(
        "abckj,jxaybzc->kxyz",
        matrices.reshape(2, 2, 2, coef_count, coef_count),
        parted,
        precision=highest,
    )


def descend_children(parent_local, matrices):
    coef_count, size_x, size_y, size_z = parent_local.shape
    spread = jnp.einsum(
        "abckj,jxyz->kxaybzc",
        matrices.reshape(2, 2, 2, coef_count, coef_count),
        parent_local,
        precision=highest,
    )
    return spread.reshape(coef_count, 2 * size_x, 2 * size_y, 2 * size_z)


def matrix_vector(matrix, vector):
    return jnp.dot(matrix, vector, precision=highest)


def pick_side(matrices, own_side):
    return lax.dynamic_index_in_dim(matrices, own_side, 0, keepdims=False)


def pair_step(matrices, own_side, current, partner):
    return matrix_vector(pick_side(matrices, own_side), current) + matrix_vector(
        pick_side(matrices, 1 - own_side), partner
    )


def chain_tree(column, tree_up, tree_down, tree_side, lattice, hook):
    climbs = tree_up.astype(jnp.float32)
    lowers = tree_down.astype(jnp.float32)
    sideways = tree_side.astype(jnp.float32)
    current = column
    visited = []
    partner = None
    for level_bit in range(lax.axis_size("gx").bit_length() - 1):
        current = hook(current, partner)
        partner = from_partner(current, "gx", level_bit)
        own_side = lax.axis_index("gx") // 2**level_bit % 2
        current = pair_step(climbs[0], own_side, current, partner)
        visited.append((0, own_side, partner))
    for level_bit in range(lax.axis_size("gy").bit_length() - 1):
        current = hook(current, partner)
        partner = from_partner(current, "gy", level_bit)
        own_side = lax.axis_index("gy") // 2**level_bit % 2
        current = pair_step(climbs[1], own_side, current, partner)
        visited.append((1, own_side, partner))
    local_exp = matrix_vector(lattice.astype(jnp.float32), current)
    for axis_num, own_side, partner in reversed(visited):
        local_exp = matrix_vector(pick_side(lowers[axis_num], own_side), local_exp) + matrix_vector(
            pick_side(sideways[axis_num], own_side), partner
        )
    return local_exp


def flip_pair(column_grid, axis_num, level_bit):
    coef_count, size_x, size_y = column_grid.shape
    span_size = 2**level_bit
    if axis_num == 0:
        parted = column_grid.reshape(coef_count, size_x // (2 * span_size), 2, span_size, size_y)
        return parted[:, :, ::-1].reshape(column_grid.shape)
    parted = column_grid.reshape(coef_count, size_x, size_y // (2 * span_size), 2, span_size)
    return parted[:, :, :, ::-1].reshape(column_grid.shape)


def side_grid(axis_num, level_bit, size_x, size_y):
    positions = jnp.arange(size_x if axis_num == 0 else size_y, dtype=jnp.int32)
    own_side = positions // 2**level_bit % 2
    return own_side[:, None] if axis_num == 0 else own_side[None, :]


def choose_side(matrices, own_side, column_grid):
    first = jnp.einsum("kj,jxy->kxy", matrices[0], column_grid, precision=highest)
    second = jnp.einsum("kj,jxy->kxy", matrices[1], column_grid, precision=highest)
    return jnp.where(own_side[None] == 0, first, second)


def gathered_tree(column, tree_up, tree_down, tree_side, lattice):
    size_x, size_y = lax.axis_size("gx"), lax.axis_size("gy")
    gathered = lax.all_gather(column, ("gx", "gy")).reshape(size_x, size_y, -1)
    current = jnp.transpose(gathered, (2, 0, 1))
    levels = [(0, bit) for bit in range(size_x.bit_length() - 1)] + [
        (1, bit) for bit in range(size_y.bit_length() - 1)
    ]
    visited = []
    for axis_num, level_bit in levels:
        partner = flip_pair(current, axis_num, level_bit)
        own_side = side_grid(axis_num, level_bit, size_x, size_y)
        climbs = tree_up[axis_num].astype(jnp.float32)
        current = choose_side(climbs, own_side, current) + choose_side(climbs, 1 - own_side, partner)
        visited.append((axis_num, own_side, partner))
    local_exp = jnp.einsum("kj,jxy->kxy", lattice.astype(jnp.float32), current, precision=highest)
    for axis_num, own_side, partner in reversed(visited):
        local_exp = choose_side(tree_down[axis_num].astype(jnp.float32), own_side, local_exp) + choose_side(
            tree_side[axis_num].astype(jnp.float32), own_side, partner
        )
    own = lax.dynamic_slice(local_exp, (0, lax.axis_index("gx"), lax.axis_index("gy")), (local_exp.shape[0], 1, 1))
    return own.reshape(-1)


def assemble(near_terms, potential, field_parts, charge, live_slots):
    rows = [coulomb * (near_terms[0] + potential) * live_slots]
    for component in range(3):
        rows.append(coulomb * charge * (near_terms[1 + component] + field_parts[component]))
    return jnp.stack(rows)


NEAR_ROWS = 64
NEAR_PIECES = 8
NEAR_UNROLL = 2


def near_pairs(tx, ty, tz, srow, mask):
    weight = srow[3:4, :]
    delta_x = tx - srow[0:1, :]
    delta_y = ty - srow[1:2, :]
    delta_z = tz - srow[2:3, :]
    inverse = lax.rsqrt(delta_x * delta_x + delta_y * delta_y + delta_z * delta_z + soften)
    pair_term = weight * inverse
    if mask is not None:
        pair_term = jnp.where(mask, pair_term, 0.0)
    cube_term = pair_term * inverse * inverse
    return (pair_term, cube_term * delta_x, cube_term * delta_y, cube_term * delta_z)


def near_kernel(first_leaf, leaf_count, listed_width, table_ref, target_ref, source_ref, shift_ref, out_ref, tile_ref):
    piece_leaves = out_ref.shape[0]
    place_start = 2 * leaf_count
    kind_start = place_start + leaf_count * listed_width
    big = NEAR_ROWS
    small = NEAR_ROWS // 2
    lanes = out_ref.shape[2]

    def leaf_body(local, carry):
        leaf = first_leaf + local
        count = table_ref[leaf]
        full_count = count // big
        rest = count - full_count * big
        listed = table_ref[leaf_count + leaf]
        base = leaf * listed_width
        tile_ref[...] = jnp.zeros(tile_ref.shape, tile_ref.dtype)

        def chunk_at(first, rows):
            lane = lax.broadcasted_iota(jnp.int32, (rows, lanes), 1)
            row = lax.broadcasted_iota(jnp.int32, (rows, lanes), 0)
            column = target_ref[local, pl.ds(first, rows), :]
            tx = jnp.broadcast_to(column[:, 0:1], (rows, lanes))
            ty = jnp.broadcast_to(column[:, 1:2], (rows, lanes))
            tz = jnp.broadcast_to(column[:, 2:3], (rows, lanes))
            acc = near_pairs(tx, ty, tz, source_ref[table_ref[place_start + base]], row + first != lane)

            def offset_body(step, acc):
                number = base + 1 + NEAR_UNROLL * step
                for extra in range(NEAR_UNROLL):
                    srow = source_ref[table_ref[place_start + number + extra]]
                    srow = srow + shift_ref[table_ref[kind_start + number + extra]]
                    terms = near_pairs(tx, ty, tz, srow, None)
                    acc = tuple(a + b for a, b in zip(acc, terms))
                return acc

            acc = lax.fori_loop(0, (listed - 1) // NEAR_UNROLL, offset_body, acc)
            sums = [jnp.sum(part, axis=1, keepdims=True) for part in acc]
            tile = jnp.where(
                lane == 0, sums[0], jnp.where(lane == 1, sums[1], jnp.where(lane == 2, sums[2], sums[3]))
            )
            tile_ref[pl.ds(first, rows), :] = jnp.where(lane < 4, tile, 0.0)

        def full_body(chunk, carry2):
            chunk_at(pl.multiple_of(chunk * big, big), big)
            return carry2

        lax.fori_loop(0, full_count, full_body, 0)
        last = pl.multiple_of(full_count * big, small)

        @pl.when(rest > small)
        def _():
            chunk_at(last, big)

        @pl.when((rest > 0) & (rest <= small))
        def _():
            chunk_at(last, small)

        out_ref[local] = jnp.transpose(tile_ref[...])[0 : out_ref.shape[1], :]
        return carry

    lax.fori_loop(0, piece_leaves, leaf_body, 0)


def near_local(charged, rimmed, counts, near_flags):
    size_x, size_y, size_z, slot_count = charged.shape[1:]
    leaf_count = size_x * size_y * size_z
    ext_y = size_y + 2
    target = jnp.transpose(charged, (1, 2, 3, 4, 0)).reshape(leaf_count, slot_count, 4)
    source = jnp.transpose(rimmed, (1, 2, 3, 0, 4)).reshape(-1, 4, slot_count)
    source = jnp.pad(source, ((0, 1), (0, 4), (0, 0)))
    empty_leaf = source.shape[0] - 1
    offsets = [(0, 0, 0)] + leaf_offsets()
    shift_rows = jnp.array([[float(v) for v in offset] + [0.0] * 5 for offset in offsets], jnp.float32)
    shift_table = jnp.broadcast_to(shift_rows[:, :, None], (len(offsets), 8, slot_count))
    leaf_x = jnp.arange(size_x, dtype=jnp.int32)[:, None, None]
    leaf_y = jnp.arange(size_y, dtype=jnp.int32)[None, :, None]
    leaf_z = jnp.arange(size_z, dtype=jnp.int32)[None, None, :]
    places = []
    for offset in offsets:
        place = ((leaf_x + 1 + offset[0]) * ext_y + leaf_y + 1 + offset[1]) * size_z + leaf_z + offset[2]
        places.append(jnp.broadcast_to(place, (size_x, size_y, size_z)))
    places = jnp.stack(places).reshape(len(offsets), leaf_count)
    layer = jnp.arange(size_z, dtype=jnp.int32)
    valid = jnp.stack([((layer + offset[2] >= 0) & (layer + offset[2] < size_z)) for offset in offsets[1:]])
    active = (near_flags != 0) & valid[:, None, None, :]
    active = jnp.concatenate([jnp.ones((1, leaf_count), bool), active.reshape(len(offsets) - 1, leaf_count)])
    listed = jnp.sum(active.astype(jnp.int32), axis=0)
    listed = listed + (NEAR_UNROLL - (listed - 1) % NEAR_UNROLL) % NEAR_UNROLL
    position = jnp.cumsum(active.astype(jnp.int32), axis=0) - 1
    width = 1 + -(-(len(offsets) - 1) // NEAR_UNROLL) * NEAR_UNROLL
    slots = jnp.arange(width, dtype=jnp.int32)
    chosen = active[None] & (position[None] == slots[:, None, None])
    kinds = jnp.arange(len(offsets), dtype=jnp.int32)
    kind_list = jnp.sum(jnp.where(chosen, kinds[None, :, None], 0), axis=1)
    place_list = jnp.sum(jnp.where(chosen, places[None], 0), axis=1)
    place_list = jnp.where(slots[:, None] < jnp.sum(active.astype(jnp.int32), axis=0)[None], place_list, empty_leaf)
    table = jnp.concatenate(
        [counts.reshape(-1), listed, jnp.transpose(place_list).reshape(-1), jnp.transpose(kind_list).reshape(-1)]
    ).astype(jnp.int32)
    piece = leaf_count // NEAR_PIECES if leaf_count % NEAR_PIECES == 0 else leaf_count
    pairs = piece * slot_count * slot_count * 10

    def run_piece(number, gate):
        first_leaf = number * piece
        own = target[first_leaf : first_leaf + piece]
        if gate is not None:
            own, unused = lax.optimization_barrier((own, gate))
        return pl.pallas_call(
            functools.partial(near_kernel, first_leaf, leaf_count, width),
            out_shape=jax.ShapeDtypeStruct((piece, 8, slot_count), jnp.float32),
            in_specs=[pl.BlockSpec(memory_space=pltpu.SMEM)] + [pl.BlockSpec(memory_space=pltpu.VMEM)] * 3,
            out_specs=pl.BlockSpec(memory_space=pltpu.VMEM),
            scratch_shapes=[pltpu.VMEM((slot_count, 128), jnp.float32)],
            cost_estimate=pl.CostEstimate(
                flops=20 * pairs, transcendentals=pairs, bytes_accessed=8 * piece * slot_count * 128
            ),
        )(table, own, source, shift_table)

    def finish_near(outs):
        out = jnp.concatenate(outs, axis=0)
        near = jnp.transpose(out[:, :4, :], (1, 0, 2))
        return near.reshape(4, size_x, size_y, size_z, slot_count)

    return leaf_count // piece, run_piece, finish_near


def body(
    atom_data,
    counts,
    near_flags,
    child_up,
    child_down,
    leaf_far,
    parent_far,
    column_up,
    column_down,
    tree_up,
    tree_down,
    tree_side,
    lattice,
):
    coef_count = lattice.shape[0]
    slot_count = atom_data.shape[4]
    size_x, size_y, size_z = (atom_data.shape[1], atom_data.shape[2], atom_data.shape[3])
    live_slots = (
        jnp.arange(slot_count, dtype=jnp.int32)[None, None, None, :] < counts[..., None]
    ).astype(jnp.float32)
    charged = jnp.concatenate([atom_data[:3], (atom_data[3] * live_slots)[None]], axis=0)
    waves = wave_table(coef_count, jnp.float32)
    half_count = waves.shape[1]
    moments = leaf_moments(charged, waves)
    parents = climb_children(moments, child_up.astype(jnp.float32))
    rimmed, parent_rim, leaf_rim = extended_joint([(charged, 1), (parents, 2), (moments, 1)], (("gx", 1), ("gy", 2)))
    parent_rim = jnp.pad(parent_rim, ((0, 0), (0, 0), (0, 0), (2, 2)))
    half_x, half_y, half_z = (parents.shape[1], parents.shape[2], parents.shape[3])
    phase_grid = block_phase(waves, half_x, half_y, half_z, jnp.float32)
    turned = jnp.sum(rotate_by(parents, phase_grid), axis=(1, 2, 3))
    column = matrix_vector(column_up.astype(jnp.float32), turned)
    piece_count, run_piece, finish_near = near_local(charged, rimmed, counts, near_flags)
    pieces = []

    def hook(value, prior):
        number = len(pieces)
        if number < piece_count:
            if number > 0:
                value, unused = lax.optimization_barrier((value, pieces[-1]))
            pieces.append(run_piece(number, prior))
        return value

    column_local = chain_tree(column, tree_up, tree_down, tree_side, lattice, hook)
    while len(pieces) < piece_count:
        pieces.append(run_piece(len(pieces), None))
    near_terms = finish_near(pieces)
    leaf_rim = jnp.pad(leaf_rim, ((0, 0), (0, 0), (0, 0), (1, 1)))
    lowered = matrix_vector(column_down.astype(jnp.float32), column_local)
    parent_local = rotate_by(
        jnp.broadcast_to(lowered[:, None, None, None], parents.shape), -phase_grid
    )
    far_parents = parent_offsets()
    parent_stack = jnp.stack(
        [
            parent_rim[
                :,
                2 + offset[0] : 2 + offset[0] + half_x,
                2 + offset[1] : 2 + offset[1] + half_y,
                2 + offset[2] : 2 + offset[2] + half_z,
            ]
            for offset in far_parents
        ]
    )
    parent_turns = offset_phases(waves, far_parents).reshape(len(far_parents), half_count, 1, 1, 1)
    parent_sum = jnp.sum(jax.vmap(rotate_by)(parent_stack, parent_turns), axis=0)
    parent_local = parent_local + jnp.einsum(
        "kj,jxyz->kxyz", parent_far.astype(jnp.float32), parent_sum, precision=highest
    )
    leaf_local = descend_children(parent_local, child_down.astype(jnp.float32))
    near_leaves = leaf_offsets()
    leaf_stack = jnp.stack(
        [
            leaf_rim[
                :,
                1 + offset[0] : 1 + offset[0] + size_x,
                1 + offset[1] : 1 + offset[1] + size_y,
                1 + offset[2] : 1 + offset[2] + size_z,
            ]
            for offset in near_leaves
        ]
    )
    leaf_stack = leaf_stack * (1.0 - near_flags.astype(jnp.float32))[:, None]
    leaf_turns = offset_phases(waves, near_leaves).reshape(len(near_leaves), half_count, 1, 1, 1)
    leaf_sum = jnp.sum(jax.vmap(rotate_by)(leaf_stack, leaf_turns), axis=0)
    leaf_local = leaf_local + jnp.einsum(
        "kj,jxyz->kxyz", leaf_far.astype(jnp.float32), leaf_sum, precision=highest
    )
    potential, field_parts = evaluate(charged, leaf_local, waves)
    return assemble(near_terms, potential, field_parts, charged[3], live_slots)


def solution(mesh):
    in_specs = (
        P(None, "gx", "gy", None, None),
        P("gx", "gy", None),
        P(None, "gx", "gy", None),
        P(),
        P(),
        P(),
        P(),
        P(),
        P(),
        P(),
        P(),
        P(),
        P(),
    )
    out_specs = P(None, "gx", "gy", None, None)
    return jax.shard_map(body, mesh=mesh, in_specs=in_specs, out_specs=out_specs, check_vma=False)
```

```python
import functools

import jax
import jax.numpy as jnp
from jax import lax
from jax.experimental import pallas as pl
from jax.experimental.pallas import tpu as pltpu
from jax.sharding import PartitionSpec as P

soften = 0.04
coulomb = 0.1
highest = lax.Precision.HIGHEST


def from_partner(value, axis, bit):
    mask = 2**bit
    pairs = [(source, source ^ mask) for source in range(lax.axis_size(axis))]
    return lax.ppermute(value, axis, pairs)


def extended_2(block, sides, width):
    return extended_joint([(block, width)], sides)[0]


def extended_joint(parts, sides):
    blocks = [block for block, width in parts]
    for axis, dim in sides:
        count = lax.axis_size(axis)
        forward = [(i, i + 1) for i in range(count - 1)]
        forward.append((count - 1, 0))
        backward = [(target, source) for source, target in forward]
        lows = [lax.slice_in_dim(b, b.shape[dim] - w, None, axis=dim) for b, (_, w) in zip(blocks, parts)]
        highs = [lax.slice_in_dim(b, 0, w, axis=dim) for b, (_, w) in zip(blocks, parts)]
        sizes = [piece.size for piece in lows]
        low_all = lax.ppermute(jnp.concatenate([piece.reshape(-1) for piece in lows]), axis, forward)
        high_all = lax.ppermute(jnp.concatenate([piece.reshape(-1) for piece in highs]), axis, backward)
        grown = []
        place = 0
        for b, piece, size in zip(blocks, lows, sizes):
            low = low_all[place : place + size].reshape(piece.shape)
            high = high_all[place : place + size].reshape(piece.shape)
            place += size
            grown.append(jnp.concatenate([low, b, high], axis=dim))
        blocks = grown
    return blocks


def extended_once(parts):
    count_x, count_y = lax.axis_size("gx"), lax.axis_size("gy")
    received = {}
    for step_x in (-1, 0, 1):
        for step_y in (-1, 0, 1):
            if (step_x, step_y) == (0, 0):
                continue
            sends = []
            for block, width in parts:
                size_x, size_y = block.shape[1], block.shape[2]
                range_x = (size_x - width, size_x) if step_x < 0 else (0, width) if step_x > 0 else (0, size_x)
                range_y = (size_y - width, size_y) if step_y < 0 else (0, width) if step_y > 0 else (0, size_y)
                sends.append(block[:, range_x[0] : range_x[1], range_y[0] : range_y[1]])
            flat = jnp.concatenate([piece.reshape(-1) for piece in sends])
            if step_y == 0:
                pairs = [(i, (i - step_x) % count_x) for i in range(count_x)]
                flat = lax.ppermute(flat, "gx", pairs)
            elif step_x == 0:
                pairs = [(j, (j - step_y) % count_y) for j in range(count_y)]
                flat = lax.ppermute(flat, "gy", pairs)
            else:
                pairs = [
                    (i * count_y + j, ((i - step_x) % count_x) * count_y + (j - step_y) % count_y)
                    for i in range(count_x)
                    for j in range(count_y)
                ]
                flat = lax.ppermute(flat, ("gx", "gy"), pairs)
            place = 0
            pieces = []
            for piece in sends:
                pieces.append(flat[place : place + piece.size].reshape(piece.shape))
                place += piece.size
            received[(step_x, step_y)] = pieces
    grown = []
    for number, (block, width) in enumerate(parts):
        bands = []
        for step_x in (-1, 0, 1):
            row = [block if (step_x, step_y) == (0, 0) else received[(step_x, step_y)][number] for step_y in (-1, 0, 1)]
            bands.append(jnp.concatenate(row, axis=2))
        grown.append(jnp.concatenate(bands, axis=1))
    return grown


def wave_table(coef_count, float_type):
    half_count = (coef_count - 1) // 2
    order_index = jnp.arange(1, half_count + 1, dtype=jnp.int32).astype(float_type)
    height = 1.0 - 2.0 * (order_index - 0.5) / half_count
    radius = jnp.sqrt(jnp.maximum(1.0 - height * height, 0.0))
    angle_turn = 2.399963 * order_index
    magnitude = 1.5 + jnp.mod(order_index, 3.0)
    return (
        jnp.stack([radius * jnp.cos(angle_turn), radius * jnp.sin(angle_turn), height])
        * magnitude[None]
    )


def waves_at(atom_data, waves):
    shape_lead = (waves.shape[1],) + (1,) * (atom_data.ndim - 1)
    phases = waves[0].reshape(shape_lead) * (atom_data[0] - 0.5)[None]
    phases = phases + waves[1].reshape(shape_lead) * (atom_data[1] - 0.5)[None]
    phases = phases + waves[2].reshape(shape_lead) * (atom_data[2] - 0.5)[None]
    return (jnp.cos(phases), jnp.sin(phases))


def rotate_by(field, phase):
    half_count = phase.shape[0]
    cosine = jnp.cos(phase)
    sine_part = jnp.sin(phase)
    cos_coef = field[1 : 1 + half_count]
    sin_coef = field[1 + half_count :]
    return jnp.concatenate(
        [
            field[0:1],
            cos_coef * cosine - sin_coef * sine_part,
            cos_coef * sine_part + sin_coef * cosine,
        ],
        axis=0,
    )


def offset_phases(waves, offsets):
    table = jnp.array(offsets, dtype=jnp.float32)
    return (
        table[:, 0:1] * waves[0][None]
        + table[:, 1:2] * waves[1][None]
        + table[:, 2:3] * waves[2][None]
    )


def block_phase(waves, size_x, size_y, size_z, float_type):
    place_x = jnp.arange(size_x, dtype=jnp.int32).astype(float_type)
    place_y = jnp.arange(size_y, dtype=jnp.int32).astype(float_type)
    place_z = jnp.arange(size_z, dtype=jnp.int32).astype(float_type)
    phase = waves[0][:, None, None, None] * place_x[None, :, None, None]
    phase = phase + waves[1][:, None, None, None] * place_y[None, None, :, None]
    return phase + waves[2][:, None, None, None] * place_z[None, None, None, :]


def leaf_moments(atom_data, waves):
    cosine, sine_part = waves_at(atom_data, waves)
    charge = atom_data[3]
    summed = jnp.sum(charge, axis=-1)[None]
    return jnp.concatenate(
        [
            summed,
            jnp.sum(cosine * charge[None], axis=-1),
            jnp.sum(sine_part * charge[None], axis=-1),
        ],
        axis=0,
    )


def evaluate(atom_data, local_exp, waves):
    cosine, sine_part = waves_at(atom_data, waves)
    half_count = waves.shape[1]
    cos_local = local_exp[1 : 1 + half_count][..., None]
    sin_local = local_exp[1 + half_count :][..., None]
    potential = local_exp[0][..., None] + jnp.sum(
        cos_local * cosine + sin_local * sine_part, axis=0
    )
    mixed_term = cos_local * sine_part - sin_local * cosine
    shape_lead = (half_count,) + (1,) * (mixed_term.ndim - 1)
    field_parts = [
        jnp.sum(waves[component].reshape(shape_lead) * mixed_term, axis=0) for component in range(3)
    ]
    return (potential, field_parts)


def near_row(target, source, flag_grid, shift_vec, keep_self):
    weight = source[3] * flag_grid[..., None]
    delta_x = target[0][..., :, None] - (source[0][..., None, :] + shift_vec[0])
    delta_y = target[1][..., :, None] - (source[1][..., None, :] + shift_vec[1])
    delta_z = target[2][..., :, None] - (source[2][..., None, :] + shift_vec[2])
    inverse = lax.rsqrt(delta_x * delta_x + delta_y * delta_y + delta_z * delta_z + soften)
    pair_term = weight[..., None, :] * keep_self * inverse
    cube_term = pair_term * inverse * inverse
    return jnp.stack(
        [
            jnp.sum(pair_term, axis=-1),
            jnp.sum(cube_term * delta_x, axis=-1),
            jnp.sum(cube_term * delta_y, axis=-1),
            jnp.sum(cube_term * delta_z, axis=-1),
        ]
    )


def full_flags(near_flags, float_type):
    flags_float = near_flags.astype(float_type)
    centre = jnp.ones((1,) + flags_float.shape[1:], float_type)
    return jnp.concatenate([flags_float[:13], centre, flags_float[13:]], axis=0)


def leaf_offsets():
    return [
        (shift_x, shift_y, shift_z)
        for shift_x in (-1, 0, 1)
        for shift_y in (-1, 0, 1)
        for shift_z in (-1, 0, 1)
        if (shift_x, shift_y, shift_z) != (0, 0, 0)
    ]


def parent_offsets():
    return [
        (shift_x, shift_y, shift_z)
        for shift_x in range(-2, 3)
        for shift_y in range(-2, 3)
        for shift_z in range(-2, 3)
        if max(abs(shift_x), abs(shift_y), abs(shift_z)) == 2
    ]


def climb_children(moments, matrices):
    coef_count, size_x, size_y, size_z = moments.shape
    parted = moments.reshape(coef_count, size_x // 2, 2, size_y // 2, 2, size_z // 2, 2)
    return jnp.einsum(
        "abckj,jxaybzc->kxyz",
        matrices.reshape(2, 2, 2, coef_count, coef_count),
        parted,
        precision=highest,
    )


def descend_children(parent_local, matrices):
    coef_count, size_x, size_y, size_z = parent_local.shape
    spread = jnp.einsum(
        "abckj,jxyz->kxaybzc",
        matrices.reshape(2, 2, 2, coef_count, coef_count),
        parent_local,
        precision=highest,
    )
    return spread.reshape(coef_count, 2 * size_x, 2 * size_y, 2 * size_z)


def matrix_vector(matrix, vector):
    return jnp.dot(matrix, vector, precision=highest)


def pick_side(matrices, own_side):
    return lax.dynamic_index_in_dim(matrices, own_side, 0, keepdims=False)


def pair_step(matrices, own_side, current, partner):
    return matrix_vector(pick_side(matrices, own_side), current) + matrix_vector(
        pick_side(matrices, 1 - own_side), partner
    )


def chain_tree(column, tree_up, tree_down, tree_side, lattice, hook):
    climbs = tree_up.astype(jnp.float32)
    lowers = tree_down.astype(jnp.float32)
    sideways = tree_side.astype(jnp.float32)
    current = column
    visited = []
    partner = None
    for level_bit in range(lax.axis_size("gx").bit_length() - 1):
        current = hook(current, partner)
        partner = from_partner(current, "gx", level_bit)
        own_side = lax.axis_index("gx") // 2**level_bit % 2
        current = pair_step(climbs[0], own_side, current, partner)
        visited.append((0, own_side, partner))
    for level_bit in range(lax.axis_size("gy").bit_length() - 1):
        current = hook(current, partner)
        partner = from_partner(current, "gy", level_bit)
        own_side = lax.axis_index("gy") // 2**level_bit % 2
        current = pair_step(climbs[1], own_side, current, partner)
        visited.append((1, own_side, partner))
    local_exp = matrix_vector(lattice.astype(jnp.float32), current)
    for axis_num, own_side, partner in reversed(visited):
        local_exp = matrix_vector(pick_side(lowers[axis_num], own_side), local_exp) + matrix_vector(
            pick_side(sideways[axis_num], own_side), partner
        )
    return local_exp


def flip_pair(column_grid, axis_num, level_bit):
    coef_count, size_x, size_y = column_grid.shape
    span_size = 2**level_bit
    if axis_num == 0:
        parted = column_grid.reshape(coef_count, size_x // (2 * span_size), 2, span_size, size_y)
        return parted[:, :, ::-1].reshape(column_grid.shape)
    parted = column_grid.reshape(coef_count, size_x, size_y // (2 * span_size), 2, span_size)
    return parted[:, :, :, ::-1].reshape(column_grid.shape)


def side_grid(axis_num, level_bit, size_x, size_y):
    positions = jnp.arange(size_x if axis_num == 0 else size_y, dtype=jnp.int32)
    own_side = positions // 2**level_bit % 2
    return own_side[:, None] if axis_num == 0 else own_side[None, :]


def choose_side(matrices, own_side, column_grid):
    first = jnp.einsum("kj,jxy->kxy", matrices[0], column_grid, precision=highest)
    second = jnp.einsum("kj,jxy->kxy", matrices[1], column_grid, precision=highest)
    return jnp.where(own_side[None] == 0, first, second)


def gathered_tree(column, tree_up, tree_down, tree_side, lattice):
    size_x, size_y = lax.axis_size("gx"), lax.axis_size("gy")
    gathered = lax.all_gather(column, ("gx", "gy")).reshape(size_x, size_y, -1)
    current = jnp.transpose(gathered, (2, 0, 1))
    levels = [(0, bit) for bit in range(size_x.bit_length() - 1)] + [
        (1, bit) for bit in range(size_y.bit_length() - 1)
    ]
    visited = []
    for axis_num, level_bit in levels:
        partner = flip_pair(current, axis_num, level_bit)
        own_side = side_grid(axis_num, level_bit, size_x, size_y)
        climbs = tree_up[axis_num].astype(jnp.float32)
        current = choose_side(climbs, own_side, current) + choose_side(climbs, 1 - own_side, partner)
        visited.append((axis_num, own_side, partner))
    local_exp = jnp.einsum("kj,jxy->kxy", lattice.astype(jnp.float32), current, precision=highest)
    for axis_num, own_side, partner in reversed(visited):
        local_exp = choose_side(tree_down[axis_num].astype(jnp.float32), own_side, local_exp) + choose_side(
            tree_side[axis_num].astype(jnp.float32), own_side, partner
        )
    own = lax.dynamic_slice(local_exp, (0, lax.axis_index("gx"), lax.axis_index("gy")), (local_exp.shape[0], 1, 1))
    return own.reshape(-1)


def assemble(near_terms, potential, field_parts, charge, live_slots):
    rows = [coulomb * (near_terms[0] + potential) * live_slots]
    for component in range(3):
        rows.append(coulomb * charge * (near_terms[1 + component] + field_parts[component]))
    return jnp.stack(rows)


NEAR_ROWS = 64
NEAR_PIECES = 8
NEAR_UNROLL = 2


def near_pairs(tx, ty, tz, srow, mask):
    weight = srow[3:4, :]
    delta_x = tx - srow[0:1, :]
    delta_y = ty - srow[1:2, :]
    delta_z = tz - srow[2:3, :]
    inverse = lax.rsqrt(delta_x * delta_x + delta_y * delta_y + delta_z * delta_z + soften)
    pair_term = weight * inverse
    if mask is not None:
        pair_term = jnp.where(mask, pair_term, 0.0)
    cube_term = pair_term * inverse * inverse
    return (pair_term, cube_term * delta_x, cube_term * delta_y, cube_term * delta_z)


def near_kernel(first_leaf, leaf_count, listed_width, table_ref, target_ref, source_ref, shift_ref, out_ref, tile_ref):
    piece_leaves = out_ref.shape[0]
    place_start = 2 * leaf_count
    kind_start = place_start + leaf_count * listed_width
    big = NEAR_ROWS
    small = NEAR_ROWS // 2
    lanes = out_ref.shape[2]

    def leaf_body(local, carry):
        leaf = first_leaf + local
        count = table_ref[leaf]
        full_count = count // big
        rest = count - full_count * big
        listed = table_ref[leaf_count + leaf]
        base = leaf * listed_width
        tile_ref[...] = jnp.zeros(tile_ref.shape, tile_ref.dtype)

        def chunk_at(first, rows):
            lane = lax.broadcasted_iota(jnp.int32, (rows, lanes), 1)
            row = lax.broadcasted_iota(jnp.int32, (rows, lanes), 0)
            column = target_ref[local, pl.ds(first, rows), :]
            tx = jnp.broadcast_to(column[:, 0:1], (rows, lanes))
            ty = jnp.broadcast_to(column[:, 1:2], (rows, lanes))
            tz = jnp.broadcast_to(column[:, 2:3], (rows, lanes))
            acc = near_pairs(tx, ty, tz, source_ref[table_ref[place_start + base]], row + first != lane)

            def offset_body(step, acc):
                number = base + 1 + NEAR_UNROLL * step
                for extra in range(NEAR_UNROLL):
                    srow = source_ref[table_ref[place_start + number + extra]]
                    srow = srow + shift_ref[table_ref[kind_start + number + extra]]
                    terms = near_pairs(tx, ty, tz, srow, None)
                    acc = tuple(a + b for a, b in zip(acc, terms))
                return acc

            acc = lax.fori_loop(0, (listed - 1) // NEAR_UNROLL, offset_body, acc)
            sums = [jnp.sum(part, axis=1, keepdims=True) for part in acc]
            tile = jnp.where(
                lane == 0, sums[0], jnp.where(lane == 1, sums[1], jnp.where(lane == 2, sums[2], sums[3]))
            )
            tile_ref[pl.ds(first, rows), :] = jnp.where(lane < 4, tile, 0.0)

        def full_body(chunk, carry2):
            chunk_at(pl.multiple_of(chunk * big, big), big)
            return carry2

        lax.fori_loop(0, full_count, full_body, 0)
        last = pl.multiple_of(full_count * big, small)

        @pl.when(rest > small)
        def _():
            chunk_at(last, big)

        @pl.when((rest > 0) & (rest <= small))
        def _():
            chunk_at(last, small)

        out_ref[local] = jnp.transpose(tile_ref[...])[0 : out_ref.shape[1], :]
        return carry

    lax.fori_loop(0, piece_leaves, leaf_body, 0)


def near_local(charged, rimmed, counts, near_flags):
    size_x, size_y, size_z, slot_count = charged.shape[1:]
    leaf_count = size_x * size_y * size_z
    ext_y = size_y + 2
    target = jnp.transpose(charged, (1, 2, 3, 4, 0)).reshape(leaf_count, slot_count, 4)
    source = jnp.transpose(rimmed, (1, 2, 3, 0, 4)).reshape(-1, 4, slot_count)
    source = jnp.pad(source, ((0, 1), (0, 4), (0, 0)))
    empty_leaf = source.shape[0] - 1
    offsets = [(0, 0, 0)] + leaf_offsets()
    shift_rows = jnp.array([[float(v) for v in offset] + [0.0] * 5 for offset in offsets], jnp.float32)
    shift_table = jnp.broadcast_to(shift_rows[:, :, None], (len(offsets), 8, slot_count))
    leaf_x = jnp.arange(size_x, dtype=jnp.int32)[:, None, None]
    leaf_y = jnp.arange(size_y, dtype=jnp.int32)[None, :, None]
    leaf_z = jnp.arange(size_z, dtype=jnp.int32)[None, None, :]
    places = []
    for offset in offsets:
        place = ((leaf_x + 1 + offset[0]) * ext_y + leaf_y + 1 + offset[1]) * size_z + leaf_z + offset[2]
        places.append(jnp.broadcast_to(place, (size_x, size_y, size_z)))
    places = jnp.stack(places).reshape(len(offsets), leaf_count)
    layer = jnp.arange(size_z, dtype=jnp.int32)
    valid = jnp.stack([((layer + offset[2] >= 0) & (layer + offset[2] < size_z)) for offset in offsets[1:]])
    active = (near_flags != 0) & valid[:, None, None, :]
    active = jnp.concatenate([jnp.ones((1, leaf_count), bool), active.reshape(len(offsets) - 1, leaf_count)])
    listed = jnp.sum(active.astype(jnp.int32), axis=0)
    listed = listed + (NEAR_UNROLL - (listed - 1) % NEAR_UNROLL) % NEAR_UNROLL
    position = jnp.cumsum(active.astype(jnp.int32), axis=0) - 1
    width = 1 + -(-(len(offsets) - 1) // NEAR_UNROLL) * NEAR_UNROLL
    slots = jnp.arange(width, dtype=jnp.int32)
    chosen = active[None] & (position[None] == slots[:, None, None])
    kinds = jnp.arange(len(offsets), dtype=jnp.int32)
    kind_list = jnp.sum(jnp.where(chosen, kinds[None, :, None], 0), axis=1)
    place_list = jnp.sum(jnp.where(chosen, places[None], 0), axis=1)
    place_list = jnp.where(slots[:, None] < jnp.sum(active.astype(jnp.int32), axis=0)[None], place_list, empty_leaf)
    table = jnp.concatenate(
        [counts.reshape(-1), listed, jnp.transpose(place_list).reshape(-1), jnp.transpose(kind_list).reshape(-1)]
    ).astype(jnp.int32)
    piece = leaf_count // NEAR_PIECES if leaf_count % NEAR_PIECES == 0 else leaf_count
    pairs = piece * slot_count * slot_count * 10

    def run_piece(number, gate):
        first_leaf = number * piece
        own = target[first_leaf : first_leaf + piece]
        if gate is not None:
            own, unused = lax.optimization_barrier((own, gate))
        return pl.pallas_call(
            functools.partial(near_kernel, first_leaf, leaf_count, width),
            out_shape=jax.ShapeDtypeStruct((piece, 8, slot_count), jnp.float32),
            in_specs=[pl.BlockSpec(memory_space=pltpu.SMEM)] + [pl.BlockSpec(memory_space=pltpu.VMEM)] * 3,
            out_specs=pl.BlockSpec(memory_space=pltpu.VMEM),
            scratch_shapes=[pltpu.VMEM((slot_count, 128), jnp.float32)],
            cost_estimate=pl.CostEstimate(
                flops=20 * pairs, transcendentals=pairs, bytes_accessed=8 * piece * slot_count * 128
            ),
        )(table, own, source, shift_table)

    def finish_near(outs):
        out = jnp.concatenate(outs, axis=0)
        near = jnp.transpose(out[:, :4, :], (1, 0, 2))
        return near.reshape(4, size_x, size_y, size_z, slot_count)

    return leaf_count // piece, run_piece, finish_near


def body(
    atom_data,
    counts,
    near_flags,
    child_up,
    child_down,
    leaf_far,
    parent_far,
    column_up,
    column_down,
    tree_up,
    tree_down,
    tree_side,
    lattice,
):
    coef_count = lattice.shape[0]
    slot_count = atom_data.shape[4]
    size_x, size_y, size_z = (atom_data.shape[1], atom_data.shape[2], atom_data.shape[3])
    live_slots = (
        jnp.arange(slot_count, dtype=jnp.int32)[None, None, None, :] < counts[..., None]
    ).astype(jnp.float32)
    charged = jnp.concatenate([atom_data[:3], (atom_data[3] * live_slots)[None]], axis=0)
    waves = wave_table(coef_count, jnp.float32)
    half_count = waves.shape[1]
    moments = leaf_moments(charged, waves)
    parents = climb_children(moments, child_up.astype(jnp.float32))
    rimmed, parent_rim, leaf_rim = extended_once([(charged, 1), (parents, 2), (moments, 1)])
    parent_rim = jnp.pad(parent_rim, ((0, 0), (0, 0), (0, 0), (2, 2)))
    half_x, half_y, half_z = (parents.shape[1], parents.shape[2], parents.shape[3])
    phase_grid = block_phase(waves, half_x, half_y, half_z, jnp.float32)
    turned = jnp.sum(rotate_by(parents, phase_grid), axis=(1, 2, 3))
    column = matrix_vector(column_up.astype(jnp.float32), turned)
    piece_count, run_piece, finish_near = near_local(charged, rimmed, counts, near_flags)
    pieces = []

    def hook(value, prior):
        number = len(pieces)
        if number < piece_count:
            if number > 0:
                value, unused = lax.optimization_barrier((value, pieces[-1]))
            pieces.append(run_piece(number, prior))
        return value

    column_local = chain_tree(column, tree_up, tree_down, tree_side, lattice, hook)
    while len(pieces) < piece_count:
        pieces.append(run_piece(len(pieces), None))
    near_terms = finish_near(pieces)
    leaf_rim = jnp.pad(leaf_rim, ((0, 0), (0, 0), (0, 0), (1, 1)))
    lowered = matrix_vector(column_down.astype(jnp.float32), column_local)
    parent_local = rotate_by(
        jnp.broadcast_to(lowered[:, None, None, None], parents.shape), -phase_grid
    )
    far_parents = parent_offsets()
    parent_stack = jnp.stack(
        [
            parent_rim[
                :,
                2 + offset[0] : 2 + offset[0] + half_x,
                2 + offset[1] : 2 + offset[1] + half_y,
                2 + offset[2] : 2 + offset[2] + half_z,
            ]
            for offset in far_parents
        ]
    )
    parent_turns = offset_phases(waves, far_parents).reshape(len(far_parents), half_count, 1, 1, 1)
    parent_sum = jnp.sum(jax.vmap(rotate_by)(parent_stack, parent_turns), axis=0)
    parent_local = parent_local + jnp.einsum(
        "kj,jxyz->kxyz", parent_far.astype(jnp.float32), parent_sum, precision=highest
    )
    leaf_local = descend_children(parent_local, child_down.astype(jnp.float32))
    near_leaves = leaf_offsets()
    leaf_stack = jnp.stack(
        [
            leaf_rim[
                :,
                1 + offset[0] : 1 + offset[0] + size_x,
                1 + offset[1] : 1 + offset[1] + size_y,
                1 + offset[2] : 1 + offset[2] + size_z,
            ]
            for offset in near_leaves
        ]
    )
    leaf_stack = leaf_stack * (1.0 - near_flags.astype(jnp.float32))[:, None]
    leaf_turns = offset_phases(waves, near_leaves).reshape(len(near_leaves), half_count, 1, 1, 1)
    leaf_sum = jnp.sum(jax.vmap(rotate_by)(leaf_stack, leaf_turns), axis=0)
    leaf_local = leaf_local + jnp.einsum(
        "kj,jxyz->kxyz", leaf_far.astype(jnp.float32), leaf_sum, precision=highest
    )
    potential, field_parts = evaluate(charged, leaf_local, waves)
    return assemble(near_terms, potential, field_parts, charged[3], live_slots)


def solution(mesh):
    in_specs = (
        P(None, "gx", "gy", None, None),
        P("gx", "gy", None),
        P(None, "gx", "gy", None),
        P(),
        P(),
        P(),
        P(),
        P(),
        P(),
        P(),
        P(),
        P(),
        P(),
    )
    out_specs = P(None, "gx", "gy", None, None)
    return jax.shard_map(body, mesh=mesh, in_specs=in_specs, out_specs=out_specs, check_vma=False)
```

```python
import functools

import jax
import numpy as np
import jax.numpy as jnp
from jax import lax
from jax.experimental import pallas as pl
from jax.experimental.pallas import tpu as pltpu
from jax.sharding import PartitionSpec as P

soften = 0.04
coulomb = 0.1
highest = lax.Precision.HIGHEST


def from_partner(value, axis, bit):
    mask = 2**bit
    pairs = [(source, source ^ mask) for source in range(lax.axis_size(axis))]
    return lax.ppermute(value, axis, pairs)


def extended_2(block, sides, width):
    return extended_joint([(block, width)], sides)[0]


def extended_joint(parts, sides):
    blocks = [block for block, width in parts]
    for axis, dim in sides:
        count = lax.axis_size(axis)
        forward = [(i, i + 1) for i in range(count - 1)]
        forward.append((count - 1, 0))
        backward = [(target, source) for source, target in forward]
        lows = [lax.slice_in_dim(b, b.shape[dim] - w, None, axis=dim) for b, (_, w) in zip(blocks, parts)]
        highs = [lax.slice_in_dim(b, 0, w, axis=dim) for b, (_, w) in zip(blocks, parts)]
        sizes = [piece.size for piece in lows]
        low_all = lax.ppermute(jnp.concatenate([piece.reshape(-1) for piece in lows]), axis, forward)
        high_all = lax.ppermute(jnp.concatenate([piece.reshape(-1) for piece in highs]), axis, backward)
        grown = []
        place = 0
        for b, piece, size in zip(blocks, lows, sizes):
            low = low_all[place : place + size].reshape(piece.shape)
            high = high_all[place : place + size].reshape(piece.shape)
            place += size
            grown.append(jnp.concatenate([low, b, high], axis=dim))
        blocks = grown
    return blocks


def wave_table(coef_count, float_type):
    half_count = (coef_count - 1) // 2
    order_index = jnp.arange(1, half_count + 1, dtype=jnp.int32).astype(float_type)
    height = 1.0 - 2.0 * (order_index - 0.5) / half_count
    radius = jnp.sqrt(jnp.maximum(1.0 - height * height, 0.0))
    angle_turn = 2.399963 * order_index
    magnitude = 1.5 + jnp.mod(order_index, 3.0)
    return (
        jnp.stack([radius * jnp.cos(angle_turn), radius * jnp.sin(angle_turn), height])
        * magnitude[None]
    )


def waves_at(atom_data, waves):
    shape_lead = (waves.shape[1],) + (1,) * (atom_data.ndim - 1)
    phases = waves[0].reshape(shape_lead) * (atom_data[0] - 0.5)[None]
    phases = phases + waves[1].reshape(shape_lead) * (atom_data[1] - 0.5)[None]
    phases = phases + waves[2].reshape(shape_lead) * (atom_data[2] - 0.5)[None]
    return (jnp.cos(phases), jnp.sin(phases))


def rotate_by(field, phase):
    half_count = phase.shape[0]
    cosine = jnp.cos(phase)
    sine_part = jnp.sin(phase)
    cos_coef = field[1 : 1 + half_count]
    sin_coef = field[1 + half_count :]
    return jnp.concatenate(
        [
            field[0:1],
            cos_coef * cosine - sin_coef * sine_part,
            cos_coef * sine_part + sin_coef * cosine,
        ],
        axis=0,
    )


def offset_phases(waves, offsets):
    table = jnp.array(offsets, dtype=jnp.float32)
    return (
        table[:, 0:1] * waves[0][None]
        + table[:, 1:2] * waves[1][None]
        + table[:, 2:3] * waves[2][None]
    )


def block_phase(waves, size_x, size_y, size_z, float_type):
    place_x = jnp.arange(size_x, dtype=jnp.int32).astype(float_type)
    place_y = jnp.arange(size_y, dtype=jnp.int32).astype(float_type)
    place_z = jnp.arange(size_z, dtype=jnp.int32).astype(float_type)
    phase = waves[0][:, None, None, None] * place_x[None, :, None, None]
    phase = phase + waves[1][:, None, None, None] * place_y[None, None, :, None]
    return phase + waves[2][:, None, None, None] * place_z[None, None, None, :]


def leaf_moments(atom_data, waves):
    cosine, sine_part = waves_at(atom_data, waves)
    charge = atom_data[3]
    summed = jnp.sum(charge, axis=-1)[None]
    return jnp.concatenate(
        [
            summed,
            jnp.sum(cosine * charge[None], axis=-1),
            jnp.sum(sine_part * charge[None], axis=-1),
        ],
        axis=0,
    )


def evaluate(atom_data, local_exp, waves):
    cosine, sine_part = waves_at(atom_data, waves)
    half_count = waves.shape[1]
    cos_local = local_exp[1 : 1 + half_count][..., None]
    sin_local = local_exp[1 + half_count :][..., None]
    potential = local_exp[0][..., None] + jnp.sum(
        cos_local * cosine + sin_local * sine_part, axis=0
    )
    mixed_term = cos_local * sine_part - sin_local * cosine
    shape_lead = (half_count,) + (1,) * (mixed_term.ndim - 1)
    field_parts = [
        jnp.sum(waves[component].reshape(shape_lead) * mixed_term, axis=0) for component in range(3)
    ]
    return (potential, field_parts)


def near_row(target, source, flag_grid, shift_vec, keep_self):
    weight = source[3] * flag_grid[..., None]
    delta_x = target[0][..., :, None] - (source[0][..., None, :] + shift_vec[0])
    delta_y = target[1][..., :, None] - (source[1][..., None, :] + shift_vec[1])
    delta_z = target[2][..., :, None] - (source[2][..., None, :] + shift_vec[2])
    inverse = lax.rsqrt(delta_x * delta_x + delta_y * delta_y + delta_z * delta_z + soften)
    pair_term = weight[..., None, :] * keep_self * inverse
    cube_term = pair_term * inverse * inverse
    return jnp.stack(
        [
            jnp.sum(pair_term, axis=-1),
            jnp.sum(cube_term * delta_x, axis=-1),
            jnp.sum(cube_term * delta_y, axis=-1),
            jnp.sum(cube_term * delta_z, axis=-1),
        ]
    )


def full_flags(near_flags, float_type):
    flags_float = near_flags.astype(float_type)
    centre = jnp.ones((1,) + flags_float.shape[1:], float_type)
    return jnp.concatenate([flags_float[:13], centre, flags_float[13:]], axis=0)


def leaf_offsets():
    return [
        (shift_x, shift_y, shift_z)
        for shift_x in (-1, 0, 1)
        for shift_y in (-1, 0, 1)
        for shift_z in (-1, 0, 1)
        if (shift_x, shift_y, shift_z) != (0, 0, 0)
    ]


def parent_offsets():
    return [
        (shift_x, shift_y, shift_z)
        for shift_x in range(-2, 3)
        for shift_y in range(-2, 3)
        for shift_z in range(-2, 3)
        if max(abs(shift_x), abs(shift_y), abs(shift_z)) == 2
    ]


def climb_children(moments, matrices):
    coef_count, size_x, size_y, size_z = moments.shape
    parted = moments.reshape(coef_count, size_x // 2, 2, size_y // 2, 2, size_z // 2, 2)
    return jnp.einsum(
        "abckj,jxaybzc->kxyz",
        matrices.reshape(2, 2, 2, coef_count, coef_count),
        parted,
        precision=highest,
    )


def descend_children(parent_local, matrices):
    coef_count, size_x, size_y, size_z = parent_local.shape
    spread = jnp.einsum(
        "abckj,jxyz->kxaybzc",
        matrices.reshape(2, 2, 2, coef_count, coef_count),
        parent_local,
        precision=highest,
    )
    return spread.reshape(coef_count, 2 * size_x, 2 * size_y, 2 * size_z)


def matrix_vector(matrix, vector):
    return jnp.dot(matrix, vector, precision=highest)


def pick_side(matrices, own_side):
    return lax.dynamic_index_in_dim(matrices, own_side, 0, keepdims=False)


def pair_step(matrices, own_side, current, partner):
    return matrix_vector(pick_side(matrices, own_side), current) + matrix_vector(
        pick_side(matrices, 1 - own_side), partner
    )


def chain_tree(column, tree_up, tree_down, tree_side, lattice, hook):
    climbs = tree_up.astype(jnp.float32)
    lowers = tree_down.astype(jnp.float32)
    sideways = tree_side.astype(jnp.float32)
    current = column
    visited = []
    partner = None
    for level_bit in range(lax.axis_size("gx").bit_length() - 1):
        current = hook(current, partner)
        partner = from_partner(current, "gx", level_bit)
        own_side = lax.axis_index("gx") // 2**level_bit % 2
        current = pair_step(climbs[0], own_side, current, partner)
        visited.append((0, own_side, partner))
    for level_bit in range(lax.axis_size("gy").bit_length() - 1):
        current = hook(current, partner)
        partner = from_partner(current, "gy", level_bit)
        own_side = lax.axis_index("gy") // 2**level_bit % 2
        current = pair_step(climbs[1], own_side, current, partner)
        visited.append((1, own_side, partner))
    local_exp = matrix_vector(lattice.astype(jnp.float32), current)
    for axis_num, own_side, partner in reversed(visited):
        local_exp = matrix_vector(pick_side(lowers[axis_num], own_side), local_exp) + matrix_vector(
            pick_side(sideways[axis_num], own_side), partner
        )
    return local_exp


def flip_pair(column_grid, axis_num, level_bit):
    coef_count, size_x, size_y = column_grid.shape
    span_size = 2**level_bit
    if axis_num == 0:
        parted = column_grid.reshape(coef_count, size_x // (2 * span_size), 2, span_size, size_y)
        return parted[:, :, ::-1].reshape(column_grid.shape)
    parted = column_grid.reshape(coef_count, size_x, size_y // (2 * span_size), 2, span_size)
    return parted[:, :, :, ::-1].reshape(column_grid.shape)


def side_grid(axis_num, level_bit, size_x, size_y):
    positions = jnp.arange(size_x if axis_num == 0 else size_y, dtype=jnp.int32)
    own_side = positions // 2**level_bit % 2
    return own_side[:, None] if axis_num == 0 else own_side[None, :]


def choose_side(matrices, own_side, column_grid):
    first = jnp.einsum("kj,jxy->kxy", matrices[0], column_grid, precision=highest)
    second = jnp.einsum("kj,jxy->kxy", matrices[1], column_grid, precision=highest)
    return jnp.where(own_side[None] == 0, first, second)


def gathered_tree(column, tree_up, tree_down, tree_side, lattice):
    size_x, size_y = lax.axis_size("gx"), lax.axis_size("gy")
    gathered = lax.all_gather(column, ("gx", "gy")).reshape(size_x, size_y, -1)
    current = jnp.transpose(gathered, (2, 0, 1))
    levels = [(0, bit) for bit in range(size_x.bit_length() - 1)] + [
        (1, bit) for bit in range(size_y.bit_length() - 1)
    ]
    visited = []
    for axis_num, level_bit in levels:
        partner = flip_pair(current, axis_num, level_bit)
        own_side = side_grid(axis_num, level_bit, size_x, size_y)
        climbs = tree_up[axis_num].astype(jnp.float32)
        current = choose_side(climbs, own_side, current) + choose_side(climbs, 1 - own_side, partner)
        visited.append((axis_num, own_side, partner))
    local_exp = jnp.einsum("kj,jxy->kxy", lattice.astype(jnp.float32), current, precision=highest)
    for axis_num, own_side, partner in reversed(visited):
        local_exp = choose_side(tree_down[axis_num].astype(jnp.float32), own_side, local_exp) + choose_side(
            tree_side[axis_num].astype(jnp.float32), own_side, partner
        )
    own = lax.dynamic_slice(local_exp, (0, lax.axis_index("gx"), lax.axis_index("gy")), (local_exp.shape[0], 1, 1))
    return own.reshape(-1)


def assemble(near_terms, potential, field_parts, charge, live_slots):
    rows = [coulomb * (near_terms[0] + potential) * live_slots]
    for component in range(3):
        rows.append(coulomb * charge * (near_terms[1 + component] + field_parts[component]))
    return jnp.stack(rows)


NEAR_ROWS = 64
NEAR_PIECES = 8
NEAR_UNROLL = 2


def near_pairs(tx, ty, tz, srow, mask):
    weight = srow[3:4, :]
    delta_x = tx - srow[0:1, :]
    delta_y = ty - srow[1:2, :]
    delta_z = tz - srow[2:3, :]
    inverse = lax.rsqrt(delta_x * delta_x + delta_y * delta_y + delta_z * delta_z + soften)
    pair_term = weight * inverse
    if mask is not None:
        pair_term = jnp.where(mask, pair_term, 0.0)
    cube_term = pair_term * inverse * inverse
    return (pair_term, cube_term * delta_x, cube_term * delta_y, cube_term * delta_z)


def near_kernel(first_leaf, piece_leaves, leaf_count, listed_width, *refs):
    if len(refs) == 7:
        table_ref, target_ref, source_ref, shift_ref, previous_ref, out_ref, tile_ref = refs
        out_ref[...] = previous_ref[...]
    else:
        table_ref, target_ref, source_ref, shift_ref, out_ref, tile_ref = refs
        out_ref[...] = jnp.zeros(out_ref.shape, out_ref.dtype)
    place_start = 2 * leaf_count
    kind_start = place_start + leaf_count * listed_width
    big = NEAR_ROWS
    small = NEAR_ROWS // 2
    lanes = out_ref.shape[2]

    def leaf_body(local, carry):
        leaf = first_leaf + local
        count = table_ref[leaf]
        full_count = count // big
        rest = count - full_count * big
        listed = table_ref[leaf_count + leaf]
        base = leaf * listed_width
        tile_ref[...] = jnp.zeros(tile_ref.shape, tile_ref.dtype)

        def chunk_at(first, rows):
            lane = lax.broadcasted_iota(jnp.int32, (rows, lanes), 1)
            row = lax.broadcasted_iota(jnp.int32, (rows, lanes), 0)
            column = target_ref[local, pl.ds(first, rows), :]
            tx = jnp.broadcast_to(column[:, 0:1], (rows, lanes))
            ty = jnp.broadcast_to(column[:, 1:2], (rows, lanes))
            tz = jnp.broadcast_to(column[:, 2:3], (rows, lanes))
            acc = near_pairs(tx, ty, tz, source_ref[table_ref[place_start + base]], row + first != lane)

            def offset_body(step, acc):
                number = base + 1 + NEAR_UNROLL * step
                for extra in range(NEAR_UNROLL):
                    srow = source_ref[table_ref[place_start + number + extra]]
                    srow = srow + shift_ref[table_ref[kind_start + number + extra]]
                    terms = near_pairs(tx, ty, tz, srow, None)
                    acc = tuple(a + b for a, b in zip(acc, terms))
                return acc

            acc = lax.fori_loop(0, (listed - 1) // NEAR_UNROLL, offset_body, acc)
            sums = [jnp.sum(part, axis=1, keepdims=True) for part in acc]
            tile = jnp.where(
                lane == 0, sums[0], jnp.where(lane == 1, sums[1], jnp.where(lane == 2, sums[2], sums[3]))
            )
            tile_ref[pl.ds(first, rows), :] = jnp.where(lane < 4, tile, 0.0)

        def full_body(chunk, carry2):
            chunk_at(pl.multiple_of(chunk * big, big), big)
            return carry2

        lax.fori_loop(0, full_count, full_body, 0)
        last = pl.multiple_of(full_count * big, small)

        @pl.when(rest > small)
        def _():
            chunk_at(last, big)

        @pl.when((rest > 0) & (rest <= small))
        def _():
            chunk_at(last, small)

        out_ref[leaf] = jnp.transpose(tile_ref[...])[0 : out_ref.shape[1], :]
        return carry

    lax.fori_loop(0, piece_leaves, leaf_body, 0)


def near_local(charged, rimmed, counts, near_flags):
    size_x, size_y, size_z, slot_count = charged.shape[1:]
    leaf_count = size_x * size_y * size_z
    ext_y = size_y + 2
    target = jnp.transpose(charged, (1, 2, 3, 4, 0)).reshape(leaf_count, slot_count, 4)
    source = jnp.transpose(rimmed, (1, 2, 3, 0, 4)).reshape(-1, 4, slot_count)
    source = jnp.pad(source, ((0, 1), (0, 4), (0, 0)))
    empty_leaf = source.shape[0] - 1
    offsets = [(0, 0, 0)] + leaf_offsets()
    shift_rows = np.array([[float(v) for v in offset] + [0.0] * 5 for offset in offsets], np.float32)
    shift_table = jnp.asarray(np.ascontiguousarray(np.broadcast_to(shift_rows[:, :, None], (len(offsets), 8, slot_count))))
    leaf_x = jnp.arange(size_x, dtype=jnp.int32)[:, None, None]
    leaf_y = jnp.arange(size_y, dtype=jnp.int32)[None, :, None]
    leaf_z = jnp.arange(size_z, dtype=jnp.int32)[None, None, :]
    places = []
    for offset in offsets:
        place = ((leaf_x + 1 + offset[0]) * ext_y + leaf_y + 1 + offset[1]) * size_z + leaf_z + offset[2]
        places.append(jnp.broadcast_to(place, (size_x, size_y, size_z)))
    places = jnp.stack(places).reshape(len(offsets), leaf_count)
    layer = jnp.arange(size_z, dtype=jnp.int32)
    valid = jnp.stack([((layer + offset[2] >= 0) & (layer + offset[2] < size_z)) for offset in offsets[1:]])
    active = (near_flags != 0) & valid[:, None, None, :]
    active = jnp.concatenate([jnp.ones((1, leaf_count), bool), active.reshape(len(offsets) - 1, leaf_count)])
    listed = jnp.sum(active.astype(jnp.int32), axis=0)
    listed = listed + (NEAR_UNROLL - (listed - 1) % NEAR_UNROLL) % NEAR_UNROLL
    position = jnp.cumsum(active.astype(jnp.int32), axis=0) - 1
    width = 1 + -(-(len(offsets) - 1) // NEAR_UNROLL) * NEAR_UNROLL
    slots = jnp.arange(width, dtype=jnp.int32)
    chosen = active[None] & (position[None] == slots[:, None, None])
    kinds = jnp.arange(len(offsets), dtype=jnp.int32)
    kind_list = jnp.sum(jnp.where(chosen, kinds[None, :, None], 0), axis=1)
    place_list = jnp.sum(jnp.where(chosen, places[None], 0), axis=1)
    place_list = jnp.where(slots[:, None] < jnp.sum(active.astype(jnp.int32), axis=0)[None], place_list, empty_leaf)
    table = jnp.concatenate(
        [counts.reshape(-1), listed, jnp.transpose(place_list).reshape(-1), jnp.transpose(kind_list).reshape(-1)]
    ).astype(jnp.int32)
    piece = leaf_count // NEAR_PIECES if leaf_count % NEAR_PIECES == 0 else leaf_count
    pairs = piece * slot_count * slot_count * 10

    chained = []

    def run_piece(number, gate):
        first_leaf = number * piece
        own = target[first_leaf : first_leaf + piece]
        if gate is not None:
            own, unused = lax.optimization_barrier((own, gate))
        operands = [table, own, source, shift_table] + chained[-1:]
        result = pl.pallas_call(
            functools.partial(near_kernel, first_leaf, piece, leaf_count, width),
            out_shape=jax.ShapeDtypeStruct((leaf_count, 8, slot_count), jnp.float32),
            in_specs=[pl.BlockSpec(memory_space=pltpu.SMEM)] + [pl.BlockSpec(memory_space=pltpu.VMEM)] * (len(operands) - 1),
            out_specs=pl.BlockSpec(memory_space=pltpu.VMEM),
            scratch_shapes=[pltpu.VMEM((slot_count, 128), jnp.float32)],
            input_output_aliases={4: 0} if chained else {},
            cost_estimate=pl.CostEstimate(
                flops=20 * pairs, transcendentals=pairs, bytes_accessed=8 * piece * slot_count * 128
            ),
        )(*operands)
        chained.append(result)
        return result

    def finish_near(outs):
        near = jnp.transpose(chained[-1][:, :4, :], (1, 0, 2))
        return near.reshape(4, size_x, size_y, size_z, slot_count)

    return leaf_count // piece, run_piece, finish_near


def body(
    atom_data,
    counts,
    near_flags,
    child_up,
    child_down,
    leaf_far,
    parent_far,
    column_up,
    column_down,
    tree_up,
    tree_down,
    tree_side,
    lattice,
):
    coef_count = lattice.shape[0]
    slot_count = atom_data.shape[4]
    size_x, size_y, size_z = (atom_data.shape[1], atom_data.shape[2], atom_data.shape[3])
    live_slots = (
        jnp.arange(slot_count, dtype=jnp.int32)[None, None, None, :] < counts[..., None]
    ).astype(jnp.float32)
    charged = jnp.concatenate([atom_data[:3], (atom_data[3] * live_slots)[None]], axis=0)
    waves = wave_table(coef_count, jnp.float32)
    half_count = waves.shape[1]
    moments = leaf_moments(charged, waves)
    parents = climb_children(moments, child_up.astype(jnp.float32))
    rimmed, parent_rim, leaf_rim = extended_joint([(charged, 1), (parents, 2), (moments, 1)], (("gx", 1), ("gy", 2)))
    parent_rim = jnp.pad(parent_rim, ((0, 0), (0, 0), (0, 0), (2, 2)))
    half_x, half_y, half_z = (parents.shape[1], parents.shape[2], parents.shape[3])
    phase_grid = block_phase(waves, half_x, half_y, half_z, jnp.float32)
    turned = jnp.sum(rotate_by(parents, phase_grid), axis=(1, 2, 3))
    column = matrix_vector(column_up.astype(jnp.float32), turned)
    piece_count, run_piece, finish_near = near_local(charged, rimmed, counts, near_flags)
    pieces = []

    def hook(value, prior):
        number = len(pieces)
        if number < piece_count:
            if number > 0:
                value, unused = lax.optimization_barrier((value, pieces[-1]))
            pieces.append(run_piece(number, prior))
        return value

    column_local = chain_tree(column, tree_up, tree_down, tree_side, lattice, hook)
    while len(pieces) < piece_count:
        pieces.append(run_piece(len(pieces), None))
    near_terms = finish_near(pieces)
    leaf_rim = jnp.pad(leaf_rim, ((0, 0), (0, 0), (0, 0), (1, 1)))
    lowered = matrix_vector(column_down.astype(jnp.float32), column_local)
    parent_local = rotate_by(
        jnp.broadcast_to(lowered[:, None, None, None], parents.shape), -phase_grid
    )
    far_parents = parent_offsets()
    parent_stack = jnp.stack(
        [
            parent_rim[
                :,
                2 + offset[0] : 2 + offset[0] + half_x,
                2 + offset[1] : 2 + offset[1] + half_y,
                2 + offset[2] : 2 + offset[2] + half_z,
            ]
            for offset in far_parents
        ]
    )
    parent_turns = offset_phases(waves, far_parents).reshape(len(far_parents), half_count, 1, 1, 1)
    parent_sum = jnp.sum(jax.vmap(rotate_by)(parent_stack, parent_turns), axis=0)
    parent_local = parent_local + jnp.einsum(
        "kj,jxyz->kxyz", parent_far.astype(jnp.float32), parent_sum, precision=highest
    )
    leaf_local = descend_children(parent_local, child_down.astype(jnp.float32))
    near_leaves = leaf_offsets()
    leaf_stack = jnp.stack(
        [
            leaf_rim[
                :,
                1 + offset[0] : 1 + offset[0] + size_x,
                1 + offset[1] : 1 + offset[1] + size_y,
                1 + offset[2] : 1 + offset[2] + size_z,
            ]
            for offset in near_leaves
        ]
    )
    leaf_stack = leaf_stack * (1.0 - near_flags.astype(jnp.float32))[:, None]
    leaf_turns = offset_phases(waves, near_leaves).reshape(len(near_leaves), half_count, 1, 1, 1)
    leaf_sum = jnp.sum(jax.vmap(rotate_by)(leaf_stack, leaf_turns), axis=0)
    leaf_local = leaf_local + jnp.einsum(
        "kj,jxyz->kxyz", leaf_far.astype(jnp.float32), leaf_sum, precision=highest
    )
    potential, field_parts = evaluate(charged, leaf_local, waves)
    return assemble(near_terms, potential, field_parts, charged[3], live_slots)


def solution(mesh):
    in_specs = (
        P(None, "gx", "gy", None, None),
        P("gx", "gy", None),
        P(None, "gx", "gy", None),
        P(),
        P(),
        P(),
        P(),
        P(),
        P(),
        P(),
        P(),
        P(),
        P(),
    )
    out_specs = P(None, "gx", "gy", None, None)
    return jax.shard_map(body, mesh=mesh, in_specs=in_specs, out_specs=out_specs, check_vma=False)
```

```python
import functools

import jax
import numpy as np
import jax.numpy as jnp
from jax import lax
from jax.experimental import pallas as pl
from jax.experimental.pallas import tpu as pltpu
from jax.sharding import PartitionSpec as P

soften = 0.04
coulomb = 0.1
highest = lax.Precision.HIGHEST


def from_partner(value, axis, bit):
    mask = 2**bit
    pairs = [(source, source ^ mask) for source in range(lax.axis_size(axis))]
    return lax.ppermute(value, axis, pairs)


def extended_2(block, sides, width):
    return extended_joint([(block, width)], sides)[0]


def extended_joint(parts, sides):
    blocks = [block for block, width in parts]
    for axis, dim in sides:
        count = lax.axis_size(axis)
        forward = [(i, i + 1) for i in range(count - 1)]
        forward.append((count - 1, 0))
        backward = [(target, source) for source, target in forward]
        lows = [lax.slice_in_dim(b, b.shape[dim] - w, None, axis=dim) for b, (_, w) in zip(blocks, parts)]
        highs = [lax.slice_in_dim(b, 0, w, axis=dim) for b, (_, w) in zip(blocks, parts)]
        sizes = [piece.size for piece in lows]
        low_all = lax.ppermute(jnp.concatenate([piece.reshape(-1) for piece in lows]), axis, forward)
        high_all = lax.ppermute(jnp.concatenate([piece.reshape(-1) for piece in highs]), axis, backward)
        grown = []
        place = 0
        for b, piece, size in zip(blocks, lows, sizes):
            low = low_all[place : place + size].reshape(piece.shape)
            high = high_all[place : place + size].reshape(piece.shape)
            place += size
            grown.append(jnp.concatenate([low, b, high], axis=dim))
        blocks = grown
    return blocks


def wave_table(coef_count, float_type):
    half_count = (coef_count - 1) // 2
    order_index = jnp.arange(1, half_count + 1, dtype=jnp.int32).astype(float_type)
    height = 1.0 - 2.0 * (order_index - 0.5) / half_count
    radius = jnp.sqrt(jnp.maximum(1.0 - height * height, 0.0))
    angle_turn = 2.399963 * order_index
    magnitude = 1.5 + jnp.mod(order_index, 3.0)
    return (
        jnp.stack([radius * jnp.cos(angle_turn), radius * jnp.sin(angle_turn), height])
        * magnitude[None]
    )


def waves_at(atom_data, waves):
    shape_lead = (waves.shape[1],) + (1,) * (atom_data.ndim - 1)
    phases = waves[0].reshape(shape_lead) * (atom_data[0] - 0.5)[None]
    phases = phases + waves[1].reshape(shape_lead) * (atom_data[1] - 0.5)[None]
    phases = phases + waves[2].reshape(shape_lead) * (atom_data[2] - 0.5)[None]
    return (jnp.cos(phases), jnp.sin(phases))


def rotate_by(field, phase):
    half_count = phase.shape[0]
    cosine = jnp.cos(phase)
    sine_part = jnp.sin(phase)
    cos_coef = field[1 : 1 + half_count]
    sin_coef = field[1 + half_count :]
    return jnp.concatenate(
        [
            field[0:1],
            cos_coef * cosine - sin_coef * sine_part,
            cos_coef * sine_part + sin_coef * cosine,
        ],
        axis=0,
    )


def offset_phases(waves, offsets):
    table = jnp.array(offsets, dtype=jnp.float32)
    return (
        table[:, 0:1] * waves[0][None]
        + table[:, 1:2] * waves[1][None]
        + table[:, 2:3] * waves[2][None]
    )


def block_phase(waves, size_x, size_y, size_z, float_type):
    place_x = jnp.arange(size_x, dtype=jnp.int32).astype(float_type)
    place_y = jnp.arange(size_y, dtype=jnp.int32).astype(float_type)
    place_z = jnp.arange(size_z, dtype=jnp.int32).astype(float_type)
    phase = waves[0][:, None, None, None] * place_x[None, :, None, None]
    phase = phase + waves[1][:, None, None, None] * place_y[None, None, :, None]
    return phase + waves[2][:, None, None, None] * place_z[None, None, None, :]


def leaf_moments(atom_data, waves):
    cosine, sine_part = waves_at(atom_data, waves)
    charge = atom_data[3]
    summed = jnp.sum(charge, axis=-1)[None]
    return jnp.concatenate(
        [
            summed,
            jnp.sum(cosine * charge[None], axis=-1),
            jnp.sum(sine_part * charge[None], axis=-1),
        ],
        axis=0,
    )


def evaluate(atom_data, local_exp, waves):
    cosine, sine_part = waves_at(atom_data, waves)
    half_count = waves.shape[1]
    cos_local = local_exp[1 : 1 + half_count][..., None]
    sin_local = local_exp[1 + half_count :][..., None]
    potential = local_exp[0][..., None] + jnp.sum(
        cos_local * cosine + sin_local * sine_part, axis=0
    )
    mixed_term = cos_local * sine_part - sin_local * cosine
    shape_lead = (half_count,) + (1,) * (mixed_term.ndim - 1)
    field_parts = [
        jnp.sum(waves[component].reshape(shape_lead) * mixed_term, axis=0) for component in range(3)
    ]
    return (potential, field_parts)


def near_row(target, source, flag_grid, shift_vec, keep_self):
    weight = source[3] * flag_grid[..., None]
    delta_x = target[0][..., :, None] - (source[0][..., None, :] + shift_vec[0])
    delta_y = target[1][..., :, None] - (source[1][..., None, :] + shift_vec[1])
    delta_z = target[2][..., :, None] - (source[2][..., None, :] + shift_vec[2])
    inverse = lax.rsqrt(delta_x * delta_x + delta_y * delta_y + delta_z * delta_z + soften)
    pair_term = weight[..., None, :] * keep_self * inverse
    cube_term = pair_term * inverse * inverse
    return jnp.stack(
        [
            jnp.sum(pair_term, axis=-1),
            jnp.sum(cube_term * delta_x, axis=-1),
            jnp.sum(cube_term * delta_y, axis=-1),
            jnp.sum(cube_term * delta_z, axis=-1),
        ]
    )


def full_flags(near_flags, float_type):
    flags_float = near_flags.astype(float_type)
    centre = jnp.ones((1,) + flags_float.shape[1:], float_type)
    return jnp.concatenate([flags_float[:13], centre, flags_float[13:]], axis=0)


def leaf_offsets():
    return [
        (shift_x, shift_y, shift_z)
        for shift_x in (-1, 0, 1)
        for shift_y in (-1, 0, 1)
        for shift_z in (-1, 0, 1)
        if (shift_x, shift_y, shift_z) != (0, 0, 0)
    ]


def parent_offsets():
    return [
        (shift_x, shift_y, shift_z)
        for shift_x in range(-2, 3)
        for shift_y in range(-2, 3)
        for shift_z in range(-2, 3)
        if max(abs(shift_x), abs(shift_y), abs(shift_z)) == 2
    ]


def climb_children(moments, matrices):
    coef_count, size_x, size_y, size_z = moments.shape
    parted = moments.reshape(coef_count, size_x // 2, 2, size_y // 2, 2, size_z // 2, 2)
    return jnp.einsum(
        "abckj,jxaybzc->kxyz",
        matrices.reshape(2, 2, 2, coef_count, coef_count),
        parted,
        precision=highest,
    )


def descend_children(parent_local, matrices):
    coef_count, size_x, size_y, size_z = parent_local.shape
    spread = jnp.einsum(
        "abckj,jxyz->kxaybzc",
        matrices.reshape(2, 2, 2, coef_count, coef_count),
        parent_local,
        precision=highest,
    )
    return spread.reshape(coef_count, 2 * size_x, 2 * size_y, 2 * size_z)


def matrix_vector(matrix, vector):
    return jnp.dot(matrix, vector, precision=highest)


def pick_side(matrices, own_side):
    return lax.dynamic_index_in_dim(matrices, own_side, 0, keepdims=False)


def pair_step(matrices, own_side, current, partner):
    return matrix_vector(pick_side(matrices, own_side), current) + matrix_vector(
        pick_side(matrices, 1 - own_side), partner
    )


def chain_tree(column, tree_up, tree_down, tree_side, lattice, hook):
    climbs = tree_up.astype(jnp.float32)
    lowers = tree_down.astype(jnp.float32)
    sideways = tree_side.astype(jnp.float32)
    current = column
    visited = []
    partner = None
    for level_bit in range(lax.axis_size("gx").bit_length() - 1):
        current = hook(current, partner)
        partner = from_partner(current, "gx", level_bit)
        own_side = lax.axis_index("gx") // 2**level_bit % 2
        current = pair_step(climbs[0], own_side, current, partner)
        visited.append((0, own_side, partner))
    for level_bit in range(lax.axis_size("gy").bit_length() - 1):
        current = hook(current, partner)
        partner = from_partner(current, "gy", level_bit)
        own_side = lax.axis_index("gy") // 2**level_bit % 2
        current = pair_step(climbs[1], own_side, current, partner)
        visited.append((1, own_side, partner))
    local_exp = matrix_vector(lattice.astype(jnp.float32), current)
    for axis_num, own_side, partner in reversed(visited):
        local_exp = matrix_vector(pick_side(lowers[axis_num], own_side), local_exp) + matrix_vector(
            pick_side(sideways[axis_num], own_side), partner
        )
    return local_exp


def flip_pair(column_grid, axis_num, level_bit):
    coef_count, size_x, size_y = column_grid.shape
    span_size = 2**level_bit
    if axis_num == 0:
        parted = column_grid.reshape(coef_count, size_x // (2 * span_size), 2, span_size, size_y)
        return parted[:, :, ::-1].reshape(column_grid.shape)
    parted = column_grid.reshape(coef_count, size_x, size_y // (2 * span_size), 2, span_size)
    return parted[:, :, :, ::-1].reshape(column_grid.shape)


def side_grid(axis_num, level_bit, size_x, size_y):
    positions = jnp.arange(size_x if axis_num == 0 else size_y, dtype=jnp.int32)
    own_side = positions // 2**level_bit % 2
    return own_side[:, None] if axis_num == 0 else own_side[None, :]


def choose_side(matrices, own_side, column_grid):
    first = jnp.einsum("kj,jxy->kxy", matrices[0], column_grid, precision=highest)
    second = jnp.einsum("kj,jxy->kxy", matrices[1], column_grid, precision=highest)
    return jnp.where(own_side[None] == 0, first, second)


def gathered_tree(column, tree_up, tree_down, tree_side, lattice):
    size_x, size_y = lax.axis_size("gx"), lax.axis_size("gy")
    gathered = lax.all_gather(column, ("gx", "gy")).reshape(size_x, size_y, -1)
    current = jnp.transpose(gathered, (2, 0, 1))
    levels = [(0, bit) for bit in range(size_x.bit_length() - 1)] + [
        (1, bit) for bit in range(size_y.bit_length() - 1)
    ]
    visited = []
    for axis_num, level_bit in levels:
        partner = flip_pair(current, axis_num, level_bit)
        own_side = side_grid(axis_num, level_bit, size_x, size_y)
        climbs = tree_up[axis_num].astype(jnp.float32)
        current = choose_side(climbs, own_side, current) + choose_side(climbs, 1 - own_side, partner)
        visited.append((axis_num, own_side, partner))
    local_exp = jnp.einsum("kj,jxy->kxy", lattice.astype(jnp.float32), current, precision=highest)
    for axis_num, own_side, partner in reversed(visited):
        local_exp = choose_side(tree_down[axis_num].astype(jnp.float32), own_side, local_exp) + choose_side(
            tree_side[axis_num].astype(jnp.float32), own_side, partner
        )
    own = lax.dynamic_slice(local_exp, (0, lax.axis_index("gx"), lax.axis_index("gy")), (local_exp.shape[0], 1, 1))
    return own.reshape(-1)


def assemble(near_terms, potential, field_parts, charge, live_slots):
    rows = [coulomb * (near_terms[0] + potential) * live_slots]
    for component in range(3):
        rows.append(coulomb * charge * (near_terms[1 + component] + field_parts[component]))
    return jnp.stack(rows)


NEAR_ROWS = 64
NEAR_PIECES = 8
NEAR_UNROLL = 2


def near_pairs(tx, ty, tz, srow, mask):
    weight = srow[3:4, :]
    delta_x = tx - srow[0:1, :]
    delta_y = ty - srow[1:2, :]
    delta_z = tz - srow[2:3, :]
    inverse = lax.rsqrt(delta_x * delta_x + delta_y * delta_y + delta_z * delta_z + soften)
    pair_term = weight * inverse
    if mask is not None:
        pair_term = jnp.where(mask, pair_term, 0.0)
    cube_term = pair_term * inverse * inverse
    return (pair_term, cube_term * delta_x, cube_term * delta_y, cube_term * delta_z)


def near_kernel(first_leaf, piece_leaves, leaf_count, listed_width, *refs):
    if len(refs) == 7:
        table_ref, target_ref, source_ref, shift_ref, previous_ref, out_ref, tile_ref = refs
        out_ref[...] = previous_ref[...]
    else:
        table_ref, target_ref, source_ref, shift_ref, out_ref, tile_ref = refs
        out_ref[...] = jnp.zeros(out_ref.shape, out_ref.dtype)
    place_start = 2 * leaf_count
    kind_start = place_start + leaf_count * listed_width
    big = NEAR_ROWS
    small = NEAR_ROWS // 2
    lanes = out_ref.shape[2]

    def leaf_body(local, carry):
        leaf = first_leaf + local
        count = table_ref[leaf]
        full_count = count // big
        rest = count - full_count * big
        listed = table_ref[leaf_count + leaf]
        base = leaf * listed_width
        tile_ref[...] = jnp.zeros(tile_ref.shape, tile_ref.dtype)

        def chunk_at(first, rows):
            lane = lax.broadcasted_iota(jnp.int32, (rows, lanes), 1)
            row = lax.broadcasted_iota(jnp.int32, (rows, lanes), 0)
            column = target_ref[local, pl.ds(first, rows), :]
            tx = jnp.broadcast_to(column[:, 0:1], (rows, lanes))
            ty = jnp.broadcast_to(column[:, 1:2], (rows, lanes))
            tz = jnp.broadcast_to(column[:, 2:3], (rows, lanes))
            acc = near_pairs(tx, ty, tz, source_ref[table_ref[place_start + base]], row + first != lane)

            def offset_body(step, acc):
                number = base + 1 + NEAR_UNROLL * step
                for extra in range(NEAR_UNROLL):
                    srow = source_ref[table_ref[place_start + number + extra]]
                    srow = srow + shift_ref[table_ref[kind_start + number + extra]]
                    terms = near_pairs(tx, ty, tz, srow, None)
                    acc = tuple(a + b for a, b in zip(acc, terms))
                return acc

            acc = lax.fori_loop(0, (listed - 1) // NEAR_UNROLL, offset_body, acc)
            sums = [jnp.sum(part, axis=1, keepdims=True) for part in acc]
            tile = jnp.where(
                lane == 0, sums[0], jnp.where(lane == 1, sums[1], jnp.where(lane == 2, sums[2], sums[3]))
            )
            tile_ref[pl.ds(first, rows), :] = jnp.where(lane < 4, tile, 0.0)

        def full_body(chunk, carry2):
            chunk_at(pl.multiple_of(chunk * big, big), big)
            return carry2

        lax.fori_loop(0, full_count, full_body, 0)
        last = pl.multiple_of(full_count * big, small)

        @pl.when(rest > small)
        def _():
            chunk_at(last, big)

        @pl.when((rest > 0) & (rest <= small))
        def _():
            chunk_at(last, small)

        out_ref[leaf] = jnp.transpose(tile_ref[...])[0 : out_ref.shape[1], :]
        return carry

    lax.fori_loop(0, piece_leaves, leaf_body, 0)


def near_local(charged, rimmed, counts, near_flags):
    size_x, size_y, size_z, slot_count = charged.shape[1:]
    leaf_count = size_x * size_y * size_z
    ext_y = size_y + 2
    target = jnp.transpose(charged, (1, 2, 3, 4, 0)).reshape(leaf_count, slot_count, 4)
    source = jnp.transpose(rimmed, (1, 2, 3, 0, 4)).reshape(-1, 4, slot_count)
    source = jnp.pad(source, ((0, 1), (0, 4), (0, 0)))
    empty_leaf = source.shape[0] - 1
    offsets = [(0, 0, 0)] + leaf_offsets()
    shift_rows = np.array([[float(v) for v in offset] + [0.0] * 5 for offset in offsets], np.float32)
    shift_table = jnp.asarray(np.ascontiguousarray(np.broadcast_to(shift_rows[:, :, None], (len(offsets), 8, slot_count))))
    leaf_x = jnp.arange(size_x, dtype=jnp.int32)[:, None, None]
    leaf_y = jnp.arange(size_y, dtype=jnp.int32)[None, :, None]
    leaf_z = jnp.arange(size_z, dtype=jnp.int32)[None, None, :]
    places = []
    for offset in offsets:
        place = ((leaf_x + 1 + offset[0]) * ext_y + leaf_y + 1 + offset[1]) * size_z + leaf_z + offset[2]
        places.append(jnp.broadcast_to(place, (size_x, size_y, size_z)))
    places = jnp.stack(places).reshape(len(offsets), leaf_count)
    layer = jnp.arange(size_z, dtype=jnp.int32)
    valid = jnp.stack([((layer + offset[2] >= 0) & (layer + offset[2] < size_z)) for offset in offsets[1:]])
    active = (near_flags != 0) & valid[:, None, None, :]
    active = jnp.concatenate([jnp.ones((1, leaf_count), bool), active.reshape(len(offsets) - 1, leaf_count)])
    listed = jnp.sum(active.astype(jnp.int32), axis=0)
    listed = listed + (NEAR_UNROLL - (listed - 1) % NEAR_UNROLL) % NEAR_UNROLL
    position = jnp.cumsum(active.astype(jnp.int32), axis=0) - 1
    width = 1 + -(-(len(offsets) - 1) // NEAR_UNROLL) * NEAR_UNROLL
    slots = jnp.arange(width, dtype=jnp.int32)
    chosen = active[None] & (position[None] == slots[:, None, None])
    kinds = jnp.arange(len(offsets), dtype=jnp.int32)
    kind_list = jnp.sum(jnp.where(chosen, kinds[None, :, None], 0), axis=1)
    place_list = jnp.sum(jnp.where(chosen, places[None], 0), axis=1)
    place_list = jnp.where(slots[:, None] < jnp.sum(active.astype(jnp.int32), axis=0)[None], place_list, empty_leaf)
    table = jnp.concatenate(
        [counts.reshape(-1), listed, jnp.transpose(place_list).reshape(-1), jnp.transpose(kind_list).reshape(-1)]
    ).astype(jnp.int32)
    piece = leaf_count // NEAR_PIECES if leaf_count % NEAR_PIECES == 0 else leaf_count
    pairs = piece * slot_count * slot_count * 10

    chained = []

    def run_piece(number, gate):
        first_leaf = number * piece
        own = target[first_leaf : first_leaf + piece]
        if gate is not None:
            own, unused = lax.optimization_barrier((own, gate))
        operands = [table, own, source, shift_table] + chained[-1:]
        result = pl.pallas_call(
            functools.partial(near_kernel, first_leaf, piece, leaf_count, width),
            out_shape=jax.ShapeDtypeStruct((leaf_count, 8, slot_count), jnp.float32),
            in_specs=[pl.BlockSpec(memory_space=pltpu.SMEM)] + [pl.BlockSpec(memory_space=pltpu.VMEM)] * (len(operands) - 1),
            out_specs=pl.BlockSpec(memory_space=pltpu.VMEM),
            scratch_shapes=[pltpu.VMEM((slot_count, 128), jnp.float32)],
            input_output_aliases={4: 0} if chained else {},
            cost_estimate=pl.CostEstimate(
                flops=20 * pairs, transcendentals=pairs, bytes_accessed=8 * piece * slot_count * 128
            ),
        )(*operands)
        chained.append(result)
        return result

    def finish_near(outs):
        near = jnp.transpose(chained[-1][:, :4, :], (1, 0, 2))
        return near.reshape(4, size_x, size_y, size_z, slot_count)

    return leaf_count // piece, run_piece, finish_near


def body(
    atom_data,
    counts,
    near_flags,
    child_up,
    child_down,
    leaf_far,
    parent_far,
    column_up,
    column_down,
    tree_up,
    tree_down,
    tree_side,
    lattice,
):
    coef_count = lattice.shape[0]
    slot_count = atom_data.shape[4]
    size_x, size_y, size_z = (atom_data.shape[1], atom_data.shape[2], atom_data.shape[3])
    live_slots = (
        jnp.arange(slot_count, dtype=jnp.int32)[None, None, None, :] < counts[..., None]
    ).astype(jnp.float32)
    charged = jnp.concatenate([atom_data[:3], (atom_data[3] * live_slots)[None]], axis=0)
    waves = wave_table(coef_count, jnp.float32)
    half_count = waves.shape[1]
    moments = leaf_moments(charged, waves)
    parents = climb_children(moments, child_up.astype(jnp.float32))
    rimmed, parent_rim, leaf_rim = extended_joint([(charged, 1), (parents, 2), (moments, 1)], (("gx", 1), ("gy", 2)))
    parent_rim = jnp.pad(parent_rim, ((0, 0), (0, 0), (0, 0), (2, 2)))
    half_x, half_y, half_z = (parents.shape[1], parents.shape[2], parents.shape[3])
    phase_grid = block_phase(waves, half_x, half_y, half_z, jnp.float32)
    turned = jnp.sum(rotate_by(parents, phase_grid), axis=(1, 2, 3))
    column = matrix_vector(column_up.astype(jnp.float32), turned)
    piece_count, run_piece, finish_near = near_local(charged, rimmed, counts, near_flags)
    pieces = []

    sent = []

    def hook(value, prior):
        number = len(pieces)
        if number < piece_count:
            if number > 0:
                value, unused = lax.optimization_barrier((value, pieces[-1]))
            pieces.append(run_piece(number, prior))
        sent.append(value)
        return value

    column_local = chain_tree(column, tree_up, tree_down, tree_side, lattice, hook)
    while len(pieces) < piece_count:
        pieces.append(run_piece(len(pieces), sent[-1]))
    near_terms = finish_near(pieces)
    leaf_rim = jnp.pad(leaf_rim, ((0, 0), (0, 0), (0, 0), (1, 1)))
    lowered = matrix_vector(column_down.astype(jnp.float32), column_local)
    parent_local = rotate_by(
        jnp.broadcast_to(lowered[:, None, None, None], parents.shape), -phase_grid
    )
    far_parents = parent_offsets()
    parent_stack = jnp.stack(
        [
            parent_rim[
                :,
                2 + offset[0] : 2 + offset[0] + half_x,
                2 + offset[1] : 2 + offset[1] + half_y,
                2 + offset[2] : 2 + offset[2] + half_z,
            ]
            for offset in far_parents
        ]
    )
    parent_turns = offset_phases(waves, far_parents).reshape(len(far_parents), half_count, 1, 1, 1)
    parent_sum = jnp.sum(jax.vmap(rotate_by)(parent_stack, parent_turns), axis=0)
    parent_local = parent_local + jnp.einsum(
        "kj,jxyz->kxyz", parent_far.astype(jnp.float32), parent_sum, precision=highest
    )
    leaf_local = descend_children(parent_local, child_down.astype(jnp.float32))
    near_leaves = leaf_offsets()
    leaf_stack = jnp.stack(
        [
            leaf_rim[
                :,
                1 + offset[0] : 1 + offset[0] + size_x,
                1 + offset[1] : 1 + offset[1] + size_y,
                1 + offset[2] : 1 + offset[2] + size_z,
            ]
            for offset in near_leaves
        ]
    )
    leaf_stack = leaf_stack * (1.0 - near_flags.astype(jnp.float32))[:, None]
    leaf_turns = offset_phases(waves, near_leaves).reshape(len(near_leaves), half_count, 1, 1, 1)
    leaf_sum = jnp.sum(jax.vmap(rotate_by)(leaf_stack, leaf_turns), axis=0)
    leaf_local = leaf_local + jnp.einsum(
        "kj,jxyz->kxyz", leaf_far.astype(jnp.float32), leaf_sum, precision=highest
    )
    potential, field_parts = evaluate(charged, leaf_local, waves)
    return assemble(near_terms, potential, field_parts, charged[3], live_slots)


def solution(mesh):
    in_specs = (
        P(None, "gx", "gy", None, None),
        P("gx", "gy", None),
        P(None, "gx", "gy", None),
        P(),
        P(),
        P(),
        P(),
        P(),
        P(),
        P(),
        P(),
        P(),
        P(),
    )
    out_specs = P(None, "gx", "gy", None, None)
    return jax.shard_map(body, mesh=mesh, in_specs=in_specs, out_specs=out_specs, check_vma=False)
```

```python
import functools

import jax
import numpy as np
import jax.numpy as jnp
from jax import lax
from jax.experimental import pallas as pl
from jax.experimental.pallas import tpu as pltpu
from jax.sharding import PartitionSpec as P

soften = 0.04
coulomb = 0.1
highest = lax.Precision.HIGHEST


def from_partner(value, axis, bit):
    mask = 2**bit
    pairs = [(source, source ^ mask) for source in range(lax.axis_size(axis))]
    return lax.ppermute(value, axis, pairs)


def extended_2(block, sides, width):
    return extended_joint([(block, width)], sides)[0]


def extended_joint(parts, sides):
    blocks = [block for block, width in parts]
    for axis, dim in sides:
        count = lax.axis_size(axis)
        forward = [(i, i + 1) for i in range(count - 1)]
        forward.append((count - 1, 0))
        backward = [(target, source) for source, target in forward]
        lows = [lax.slice_in_dim(b, b.shape[dim] - w, None, axis=dim) for b, (_, w) in zip(blocks, parts)]
        highs = [lax.slice_in_dim(b, 0, w, axis=dim) for b, (_, w) in zip(blocks, parts)]
        sizes = [piece.size for piece in lows]
        low_all = lax.ppermute(jnp.concatenate([piece.reshape(-1) for piece in lows]), axis, forward)
        high_all = lax.ppermute(jnp.concatenate([piece.reshape(-1) for piece in highs]), axis, backward)
        grown = []
        place = 0
        for b, piece, size in zip(blocks, lows, sizes):
            low = low_all[place : place + size].reshape(piece.shape)
            high = high_all[place : place + size].reshape(piece.shape)
            place += size
            grown.append(jnp.concatenate([low, b, high], axis=dim))
        blocks = grown
    return blocks


def wave_table(coef_count, float_type):
    half_count = (coef_count - 1) // 2
    order_index = jnp.arange(1, half_count + 1, dtype=jnp.int32).astype(float_type)
    height = 1.0 - 2.0 * (order_index - 0.5) / half_count
    radius = jnp.sqrt(jnp.maximum(1.0 - height * height, 0.0))
    angle_turn = 2.399963 * order_index
    magnitude = 1.5 + jnp.mod(order_index, 3.0)
    return (
        jnp.stack([radius * jnp.cos(angle_turn), radius * jnp.sin(angle_turn), height])
        * magnitude[None]
    )


def waves_at(atom_data, waves):
    shape_lead = (waves.shape[1],) + (1,) * (atom_data.ndim - 1)
    phases = waves[0].reshape(shape_lead) * (atom_data[0] - 0.5)[None]
    phases = phases + waves[1].reshape(shape_lead) * (atom_data[1] - 0.5)[None]
    phases = phases + waves[2].reshape(shape_lead) * (atom_data[2] - 0.5)[None]
    return (jnp.cos(phases), jnp.sin(phases))


def rotate_by(field, phase):
    half_count = phase.shape[0]
    cosine = jnp.cos(phase)
    sine_part = jnp.sin(phase)
    cos_coef = field[1 : 1 + half_count]
    sin_coef = field[1 + half_count :]
    return jnp.concatenate(
        [
            field[0:1],
            cos_coef * cosine - sin_coef * sine_part,
            cos_coef * sine_part + sin_coef * cosine,
        ],
        axis=0,
    )


def offset_phases(waves, offsets):
    table = jnp.array(offsets, dtype=jnp.float32)
    return (
        table[:, 0:1] * waves[0][None]
        + table[:, 1:2] * waves[1][None]
        + table[:, 2:3] * waves[2][None]
    )


def block_phase(waves, size_x, size_y, size_z, float_type):
    place_x = jnp.arange(size_x, dtype=jnp.int32).astype(float_type)
    place_y = jnp.arange(size_y, dtype=jnp.int32).astype(float_type)
    place_z = jnp.arange(size_z, dtype=jnp.int32).astype(float_type)
    phase = waves[0][:, None, None, None] * place_x[None, :, None, None]
    phase = phase + waves[1][:, None, None, None] * place_y[None, None, :, None]
    return phase + waves[2][:, None, None, None] * place_z[None, None, None, :]


def leaf_moments(atom_data, waves, basis=None):
    cosine, sine_part = waves_at(atom_data, waves) if basis is None else basis
    charge = atom_data[3]
    summed = jnp.sum(charge, axis=-1)[None]
    return jnp.concatenate(
        [
            summed,
            jnp.sum(cosine * charge[None], axis=-1),
            jnp.sum(sine_part * charge[None], axis=-1),
        ],
        axis=0,
    )


def evaluate(atom_data, local_exp, waves, basis=None):
    cosine, sine_part = waves_at(atom_data, waves) if basis is None else basis
    half_count = waves.shape[1]
    cos_local = local_exp[1 : 1 + half_count][..., None]
    sin_local = local_exp[1 + half_count :][..., None]
    potential = local_exp[0][..., None] + jnp.sum(
        cos_local * cosine + sin_local * sine_part, axis=0
    )
    mixed_term = cos_local * sine_part - sin_local * cosine
    shape_lead = (half_count,) + (1,) * (mixed_term.ndim - 1)
    field_parts = [
        jnp.sum(waves[component].reshape(shape_lead) * mixed_term, axis=0) for component in range(3)
    ]
    return (potential, field_parts)


def near_row(target, source, flag_grid, shift_vec, keep_self):
    weight = source[3] * flag_grid[..., None]
    delta_x = target[0][..., :, None] - (source[0][..., None, :] + shift_vec[0])
    delta_y = target[1][..., :, None] - (source[1][..., None, :] + shift_vec[1])
    delta_z = target[2][..., :, None] - (source[2][..., None, :] + shift_vec[2])
    inverse = lax.rsqrt(delta_x * delta_x + delta_y * delta_y + delta_z * delta_z + soften)
    pair_term = weight[..., None, :] * keep_self * inverse
    cube_term = pair_term * inverse * inverse
    return jnp.stack(
        [
            jnp.sum(pair_term, axis=-1),
            jnp.sum(cube_term * delta_x, axis=-1),
            jnp.sum(cube_term * delta_y, axis=-1),
            jnp.sum(cube_term * delta_z, axis=-1),
        ]
    )


def full_flags(near_flags, float_type):
    flags_float = near_flags.astype(float_type)
    centre = jnp.ones((1,) + flags_float.shape[1:], float_type)
    return jnp.concatenate([flags_float[:13], centre, flags_float[13:]], axis=0)


def leaf_offsets():
    return [
        (shift_x, shift_y, shift_z)
        for shift_x in (-1, 0, 1)
        for shift_y in (-1, 0, 1)
        for shift_z in (-1, 0, 1)
        if (shift_x, shift_y, shift_z) != (0, 0, 0)
    ]


def parent_offsets():
    return [
        (shift_x, shift_y, shift_z)
        for shift_x in range(-2, 3)
        for shift_y in range(-2, 3)
        for shift_z in range(-2, 3)
        if max(abs(shift_x), abs(shift_y), abs(shift_z)) == 2
    ]


def climb_children(moments, matrices):
    coef_count, size_x, size_y, size_z = moments.shape
    parted = moments.reshape(coef_count, size_x // 2, 2, size_y // 2, 2, size_z // 2, 2)
    return jnp.einsum(
        "abckj,jxaybzc->kxyz",
        matrices.reshape(2, 2, 2, coef_count, coef_count),
        parted,
        precision=highest,
    )


def descend_children(parent_local, matrices):
    coef_count, size_x, size_y, size_z = parent_local.shape
    spread = jnp.einsum(
        "abckj,jxyz->kxaybzc",
        matrices.reshape(2, 2, 2, coef_count, coef_count),
        parent_local,
        precision=highest,
    )
    return spread.reshape(coef_count, 2 * size_x, 2 * size_y, 2 * size_z)


def matrix_vector(matrix, vector):
    return jnp.dot(matrix, vector, precision=highest)


def pick_side(matrices, own_side):
    return lax.dynamic_index_in_dim(matrices, own_side, 0, keepdims=False)


def pair_step(matrices, own_side, current, partner):
    return matrix_vector(pick_side(matrices, own_side), current) + matrix_vector(
        pick_side(matrices, 1 - own_side), partner
    )


def chain_tree(column, tree_up, tree_down, tree_side, lattice, hook):
    climbs = tree_up.astype(jnp.float32)
    lowers = tree_down.astype(jnp.float32)
    sideways = tree_side.astype(jnp.float32)
    current = column
    visited = []
    partner = None
    for level_bit in range(lax.axis_size("gx").bit_length() - 1):
        current = hook(current, partner)
        partner = from_partner(current, "gx", level_bit)
        own_side = lax.axis_index("gx") // 2**level_bit % 2
        current = pair_step(climbs[0], own_side, current, partner)
        visited.append((0, own_side, partner))
    for level_bit in range(lax.axis_size("gy").bit_length() - 1):
        current = hook(current, partner)
        partner = from_partner(current, "gy", level_bit)
        own_side = lax.axis_index("gy") // 2**level_bit % 2
        current = pair_step(climbs[1], own_side, current, partner)
        visited.append((1, own_side, partner))
    local_exp = matrix_vector(lattice.astype(jnp.float32), current)
    for axis_num, own_side, partner in reversed(visited):
        local_exp = matrix_vector(pick_side(lowers[axis_num], own_side), local_exp) + matrix_vector(
            pick_side(sideways[axis_num], own_side), partner
        )
    return local_exp


def flip_pair(column_grid, axis_num, level_bit):
    coef_count, size_x, size_y = column_grid.shape
    span_size = 2**level_bit
    if axis_num == 0:
        parted = column_grid.reshape(coef_count, size_x // (2 * span_size), 2, span_size, size_y)
        return parted[:, :, ::-1].reshape(column_grid.shape)
    parted = column_grid.reshape(coef_count, size_x, size_y // (2 * span_size), 2, span_size)
    return parted[:, :, :, ::-1].reshape(column_grid.shape)


def side_grid(axis_num, level_bit, size_x, size_y):
    positions = jnp.arange(size_x if axis_num == 0 else size_y, dtype=jnp.int32)
    own_side = positions // 2**level_bit % 2
    return own_side[:, None] if axis_num == 0 else own_side[None, :]


def choose_side(matrices, own_side, column_grid):
    first = jnp.einsum("kj,jxy->kxy", matrices[0], column_grid, precision=highest)
    second = jnp.einsum("kj,jxy->kxy", matrices[1], column_grid, precision=highest)
    return jnp.where(own_side[None] == 0, first, second)


def gathered_tree(column, tree_up, tree_down, tree_side, lattice):
    size_x, size_y = lax.axis_size("gx"), lax.axis_size("gy")
    gathered = lax.all_gather(column, ("gx", "gy")).reshape(size_x, size_y, -1)
    current = jnp.transpose(gathered, (2, 0, 1))
    levels = [(0, bit) for bit in range(size_x.bit_length() - 1)] + [
        (1, bit) for bit in range(size_y.bit_length() - 1)
    ]
    visited = []
    for axis_num, level_bit in levels:
        partner = flip_pair(current, axis_num, level_bit)
        own_side = side_grid(axis_num, level_bit, size_x, size_y)
        climbs = tree_up[axis_num].astype(jnp.float32)
        current = choose_side(climbs, own_side, current) + choose_side(climbs, 1 - own_side, partner)
        visited.append((axis_num, own_side, partner))
    local_exp = jnp.einsum("kj,jxy->kxy", lattice.astype(jnp.float32), current, precision=highest)
    for axis_num, own_side, partner in reversed(visited):
        local_exp = choose_side(tree_down[axis_num].astype(jnp.float32), own_side, local_exp) + choose_side(
            tree_side[axis_num].astype(jnp.float32), own_side, partner
        )
    own = lax.dynamic_slice(local_exp, (0, lax.axis_index("gx"), lax.axis_index("gy")), (local_exp.shape[0], 1, 1))
    return own.reshape(-1)


def assemble(near_terms, potential, field_parts, charge, live_slots):
    rows = [coulomb * (near_terms[0] + potential) * live_slots]
    for component in range(3):
        rows.append(coulomb * charge * (near_terms[1 + component] + field_parts[component]))
    return jnp.stack(rows)


NEAR_ROWS = 64
NEAR_PIECES = 8
NEAR_UNROLL = 2


def near_pairs(tx, ty, tz, srow, mask):
    weight = srow[3:4, :]
    delta_x = tx - srow[0:1, :]
    delta_y = ty - srow[1:2, :]
    delta_z = tz - srow[2:3, :]
    inverse = lax.rsqrt(delta_x * delta_x + delta_y * delta_y + delta_z * delta_z + soften)
    pair_term = weight * inverse
    if mask is not None:
        pair_term = jnp.where(mask, pair_term, 0.0)
    cube_term = pair_term * inverse * inverse
    return (pair_term, cube_term * delta_x, cube_term * delta_y, cube_term * delta_z)


def near_kernel(first_leaf, piece_leaves, leaf_count, listed_width, *refs):
    if len(refs) == 7:
        table_ref, target_ref, source_ref, shift_ref, previous_ref, out_ref, tile_ref = refs
        out_ref[...] = previous_ref[...]
    else:
        table_ref, target_ref, source_ref, shift_ref, out_ref, tile_ref = refs
        out_ref[...] = jnp.zeros(out_ref.shape, out_ref.dtype)
    place_start = 2 * leaf_count
    kind_start = place_start + leaf_count * listed_width
    big = NEAR_ROWS
    small = NEAR_ROWS // 2
    lanes = out_ref.shape[2]

    def leaf_body(local, carry):
        leaf = first_leaf + local
        count = table_ref[leaf]
        full_count = count // big
        rest = count - full_count * big
        listed = table_ref[leaf_count + leaf]
        base = leaf * listed_width
        tile_ref[...] = jnp.zeros(tile_ref.shape, tile_ref.dtype)

        def chunk_at(first, rows):
            lane = lax.broadcasted_iota(jnp.int32, (rows, lanes), 1)
            row = lax.broadcasted_iota(jnp.int32, (rows, lanes), 0)
            column = target_ref[local, pl.ds(first, rows), :]
            tx = jnp.broadcast_to(column[:, 0:1], (rows, lanes))
            ty = jnp.broadcast_to(column[:, 1:2], (rows, lanes))
            tz = jnp.broadcast_to(column[:, 2:3], (rows, lanes))
            acc = near_pairs(tx, ty, tz, source_ref[table_ref[place_start + base]], row + first != lane)

            def offset_body(step, acc):
                number = base + 1 + NEAR_UNROLL * step
                for extra in range(NEAR_UNROLL):
                    srow = source_ref[table_ref[place_start + number + extra]]
                    srow = srow + shift_ref[table_ref[kind_start + number + extra]]
                    terms = near_pairs(tx, ty, tz, srow, None)
                    acc = tuple(a + b for a, b in zip(acc, terms))
                return acc

            acc = lax.fori_loop(0, (listed - 1) // NEAR_UNROLL, offset_body, acc)
            sums = [jnp.sum(part, axis=1, keepdims=True) for part in acc]
            tile = jnp.where(
                lane == 0, sums[0], jnp.where(lane == 1, sums[1], jnp.where(lane == 2, sums[2], sums[3]))
            )
            tile_ref[pl.ds(first, rows), :] = jnp.where(lane < 4, tile, 0.0)

        def full_body(chunk, carry2):
            chunk_at(pl.multiple_of(chunk * big, big), big)
            return carry2

        lax.fori_loop(0, full_count, full_body, 0)
        last = pl.multiple_of(full_count * big, small)

        @pl.when(rest > small)
        def _():
            chunk_at(last, big)

        @pl.when((rest > 0) & (rest <= small))
        def _():
            chunk_at(last, small)

        out_ref[leaf] = jnp.transpose(tile_ref[...])[0 : out_ref.shape[1], :]
        return carry

    lax.fori_loop(0, piece_leaves, leaf_body, 0)


def near_local(charged, rimmed, counts, near_flags):
    size_x, size_y, size_z, slot_count = charged.shape[1:]
    leaf_count = size_x * size_y * size_z
    ext_y = size_y + 2
    target = jnp.transpose(charged, (1, 2, 3, 4, 0)).reshape(leaf_count, slot_count, 4)
    source = jnp.transpose(rimmed, (1, 2, 3, 0, 4)).reshape(-1, 4, slot_count)
    source = jnp.pad(source, ((0, 1), (0, 4), (0, 0)))
    empty_leaf = source.shape[0] - 1
    offsets = [(0, 0, 0)] + leaf_offsets()
    shift_rows = np.array([[float(v) for v in offset] + [0.0] * 5 for offset in offsets], np.float32)
    shift_table = jnp.asarray(np.ascontiguousarray(np.broadcast_to(shift_rows[:, :, None], (len(offsets), 8, slot_count))))
    leaf_x = jnp.arange(size_x, dtype=jnp.int32)[:, None, None]
    leaf_y = jnp.arange(size_y, dtype=jnp.int32)[None, :, None]
    leaf_z = jnp.arange(size_z, dtype=jnp.int32)[None, None, :]
    places = []
    for offset in offsets:
        place = ((leaf_x + 1 + offset[0]) * ext_y + leaf_y + 1 + offset[1]) * size_z + leaf_z + offset[2]
        places.append(jnp.broadcast_to(place, (size_x, size_y, size_z)))
    places = jnp.stack(places).reshape(len(offsets), leaf_count)
    layer = jnp.arange(size_z, dtype=jnp.int32)
    valid = jnp.stack([((layer + offset[2] >= 0) & (layer + offset[2] < size_z)) for offset in offsets[1:]])
    active = (near_flags != 0) & valid[:, None, None, :]
    active = jnp.concatenate([jnp.ones((1, leaf_count), bool), active.reshape(len(offsets) - 1, leaf_count)])
    listed = jnp.sum(active.astype(jnp.int32), axis=0)
    listed = listed + (NEAR_UNROLL - (listed - 1) % NEAR_UNROLL) % NEAR_UNROLL
    position = jnp.cumsum(active.astype(jnp.int32), axis=0) - 1
    width = 1 + -(-(len(offsets) - 1) // NEAR_UNROLL) * NEAR_UNROLL
    slots = jnp.arange(width, dtype=jnp.int32)
    chosen = active[None] & (position[None] == slots[:, None, None])
    kinds = jnp.arange(len(offsets), dtype=jnp.int32)
    kind_list = jnp.sum(jnp.where(chosen, kinds[None, :, None], 0), axis=1)
    place_list = jnp.sum(jnp.where(chosen, places[None], 0), axis=1)
    place_list = jnp.where(slots[:, None] < jnp.sum(active.astype(jnp.int32), axis=0)[None], place_list, empty_leaf)
    table = jnp.concatenate(
        [counts.reshape(-1), listed, jnp.transpose(place_list).reshape(-1), jnp.transpose(kind_list).reshape(-1)]
    ).astype(jnp.int32)
    piece = leaf_count // NEAR_PIECES if leaf_count % NEAR_PIECES == 0 else leaf_count
    pairs = piece * slot_count * slot_count * 10

    chained = []

    def run_piece(number, gate):
        first_leaf = number * piece
        own = target[first_leaf : first_leaf + piece]
        if gate is not None:
            own, unused = lax.optimization_barrier((own, gate))
        operands = [table, own, source, shift_table] + chained[-1:]
        result = pl.pallas_call(
            functools.partial(near_kernel, first_leaf, piece, leaf_count, width),
            out_shape=jax.ShapeDtypeStruct((leaf_count, 8, slot_count), jnp.float32),
            in_specs=[pl.BlockSpec(memory_space=pltpu.SMEM)] + [pl.BlockSpec(memory_space=pltpu.VMEM)] * (len(operands) - 1),
            out_specs=pl.BlockSpec(memory_space=pltpu.VMEM),
            scratch_shapes=[pltpu.VMEM((slot_count, 128), jnp.float32)],
            input_output_aliases={4: 0} if chained else {},
            cost_estimate=pl.CostEstimate(
                flops=20 * pairs, transcendentals=pairs, bytes_accessed=8 * piece * slot_count * 128
            ),
        )(*operands)
        chained.append(result)
        return result

    def finish_near(outs):
        near = jnp.transpose(chained[-1][:, :4, :], (1, 0, 2))
        return near.reshape(4, size_x, size_y, size_z, slot_count)

    return leaf_count // piece, run_piece, finish_near


def body(
    atom_data,
    counts,
    near_flags,
    child_up,
    child_down,
    leaf_far,
    parent_far,
    column_up,
    column_down,
    tree_up,
    tree_down,
    tree_side,
    lattice,
):
    coef_count = lattice.shape[0]
    slot_count = atom_data.shape[4]
    size_x, size_y, size_z = (atom_data.shape[1], atom_data.shape[2], atom_data.shape[3])
    live_slots = (
        jnp.arange(slot_count, dtype=jnp.int32)[None, None, None, :] < counts[..., None]
    ).astype(jnp.float32)
    charged = jnp.concatenate([atom_data[:3], (atom_data[3] * live_slots)[None]], axis=0)
    waves = wave_table(coef_count, jnp.float32)
    half_count = waves.shape[1]
    basis = lax.optimization_barrier(waves_at(charged, waves))
    moments = leaf_moments(charged, waves, basis)
    parents = climb_children(moments, child_up.astype(jnp.float32))
    rimmed, parent_rim, leaf_rim = extended_joint([(charged, 1), (parents, 2), (moments, 1)], (("gx", 1), ("gy", 2)))
    parent_rim = jnp.pad(parent_rim, ((0, 0), (0, 0), (0, 0), (2, 2)))
    half_x, half_y, half_z = (parents.shape[1], parents.shape[2], parents.shape[3])
    phase_grid = block_phase(waves, half_x, half_y, half_z, jnp.float32)
    turned = jnp.sum(rotate_by(parents, phase_grid), axis=(1, 2, 3))
    column = matrix_vector(column_up.astype(jnp.float32), turned)
    piece_count, run_piece, finish_near = near_local(charged, rimmed, counts, near_flags)
    pieces = []

    sent = []

    def hook(value, prior):
        number = len(pieces)
        if number < piece_count:
            if number > 0:
                value, unused = lax.optimization_barrier((value, pieces[-1]))
            pieces.append(run_piece(number, prior))
        sent.append(value)
        return value

    column_local = chain_tree(column, tree_up, tree_down, tree_side, lattice, hook)
    while len(pieces) < piece_count:
        pieces.append(run_piece(len(pieces), sent[-1]))
    near_terms = finish_near(pieces)
    leaf_rim = jnp.pad(leaf_rim, ((0, 0), (0, 0), (0, 0), (1, 1)))
    lowered = matrix_vector(column_down.astype(jnp.float32), column_local)
    parent_local = rotate_by(
        jnp.broadcast_to(lowered[:, None, None, None], parents.shape), -phase_grid
    )
    far_parents = parent_offsets()
    parent_stack = jnp.stack(
        [
            parent_rim[
                :,
                2 + offset[0] : 2 + offset[0] + half_x,
                2 + offset[1] : 2 + offset[1] + half_y,
                2 + offset[2] : 2 + offset[2] + half_z,
            ]
            for offset in far_parents
        ]
    )
    parent_turns = offset_phases(waves, far_parents).reshape(len(far_parents), half_count, 1, 1, 1)
    parent_sum = jnp.sum(jax.vmap(rotate_by)(parent_stack, parent_turns), axis=0)
    parent_local = parent_local + jnp.einsum(
        "kj,jxyz->kxyz", parent_far.astype(jnp.float32), parent_sum, precision=highest
    )
    leaf_local = descend_children(parent_local, child_down.astype(jnp.float32))
    near_leaves = leaf_offsets()
    leaf_stack = jnp.stack(
        [
            leaf_rim[
                :,
                1 + offset[0] : 1 + offset[0] + size_x,
                1 + offset[1] : 1 + offset[1] + size_y,
                1 + offset[2] : 1 + offset[2] + size_z,
            ]
            for offset in near_leaves
        ]
    )
    leaf_stack = leaf_stack * (1.0 - near_flags.astype(jnp.float32))[:, None]
    leaf_turns = offset_phases(waves, near_leaves).reshape(len(near_leaves), half_count, 1, 1, 1)
    leaf_sum = jnp.sum(jax.vmap(rotate_by)(leaf_stack, leaf_turns), axis=0)
    leaf_local = leaf_local + jnp.einsum(
        "kj,jxyz->kxyz", leaf_far.astype(jnp.float32), leaf_sum, precision=highest
    )
    potential, field_parts = evaluate(charged, leaf_local, waves, basis)
    return assemble(near_terms, potential, field_parts, charged[3], live_slots)


def solution(mesh):
    in_specs = (
        P(None, "gx", "gy", None, None),
        P("gx", "gy", None),
        P(None, "gx", "gy", None),
        P(),
        P(),
        P(),
        P(),
        P(),
        P(),
        P(),
        P(),
        P(),
        P(),
    )
    out_specs = P(None, "gx", "gy", None, None)
    return jax.shard_map(body, mesh=mesh, in_specs=in_specs, out_specs=out_specs, check_vma=False)
```

```python
import functools

import jax
import numpy as np
import jax.numpy as jnp
from jax import lax
from jax.experimental import pallas as pl
from jax.experimental.pallas import tpu as pltpu
from jax.sharding import PartitionSpec as P

soften = 0.04
coulomb = 0.1
highest = lax.Precision.HIGHEST


def from_partner(value, axis, bit):
    mask = 2**bit
    pairs = [(source, source ^ mask) for source in range(lax.axis_size(axis))]
    return lax.ppermute(value, axis, pairs)


def extended_2(block, sides, width):
    return extended_joint([(block, width)], sides)[0]


def extended_joint(parts, sides):
    blocks = [block for block, width in parts]
    for axis, dim in sides:
        count = lax.axis_size(axis)
        forward = [(i, i + 1) for i in range(count - 1)]
        forward.append((count - 1, 0))
        backward = [(target, source) for source, target in forward]
        lows = [lax.slice_in_dim(b, b.shape[dim] - w, None, axis=dim) for b, (_, w) in zip(blocks, parts)]
        highs = [lax.slice_in_dim(b, 0, w, axis=dim) for b, (_, w) in zip(blocks, parts)]
        sizes = [piece.size for piece in lows]
        low_all = lax.ppermute(jnp.concatenate([piece.reshape(-1) for piece in lows]), axis, forward)
        high_all = lax.ppermute(jnp.concatenate([piece.reshape(-1) for piece in highs]), axis, backward)
        grown = []
        place = 0
        for b, piece, size in zip(blocks, lows, sizes):
            low = low_all[place : place + size].reshape(piece.shape)
            high = high_all[place : place + size].reshape(piece.shape)
            place += size
            grown.append(jnp.concatenate([low, b, high], axis=dim))
        blocks = grown
    return blocks


def wave_table(coef_count, float_type):
    half_count = (coef_count - 1) // 2
    order_index = jnp.arange(1, half_count + 1, dtype=jnp.int32).astype(float_type)
    height = 1.0 - 2.0 * (order_index - 0.5) / half_count
    radius = jnp.sqrt(jnp.maximum(1.0 - height * height, 0.0))
    angle_turn = 2.399963 * order_index
    magnitude = 1.5 + jnp.mod(order_index, 3.0)
    return (
        jnp.stack([radius * jnp.cos(angle_turn), radius * jnp.sin(angle_turn), height])
        * magnitude[None]
    )


def waves_at(atom_data, waves):
    shape_lead = (waves.shape[1],) + (1,) * (atom_data.ndim - 1)
    phases = waves[0].reshape(shape_lead) * (atom_data[0] - 0.5)[None]
    phases = phases + waves[1].reshape(shape_lead) * (atom_data[1] - 0.5)[None]
    phases = phases + waves[2].reshape(shape_lead) * (atom_data[2] - 0.5)[None]
    return (jnp.cos(phases), jnp.sin(phases))


def rotate_by(field, phase):
    half_count = phase.shape[0]
    cosine = jnp.cos(phase)
    sine_part = jnp.sin(phase)
    cos_coef = field[1 : 1 + half_count]
    sin_coef = field[1 + half_count :]
    return jnp.concatenate(
        [
            field[0:1],
            cos_coef * cosine - sin_coef * sine_part,
            cos_coef * sine_part + sin_coef * cosine,
        ],
        axis=0,
    )


def offset_phases(waves, offsets):
    table = jnp.array(offsets, dtype=jnp.float32)
    return (
        table[:, 0:1] * waves[0][None]
        + table[:, 1:2] * waves[1][None]
        + table[:, 2:3] * waves[2][None]
    )


def block_phase(waves, size_x, size_y, size_z, float_type):
    place_x = jnp.arange(size_x, dtype=jnp.int32).astype(float_type)
    place_y = jnp.arange(size_y, dtype=jnp.int32).astype(float_type)
    place_z = jnp.arange(size_z, dtype=jnp.int32).astype(float_type)
    phase = waves[0][:, None, None, None] * place_x[None, :, None, None]
    phase = phase + waves[1][:, None, None, None] * place_y[None, None, :, None]
    return phase + waves[2][:, None, None, None] * place_z[None, None, None, :]


def leaf_moments(atom_data, waves):
    cosine, sine_part = waves_at(atom_data, waves)
    charge = atom_data[3]
    summed = jnp.sum(charge, axis=-1)[None]
    return jnp.concatenate(
        [
            summed,
            jnp.sum(cosine * charge[None], axis=-1),
            jnp.sum(sine_part * charge[None], axis=-1),
        ],
        axis=0,
    )


def evaluate(atom_data, local_exp, waves):
    cosine, sine_part = waves_at(atom_data, waves)
    half_count = waves.shape[1]
    cos_local = local_exp[1 : 1 + half_count][..., None]
    sin_local = local_exp[1 + half_count :][..., None]
    potential = local_exp[0][..., None] + jnp.sum(
        cos_local * cosine + sin_local * sine_part, axis=0
    )
    mixed_term = cos_local * sine_part - sin_local * cosine
    shape_lead = (half_count,) + (1,) * (mixed_term.ndim - 1)
    field_parts = [
        jnp.sum(waves[component].reshape(shape_lead) * mixed_term, axis=0) for component in range(3)
    ]
    return (potential, field_parts)


def near_row(target, source, flag_grid, shift_vec, keep_self):
    weight = source[3] * flag_grid[..., None]
    delta_x = target[0][..., :, None] - (source[0][..., None, :] + shift_vec[0])
    delta_y = target[1][..., :, None] - (source[1][..., None, :] + shift_vec[1])
    delta_z = target[2][..., :, None] - (source[2][..., None, :] + shift_vec[2])
    inverse = lax.rsqrt(delta_x * delta_x + delta_y * delta_y + delta_z * delta_z + soften)
    pair_term = weight[..., None, :] * keep_self * inverse
    cube_term = pair_term * inverse * inverse
    return jnp.stack(
        [
            jnp.sum(pair_term, axis=-1),
            jnp.sum(cube_term * delta_x, axis=-1),
            jnp.sum(cube_term * delta_y, axis=-1),
            jnp.sum(cube_term * delta_z, axis=-1),
        ]
    )


def full_flags(near_flags, float_type):
    flags_float = near_flags.astype(float_type)
    centre = jnp.ones((1,) + flags_float.shape[1:], float_type)
    return jnp.concatenate([flags_float[:13], centre, flags_float[13:]], axis=0)


def leaf_offsets():
    return [
        (shift_x, shift_y, shift_z)
        for shift_x in (-1, 0, 1)
        for shift_y in (-1, 0, 1)
        for shift_z in (-1, 0, 1)
        if (shift_x, shift_y, shift_z) != (0, 0, 0)
    ]


def parent_offsets():
    return [
        (shift_x, shift_y, shift_z)
        for shift_x in range(-2, 3)
        for shift_y in range(-2, 3)
        for shift_z in range(-2, 3)
        if max(abs(shift_x), abs(shift_y), abs(shift_z)) == 2
    ]


def climb_children(moments, matrices):
    coef_count, size_x, size_y, size_z = moments.shape
    parted = moments.reshape(coef_count, size_x // 2, 2, size_y // 2, 2, size_z // 2, 2)
    return jnp.einsum(
        "abckj,jxaybzc->kxyz",
        matrices.reshape(2, 2, 2, coef_count, coef_count),
        parted,
        precision=highest,
    )


def descend_children(parent_local, matrices):
    coef_count, size_x, size_y, size_z = parent_local.shape
    spread = jnp.einsum(
        "abckj,jxyz->kxaybzc",
        matrices.reshape(2, 2, 2, coef_count, coef_count),
        parent_local,
        precision=highest,
    )
    return spread.reshape(coef_count, 2 * size_x, 2 * size_y, 2 * size_z)


def matrix_vector(matrix, vector):
    return jnp.dot(matrix, vector, precision=highest)


def pick_side(matrices, own_side):
    return lax.dynamic_index_in_dim(matrices, own_side, 0, keepdims=False)


def pair_step(matrices, own_side, current, partner):
    return matrix_vector(pick_side(matrices, own_side), current) + matrix_vector(
        pick_side(matrices, 1 - own_side), partner
    )


def chain_tree(column, tree_up, tree_down, tree_side, lattice, hook):
    climbs = tree_up.astype(jnp.float32)
    lowers = tree_down.astype(jnp.float32)
    sideways = tree_side.astype(jnp.float32)
    current = column
    visited = []
    partner = None
    for level_bit in range(lax.axis_size("gx").bit_length() - 1):
        current = hook(current, partner)
        partner = from_partner(current, "gx", level_bit)
        own_side = lax.axis_index("gx") // 2**level_bit % 2
        current = pair_step(climbs[0], own_side, current, partner)
        visited.append((0, own_side, partner))
    for level_bit in range(lax.axis_size("gy").bit_length() - 1):
        current = hook(current, partner)
        partner = from_partner(current, "gy", level_bit)
        own_side = lax.axis_index("gy") // 2**level_bit % 2
        current = pair_step(climbs[1], own_side, current, partner)
        visited.append((1, own_side, partner))
    local_exp = matrix_vector(lattice.astype(jnp.float32), current)
    for axis_num, own_side, partner in reversed(visited):
        local_exp = matrix_vector(pick_side(lowers[axis_num], own_side), local_exp) + matrix_vector(
            pick_side(sideways[axis_num], own_side), partner
        )
    return local_exp


def flip_pair(column_grid, axis_num, level_bit):
    coef_count, size_x, size_y = column_grid.shape
    span_size = 2**level_bit
    if axis_num == 0:
        parted = column_grid.reshape(coef_count, size_x // (2 * span_size), 2, span_size, size_y)
        return parted[:, :, ::-1].reshape(column_grid.shape)
    parted = column_grid.reshape(coef_count, size_x, size_y // (2 * span_size), 2, span_size)
    return parted[:, :, :, ::-1].reshape(column_grid.shape)


def side_grid(axis_num, level_bit, size_x, size_y):
    positions = jnp.arange(size_x if axis_num == 0 else size_y, dtype=jnp.int32)
    own_side = positions // 2**level_bit % 2
    return own_side[:, None] if axis_num == 0 else own_side[None, :]


def choose_side(matrices, own_side, column_grid):
    first = jnp.einsum("kj,jxy->kxy", matrices[0], column_grid, precision=highest)
    second = jnp.einsum("kj,jxy->kxy", matrices[1], column_grid, precision=highest)
    return jnp.where(own_side[None] == 0, first, second)


def gathered_tree(column, tree_up, tree_down, tree_side, lattice):
    size_x, size_y = lax.axis_size("gx"), lax.axis_size("gy")
    gathered = lax.all_gather(column, ("gx", "gy")).reshape(size_x, size_y, -1)
    current = jnp.transpose(gathered, (2, 0, 1))
    levels = [(0, bit) for bit in range(size_x.bit_length() - 1)] + [
        (1, bit) for bit in range(size_y.bit_length() - 1)
    ]
    visited = []
    for axis_num, level_bit in levels:
        partner = flip_pair(current, axis_num, level_bit)
        own_side = side_grid(axis_num, level_bit, size_x, size_y)
        climbs = tree_up[axis_num].astype(jnp.float32)
        current = choose_side(climbs, own_side, current) + choose_side(climbs, 1 - own_side, partner)
        visited.append((axis_num, own_side, partner))
    local_exp = jnp.einsum("kj,jxy->kxy", lattice.astype(jnp.float32), current, precision=highest)
    for axis_num, own_side, partner in reversed(visited):
        local_exp = choose_side(tree_down[axis_num].astype(jnp.float32), own_side, local_exp) + choose_side(
            tree_side[axis_num].astype(jnp.float32), own_side, partner
        )
    own = lax.dynamic_slice(local_exp, (0, lax.axis_index("gx"), lax.axis_index("gy")), (local_exp.shape[0], 1, 1))
    return own.reshape(-1)


def assemble(near_terms, potential, field_parts, charge, live_slots):
    rows = [coulomb * (near_terms[0] + potential) * live_slots]
    for component in range(3):
        rows.append(coulomb * charge * (near_terms[1 + component] + field_parts[component]))
    return jnp.stack(rows)


NEAR_ROWS = 64
NEAR_PIECES = 8
NEAR_HOOKED = 5
NEAR_UNROLL = 2


def near_pairs(tx, ty, tz, srow, mask):
    weight = srow[3:4, :]
    delta_x = tx - srow[0:1, :]
    delta_y = ty - srow[1:2, :]
    delta_z = tz - srow[2:3, :]
    inverse = lax.rsqrt(delta_x * delta_x + delta_y * delta_y + delta_z * delta_z + soften)
    pair_term = weight * inverse
    if mask is not None:
        pair_term = jnp.where(mask, pair_term, 0.0)
    cube_term = pair_term * inverse * inverse
    return (pair_term, cube_term * delta_x, cube_term * delta_y, cube_term * delta_z)


def near_kernel(first_leaf, piece_leaves, leaf_count, listed_width, *refs):
    if len(refs) == 7:
        table_ref, target_ref, source_ref, shift_ref, previous_ref, out_ref, tile_ref = refs
        out_ref[...] = previous_ref[...]
    else:
        table_ref, target_ref, source_ref, shift_ref, out_ref, tile_ref = refs
        out_ref[...] = jnp.zeros(out_ref.shape, out_ref.dtype)
    place_start = 2 * leaf_count
    kind_start = place_start + leaf_count * listed_width
    big = NEAR_ROWS
    small = NEAR_ROWS // 2
    lanes = out_ref.shape[2]

    def leaf_body(local, carry):
        leaf = first_leaf + local
        count = table_ref[leaf]
        full_count = count // big
        rest = count - full_count * big
        listed = table_ref[leaf_count + leaf]
        base = leaf * listed_width
        tile_ref[...] = jnp.zeros(tile_ref.shape, tile_ref.dtype)

        def chunk_at(first, rows):
            lane = lax.broadcasted_iota(jnp.int32, (rows, lanes), 1)
            row = lax.broadcasted_iota(jnp.int32, (rows, lanes), 0)
            column = target_ref[local, pl.ds(first, rows), :]
            tx = jnp.broadcast_to(column[:, 0:1], (rows, lanes))
            ty = jnp.broadcast_to(column[:, 1:2], (rows, lanes))
            tz = jnp.broadcast_to(column[:, 2:3], (rows, lanes))
            acc = near_pairs(tx, ty, tz, source_ref[table_ref[place_start + base]], row + first != lane)

            def offset_body(step, acc):
                number = base + 1 + NEAR_UNROLL * step
                for extra in range(NEAR_UNROLL):
                    srow = source_ref[table_ref[place_start + number + extra]]
                    srow = srow + shift_ref[table_ref[kind_start + number + extra]]
                    terms = near_pairs(tx, ty, tz, srow, None)
                    acc = tuple(a + b for a, b in zip(acc, terms))
                return acc

            acc = lax.fori_loop(0, (listed - 1) // NEAR_UNROLL, offset_body, acc)
            sums = [jnp.sum(part, axis=1, keepdims=True) for part in acc]
            tile = jnp.where(
                lane == 0, sums[0], jnp.where(lane == 1, sums[1], jnp.where(lane == 2, sums[2], sums[3]))
            )
            tile_ref[pl.ds(first, rows), :] = jnp.where(lane < 4, tile, 0.0)

        def full_body(chunk, carry2):
            chunk_at(pl.multiple_of(chunk * big, big), big)
            return carry2

        lax.fori_loop(0, full_count, full_body, 0)
        last = pl.multiple_of(full_count * big, small)

        @pl.when(rest > small)
        def _():
            chunk_at(last, big)

        @pl.when((rest > 0) & (rest <= small))
        def _():
            chunk_at(last, small)

        out_ref[leaf] = jnp.transpose(tile_ref[...])[0 : out_ref.shape[1], :]
        return carry

    lax.fori_loop(0, piece_leaves, leaf_body, 0)


def near_local(charged, rimmed, counts, near_flags):
    size_x, size_y, size_z, slot_count = charged.shape[1:]
    leaf_count = size_x * size_y * size_z
    ext_y = size_y + 2
    target = jnp.transpose(charged, (1, 2, 3, 4, 0)).reshape(leaf_count, slot_count, 4)
    source = jnp.transpose(rimmed, (1, 2, 3, 0, 4)).reshape(-1, 4, slot_count)
    source = jnp.pad(source, ((0, 1), (0, 4), (0, 0)))
    empty_leaf = source.shape[0] - 1
    offsets = [(0, 0, 0)] + leaf_offsets()
    shift_rows = np.array([[float(v) for v in offset] + [0.0] * 5 for offset in offsets], np.float32)
    shift_table = jnp.asarray(np.ascontiguousarray(np.broadcast_to(shift_rows[:, :, None], (len(offsets), 8, slot_count))))
    leaf_x = jnp.arange(size_x, dtype=jnp.int32)[:, None, None]
    leaf_y = jnp.arange(size_y, dtype=jnp.int32)[None, :, None]
    leaf_z = jnp.arange(size_z, dtype=jnp.int32)[None, None, :]
    places = []
    for offset in offsets:
        place = ((leaf_x + 1 + offset[0]) * ext_y + leaf_y + 1 + offset[1]) * size_z + leaf_z + offset[2]
        places.append(jnp.broadcast_to(place, (size_x, size_y, size_z)))
    places = jnp.stack(places).reshape(len(offsets), leaf_count)
    layer = jnp.arange(size_z, dtype=jnp.int32)
    valid = jnp.stack([((layer + offset[2] >= 0) & (layer + offset[2] < size_z)) for offset in offsets[1:]])
    active = (near_flags != 0) & valid[:, None, None, :]
    active = jnp.concatenate([jnp.ones((1, leaf_count), bool), active.reshape(len(offsets) - 1, leaf_count)])
    listed = jnp.sum(active.astype(jnp.int32), axis=0)
    listed = listed + (NEAR_UNROLL - (listed - 1) % NEAR_UNROLL) % NEAR_UNROLL
    position = jnp.cumsum(active.astype(jnp.int32), axis=0) - 1
    width = 1 + -(-(len(offsets) - 1) // NEAR_UNROLL) * NEAR_UNROLL
    slots = jnp.arange(width, dtype=jnp.int32)
    chosen = active[None] & (position[None] == slots[:, None, None])
    kinds = jnp.arange(len(offsets), dtype=jnp.int32)
    kind_list = jnp.sum(jnp.where(chosen, kinds[None, :, None], 0), axis=1)
    place_list = jnp.sum(jnp.where(chosen, places[None], 0), axis=1)
    place_list = jnp.where(slots[:, None] < jnp.sum(active.astype(jnp.int32), axis=0)[None], place_list, empty_leaf)
    table = jnp.concatenate(
        [counts.reshape(-1), listed, jnp.transpose(place_list).reshape(-1), jnp.transpose(kind_list).reshape(-1)]
    ).astype(jnp.int32)
    piece = leaf_count // NEAR_PIECES if leaf_count % NEAR_PIECES == 0 else leaf_count
    sizes = [piece] * min(NEAR_HOOKED, leaf_count // piece - 1)
    sizes.append(leaf_count - sum(sizes))
    starts = [sum(sizes[:number]) for number in range(len(sizes))]

    chained = []

    def run_piece(number, gate):
        first_leaf, size = starts[number], sizes[number]
        pairs = size * slot_count * slot_count * 10
        own = target[first_leaf : first_leaf + size]
        if gate is not None:
            own, unused = lax.optimization_barrier((own, gate))
        operands = [table, own, source, shift_table] + chained[-1:]
        result = pl.pallas_call(
            functools.partial(near_kernel, first_leaf, size, leaf_count, width),
            out_shape=jax.ShapeDtypeStruct((leaf_count, 8, slot_count), jnp.float32),
            in_specs=[pl.BlockSpec(memory_space=pltpu.SMEM)] + [pl.BlockSpec(memory_space=pltpu.VMEM)] * (len(operands) - 1),
            out_specs=pl.BlockSpec(memory_space=pltpu.VMEM),
            scratch_shapes=[pltpu.VMEM((slot_count, 128), jnp.float32)],
            input_output_aliases={4: 0} if chained else {},
            cost_estimate=pl.CostEstimate(
                flops=20 * pairs, transcendentals=pairs, bytes_accessed=8 * size * slot_count * 128
            ),
        )(*operands)
        chained.append(result)
        return result

    def finish_near(outs):
        near = jnp.transpose(chained[-1][:, :4, :], (1, 0, 2))
        return near.reshape(4, size_x, size_y, size_z, slot_count)

    return len(sizes), run_piece, finish_near


def body(
    atom_data,
    counts,
    near_flags,
    child_up,
    child_down,
    leaf_far,
    parent_far,
    column_up,
    column_down,
    tree_up,
    tree_down,
    tree_side,
    lattice,
):
    coef_count = lattice.shape[0]
    slot_count = atom_data.shape[4]
    size_x, size_y, size_z = (atom_data.shape[1], atom_data.shape[2], atom_data.shape[3])
    live_slots = (
        jnp.arange(slot_count, dtype=jnp.int32)[None, None, None, :] < counts[..., None]
    ).astype(jnp.float32)
    charged = jnp.concatenate([atom_data[:3], (atom_data[3] * live_slots)[None]], axis=0)
    waves = wave_table(coef_count, jnp.float32)
    half_count = waves.shape[1]
    moments = leaf_moments(charged, waves)
    parents = climb_children(moments, child_up.astype(jnp.float32))
    rimmed, parent_rim, leaf_rim = extended_joint([(charged, 1), (parents, 2), (moments, 1)], (("gx", 1), ("gy", 2)))
    parent_rim = jnp.pad(parent_rim, ((0, 0), (0, 0), (0, 0), (2, 2)))
    half_x, half_y, half_z = (parents.shape[1], parents.shape[2], parents.shape[3])
    phase_grid = block_phase(waves, half_x, half_y, half_z, jnp.float32)
    turned = jnp.sum(rotate_by(parents, phase_grid), axis=(1, 2, 3))
    column = matrix_vector(column_up.astype(jnp.float32), turned)
    piece_count, run_piece, finish_near = near_local(charged, rimmed, counts, near_flags)
    pieces = []

    sent = []

    def hook(value, prior):
        number = len(pieces)
        if number < piece_count:
            if number > 0:
                value, unused = lax.optimization_barrier((value, pieces[-1]))
            pieces.append(run_piece(number, prior))
        sent.append(value)
        return value

    column_local = chain_tree(column, tree_up, tree_down, tree_side, lattice, hook)
    while len(pieces) < piece_count:
        pieces.append(run_piece(len(pieces), sent[-1]))
    near_terms = finish_near(pieces)
    leaf_rim = jnp.pad(leaf_rim, ((0, 0), (0, 0), (0, 0), (1, 1)))
    lowered = matrix_vector(column_down.astype(jnp.float32), column_local)
    parent_local = rotate_by(
        jnp.broadcast_to(lowered[:, None, None, None], parents.shape), -phase_grid
    )
    far_parents = parent_offsets()
    parent_stack = jnp.stack(
        [
            parent_rim[
                :,
                2 + offset[0] : 2 + offset[0] + half_x,
                2 + offset[1] : 2 + offset[1] + half_y,
                2 + offset[2] : 2 + offset[2] + half_z,
            ]
            for offset in far_parents
        ]
    )
    parent_turns = offset_phases(waves, far_parents).reshape(len(far_parents), half_count, 1, 1, 1)
    parent_sum = jnp.sum(jax.vmap(rotate_by)(parent_stack, parent_turns), axis=0)
    parent_local = parent_local + jnp.einsum(
        "kj,jxyz->kxyz", parent_far.astype(jnp.float32), parent_sum, precision=highest
    )
    leaf_local = descend_children(parent_local, child_down.astype(jnp.float32))
    near_leaves = leaf_offsets()
    leaf_stack = jnp.stack(
        [
            leaf_rim[
                :,
                1 + offset[0] : 1 + offset[0] + size_x,
                1 + offset[1] : 1 + offset[1] + size_y,
                1 + offset[2] : 1 + offset[2] + size_z,
            ]
            for offset in near_leaves
        ]
    )
    leaf_stack = leaf_stack * (1.0 - near_flags.astype(jnp.float32))[:, None]
    leaf_turns = offset_phases(waves, near_leaves).reshape(len(near_leaves), half_count, 1, 1, 1)
    leaf_sum = jnp.sum(jax.vmap(rotate_by)(leaf_stack, leaf_turns), axis=0)
    leaf_local = leaf_local + jnp.einsum(
        "kj,jxyz->kxyz", leaf_far.astype(jnp.float32), leaf_sum, precision=highest
    )
    potential, field_parts = evaluate(charged, leaf_local, waves)
    return assemble(near_terms, potential, field_parts, charged[3], live_slots)


def solution(mesh):
    in_specs = (
        P(None, "gx", "gy", None, None),
        P("gx", "gy", None),
        P(None, "gx", "gy", None),
        P(),
        P(),
        P(),
        P(),
        P(),
        P(),
        P(),
        P(),
        P(),
        P(),
    )
    out_specs = P(None, "gx", "gy", None, None)
    return jax.shard_map(body, mesh=mesh, in_specs=in_specs, out_specs=out_specs, check_vma=False)
```

```python
import functools

import jax
import numpy as np
import jax.numpy as jnp
from jax import lax
from jax.experimental import pallas as pl
from jax.experimental.pallas import tpu as pltpu
from jax.sharding import PartitionSpec as P

soften = 0.04
coulomb = 0.1
highest = lax.Precision.HIGHEST


def from_partner(value, axis, bit):
    mask = 2**bit
    pairs = [(source, source ^ mask) for source in range(lax.axis_size(axis))]
    return lax.ppermute(value, axis, pairs)


def extended_2(block, sides, width):
    return extended_joint([(block, width)], sides)[0]


def extended_joint(parts, sides):
    blocks = [block for block, width in parts]
    for axis, dim in sides:
        count = lax.axis_size(axis)
        forward = [(i, i + 1) for i in range(count - 1)]
        forward.append((count - 1, 0))
        backward = [(target, source) for source, target in forward]
        lows = [lax.slice_in_dim(b, b.shape[dim] - w, None, axis=dim) for b, (_, w) in zip(blocks, parts)]
        highs = [lax.slice_in_dim(b, 0, w, axis=dim) for b, (_, w) in zip(blocks, parts)]
        sizes = [piece.size for piece in lows]
        low_all = lax.ppermute(jnp.concatenate([piece.reshape(-1) for piece in lows]), axis, forward)
        high_all = lax.ppermute(jnp.concatenate([piece.reshape(-1) for piece in highs]), axis, backward)
        grown = []
        place = 0
        for b, piece, size in zip(blocks, lows, sizes):
            low = low_all[place : place + size].reshape(piece.shape)
            high = high_all[place : place + size].reshape(piece.shape)
            place += size
            grown.append(jnp.concatenate([low, b, high], axis=dim))
        blocks = grown
    return blocks


def wave_table(coef_count, float_type):
    half_count = (coef_count - 1) // 2
    order_index = jnp.arange(1, half_count + 1, dtype=jnp.int32).astype(float_type)
    height = 1.0 - 2.0 * (order_index - 0.5) / half_count
    radius = jnp.sqrt(jnp.maximum(1.0 - height * height, 0.0))
    angle_turn = 2.399963 * order_index
    magnitude = 1.5 + jnp.mod(order_index, 3.0)
    return (
        jnp.stack([radius * jnp.cos(angle_turn), radius * jnp.sin(angle_turn), height])
        * magnitude[None]
    )


def waves_at(atom_data, waves):
    shape_lead = (waves.shape[1],) + (1,) * (atom_data.ndim - 1)
    phases = waves[0].reshape(shape_lead) * (atom_data[0] - 0.5)[None]
    phases = phases + waves[1].reshape(shape_lead) * (atom_data[1] - 0.5)[None]
    phases = phases + waves[2].reshape(shape_lead) * (atom_data[2] - 0.5)[None]
    return (jnp.cos(phases), jnp.sin(phases))


def rotate_by(field, phase):
    half_count = phase.shape[0]
    cosine = jnp.cos(phase)
    sine_part = jnp.sin(phase)
    cos_coef = field[1 : 1 + half_count]
    sin_coef = field[1 + half_count :]
    return jnp.concatenate(
        [
            field[0:1],
            cos_coef * cosine - sin_coef * sine_part,
            cos_coef * sine_part + sin_coef * cosine,
        ],
        axis=0,
    )


def offset_phases(waves, offsets):
    table = jnp.array(offsets, dtype=jnp.float32)
    return (
        table[:, 0:1] * waves[0][None]
        + table[:, 1:2] * waves[1][None]
        + table[:, 2:3] * waves[2][None]
    )


def block_phase(waves, size_x, size_y, size_z, float_type):
    place_x = jnp.arange(size_x, dtype=jnp.int32).astype(float_type)
    place_y = jnp.arange(size_y, dtype=jnp.int32).astype(float_type)
    place_z = jnp.arange(size_z, dtype=jnp.int32).astype(float_type)
    phase = waves[0][:, None, None, None] * place_x[None, :, None, None]
    phase = phase + waves[1][:, None, None, None] * place_y[None, None, :, None]
    return phase + waves[2][:, None, None, None] * place_z[None, None, None, :]


def leaf_moments(atom_data, waves):
    cosine, sine_part = waves_at(atom_data, waves)
    charge = atom_data[3]
    summed = jnp.sum(charge, axis=-1)[None]
    return jnp.concatenate(
        [
            summed,
            jnp.sum(cosine * charge[None], axis=-1),
            jnp.sum(sine_part * charge[None], axis=-1),
        ],
        axis=0,
    )


def evaluate(atom_data, local_exp, waves):
    cosine, sine_part = waves_at(atom_data, waves)
    half_count = waves.shape[1]
    cos_local = local_exp[1 : 1 + half_count][..., None]
    sin_local = local_exp[1 + half_count :][..., None]
    potential = local_exp[0][..., None] + jnp.sum(
        cos_local * cosine + sin_local * sine_part, axis=0
    )
    mixed_term = cos_local * sine_part - sin_local * cosine
    shape_lead = (half_count,) + (1,) * (mixed_term.ndim - 1)
    field_parts = [
        jnp.sum(waves[component].reshape(shape_lead) * mixed_term, axis=0) for component in range(3)
    ]
    return (potential, field_parts)


def near_row(target, source, flag_grid, shift_vec, keep_self):
    weight = source[3] * flag_grid[..., None]
    delta_x = target[0][..., :, None] - (source[0][..., None, :] + shift_vec[0])
    delta_y = target[1][..., :, None] - (source[1][..., None, :] + shift_vec[1])
    delta_z = target[2][..., :, None] - (source[2][..., None, :] + shift_vec[2])
    inverse = lax.rsqrt(delta_x * delta_x + delta_y * delta_y + delta_z * delta_z + soften)
    pair_term = weight[..., None, :] * keep_self * inverse
    cube_term = pair_term * inverse * inverse
    return jnp.stack(
        [
            jnp.sum(pair_term, axis=-1),
            jnp.sum(cube_term * delta_x, axis=-1),
            jnp.sum(cube_term * delta_y, axis=-1),
            jnp.sum(cube_term * delta_z, axis=-1),
        ]
    )


def full_flags(near_flags, float_type):
    flags_float = near_flags.astype(float_type)
    centre = jnp.ones((1,) + flags_float.shape[1:], float_type)
    return jnp.concatenate([flags_float[:13], centre, flags_float[13:]], axis=0)


def leaf_offsets():
    return [
        (shift_x, shift_y, shift_z)
        for shift_x in (-1, 0, 1)
        for shift_y in (-1, 0, 1)
        for shift_z in (-1, 0, 1)
        if (shift_x, shift_y, shift_z) != (0, 0, 0)
    ]


def parent_offsets():
    return [
        (shift_x, shift_y, shift_z)
        for shift_x in range(-2, 3)
        for shift_y in range(-2, 3)
        for shift_z in range(-2, 3)
        if max(abs(shift_x), abs(shift_y), abs(shift_z)) == 2
    ]


def climb_children(moments, matrices):
    coef_count, size_x, size_y, size_z = moments.shape
    parted = moments.reshape(coef_count, size_x // 2, 2, size_y // 2, 2, size_z // 2, 2)
    return jnp.einsum(
        "abckj,jxaybzc->kxyz",
        matrices.reshape(2, 2, 2, coef_count, coef_count),
        parted,
        precision=highest,
    )


def descend_children(parent_local, matrices):
    coef_count, size_x, size_y, size_z = parent_local.shape
    spread = jnp.einsum(
        "abckj,jxyz->kxaybzc",
        matrices.reshape(2, 2, 2, coef_count, coef_count),
        parent_local,
        precision=highest,
    )
    return spread.reshape(coef_count, 2 * size_x, 2 * size_y, 2 * size_z)


def matrix_vector(matrix, vector):
    return jnp.dot(matrix, vector, precision=highest)


def pick_side(matrices, own_side):
    return lax.dynamic_index_in_dim(matrices, own_side, 0, keepdims=False)


def pair_step(matrices, own_side, current, partner):
    return matrix_vector(pick_side(matrices, own_side), current) + matrix_vector(
        pick_side(matrices, 1 - own_side), partner
    )


def chain_tree(column, tree_up, tree_down, tree_side, lattice, hook):
    climbs = tree_up.astype(jnp.float32)
    lowers = tree_down.astype(jnp.float32)
    sideways = tree_side.astype(jnp.float32)
    current = column
    visited = []
    partner = None
    for level_bit in range(lax.axis_size("gx").bit_length() - 1):
        current = hook(current, partner)
        partner = from_partner(current, "gx", level_bit)
        own_side = lax.axis_index("gx") // 2**level_bit % 2
        current = pair_step(climbs[0], own_side, current, partner)
        visited.append((0, own_side, partner))
    for level_bit in range(lax.axis_size("gy").bit_length() - 1):
        current = hook(current, partner)
        partner = from_partner(current, "gy", level_bit)
        own_side = lax.axis_index("gy") // 2**level_bit % 2
        current = pair_step(climbs[1], own_side, current, partner)
        visited.append((1, own_side, partner))
    local_exp = matrix_vector(lattice.astype(jnp.float32), current)
    for axis_num, own_side, partner in reversed(visited):
        local_exp = matrix_vector(pick_side(lowers[axis_num], own_side), local_exp) + matrix_vector(
            pick_side(sideways[axis_num], own_side), partner
        )
    return local_exp


def flip_pair(column_grid, axis_num, level_bit):
    coef_count, size_x, size_y = column_grid.shape
    span_size = 2**level_bit
    if axis_num == 0:
        parted = column_grid.reshape(coef_count, size_x // (2 * span_size), 2, span_size, size_y)
        return parted[:, :, ::-1].reshape(column_grid.shape)
    parted = column_grid.reshape(coef_count, size_x, size_y // (2 * span_size), 2, span_size)
    return parted[:, :, :, ::-1].reshape(column_grid.shape)


def side_grid(axis_num, level_bit, size_x, size_y):
    positions = jnp.arange(size_x if axis_num == 0 else size_y, dtype=jnp.int32)
    own_side = positions // 2**level_bit % 2
    return own_side[:, None] if axis_num == 0 else own_side[None, :]


def choose_side(matrices, own_side, column_grid):
    first = jnp.einsum("kj,jxy->kxy", matrices[0], column_grid, precision=highest)
    second = jnp.einsum("kj,jxy->kxy", matrices[1], column_grid, precision=highest)
    return jnp.where(own_side[None] == 0, first, second)


def gathered_tree(column, tree_up, tree_down, tree_side, lattice):
    size_x, size_y = lax.axis_size("gx"), lax.axis_size("gy")
    gathered = lax.all_gather(column, ("gx", "gy")).reshape(size_x, size_y, -1)
    current = jnp.transpose(gathered, (2, 0, 1))
    levels = [(0, bit) for bit in range(size_x.bit_length() - 1)] + [
        (1, bit) for bit in range(size_y.bit_length() - 1)
    ]
    visited = []
    for axis_num, level_bit in levels:
        partner = flip_pair(current, axis_num, level_bit)
        own_side = side_grid(axis_num, level_bit, size_x, size_y)
        climbs = tree_up[axis_num].astype(jnp.float32)
        current = choose_side(climbs, own_side, current) + choose_side(climbs, 1 - own_side, partner)
        visited.append((axis_num, own_side, partner))
    local_exp = jnp.einsum("kj,jxy->kxy", lattice.astype(jnp.float32), current, precision=highest)
    for axis_num, own_side, partner in reversed(visited):
        local_exp = choose_side(tree_down[axis_num].astype(jnp.float32), own_side, local_exp) + choose_side(
            tree_side[axis_num].astype(jnp.float32), own_side, partner
        )
    own = lax.dynamic_slice(local_exp, (0, lax.axis_index("gx"), lax.axis_index("gy")), (local_exp.shape[0], 1, 1))
    return own.reshape(-1)


def assemble(near_terms, potential, field_parts, charge, live_slots):
    rows = [coulomb * (near_terms[0] + potential) * live_slots]
    for component in range(3):
        rows.append(coulomb * charge * (near_terms[1 + component] + field_parts[component]))
    return jnp.stack(rows)


NEAR_ROWS = 64
NEAR_PIECES = 8
NEAR_UNROLL = 2


def near_pairs(tx, ty, tz, srow, mask):
    weight = srow[3:4, :]
    delta_x = tx - srow[0:1, :]
    delta_y = ty - srow[1:2, :]
    delta_z = tz - srow[2:3, :]
    inverse = lax.rsqrt(delta_x * delta_x + delta_y * delta_y + delta_z * delta_z + soften)
    pair_term = weight * inverse
    if mask is not None:
        pair_term = jnp.where(mask, pair_term, 0.0)
    cube_term = pair_term * inverse * inverse
    return (pair_term, cube_term * delta_x, cube_term * delta_y, cube_term * delta_z)


def near_kernel(first_leaf, piece_leaves, leaf_count, listed_width, *refs):
    if len(refs) == 7:
        table_ref, target_ref, source_ref, shift_ref, previous_ref, out_ref, tile_ref = refs
        out_ref[...] = previous_ref[...]
    else:
        table_ref, target_ref, source_ref, shift_ref, out_ref, tile_ref = refs
        out_ref[...] = jnp.zeros(out_ref.shape, out_ref.dtype)
    place_start = 2 * leaf_count
    kind_start = place_start + leaf_count * listed_width
    big = NEAR_ROWS
    small = NEAR_ROWS // 2
    lanes = out_ref.shape[2]

    def leaf_body(local, carry):
        leaf = first_leaf + local
        count = table_ref[leaf]
        full_count = count // big
        rest = count - full_count * big
        listed = table_ref[leaf_count + leaf]
        base = leaf * listed_width
        tile_ref[...] = jnp.zeros(tile_ref.shape, tile_ref.dtype)

        def chunk_at(first, rows):
            lane = lax.broadcasted_iota(jnp.int32, (rows, lanes), 1)
            row = lax.broadcasted_iota(jnp.int32, (rows, lanes), 0)
            column = target_ref[local, pl.ds(first, rows), :]
            tx = jnp.broadcast_to(column[:, 0:1], (rows, lanes))
            ty = jnp.broadcast_to(column[:, 1:2], (rows, lanes))
            tz = jnp.broadcast_to(column[:, 2:3], (rows, lanes))
            acc = near_pairs(tx, ty, tz, source_ref[table_ref[place_start + base]], row + first != lane)

            def offset_body(step, acc):
                number = base + 1 + NEAR_UNROLL * step
                for extra in range(NEAR_UNROLL):
                    srow = source_ref[table_ref[place_start + number + extra]]
                    srow = srow + shift_ref[table_ref[kind_start + number + extra]]
                    terms = near_pairs(tx, ty, tz, srow, None)
                    acc = tuple(a + b for a, b in zip(acc, terms))
                return acc

            acc = lax.fori_loop(0, (listed - 1) // NEAR_UNROLL, offset_body, acc)
            sums = [jnp.sum(part, axis=1, keepdims=True) for part in acc]
            tile = jnp.where(
                lane == 0, sums[0], jnp.where(lane == 1, sums[1], jnp.where(lane == 2, sums[2], sums[3]))
            )
            tile_ref[pl.ds(first, rows), :] = jnp.where(lane < 4, tile, 0.0)

        def full_body(chunk, carry2):
            chunk_at(pl.multiple_of(chunk * big, big), big)
            return carry2

        lax.fori_loop(0, full_count, full_body, 0)
        last = pl.multiple_of(full_count * big, small)

        @pl.when(rest > small)
        def _():
            chunk_at(last, big)

        @pl.when((rest > 0) & (rest <= small))
        def _():
            chunk_at(last, small)

        out_ref[leaf] = jnp.transpose(tile_ref[...])[0 : out_ref.shape[1], :]
        return carry

    lax.fori_loop(0, piece_leaves, leaf_body, 0)


def near_local(charged, rimmed, counts, near_flags):
    size_x, size_y, size_z, slot_count = charged.shape[1:]
    leaf_count = size_x * size_y * size_z
    ext_y = size_y + 2
    target = jnp.transpose(charged, (1, 2, 3, 4, 0)).reshape(leaf_count, slot_count, 4)
    source = jnp.transpose(rimmed, (1, 2, 3, 0, 4)).reshape(-1, 4, slot_count)
    source = jnp.pad(source, ((0, 1), (0, 4), (0, 0)))
    empty_leaf = source.shape[0] - 1
    offsets = [(0, 0, 0)] + leaf_offsets()
    shift_rows = np.array([[float(v) for v in offset] + [0.0] * 5 for offset in offsets], np.float32)
    shift_table = jnp.asarray(np.ascontiguousarray(np.broadcast_to(shift_rows[:, :, None], (len(offsets), 8, slot_count))))
    leaf_x = jnp.arange(size_x, dtype=jnp.int32)[:, None, None]
    leaf_y = jnp.arange(size_y, dtype=jnp.int32)[None, :, None]
    leaf_z = jnp.arange(size_z, dtype=jnp.int32)[None, None, :]
    places = []
    for offset in offsets:
        place = ((leaf_x + 1 + offset[0]) * ext_y + leaf_y + 1 + offset[1]) * size_z + leaf_z + offset[2]
        places.append(jnp.broadcast_to(place, (size_x, size_y, size_z)))
    places = jnp.stack(places).reshape(len(offsets), leaf_count)
    layer = jnp.arange(size_z, dtype=jnp.int32)
    valid = jnp.stack([((layer + offset[2] >= 0) & (layer + offset[2] < size_z)) for offset in offsets[1:]])
    active = (near_flags != 0) & valid[:, None, None, :]
    active = jnp.concatenate([jnp.ones((1, leaf_count), bool), active.reshape(len(offsets) - 1, leaf_count)])
    listed = jnp.sum(active.astype(jnp.int32), axis=0)
    listed = listed + (NEAR_UNROLL - (listed - 1) % NEAR_UNROLL) % NEAR_UNROLL
    position = jnp.cumsum(active.astype(jnp.int32), axis=0) - 1
    width = 1 + -(-(len(offsets) - 1) // NEAR_UNROLL) * NEAR_UNROLL
    slots = jnp.arange(width, dtype=jnp.int32)
    chosen = active[None] & (position[None] == slots[:, None, None])
    kinds = jnp.arange(len(offsets), dtype=jnp.int32)
    kind_list = jnp.sum(jnp.where(chosen, kinds[None, :, None], 0), axis=1)
    place_list = jnp.sum(jnp.where(chosen, places[None], 0), axis=1)
    place_list = jnp.where(slots[:, None] < jnp.sum(active.astype(jnp.int32), axis=0)[None], place_list, empty_leaf)
    table = jnp.concatenate(
        [counts.reshape(-1), listed, jnp.transpose(place_list).reshape(-1), jnp.transpose(kind_list).reshape(-1)]
    ).astype(jnp.int32)
    piece = leaf_count // NEAR_PIECES if leaf_count % NEAR_PIECES == 0 else leaf_count
    pairs = piece * slot_count * slot_count * 10

    chained = []

    def run_piece(number, gate):
        first_leaf = number * piece
        own = target[first_leaf : first_leaf + piece]
        if gate is not None:
            own, unused = lax.optimization_barrier((own, gate))
        operands = [table, own, source, shift_table] + chained[-1:]
        result = pl.pallas_call(
            functools.partial(near_kernel, first_leaf, piece, leaf_count, width),
            out_shape=jax.ShapeDtypeStruct((leaf_count, 8, slot_count), jnp.float32),
            in_specs=[pl.BlockSpec(memory_space=pltpu.SMEM)] + [pl.BlockSpec(memory_space=pltpu.VMEM)] * (len(operands) - 1),
            out_specs=pl.BlockSpec(memory_space=pltpu.VMEM),
            scratch_shapes=[pltpu.VMEM((slot_count, 128), jnp.float32)],
            input_output_aliases={4: 0} if chained else {},
            cost_estimate=pl.CostEstimate(
                flops=20 * pairs, transcendentals=pairs, bytes_accessed=8 * piece * slot_count * 128
            ),
        )(*operands)
        chained.append(result)
        return result

    def finish_near(outs):
        near = jnp.transpose(chained[-1][:, :4, :], (1, 0, 2))
        return near.reshape(4, size_x, size_y, size_z, slot_count)

    return leaf_count // piece, run_piece, finish_near


def body(
    atom_data,
    counts,
    near_flags,
    child_up,
    child_down,
    leaf_far,
    parent_far,
    column_up,
    column_down,
    tree_up,
    tree_down,
    tree_side,
    lattice,
):
    coef_count = lattice.shape[0]
    slot_count = atom_data.shape[4]
    size_x, size_y, size_z = (atom_data.shape[1], atom_data.shape[2], atom_data.shape[3])
    live_slots = (
        jnp.arange(slot_count, dtype=jnp.int32)[None, None, None, :] < counts[..., None]
    ).astype(jnp.float32)
    charged = jnp.concatenate([atom_data[:3], (atom_data[3] * live_slots)[None]], axis=0)
    waves = wave_table(coef_count, jnp.float32)
    rimmed = extended_2(charged, (("gx", 1), ("gy", 2)), 1)
    half_count = waves.shape[1]
    moments = leaf_moments(charged, waves)
    parents = climb_children(moments, child_up.astype(jnp.float32))
    sent_parents, sent_moments, unused = lax.optimization_barrier((parents, moments, rimmed))
    parent_rim, leaf_rim = extended_joint([(sent_parents, 2), (sent_moments, 1)], (("gx", 1), ("gy", 2)))
    parent_rim = jnp.pad(parent_rim, ((0, 0), (0, 0), (0, 0), (2, 2)))
    half_x, half_y, half_z = (parents.shape[1], parents.shape[2], parents.shape[3])
    phase_grid = block_phase(waves, half_x, half_y, half_z, jnp.float32)
    turned = jnp.sum(rotate_by(parents, phase_grid), axis=(1, 2, 3))
    column = matrix_vector(column_up.astype(jnp.float32), turned)
    piece_count, run_piece, finish_near = near_local(charged, rimmed, counts, near_flags)
    pieces = []

    sent = []

    def hook(value, prior):
        number = len(pieces)
        if number < piece_count:
            if number > 0:
                value, unused = lax.optimization_barrier((value, pieces[-1]))
            pieces.append(run_piece(number, prior))
        sent.append(value)
        return value

    column_local = chain_tree(column, tree_up, tree_down, tree_side, lattice, hook)
    while len(pieces) < piece_count:
        pieces.append(run_piece(len(pieces), (sent[-1], parent_rim, leaf_rim)))
    near_terms = finish_near(pieces)
    leaf_rim = jnp.pad(leaf_rim, ((0, 0), (0, 0), (0, 0), (1, 1)))
    lowered = matrix_vector(column_down.astype(jnp.float32), column_local)
    parent_local = rotate_by(
        jnp.broadcast_to(lowered[:, None, None, None], parents.shape), -phase_grid
    )
    far_parents = parent_offsets()
    parent_stack = jnp.stack(
        [
            parent_rim[
                :,
                2 + offset[0] : 2 + offset[0] + half_x,
                2 + offset[1] : 2 + offset[1] + half_y,
                2 + offset[2] : 2 + offset[2] + half_z,
            ]
            for offset in far_parents
        ]
    )
    parent_turns = offset_phases(waves, far_parents).reshape(len(far_parents), half_count, 1, 1, 1)
    parent_sum = jnp.sum(jax.vmap(rotate_by)(parent_stack, parent_turns), axis=0)
    parent_local = parent_local + jnp.einsum(
        "kj,jxyz->kxyz", parent_far.astype(jnp.float32), parent_sum, precision=highest
    )
    leaf_local = descend_children(parent_local, child_down.astype(jnp.float32))
    near_leaves = leaf_offsets()
    leaf_stack = jnp.stack(
        [
            leaf_rim[
                :,
                1 + offset[0] : 1 + offset[0] + size_x,
                1 + offset[1] : 1 + offset[1] + size_y,
                1 + offset[2] : 1 + offset[2] + size_z,
            ]
            for offset in near_leaves
        ]
    )
    leaf_stack = leaf_stack * (1.0 - near_flags.astype(jnp.float32))[:, None]
    leaf_turns = offset_phases(waves, near_leaves).reshape(len(near_leaves), half_count, 1, 1, 1)
    leaf_sum = jnp.sum(jax.vmap(rotate_by)(leaf_stack, leaf_turns), axis=0)
    leaf_local = leaf_local + jnp.einsum(
        "kj,jxyz->kxyz", leaf_far.astype(jnp.float32), leaf_sum, precision=highest
    )
    potential, field_parts = evaluate(charged, leaf_local, waves)
    return assemble(near_terms, potential, field_parts, charged[3], live_slots)


def solution(mesh):
    in_specs = (
        P(None, "gx", "gy", None, None),
        P("gx", "gy", None),
        P(None, "gx", "gy", None),
        P(),
        P(),
        P(),
        P(),
        P(),
        P(),
        P(),
        P(),
        P(),
        P(),
    )
    out_specs = P(None, "gx", "gy", None, None)
    return jax.shard_map(body, mesh=mesh, in_specs=in_specs, out_specs=out_specs, check_vma=False)
```

```python
import functools

import jax
import numpy as np
import jax.numpy as jnp
from jax import lax
from jax.experimental import pallas as pl
from jax.experimental.pallas import tpu as pltpu
from jax.sharding import PartitionSpec as P

soften = 0.04
coulomb = 0.1
highest = lax.Precision.HIGHEST


def from_partner(value, axis, bit):
    mask = 2**bit
    pairs = [(source, source ^ mask) for source in range(lax.axis_size(axis))]
    return lax.ppermute(value, axis, pairs)


def extended_2(block, sides, width):
    return extended_joint([(block, width)], sides)[0]


def extended_joint(parts, sides):
    blocks = [block for block, width in parts]
    for axis, dim in sides:
        count = lax.axis_size(axis)
        forward = [(i, i + 1) for i in range(count - 1)]
        forward.append((count - 1, 0))
        backward = [(target, source) for source, target in forward]
        lows = [lax.slice_in_dim(b, b.shape[dim] - w, None, axis=dim) for b, (_, w) in zip(blocks, parts)]
        highs = [lax.slice_in_dim(b, 0, w, axis=dim) for b, (_, w) in zip(blocks, parts)]
        sizes = [piece.size for piece in lows]
        low_all = lax.ppermute(jnp.concatenate([piece.reshape(-1) for piece in lows]), axis, forward)
        high_all = lax.ppermute(jnp.concatenate([piece.reshape(-1) for piece in highs]), axis, backward)
        grown = []
        place = 0
        for b, piece, size in zip(blocks, lows, sizes):
            low = low_all[place : place + size].reshape(piece.shape)
            high = high_all[place : place + size].reshape(piece.shape)
            place += size
            grown.append(jnp.concatenate([low, b, high], axis=dim))
        blocks = grown
    return blocks


def wave_table(coef_count, float_type):
    half_count = (coef_count - 1) // 2
    order_index = jnp.arange(1, half_count + 1, dtype=jnp.int32).astype(float_type)
    height = 1.0 - 2.0 * (order_index - 0.5) / half_count
    radius = jnp.sqrt(jnp.maximum(1.0 - height * height, 0.0))
    angle_turn = 2.399963 * order_index
    magnitude = 1.5 + jnp.mod(order_index, 3.0)
    return (
        jnp.stack([radius * jnp.cos(angle_turn), radius * jnp.sin(angle_turn), height])
        * magnitude[None]
    )


def waves_at(atom_data, waves):
    shape_lead = (waves.shape[1],) + (1,) * (atom_data.ndim - 1)
    phases = waves[0].reshape(shape_lead) * (atom_data[0] - 0.5)[None]
    phases = phases + waves[1].reshape(shape_lead) * (atom_data[1] - 0.5)[None]
    phases = phases + waves[2].reshape(shape_lead) * (atom_data[2] - 0.5)[None]
    return (jnp.cos(phases), jnp.sin(phases))


def rotate_by(field, phase):
    half_count = phase.shape[0]
    cosine = jnp.cos(phase)
    sine_part = jnp.sin(phase)
    cos_coef = field[1 : 1 + half_count]
    sin_coef = field[1 + half_count :]
    return jnp.concatenate(
        [
            field[0:1],
            cos_coef * cosine - sin_coef * sine_part,
            cos_coef * sine_part + sin_coef * cosine,
        ],
        axis=0,
    )


def offset_phases(waves, offsets):
    table = jnp.array(offsets, dtype=jnp.float32)
    return (
        table[:, 0:1] * waves[0][None]
        + table[:, 1:2] * waves[1][None]
        + table[:, 2:3] * waves[2][None]
    )


def block_phase(waves, size_x, size_y, size_z, float_type):
    place_x = jnp.arange(size_x, dtype=jnp.int32).astype(float_type)
    place_y = jnp.arange(size_y, dtype=jnp.int32).astype(float_type)
    place_z = jnp.arange(size_z, dtype=jnp.int32).astype(float_type)
    phase = waves[0][:, None, None, None] * place_x[None, :, None, None]
    phase = phase + waves[1][:, None, None, None] * place_y[None, None, :, None]
    return phase + waves[2][:, None, None, None] * place_z[None, None, None, :]


def leaf_moments(atom_data, waves):
    cosine, sine_part = waves_at(atom_data, waves)
    charge = atom_data[3]
    summed = jnp.sum(charge, axis=-1)[None]
    return jnp.concatenate(
        [
            summed,
            jnp.sum(cosine * charge[None], axis=-1),
            jnp.sum(sine_part * charge[None], axis=-1),
        ],
        axis=0,
    )


def evaluate(atom_data, local_exp, waves):
    cosine, sine_part = waves_at(atom_data, waves)
    half_count = waves.shape[1]
    cos_local = local_exp[1 : 1 + half_count][..., None]
    sin_local = local_exp[1 + half_count :][..., None]
    potential = local_exp[0][..., None] + jnp.sum(
        cos_local * cosine + sin_local * sine_part, axis=0
    )
    mixed_term = cos_local * sine_part - sin_local * cosine
    shape_lead = (half_count,) + (1,) * (mixed_term.ndim - 1)
    field_parts = [
        jnp.sum(waves[component].reshape(shape_lead) * mixed_term, axis=0) for component in range(3)
    ]
    return (potential, field_parts)


def near_row(target, source, flag_grid, shift_vec, keep_self):
    weight = source[3] * flag_grid[..., None]
    delta_x = target[0][..., :, None] - (source[0][..., None, :] + shift_vec[0])
    delta_y = target[1][..., :, None] - (source[1][..., None, :] + shift_vec[1])
    delta_z = target[2][..., :, None] - (source[2][..., None, :] + shift_vec[2])
    inverse = lax.rsqrt(delta_x * delta_x + delta_y * delta_y + delta_z * delta_z + soften)
    pair_term = weight[..., None, :] * keep_self * inverse
    cube_term = pair_term * inverse * inverse
    return jnp.stack(
        [
            jnp.sum(pair_term, axis=-1),
            jnp.sum(cube_term * delta_x, axis=-1),
            jnp.sum(cube_term * delta_y, axis=-1),
            jnp.sum(cube_term * delta_z, axis=-1),
        ]
    )


def full_flags(near_flags, float_type):
    flags_float = near_flags.astype(float_type)
    centre = jnp.ones((1,) + flags_float.shape[1:], float_type)
    return jnp.concatenate([flags_float[:13], centre, flags_float[13:]], axis=0)


def leaf_offsets():
    return [
        (shift_x, shift_y, shift_z)
        for shift_x in (-1, 0, 1)
        for shift_y in (-1, 0, 1)
        for shift_z in (-1, 0, 1)
        if (shift_x, shift_y, shift_z) != (0, 0, 0)
    ]


def parent_offsets():
    return [
        (shift_x, shift_y, shift_z)
        for shift_x in range(-2, 3)
        for shift_y in range(-2, 3)
        for shift_z in range(-2, 3)
        if max(abs(shift_x), abs(shift_y), abs(shift_z)) == 2
    ]


def climb_children(moments, matrices):
    coef_count, size_x, size_y, size_z = moments.shape
    parted = moments.reshape(coef_count, size_x // 2, 2, size_y // 2, 2, size_z // 2, 2)
    return jnp.einsum(
        "abckj,jxaybzc->kxyz",
        matrices.reshape(2, 2, 2, coef_count, coef_count),
        parted,
        precision=highest,
    )


def descend_children(parent_local, matrices):
    coef_count, size_x, size_y, size_z = parent_local.shape
    spread = jnp.einsum(
        "abckj,jxyz->kxaybzc",
        matrices.reshape(2, 2, 2, coef_count, coef_count),
        parent_local,
        precision=highest,
    )
    return spread.reshape(coef_count, 2 * size_x, 2 * size_y, 2 * size_z)


def matrix_vector(matrix, vector):
    return jnp.dot(matrix, vector, precision=highest)


def pick_side(matrices, own_side):
    return lax.dynamic_index_in_dim(matrices, own_side, 0, keepdims=False)


def pair_step(matrices, own_side, current, partner):
    return matrix_vector(pick_side(matrices, own_side), current) + matrix_vector(
        pick_side(matrices, 1 - own_side), partner
    )


def chain_tree(column, tree_up, tree_down, tree_side, lattice, hook):
    climbs = tree_up.astype(jnp.float32)
    lowers = tree_down.astype(jnp.float32)
    sideways = tree_side.astype(jnp.float32)
    current = column
    visited = []
    partner = None
    for level_bit in range(lax.axis_size("gx").bit_length() - 1):
        current = hook(current, partner)
        partner = from_partner(current, "gx", level_bit)
        own_side = lax.axis_index("gx") // 2**level_bit % 2
        current = pair_step(climbs[0], own_side, current, partner)
        visited.append((0, own_side, partner))
    for level_bit in range(lax.axis_size("gy").bit_length() - 1):
        current = hook(current, partner)
        partner = from_partner(current, "gy", level_bit)
        own_side = lax.axis_index("gy") // 2**level_bit % 2
        current = pair_step(climbs[1], own_side, current, partner)
        visited.append((1, own_side, partner))
    local_exp = matrix_vector(lattice.astype(jnp.float32), current)
    for axis_num, own_side, partner in reversed(visited):
        local_exp = matrix_vector(pick_side(lowers[axis_num], own_side), local_exp) + matrix_vector(
            pick_side(sideways[axis_num], own_side), partner
        )
    return local_exp


def flip_pair(column_grid, axis_num, level_bit):
    coef_count, size_x, size_y = column_grid.shape
    span_size = 2**level_bit
    if axis_num == 0:
        parted = column_grid.reshape(coef_count, size_x // (2 * span_size), 2, span_size, size_y)
        return parted[:, :, ::-1].reshape(column_grid.shape)
    parted = column_grid.reshape(coef_count, size_x, size_y // (2 * span_size), 2, span_size)
    return parted[:, :, :, ::-1].reshape(column_grid.shape)


def side_grid(axis_num, level_bit, size_x, size_y):
    positions = jnp.arange(size_x if axis_num == 0 else size_y, dtype=jnp.int32)
    own_side = positions // 2**level_bit % 2
    return own_side[:, None] if axis_num == 0 else own_side[None, :]


def choose_side(matrices, own_side, column_grid):
    first = jnp.einsum("kj,jxy->kxy", matrices[0], column_grid, precision=highest)
    second = jnp.einsum("kj,jxy->kxy", matrices[1], column_grid, precision=highest)
    return jnp.where(own_side[None] == 0, first, second)


def gathered_tree(column, tree_up, tree_down, tree_side, lattice):
    size_x, size_y = lax.axis_size("gx"), lax.axis_size("gy")
    gathered = lax.all_gather(column, ("gx", "gy")).reshape(size_x, size_y, -1)
    current = jnp.transpose(gathered, (2, 0, 1))
    levels = [(0, bit) for bit in range(size_x.bit_length() - 1)] + [
        (1, bit) for bit in range(size_y.bit_length() - 1)
    ]
    visited = []
    for axis_num, level_bit in levels:
        partner = flip_pair(current, axis_num, level_bit)
        own_side = side_grid(axis_num, level_bit, size_x, size_y)
        climbs = tree_up[axis_num].astype(jnp.float32)
        current = choose_side(climbs, own_side, current) + choose_side(climbs, 1 - own_side, partner)
        visited.append((axis_num, own_side, partner))
    local_exp = jnp.einsum("kj,jxy->kxy", lattice.astype(jnp.float32), current, precision=highest)
    for axis_num, own_side, partner in reversed(visited):
        local_exp = choose_side(tree_down[axis_num].astype(jnp.float32), own_side, local_exp) + choose_side(
            tree_side[axis_num].astype(jnp.float32), own_side, partner
        )
    own = lax.dynamic_slice(local_exp, (0, lax.axis_index("gx"), lax.axis_index("gy")), (local_exp.shape[0], 1, 1))
    return own.reshape(-1)


def assemble(near_terms, potential, field_parts, charge, live_slots):
    rows = [coulomb * (near_terms[0] + potential) * live_slots]
    for component in range(3):
        rows.append(coulomb * charge * (near_terms[1 + component] + field_parts[component]))
    return jnp.stack(rows)


NEAR_ROWS = 64
NEAR_PIECES = 8
NEAR_UNROLL = 2


def near_pairs(tx, ty, tz, srow, mask):
    weight = srow[3:4, :]
    delta_x = tx - srow[0:1, :]
    delta_y = ty - srow[1:2, :]
    delta_z = tz - srow[2:3, :]
    inverse = lax.rsqrt(delta_x * delta_x + delta_y * delta_y + delta_z * delta_z + soften)
    pair_term = weight * inverse
    if mask is not None:
        pair_term = jnp.where(mask, pair_term, 0.0)
    cube_term = pair_term * inverse * inverse
    return (pair_term, cube_term * delta_x, cube_term * delta_y, cube_term * delta_z)


def near_kernel(first_leaf, piece_leaves, leaf_count, listed_width, *refs):
    if len(refs) == 7:
        table_ref, target_ref, source_ref, shift_ref, previous_ref, out_ref, tile_ref = refs
        out_ref[...] = previous_ref[...]
    else:
        table_ref, target_ref, source_ref, shift_ref, out_ref, tile_ref = refs
        out_ref[...] = jnp.zeros(out_ref.shape, out_ref.dtype)
    place_start = 2 * leaf_count
    kind_start = place_start + leaf_count * listed_width
    big = NEAR_ROWS
    small = NEAR_ROWS // 2
    lanes = out_ref.shape[2]

    def leaf_body(local, carry):
        leaf = first_leaf + local
        count = table_ref[leaf]
        full_count = count // big
        rest = count - full_count * big
        listed = table_ref[leaf_count + leaf]
        base = leaf * listed_width
        tile_ref[...] = jnp.zeros(tile_ref.shape, tile_ref.dtype)

        def chunk_at(first, rows):
            lane = lax.broadcasted_iota(jnp.int32, (rows, lanes), 1)
            row = lax.broadcasted_iota(jnp.int32, (rows, lanes), 0)
            column = target_ref[local, pl.ds(first, rows), :]
            tx = jnp.broadcast_to(column[:, 0:1], (rows, lanes))
            ty = jnp.broadcast_to(column[:, 1:2], (rows, lanes))
            tz = jnp.broadcast_to(column[:, 2:3], (rows, lanes))
            acc = near_pairs(tx, ty, tz, source_ref[table_ref[place_start + base]], row + first != lane)

            def offset_body(step, acc):
                number = base + 1 + NEAR_UNROLL * step
                for extra in range(NEAR_UNROLL):
                    srow = source_ref[table_ref[place_start + number + extra]]
                    srow = srow + shift_ref[table_ref[kind_start + number + extra]]
                    terms = near_pairs(tx, ty, tz, srow, None)
                    acc = tuple(a + b for a, b in zip(acc, terms))
                return acc

            acc = lax.fori_loop(0, (listed - 1) // NEAR_UNROLL, offset_body, acc)
            sums = [jnp.sum(part, axis=1, keepdims=True) for part in acc]
            tile = jnp.where(
                lane == 0, sums[0], jnp.where(lane == 1, sums[1], jnp.where(lane == 2, sums[2], sums[3]))
            )
            tile_ref[pl.ds(first, rows), :] = jnp.where(lane < 4, tile, 0.0)

        def full_body(chunk, carry2):
            chunk_at(pl.multiple_of(chunk * big, big), big)
            return carry2

        lax.fori_loop(0, full_count, full_body, 0)
        last = pl.multiple_of(full_count * big, small)

        @pl.when(rest > small)
        def _():
            chunk_at(last, big)

        @pl.when((rest > 0) & (rest <= small))
        def _():
            chunk_at(last, small)

        out_ref[:, pl.ds(leaf, 1), :] = jnp.transpose(tile_ref[...])[0 : out_ref.shape[0], None, :]
        return carry

    lax.fori_loop(0, piece_leaves, leaf_body, 0)


def near_local(charged, rimmed, counts, near_flags):
    size_x, size_y, size_z, slot_count = charged.shape[1:]
    leaf_count = size_x * size_y * size_z
    ext_y = size_y + 2
    target = jnp.transpose(charged, (1, 2, 3, 4, 0)).reshape(leaf_count, slot_count, 4)
    source = jnp.transpose(rimmed, (1, 2, 3, 0, 4)).reshape(-1, 4, slot_count)
    source = jnp.pad(source, ((0, 1), (0, 4), (0, 0)))
    empty_leaf = source.shape[0] - 1
    offsets = [(0, 0, 0)] + leaf_offsets()
    shift_rows = np.array([[float(v) for v in offset] + [0.0] * 5 for offset in offsets], np.float32)
    shift_table = jnp.asarray(np.ascontiguousarray(np.broadcast_to(shift_rows[:, :, None], (len(offsets), 8, slot_count))))
    leaf_x = jnp.arange(size_x, dtype=jnp.int32)[:, None, None]
    leaf_y = jnp.arange(size_y, dtype=jnp.int32)[None, :, None]
    leaf_z = jnp.arange(size_z, dtype=jnp.int32)[None, None, :]
    places = []
    for offset in offsets:
        place = ((leaf_x + 1 + offset[0]) * ext_y + leaf_y + 1 + offset[1]) * size_z + leaf_z + offset[2]
        places.append(jnp.broadcast_to(place, (size_x, size_y, size_z)))
    places = jnp.stack(places).reshape(len(offsets), leaf_count)
    layer = jnp.arange(size_z, dtype=jnp.int32)
    valid = jnp.stack([((layer + offset[2] >= 0) & (layer + offset[2] < size_z)) for offset in offsets[1:]])
    active = (near_flags != 0) & valid[:, None, None, :]
    active = jnp.concatenate([jnp.ones((1, leaf_count), bool), active.reshape(len(offsets) - 1, leaf_count)])
    listed = jnp.sum(active.astype(jnp.int32), axis=0)
    listed = listed + (NEAR_UNROLL - (listed - 1) % NEAR_UNROLL) % NEAR_UNROLL
    position = jnp.cumsum(active.astype(jnp.int32), axis=0) - 1
    width = 1 + -(-(len(offsets) - 1) // NEAR_UNROLL) * NEAR_UNROLL
    slots = jnp.arange(width, dtype=jnp.int32)
    chosen = active[None] & (position[None] == slots[:, None, None])
    kinds = jnp.arange(len(offsets), dtype=jnp.int32)
    kind_list = jnp.sum(jnp.where(chosen, kinds[None, :, None], 0), axis=1)
    place_list = jnp.sum(jnp.where(chosen, places[None], 0), axis=1)
    place_list = jnp.where(slots[:, None] < jnp.sum(active.astype(jnp.int32), axis=0)[None], place_list, empty_leaf)
    table = jnp.concatenate(
        [counts.reshape(-1), listed, jnp.transpose(place_list).reshape(-1), jnp.transpose(kind_list).reshape(-1)]
    ).astype(jnp.int32)
    piece = leaf_count // NEAR_PIECES if leaf_count % NEAR_PIECES == 0 else leaf_count
    pairs = piece * slot_count * slot_count * 10

    chained = []

    def run_piece(number, gate):
        first_leaf = number * piece
        own = target[first_leaf : first_leaf + piece]
        if gate is not None:
            own, unused = lax.optimization_barrier((own, gate))
        operands = [table, own, source, shift_table] + chained[-1:]
        result = pl.pallas_call(
            functools.partial(near_kernel, first_leaf, piece, leaf_count, width),
            out_shape=jax.ShapeDtypeStruct((8, leaf_count, slot_count), jnp.float32),
            in_specs=[pl.BlockSpec(memory_space=pltpu.SMEM)] + [pl.BlockSpec(memory_space=pltpu.VMEM)] * (len(operands) - 1),
            out_specs=pl.BlockSpec(memory_space=pltpu.VMEM),
            scratch_shapes=[pltpu.VMEM((slot_count, 128), jnp.float32)],
            input_output_aliases={4: 0} if chained else {},
            cost_estimate=pl.CostEstimate(
                flops=20 * pairs, transcendentals=pairs, bytes_accessed=8 * piece * slot_count * 128
            ),
        )(*operands)
        chained.append(result)
        return result

    def finish_near(outs):
        near = chained[-1][:4]
        return near.reshape(4, size_x, size_y, size_z, slot_count)

    return leaf_count // piece, run_piece, finish_near


def body(
    atom_data,
    counts,
    near_flags,
    child_up,
    child_down,
    leaf_far,
    parent_far,
    column_up,
    column_down,
    tree_up,
    tree_down,
    tree_side,
    lattice,
):
    coef_count = lattice.shape[0]
    slot_count = atom_data.shape[4]
    size_x, size_y, size_z = (atom_data.shape[1], atom_data.shape[2], atom_data.shape[3])
    live_slots = (
        jnp.arange(slot_count, dtype=jnp.int32)[None, None, None, :] < counts[..., None]
    ).astype(jnp.float32)
    charged = jnp.concatenate([atom_data[:3], (atom_data[3] * live_slots)[None]], axis=0)
    waves = wave_table(coef_count, jnp.float32)
    half_count = waves.shape[1]
    moments = leaf_moments(charged, waves)
    parents = climb_children(moments, child_up.astype(jnp.float32))
    rimmed, parent_rim, leaf_rim = extended_joint([(charged, 1), (parents, 2), (moments, 1)], (("gx", 1), ("gy", 2)))
    parent_rim = jnp.pad(parent_rim, ((0, 0), (0, 0), (0, 0), (2, 2)))
    half_x, half_y, half_z = (parents.shape[1], parents.shape[2], parents.shape[3])
    phase_grid = block_phase(waves, half_x, half_y, half_z, jnp.float32)
    turned = jnp.sum(rotate_by(parents, phase_grid), axis=(1, 2, 3))
    column = matrix_vector(column_up.astype(jnp.float32), turned)
    piece_count, run_piece, finish_near = near_local(charged, rimmed, counts, near_flags)
    pieces = []

    sent = []

    def hook(value, prior):
        number = len(pieces)
        if number < piece_count:
            if number > 0:
                value, unused = lax.optimization_barrier((value, pieces[-1]))
            pieces.append(run_piece(number, prior))
        sent.append(value)
        return value

    column_local = chain_tree(column, tree_up, tree_down, tree_side, lattice, hook)
    while len(pieces) < piece_count:
        pieces.append(run_piece(len(pieces), sent[-1]))
    near_terms = finish_near(pieces)
    leaf_rim = jnp.pad(leaf_rim, ((0, 0), (0, 0), (0, 0), (1, 1)))
    lowered = matrix_vector(column_down.astype(jnp.float32), column_local)
    parent_local = rotate_by(
        jnp.broadcast_to(lowered[:, None, None, None], parents.shape), -phase_grid
    )
    far_parents = parent_offsets()
    parent_stack = jnp.stack(
        [
            parent_rim[
                :,
                2 + offset[0] : 2 + offset[0] + half_x,
                2 + offset[1] : 2 + offset[1] + half_y,
                2 + offset[2] : 2 + offset[2] + half_z,
            ]
            for offset in far_parents
        ]
    )
    parent_turns = offset_phases(waves, far_parents).reshape(len(far_parents), half_count, 1, 1, 1)
    parent_sum = jnp.sum(jax.vmap(rotate_by)(parent_stack, parent_turns), axis=0)
    parent_local = parent_local + jnp.einsum(
        "kj,jxyz->kxyz", parent_far.astype(jnp.float32), parent_sum, precision=highest
    )
    leaf_local = descend_children(parent_local, child_down.astype(jnp.float32))
    near_leaves = leaf_offsets()
    leaf_stack = jnp.stack(
        [
            leaf_rim[
                :,
                1 + offset[0] : 1 + offset[0] + size_x,
                1 + offset[1] : 1 + offset[1] + size_y,
                1 + offset[2] : 1 + offset[2] + size_z,
            ]
            for offset in near_leaves
        ]
    )
    leaf_stack = leaf_stack * (1.0 - near_flags.astype(jnp.float32))[:, None]
    leaf_turns = offset_phases(waves, near_leaves).reshape(len(near_leaves), half_count, 1, 1, 1)
    leaf_sum = jnp.sum(jax.vmap(rotate_by)(leaf_stack, leaf_turns), axis=0)
    leaf_local = leaf_local + jnp.einsum(
        "kj,jxyz->kxyz", leaf_far.astype(jnp.float32), leaf_sum, precision=highest
    )
    potential, field_parts = evaluate(charged, leaf_local, waves)
    return assemble(near_terms, potential, field_parts, charged[3], live_slots)


def solution(mesh):
    in_specs = (
        P(None, "gx", "gy", None, None),
        P("gx", "gy", None),
        P(None, "gx", "gy", None),
        P(),
        P(),
        P(),
        P(),
        P(),
        P(),
        P(),
        P(),
        P(),
        P(),
    )
    out_specs = P(None, "gx", "gy", None, None)
    return jax.shard_map(body, mesh=mesh, in_specs=in_specs, out_specs=out_specs, check_vma=False)
```

```python
import functools

import jax
import numpy as np
import jax.numpy as jnp
from jax import lax
from jax.experimental import pallas as pl
from jax.experimental.pallas import tpu as pltpu
from jax.sharding import PartitionSpec as P

soften = 0.04
coulomb = 0.1
highest = lax.Precision.HIGHEST


def from_partner(value, axis, bit):
    mask = 2**bit
    pairs = [(source, source ^ mask) for source in range(lax.axis_size(axis))]
    return lax.ppermute(value, axis, pairs)


def extended_2(block, sides, width):
    return extended_joint([(block, width)], sides)[0]


def extended_joint(parts, sides, outgoing=None):
    blocks = [block for block, width in parts]
    for axis, dim in sides:
        count = lax.axis_size(axis)
        forward = [(i, i + 1) for i in range(count - 1)]
        forward.append((count - 1, 0))
        backward = [(target, source) for source, target in forward]
        lows = [lax.slice_in_dim(b, b.shape[dim] - w, None, axis=dim) for b, (_, w) in zip(blocks, parts)]
        highs = [lax.slice_in_dim(b, 0, w, axis=dim) for b, (_, w) in zip(blocks, parts)]
        sizes = [piece.size for piece in lows]
        low_flat = jnp.concatenate([piece.reshape(-1) for piece in lows])
        if outgoing is not None:
            outgoing.append(low_flat)
        low_all = lax.ppermute(low_flat, axis, forward)
        high_all = lax.ppermute(jnp.concatenate([piece.reshape(-1) for piece in highs]), axis, backward)
        grown = []
        place = 0
        for b, piece, size in zip(blocks, lows, sizes):
            low = low_all[place : place + size].reshape(piece.shape)
            high = high_all[place : place + size].reshape(piece.shape)
            place += size
            grown.append(jnp.concatenate([low, b, high], axis=dim))
        blocks = grown
    return blocks


def wave_table(coef_count, float_type):
    half_count = (coef_count - 1) // 2
    order_index = jnp.arange(1, half_count + 1, dtype=jnp.int32).astype(float_type)
    height = 1.0 - 2.0 * (order_index - 0.5) / half_count
    radius = jnp.sqrt(jnp.maximum(1.0 - height * height, 0.0))
    angle_turn = 2.399963 * order_index
    magnitude = 1.5 + jnp.mod(order_index, 3.0)
    return (
        jnp.stack([radius * jnp.cos(angle_turn), radius * jnp.sin(angle_turn), height])
        * magnitude[None]
    )


def waves_at(atom_data, waves):
    shape_lead = (waves.shape[1],) + (1,) * (atom_data.ndim - 1)
    phases = waves[0].reshape(shape_lead) * (atom_data[0] - 0.5)[None]
    phases = phases + waves[1].reshape(shape_lead) * (atom_data[1] - 0.5)[None]
    phases = phases + waves[2].reshape(shape_lead) * (atom_data[2] - 0.5)[None]
    return (jnp.cos(phases), jnp.sin(phases))


def rotate_by(field, phase):
    half_count = phase.shape[0]
    cosine = jnp.cos(phase)
    sine_part = jnp.sin(phase)
    cos_coef = field[1 : 1 + half_count]
    sin_coef = field[1 + half_count :]
    return jnp.concatenate(
        [
            field[0:1],
            cos_coef * cosine - sin_coef * sine_part,
            cos_coef * sine_part + sin_coef * cosine,
        ],
        axis=0,
    )


def offset_phases(waves, offsets):
    table = jnp.array(offsets, dtype=jnp.float32)
    return (
        table[:, 0:1] * waves[0][None]
        + table[:, 1:2] * waves[1][None]
        + table[:, 2:3] * waves[2][None]
    )


def block_phase(waves, size_x, size_y, size_z, float_type):
    place_x = jnp.arange(size_x, dtype=jnp.int32).astype(float_type)
    place_y = jnp.arange(size_y, dtype=jnp.int32).astype(float_type)
    place_z = jnp.arange(size_z, dtype=jnp.int32).astype(float_type)
    phase = waves[0][:, None, None, None] * place_x[None, :, None, None]
    phase = phase + waves[1][:, None, None, None] * place_y[None, None, :, None]
    return phase + waves[2][:, None, None, None] * place_z[None, None, None, :]


def leaf_moments(atom_data, waves):
    cosine, sine_part = waves_at(atom_data, waves)
    charge = atom_data[3]
    summed = jnp.sum(charge, axis=-1)[None]
    return jnp.concatenate(
        [
            summed,
            jnp.sum(cosine * charge[None], axis=-1),
            jnp.sum(sine_part * charge[None], axis=-1),
        ],
        axis=0,
    )


def evaluate(atom_data, local_exp, waves):
    cosine, sine_part = waves_at(atom_data, waves)
    half_count = waves.shape[1]
    cos_local = local_exp[1 : 1 + half_count][..., None]
    sin_local = local_exp[1 + half_count :][..., None]
    potential = local_exp[0][..., None] + jnp.sum(
        cos_local * cosine + sin_local * sine_part, axis=0
    )
    mixed_term = cos_local * sine_part - sin_local * cosine
    shape_lead = (half_count,) + (1,) * (mixed_term.ndim - 1)
    field_parts = [
        jnp.sum(waves[component].reshape(shape_lead) * mixed_term, axis=0) for component in range(3)
    ]
    return (potential, field_parts)


def near_row(target, source, flag_grid, shift_vec, keep_self):
    weight = source[3] * flag_grid[..., None]
    delta_x = target[0][..., :, None] - (source[0][..., None, :] + shift_vec[0])
    delta_y = target[1][..., :, None] - (source[1][..., None, :] + shift_vec[1])
    delta_z = target[2][..., :, None] - (source[2][..., None, :] + shift_vec[2])
    inverse = lax.rsqrt(delta_x * delta_x + delta_y * delta_y + delta_z * delta_z + soften)
    pair_term = weight[..., None, :] * keep_self * inverse
    cube_term = pair_term * inverse * inverse
    return jnp.stack(
        [
            jnp.sum(pair_term, axis=-1),
            jnp.sum(cube_term * delta_x, axis=-1),
            jnp.sum(cube_term * delta_y, axis=-1),
            jnp.sum(cube_term * delta_z, axis=-1),
        ]
    )


def full_flags(near_flags, float_type):
    flags_float = near_flags.astype(float_type)
    centre = jnp.ones((1,) + flags_float.shape[1:], float_type)
    return jnp.concatenate([flags_float[:13], centre, flags_float[13:]], axis=0)


def leaf_offsets():
    return [
        (shift_x, shift_y, shift_z)
        for shift_x in (-1, 0, 1)
        for shift_y in (-1, 0, 1)
        for shift_z in (-1, 0, 1)
        if (shift_x, shift_y, shift_z) != (0, 0, 0)
    ]


def parent_offsets():
    return [
        (shift_x, shift_y, shift_z)
        for shift_x in range(-2, 3)
        for shift_y in range(-2, 3)
        for shift_z in range(-2, 3)
        if max(abs(shift_x), abs(shift_y), abs(shift_z)) == 2
    ]


def climb_children(moments, matrices):
    coef_count, size_x, size_y, size_z = moments.shape
    parted = moments.reshape(coef_count, size_x // 2, 2, size_y // 2, 2, size_z // 2, 2)
    return jnp.einsum(
        "abckj,jxaybzc->kxyz",
        matrices.reshape(2, 2, 2, coef_count, coef_count),
        parted,
        precision=highest,
    )


def descend_children(parent_local, matrices):
    coef_count, size_x, size_y, size_z = parent_local.shape
    spread = jnp.einsum(
        "abckj,jxyz->kxaybzc",
        matrices.reshape(2, 2, 2, coef_count, coef_count),
        parent_local,
        precision=highest,
    )
    return spread.reshape(coef_count, 2 * size_x, 2 * size_y, 2 * size_z)


def matrix_vector(matrix, vector):
    return jnp.dot(matrix, vector, precision=highest)


def pick_side(matrices, own_side):
    return lax.dynamic_index_in_dim(matrices, own_side, 0, keepdims=False)


def pair_step(matrices, own_side, current, partner):
    return matrix_vector(pick_side(matrices, own_side), current) + matrix_vector(
        pick_side(matrices, 1 - own_side), partner
    )


def chain_tree(column, tree_up, tree_down, tree_side, lattice, hook):
    climbs = tree_up.astype(jnp.float32)
    lowers = tree_down.astype(jnp.float32)
    sideways = tree_side.astype(jnp.float32)
    current = column
    visited = []
    partner = None
    for level_bit in range(lax.axis_size("gx").bit_length() - 1):
        current = hook(current, partner)
        partner = from_partner(current, "gx", level_bit)
        own_side = lax.axis_index("gx") // 2**level_bit % 2
        current = pair_step(climbs[0], own_side, current, partner)
        visited.append((0, own_side, partner))
    for level_bit in range(lax.axis_size("gy").bit_length() - 1):
        current = hook(current, partner)
        partner = from_partner(current, "gy", level_bit)
        own_side = lax.axis_index("gy") // 2**level_bit % 2
        current = pair_step(climbs[1], own_side, current, partner)
        visited.append((1, own_side, partner))
    local_exp = matrix_vector(lattice.astype(jnp.float32), current)
    for axis_num, own_side, partner in reversed(visited):
        local_exp = matrix_vector(pick_side(lowers[axis_num], own_side), local_exp) + matrix_vector(
            pick_side(sideways[axis_num], own_side), partner
        )
    return local_exp


def flip_pair(column_grid, axis_num, level_bit):
    coef_count, size_x, size_y = column_grid.shape
    span_size = 2**level_bit
    if axis_num == 0:
        parted = column_grid.reshape(coef_count, size_x // (2 * span_size), 2, span_size, size_y)
        return parted[:, :, ::-1].reshape(column_grid.shape)
    parted = column_grid.reshape(coef_count, size_x, size_y // (2 * span_size), 2, span_size)
    return parted[:, :, :, ::-1].reshape(column_grid.shape)


def side_grid(axis_num, level_bit, size_x, size_y):
    positions = jnp.arange(size_x if axis_num == 0 else size_y, dtype=jnp.int32)
    own_side = positions // 2**level_bit % 2
    return own_side[:, None] if axis_num == 0 else own_side[None, :]


def choose_side(matrices, own_side, column_grid):
    first = jnp.einsum("kj,jxy->kxy", matrices[0], column_grid, precision=highest)
    second = jnp.einsum("kj,jxy->kxy", matrices[1], column_grid, precision=highest)
    return jnp.where(own_side[None] == 0, first, second)


def gathered_tree(column, tree_up, tree_down, tree_side, lattice):
    size_x, size_y = lax.axis_size("gx"), lax.axis_size("gy")
    gathered = lax.all_gather(column, ("gx", "gy")).reshape(size_x, size_y, -1)
    current = jnp.transpose(gathered, (2, 0, 1))
    levels = [(0, bit) for bit in range(size_x.bit_length() - 1)] + [
        (1, bit) for bit in range(size_y.bit_length() - 1)
    ]
    visited = []
    for axis_num, level_bit in levels:
        partner = flip_pair(current, axis_num, level_bit)
        own_side = side_grid(axis_num, level_bit, size_x, size_y)
        climbs = tree_up[axis_num].astype(jnp.float32)
        current = choose_side(climbs, own_side, current) + choose_side(climbs, 1 - own_side, partner)
        visited.append((axis_num, own_side, partner))
    local_exp = jnp.einsum("kj,jxy->kxy", lattice.astype(jnp.float32), current, precision=highest)
    for axis_num, own_side, partner in reversed(visited):
        local_exp = choose_side(tree_down[axis_num].astype(jnp.float32), own_side, local_exp) + choose_side(
            tree_side[axis_num].astype(jnp.float32), own_side, partner
        )
    own = lax.dynamic_slice(local_exp, (0, lax.axis_index("gx"), lax.axis_index("gy")), (local_exp.shape[0], 1, 1))
    return own.reshape(-1)


def assemble(near_terms, potential, field_parts, charge, live_slots):
    rows = [coulomb * (near_terms[0] + potential) * live_slots]
    for component in range(3):
        rows.append(coulomb * charge * (near_terms[1 + component] + field_parts[component]))
    return jnp.stack(rows)


NEAR_ROWS = 64
NEAR_PIECES = 8
NEAR_UNROLL = 2


def near_pairs(tx, ty, tz, srow, mask):
    weight = srow[3:4, :]
    delta_x = tx - srow[0:1, :]
    delta_y = ty - srow[1:2, :]
    delta_z = tz - srow[2:3, :]
    inverse = lax.rsqrt(delta_x * delta_x + delta_y * delta_y + delta_z * delta_z + soften)
    pair_term = weight * inverse
    if mask is not None:
        pair_term = jnp.where(mask, pair_term, 0.0)
    cube_term = pair_term * inverse * inverse
    return (pair_term, cube_term * delta_x, cube_term * delta_y, cube_term * delta_z)


def near_kernel(first_leaf, piece_leaves, leaf_count, listed_width, *refs):
    if len(refs) == 7:
        table_ref, target_ref, source_ref, shift_ref, previous_ref, out_ref, tile_ref = refs
        out_ref[...] = previous_ref[...]
    else:
        table_ref, target_ref, source_ref, shift_ref, out_ref, tile_ref = refs
        out_ref[...] = jnp.zeros(out_ref.shape, out_ref.dtype)
    place_start = 2 * leaf_count
    kind_start = place_start + leaf_count * listed_width
    order_start = kind_start + leaf_count * listed_width
    big = NEAR_ROWS
    small = NEAR_ROWS // 2
    lanes = out_ref.shape[2]

    def leaf_body(local, carry):
        leaf = table_ref[order_start + first_leaf + local]
        count = table_ref[leaf]
        full_count = count // big
        rest = count - full_count * big
        listed = table_ref[leaf_count + leaf]
        base = leaf * listed_width
        tile_ref[...] = jnp.zeros(tile_ref.shape, tile_ref.dtype)

        def chunk_at(first, rows):
            lane = lax.broadcasted_iota(jnp.int32, (rows, lanes), 1)
            row = lax.broadcasted_iota(jnp.int32, (rows, lanes), 0)
            column = target_ref[local, pl.ds(first, rows), :]
            tx = jnp.broadcast_to(column[:, 0:1], (rows, lanes))
            ty = jnp.broadcast_to(column[:, 1:2], (rows, lanes))
            tz = jnp.broadcast_to(column[:, 2:3], (rows, lanes))
            acc = near_pairs(tx, ty, tz, source_ref[table_ref[place_start + base]], row + first != lane)

            def offset_body(step, acc):
                number = base + 1 + NEAR_UNROLL * step
                for extra in range(NEAR_UNROLL):
                    srow = source_ref[table_ref[place_start + number + extra]]
                    srow = srow + shift_ref[table_ref[kind_start + number + extra]]
                    terms = near_pairs(tx, ty, tz, srow, None)
                    acc = tuple(a + b for a, b in zip(acc, terms))
                return acc

            acc = lax.fori_loop(0, (listed - 1) // NEAR_UNROLL, offset_body, acc)
            sums = [jnp.sum(part, axis=1, keepdims=True) for part in acc]
            tile = jnp.where(
                lane == 0, sums[0], jnp.where(lane == 1, sums[1], jnp.where(lane == 2, sums[2], sums[3]))
            )
            tile_ref[pl.ds(first, rows), :] = jnp.where(lane < 4, tile, 0.0)

        def full_body(chunk, carry2):
            chunk_at(pl.multiple_of(chunk * big, big), big)
            return carry2

        lax.fori_loop(0, full_count, full_body, 0)
        last = pl.multiple_of(full_count * big, small)

        @pl.when(rest > small)
        def _():
            chunk_at(last, big)

        @pl.when((rest > 0) & (rest <= small))
        def _():
            chunk_at(last, small)

        out_ref[leaf] = jnp.transpose(tile_ref[...])[0 : out_ref.shape[1], :]
        return carry

    lax.fori_loop(0, piece_leaves, leaf_body, 0)


def near_local(charged, rimmed, counts, near_flags, early_gate):
    size_x, size_y, size_z, slot_count = charged.shape[1:]
    leaf_count = size_x * size_y * size_z
    ext_y = size_y + 2
    target = jnp.transpose(charged, (1, 2, 3, 4, 0)).reshape(leaf_count, slot_count, 4)
    source = jnp.transpose(rimmed, (1, 2, 3, 0, 4)).reshape(-1, 4, slot_count)
    source = jnp.pad(source, ((0, 1), (0, 4), (0, 0)))
    inner = [
        leaf
        for leaf in range(leaf_count)
        if 0 < leaf // (size_y * size_z) < size_x - 1 and 0 < leaf // size_z % size_y < size_y - 1
    ]
    order = inner + [leaf for leaf in range(leaf_count) if leaf not in inner]
    target = jnp.concatenate([target[leaf : leaf + 1] for leaf in order], axis=0)
    early_source = jnp.transpose(jnp.pad(charged, ((0, 0), (1, 1), (1, 1), (0, 0), (0, 0))), (1, 2, 3, 0, 4))
    early_source = jnp.pad(early_source.reshape(-1, 4, slot_count), ((0, 1), (0, 4), (0, 0)))
    empty_leaf = source.shape[0] - 1
    offsets = [(0, 0, 0)] + leaf_offsets()
    shift_rows = np.array([[float(v) for v in offset] + [0.0] * 5 for offset in offsets], np.float32)
    shift_table = jnp.asarray(np.ascontiguousarray(np.broadcast_to(shift_rows[:, :, None], (len(offsets), 8, slot_count))))
    leaf_x = jnp.arange(size_x, dtype=jnp.int32)[:, None, None]
    leaf_y = jnp.arange(size_y, dtype=jnp.int32)[None, :, None]
    leaf_z = jnp.arange(size_z, dtype=jnp.int32)[None, None, :]
    places = []
    for offset in offsets:
        place = ((leaf_x + 1 + offset[0]) * ext_y + leaf_y + 1 + offset[1]) * size_z + leaf_z + offset[2]
        places.append(jnp.broadcast_to(place, (size_x, size_y, size_z)))
    places = jnp.stack(places).reshape(len(offsets), leaf_count)
    layer = jnp.arange(size_z, dtype=jnp.int32)
    valid = jnp.stack([((layer + offset[2] >= 0) & (layer + offset[2] < size_z)) for offset in offsets[1:]])
    active = (near_flags != 0) & valid[:, None, None, :]
    active = jnp.concatenate([jnp.ones((1, leaf_count), bool), active.reshape(len(offsets) - 1, leaf_count)])
    listed = jnp.sum(active.astype(jnp.int32), axis=0)
    listed = listed + (NEAR_UNROLL - (listed - 1) % NEAR_UNROLL) % NEAR_UNROLL
    position = jnp.cumsum(active.astype(jnp.int32), axis=0) - 1
    width = 1 + -(-(len(offsets) - 1) // NEAR_UNROLL) * NEAR_UNROLL
    slots = jnp.arange(width, dtype=jnp.int32)
    chosen = active[None] & (position[None] == slots[:, None, None])
    kinds = jnp.arange(len(offsets), dtype=jnp.int32)
    kind_list = jnp.sum(jnp.where(chosen, kinds[None, :, None], 0), axis=1)
    place_list = jnp.sum(jnp.where(chosen, places[None], 0), axis=1)
    place_list = jnp.where(slots[:, None] < jnp.sum(active.astype(jnp.int32), axis=0)[None], place_list, empty_leaf)
    table = jnp.concatenate(
        [counts.reshape(-1), listed, jnp.transpose(place_list).reshape(-1), jnp.transpose(kind_list).reshape(-1), jnp.array(order, jnp.int32)]
    ).astype(jnp.int32)
    piece = leaf_count // NEAR_PIECES if leaf_count % NEAR_PIECES == 0 else leaf_count
    pairs = piece * slot_count * slot_count * 10

    chained = []

    def run_piece(number, gate):
        first_leaf = number * piece
        own = target[first_leaf : first_leaf + piece]
        early = all(leaf in inner for leaf in order[first_leaf : first_leaf + piece])
        if number == 0 and early:
            gate = early_gate
        if gate is not None:
            own, unused = lax.optimization_barrier((own, gate))
        operands = [table, own, early_source if early else source, shift_table] + chained[-1:]
        result = pl.pallas_call(
            functools.partial(near_kernel, first_leaf, piece, leaf_count, width),
            out_shape=jax.ShapeDtypeStruct((leaf_count, 8, slot_count), jnp.float32),
            in_specs=[pl.BlockSpec(memory_space=pltpu.SMEM)] + [pl.BlockSpec(memory_space=pltpu.VMEM)] * (len(operands) - 1),
            out_specs=pl.BlockSpec(memory_space=pltpu.VMEM),
            scratch_shapes=[pltpu.VMEM((slot_count, 128), jnp.float32)],
            input_output_aliases={4: 0} if chained else {},
            cost_estimate=pl.CostEstimate(
                flops=20 * pairs, transcendentals=pairs, bytes_accessed=8 * piece * slot_count * 128
            ),
        )(*operands)
        chained.append(result)
        return result

    def finish_near(outs):
        near = jnp.transpose(chained[-1][:, :4, :], (1, 0, 2))
        return near.reshape(4, size_x, size_y, size_z, slot_count)

    return leaf_count // piece, run_piece, finish_near


def body(
    atom_data,
    counts,
    near_flags,
    child_up,
    child_down,
    leaf_far,
    parent_far,
    column_up,
    column_down,
    tree_up,
    tree_down,
    tree_side,
    lattice,
):
    coef_count = lattice.shape[0]
    slot_count = atom_data.shape[4]
    size_x, size_y, size_z = (atom_data.shape[1], atom_data.shape[2], atom_data.shape[3])
    live_slots = (
        jnp.arange(slot_count, dtype=jnp.int32)[None, None, None, :] < counts[..., None]
    ).astype(jnp.float32)
    charged = jnp.concatenate([atom_data[:3], (atom_data[3] * live_slots)[None]], axis=0)
    waves = wave_table(coef_count, jnp.float32)
    half_count = waves.shape[1]
    moments = leaf_moments(charged, waves)
    parents = climb_children(moments, child_up.astype(jnp.float32))
    outgoing = []
    rimmed, parent_rim, leaf_rim = extended_joint([(charged, 1), (parents, 2), (moments, 1)], (("gx", 1), ("gy", 2)), outgoing)
    parent_rim = jnp.pad(parent_rim, ((0, 0), (0, 0), (0, 0), (2, 2)))
    half_x, half_y, half_z = (parents.shape[1], parents.shape[2], parents.shape[3])
    phase_grid = block_phase(waves, half_x, half_y, half_z, jnp.float32)
    turned = jnp.sum(rotate_by(parents, phase_grid), axis=(1, 2, 3))
    column = matrix_vector(column_up.astype(jnp.float32), turned)
    piece_count, run_piece, finish_near = near_local(charged, rimmed, counts, near_flags, outgoing[-1])
    pieces = []

    sent = []

    def hook(value, prior):
        number = len(pieces)
        if number < piece_count:
            if number > 0:
                value, unused = lax.optimization_barrier((value, pieces[-1]))
            pieces.append(run_piece(number, prior))
        sent.append(value)
        return value

    column_local = chain_tree(column, tree_up, tree_down, tree_side, lattice, hook)
    while len(pieces) < piece_count:
        pieces.append(run_piece(len(pieces), sent[-1]))
    near_terms = finish_near(pieces)
    leaf_rim = jnp.pad(leaf_rim, ((0, 0), (0, 0), (0, 0), (1, 1)))
    lowered = matrix_vector(column_down.astype(jnp.float32), column_local)
    parent_local = rotate_by(
        jnp.broadcast_to(lowered[:, None, None, None], parents.shape), -phase_grid
    )
    far_parents = parent_offsets()
    parent_stack = jnp.stack(
        [
            parent_rim[
                :,
                2 + offset[0] : 2 + offset[0] + half_x,
                2 + offset[1] : 2 + offset[1] + half_y,
                2 + offset[2] : 2 + offset[2] + half_z,
            ]
            for offset in far_parents
        ]
    )
    parent_turns = offset_phases(waves, far_parents).reshape(len(far_parents), half_count, 1, 1, 1)
    parent_sum = jnp.sum(jax.vmap(rotate_by)(parent_stack, parent_turns), axis=0)
    parent_local = parent_local + jnp.einsum(
        "kj,jxyz->kxyz", parent_far.astype(jnp.float32), parent_sum, precision=highest
    )
    leaf_local = descend_children(parent_local, child_down.astype(jnp.float32))
    near_leaves = leaf_offsets()
    leaf_stack = jnp.stack(
        [
            leaf_rim[
                :,
                1 + offset[0] : 1 + offset[0] + size_x,
                1 + offset[1] : 1 + offset[1] + size_y,
                1 + offset[2] : 1 + offset[2] + size_z,
            ]
            for offset in near_leaves
        ]
    )
    leaf_stack = leaf_stack * (1.0 - near_flags.astype(jnp.float32))[:, None]
    leaf_turns = offset_phases(waves, near_leaves).reshape(len(near_leaves), half_count, 1, 1, 1)
    leaf_sum = jnp.sum(jax.vmap(rotate_by)(leaf_stack, leaf_turns), axis=0)
    leaf_local = leaf_local + jnp.einsum(
        "kj,jxyz->kxyz", leaf_far.astype(jnp.float32), leaf_sum, precision=highest
    )
    potential, field_parts = evaluate(charged, leaf_local, waves)
    return assemble(near_terms, potential, field_parts, charged[3], live_slots)


def solution(mesh):
    in_specs = (
        P(None, "gx", "gy", None, None),
        P("gx", "gy", None),
        P(None, "gx", "gy", None),
        P(),
        P(),
        P(),
        P(),
        P(),
        P(),
        P(),
        P(),
        P(),
        P(),
    )
    out_specs = P(None, "gx", "gy", None, None)
    return jax.shard_map(body, mesh=mesh, in_specs=in_specs, out_specs=out_specs, check_vma=False)
```

```python
import functools

import jax
import numpy as np
import jax.numpy as jnp
from jax import lax
from jax.experimental import pallas as pl
from jax.experimental.pallas import tpu as pltpu
from jax.sharding import PartitionSpec as P

soften = 0.04
coulomb = 0.1
highest = lax.Precision.HIGHEST


def from_partner(value, axis, bit):
    mask = 2**bit
    pairs = [(source, source ^ mask) for source in range(lax.axis_size(axis))]
    return lax.ppermute(value, axis, pairs)


def extended_2(block, sides, width):
    return extended_joint([(block, width)], sides)[0]


def extended_joint(parts, sides):
    blocks = [block for block, width in parts]
    for axis, dim in sides:
        count = lax.axis_size(axis)
        forward = [(i, i + 1) for i in range(count - 1)]
        forward.append((count - 1, 0))
        backward = [(target, source) for source, target in forward]
        lows = [lax.slice_in_dim(b, b.shape[dim] - w, None, axis=dim) for b, (_, w) in zip(blocks, parts)]
        highs = [lax.slice_in_dim(b, 0, w, axis=dim) for b, (_, w) in zip(blocks, parts)]
        sizes = [piece.size for piece in lows]
        low_all = lax.ppermute(jnp.concatenate([piece.reshape(-1) for piece in lows]), axis, forward)
        high_all = lax.ppermute(jnp.concatenate([piece.reshape(-1) for piece in highs]), axis, backward)
        grown = []
        place = 0
        for b, piece, size in zip(blocks, lows, sizes):
            low = low_all[place : place + size].reshape(piece.shape)
            high = high_all[place : place + size].reshape(piece.shape)
            place += size
            grown.append(jnp.concatenate([low, b, high], axis=dim))
        blocks = grown
    return blocks


def wave_table(coef_count, float_type):
    half_count = (coef_count - 1) // 2
    order_index = jnp.arange(1, half_count + 1, dtype=jnp.int32).astype(float_type)
    height = 1.0 - 2.0 * (order_index - 0.5) / half_count
    radius = jnp.sqrt(jnp.maximum(1.0 - height * height, 0.0))
    angle_turn = 2.399963 * order_index
    magnitude = 1.5 + jnp.mod(order_index, 3.0)
    return (
        jnp.stack([radius * jnp.cos(angle_turn), radius * jnp.sin(angle_turn), height])
        * magnitude[None]
    )


def waves_at(atom_data, waves):
    shape_lead = (waves.shape[1],) + (1,) * (atom_data.ndim - 1)
    phases = waves[0].reshape(shape_lead) * (atom_data[0] - 0.5)[None]
    phases = phases + waves[1].reshape(shape_lead) * (atom_data[1] - 0.5)[None]
    phases = phases + waves[2].reshape(shape_lead) * (atom_data[2] - 0.5)[None]
    return (jnp.cos(phases), jnp.sin(phases))


def rotate_by(field, phase):
    half_count = phase.shape[0]
    cosine = jnp.cos(phase)
    sine_part = jnp.sin(phase)
    cos_coef = field[1 : 1 + half_count]
    sin_coef = field[1 + half_count :]
    return jnp.concatenate(
        [
            field[0:1],
            cos_coef * cosine - sin_coef * sine_part,
            cos_coef * sine_part + sin_coef * cosine,
        ],
        axis=0,
    )


def offset_phases(waves, offsets):
    table = jnp.array(offsets, dtype=jnp.float32)
    return (
        table[:, 0:1] * waves[0][None]
        + table[:, 1:2] * waves[1][None]
        + table[:, 2:3] * waves[2][None]
    )


def block_phase(waves, size_x, size_y, size_z, float_type):
    place_x = jnp.arange(size_x, dtype=jnp.int32).astype(float_type)
    place_y = jnp.arange(size_y, dtype=jnp.int32).astype(float_type)
    place_z = jnp.arange(size_z, dtype=jnp.int32).astype(float_type)
    phase = waves[0][:, None, None, None] * place_x[None, :, None, None]
    phase = phase + waves[1][:, None, None, None] * place_y[None, None, :, None]
    return phase + waves[2][:, None, None, None] * place_z[None, None, None, :]


def leaf_moments(atom_data, waves):
    cosine, sine_part = waves_at(atom_data, waves)
    charge = atom_data[3]
    summed = jnp.sum(charge, axis=-1)[None]
    return jnp.concatenate(
        [
            summed,
            jnp.sum(cosine * charge[None], axis=-1),
            jnp.sum(sine_part * charge[None], axis=-1),
        ],
        axis=0,
    )


def evaluate(atom_data, local_exp, waves):
    cosine, sine_part = waves_at(atom_data, waves)
    half_count = waves.shape[1]
    cos_local = local_exp[1 : 1 + half_count][..., None]
    sin_local = local_exp[1 + half_count :][..., None]
    potential = local_exp[0][..., None] + jnp.sum(
        cos_local * cosine + sin_local * sine_part, axis=0
    )
    mixed_term = cos_local * sine_part - sin_local * cosine
    shape_lead = (half_count,) + (1,) * (mixed_term.ndim - 1)
    field_parts = [
        jnp.sum(waves[component].reshape(shape_lead) * mixed_term, axis=0) for component in range(3)
    ]
    return (potential, field_parts)


def near_row(target, source, flag_grid, shift_vec, keep_self):
    weight = source[3] * flag_grid[..., None]
    delta_x = target[0][..., :, None] - (source[0][..., None, :] + shift_vec[0])
    delta_y = target[1][..., :, None] - (source[1][..., None, :] + shift_vec[1])
    delta_z = target[2][..., :, None] - (source[2][..., None, :] + shift_vec[2])
    inverse = lax.rsqrt(delta_x * delta_x + delta_y * delta_y + delta_z * delta_z + soften)
    pair_term = weight[..., None, :] * keep_self * inverse
    cube_term = pair_term * inverse * inverse
    return jnp.stack(
        [
            jnp.sum(pair_term, axis=-1),
            jnp.sum(cube_term * delta_x, axis=-1),
            jnp.sum(cube_term * delta_y, axis=-1),
            jnp.sum(cube_term * delta_z, axis=-1),
        ]
    )


def full_flags(near_flags, float_type):
    flags_float = near_flags.astype(float_type)
    centre = jnp.ones((1,) + flags_float.shape[1:], float_type)
    return jnp.concatenate([flags_float[:13], centre, flags_float[13:]], axis=0)


def leaf_offsets():
    return [
        (shift_x, shift_y, shift_z)
        for shift_x in (-1, 0, 1)
        for shift_y in (-1, 0, 1)
        for shift_z in (-1, 0, 1)
        if (shift_x, shift_y, shift_z) != (0, 0, 0)
    ]


def parent_offsets():
    return [
        (shift_x, shift_y, shift_z)
        for shift_x in range(-2, 3)
        for shift_y in range(-2, 3)
        for shift_z in range(-2, 3)
        if max(abs(shift_x), abs(shift_y), abs(shift_z)) == 2
    ]


def climb_children(moments, matrices):
    coef_count, size_x, size_y, size_z = moments.shape
    parted = moments.reshape(coef_count, size_x // 2, 2, size_y // 2, 2, size_z // 2, 2)
    return jnp.einsum(
        "abckj,jxaybzc->kxyz",
        matrices.reshape(2, 2, 2, coef_count, coef_count),
        parted,
        precision=highest,
    )


def descend_children(parent_local, matrices):
    coef_count, size_x, size_y, size_z = parent_local.shape
    spread = jnp.einsum(
        "abckj,jxyz->kxaybzc",
        matrices.reshape(2, 2, 2, coef_count, coef_count),
        parent_local,
        precision=highest,
    )
    return spread.reshape(coef_count, 2 * size_x, 2 * size_y, 2 * size_z)


def matrix_vector(matrix, vector):
    return jnp.dot(matrix, vector, precision=highest)


def pick_side(matrices, own_side):
    return lax.dynamic_index_in_dim(matrices, own_side, 0, keepdims=False)


def pair_step(matrices, own_side, current, partner):
    return matrix_vector(pick_side(matrices, own_side), current) + matrix_vector(
        pick_side(matrices, 1 - own_side), partner
    )


def chain_tree(column, tree_up, tree_down, tree_side, lattice, hook):
    climbs = tree_up.astype(jnp.float32)
    lowers = tree_down.astype(jnp.float32)
    sideways = tree_side.astype(jnp.float32)
    current = column
    visited = []
    partner = None
    for level_bit in range(lax.axis_size("gx").bit_length() - 1):
        current = hook(current, partner)
        partner = from_partner(current, "gx", level_bit)
        own_side = lax.axis_index("gx") // 2**level_bit % 2
        current = pair_step(climbs[0], own_side, current, partner)
        visited.append((0, own_side, partner))
    for level_bit in range(lax.axis_size("gy").bit_length() - 1):
        current = hook(current, partner)
        partner = from_partner(current, "gy", level_bit)
        own_side = lax.axis_index("gy") // 2**level_bit % 2
        current = pair_step(climbs[1], own_side, current, partner)
        visited.append((1, own_side, partner))
    local_exp = matrix_vector(lattice.astype(jnp.float32), current)
    for axis_num, own_side, partner in reversed(visited):
        local_exp = matrix_vector(pick_side(lowers[axis_num], own_side), local_exp) + matrix_vector(
            pick_side(sideways[axis_num], own_side), partner
        )
    return local_exp


def flip_pair(column_grid, axis_num, level_bit):
    coef_count, size_x, size_y = column_grid.shape
    span_size = 2**level_bit
    if axis_num == 0:
        parted = column_grid.reshape(coef_count, size_x // (2 * span_size), 2, span_size, size_y)
        return parted[:, :, ::-1].reshape(column_grid.shape)
    parted = column_grid.reshape(coef_count, size_x, size_y // (2 * span_size), 2, span_size)
    return parted[:, :, :, ::-1].reshape(column_grid.shape)


def side_grid(axis_num, level_bit, size_x, size_y):
    positions = jnp.arange(size_x if axis_num == 0 else size_y, dtype=jnp.int32)
    own_side = positions // 2**level_bit % 2
    return own_side[:, None] if axis_num == 0 else own_side[None, :]


def choose_side(matrices, own_side, column_grid):
    first = jnp.einsum("kj,jxy->kxy", matrices[0], column_grid, precision=highest)
    second = jnp.einsum("kj,jxy->kxy", matrices[1], column_grid, precision=highest)
    return jnp.where(own_side[None] == 0, first, second)


def gathered_tree(column, tree_up, tree_down, tree_side, lattice):
    size_x, size_y = lax.axis_size("gx"), lax.axis_size("gy")
    gathered = lax.all_gather(column, ("gx", "gy")).reshape(size_x, size_y, -1)
    current = jnp.transpose(gathered, (2, 0, 1))
    levels = [(0, bit) for bit in range(size_x.bit_length() - 1)] + [
        (1, bit) for bit in range(size_y.bit_length() - 1)
    ]
    visited = []
    for axis_num, level_bit in levels:
        partner = flip_pair(current, axis_num, level_bit)
        own_side = side_grid(axis_num, level_bit, size_x, size_y)
        climbs = tree_up[axis_num].astype(jnp.float32)
        current = choose_side(climbs, own_side, current) + choose_side(climbs, 1 - own_side, partner)
        visited.append((axis_num, own_side, partner))
    local_exp = jnp.einsum("kj,jxy->kxy", lattice.astype(jnp.float32), current, precision=highest)
    for axis_num, own_side, partner in reversed(visited):
        local_exp = choose_side(tree_down[axis_num].astype(jnp.float32), own_side, local_exp) + choose_side(
            tree_side[axis_num].astype(jnp.float32), own_side, partner
        )
    own = lax.dynamic_slice(local_exp, (0, lax.axis_index("gx"), lax.axis_index("gy")), (local_exp.shape[0], 1, 1))
    return own.reshape(-1)


def assemble(near_terms, potential, field_parts, charge, live_slots):
    rows = [coulomb * (near_terms[0] + potential) * live_slots]
    for component in range(3):
        rows.append(coulomb * charge * (near_terms[1 + component] + field_parts[component]))
    return jnp.stack(rows)


NEAR_ROWS = 64
NEAR_PIECES = 8
NEAR_UNROLL = 2


def near_pairs(tx, ty, tz, srow, mask):
    weight = srow[3:4, :]
    delta_x = tx - srow[0:1, :]
    delta_y = ty - srow[1:2, :]
    delta_z = tz - srow[2:3, :]
    inverse = lax.rsqrt(delta_x * delta_x + delta_y * delta_y + delta_z * delta_z + soften)
    pair_term = weight * inverse
    if mask is not None:
        pair_term = jnp.where(mask, pair_term, 0.0)
    cube_term = pair_term * inverse * inverse
    return (pair_term, cube_term * delta_x, cube_term * delta_y, cube_term * delta_z)


def near_kernel(first_leaf, piece_leaves, leaf_count, listed_width, *refs):
    if len(refs) == 7:
        table_ref, target_ref, source_ref, shift_ref, previous_ref, out_ref, tile_ref = refs
        out_ref[...] = previous_ref[...]
    else:
        table_ref, target_ref, source_ref, shift_ref, out_ref, tile_ref = refs
        out_ref[...] = jnp.zeros(out_ref.shape, out_ref.dtype)
    place_start = 2 * leaf_count
    kind_start = place_start + leaf_count * listed_width
    big = NEAR_ROWS
    small = NEAR_ROWS // 2
    lanes = out_ref.shape[2]

    def leaf_body(local, carry):
        leaf = first_leaf + local
        count = table_ref[leaf]
        full_count = count // big
        rest = count - full_count * big
        listed = table_ref[leaf_count + leaf]
        base = leaf * listed_width
        tile_ref[...] = jnp.zeros(tile_ref.shape, tile_ref.dtype)

        def chunk_at(first, rows):
            lane = lax.broadcasted_iota(jnp.int32, (rows, lanes), 1)
            row = lax.broadcasted_iota(jnp.int32, (rows, lanes), 0)
            column = target_ref[local, pl.ds(first, rows), :]
            tx = jnp.broadcast_to(column[:, 0:1], (rows, lanes))
            ty = jnp.broadcast_to(column[:, 1:2], (rows, lanes))
            tz = jnp.broadcast_to(column[:, 2:3], (rows, lanes))
            acc = near_pairs(tx, ty, tz, source_ref[table_ref[place_start + base]], row + first != lane)

            def offset_body(step, acc):
                number = base + 1 + NEAR_UNROLL * step
                for extra in range(NEAR_UNROLL):
                    srow = source_ref[table_ref[place_start + number + extra]]
                    srow = srow + shift_ref[table_ref[kind_start + number + extra]]
                    terms = near_pairs(tx, ty, tz, srow, None)
                    acc = tuple(a + b for a, b in zip(acc, terms))
                return acc

            acc = lax.fori_loop(0, (listed - 1) // NEAR_UNROLL, offset_body, acc)
            sums = [jnp.sum(part, axis=1, keepdims=True) for part in acc]
            tile = jnp.where(
                lane == 0, sums[0], jnp.where(lane == 1, sums[1], jnp.where(lane == 2, sums[2], sums[3]))
            )
            tile_ref[pl.ds(first, rows), :] = jnp.where(lane < 4, tile, 0.0)

        def full_body(chunk, carry2):
            chunk_at(pl.multiple_of(chunk * big, big), big)
            return carry2

        lax.fori_loop(0, full_count, full_body, 0)
        last = pl.multiple_of(full_count * big, small)

        middle = small + small // 2

        @pl.when(rest > middle)
        def _():
            chunk_at(last, big)

        @pl.when((rest > small) & (rest <= middle))
        def _():
            chunk_at(last, middle)

        @pl.when((rest > 0) & (rest <= small))
        def _():
            chunk_at(last, small)

        out_ref[leaf] = jnp.transpose(tile_ref[...])[0 : out_ref.shape[1], :]
        return carry

    lax.fori_loop(0, piece_leaves, leaf_body, 0)


def near_local(charged, rimmed, counts, near_flags):
    size_x, size_y, size_z, slot_count = charged.shape[1:]
    leaf_count = size_x * size_y * size_z
    ext_y = size_y + 2
    target = jnp.transpose(charged, (1, 2, 3, 4, 0)).reshape(leaf_count, slot_count, 4)
    source = jnp.transpose(rimmed, (1, 2, 3, 0, 4)).reshape(-1, 4, slot_count)
    source = jnp.pad(source, ((0, 1), (0, 4), (0, 0)))
    empty_leaf = source.shape[0] - 1
    offsets = [(0, 0, 0)] + leaf_offsets()
    shift_rows = np.array([[float(v) for v in offset] + [0.0] * 5 for offset in offsets], np.float32)
    shift_table = jnp.asarray(np.ascontiguousarray(np.broadcast_to(shift_rows[:, :, None], (len(offsets), 8, slot_count))))
    leaf_x = jnp.arange(size_x, dtype=jnp.int32)[:, None, None]
    leaf_y = jnp.arange(size_y, dtype=jnp.int32)[None, :, None]
    leaf_z = jnp.arange(size_z, dtype=jnp.int32)[None, None, :]
    places = []
    for offset in offsets:
        place = ((leaf_x + 1 + offset[0]) * ext_y + leaf_y + 1 + offset[1]) * size_z + leaf_z + offset[2]
        places.append(jnp.broadcast_to(place, (size_x, size_y, size_z)))
    places = jnp.stack(places).reshape(len(offsets), leaf_count)
    layer = jnp.arange(size_z, dtype=jnp.int32)
    valid = jnp.stack([((layer + offset[2] >= 0) & (layer + offset[2] < size_z)) for offset in offsets[1:]])
    active = (near_flags != 0) & valid[:, None, None, :]
    active = jnp.concatenate([jnp.ones((1, leaf_count), bool), active.reshape(len(offsets) - 1, leaf_count)])
    listed = jnp.sum(active.astype(jnp.int32), axis=0)
    listed = listed + (NEAR_UNROLL - (listed - 1) % NEAR_UNROLL) % NEAR_UNROLL
    position = jnp.cumsum(active.astype(jnp.int32), axis=0) - 1
    width = 1 + -(-(len(offsets) - 1) // NEAR_UNROLL) * NEAR_UNROLL
    slots = jnp.arange(width, dtype=jnp.int32)
    chosen = active[None] & (position[None] == slots[:, None, None])
    kinds = jnp.arange(len(offsets), dtype=jnp.int32)
    kind_list = jnp.sum(jnp.where(chosen, kinds[None, :, None], 0), axis=1)
    place_list = jnp.sum(jnp.where(chosen, places[None], 0), axis=1)
    place_list = jnp.where(slots[:, None] < jnp.sum(active.astype(jnp.int32), axis=0)[None], place_list, empty_leaf)
    table = jnp.concatenate(
        [counts.reshape(-1), listed, jnp.transpose(place_list).reshape(-1), jnp.transpose(kind_list).reshape(-1)]
    ).astype(jnp.int32)
    piece = leaf_count // NEAR_PIECES if leaf_count % NEAR_PIECES == 0 else leaf_count
    pairs = piece * slot_count * slot_count * 10

    chained = []

    def run_piece(number, gate):
        first_leaf = number * piece
        own = target[first_leaf : first_leaf + piece]
        if gate is not None:
            own, unused = lax.optimization_barrier((own, gate))
        operands = [table, own, source, shift_table] + chained[-1:]
        result = pl.pallas_call(
            functools.partial(near_kernel, first_leaf, piece, leaf_count, width),
            out_shape=jax.ShapeDtypeStruct((leaf_count, 8, slot_count), jnp.float32),
            in_specs=[pl.BlockSpec(memory_space=pltpu.SMEM)] + [pl.BlockSpec(memory_space=pltpu.VMEM)] * (len(operands) - 1),
            out_specs=pl.BlockSpec(memory_space=pltpu.VMEM),
            scratch_shapes=[pltpu.VMEM((slot_count, 128), jnp.float32)],
            input_output_aliases={4: 0} if chained else {},
            cost_estimate=pl.CostEstimate(
                flops=20 * pairs, transcendentals=pairs, bytes_accessed=8 * piece * slot_count * 128
            ),
        )(*operands)
        chained.append(result)
        return result

    def finish_near(outs):
        near = jnp.transpose(chained[-1][:, :4, :], (1, 0, 2))
        return near.reshape(4, size_x, size_y, size_z, slot_count)

    return leaf_count // piece, run_piece, finish_near


def body(
    atom_data,
    counts,
    near_flags,
    child_up,
    child_down,
    leaf_far,
    parent_far,
    column_up,
    column_down,
    tree_up,
    tree_down,
    tree_side,
    lattice,
):
    coef_count = lattice.shape[0]
    slot_count = atom_data.shape[4]
    size_x, size_y, size_z = (atom_data.shape[1], atom_data.shape[2], atom_data.shape[3])
    live_slots = (
        jnp.arange(slot_count, dtype=jnp.int32)[None, None, None, :] < counts[..., None]
    ).astype(jnp.float32)
    charged = jnp.concatenate([atom_data[:3], (atom_data[3] * live_slots)[None]], axis=0)
    waves = wave_table(coef_count, jnp.float32)
    half_count = waves.shape[1]
    moments = leaf_moments(charged, waves)
    parents = climb_children(moments, child_up.astype(jnp.float32))
    rimmed, parent_rim, leaf_rim = extended_joint([(charged, 1), (parents, 2), (moments, 1)], (("gx", 1), ("gy", 2)))
    parent_rim = jnp.pad(parent_rim, ((0, 0), (0, 0), (0, 0), (2, 2)))
    half_x, half_y, half_z = (parents.shape[1], parents.shape[2], parents.shape[3])
    phase_grid = block_phase(waves, half_x, half_y, half_z, jnp.float32)
    turned = jnp.sum(rotate_by(parents, phase_grid), axis=(1, 2, 3))
    column = matrix_vector(column_up.astype(jnp.float32), turned)
    piece_count, run_piece, finish_near = near_local(charged, rimmed, counts, near_flags)
    pieces = []

    sent = []

    def hook(value, prior):
        number = len(pieces)
        if number < piece_count:
            if number > 0:
                value, unused = lax.optimization_barrier((value, pieces[-1]))
            pieces.append(run_piece(number, prior))
        sent.append(value)
        return value

    column_local = chain_tree(column, tree_up, tree_down, tree_side, lattice, hook)
    while len(pieces) < piece_count:
        pieces.append(run_piece(len(pieces), sent[-1]))
    near_terms = finish_near(pieces)
    leaf_rim = jnp.pad(leaf_rim, ((0, 0), (0, 0), (0, 0), (1, 1)))
    lowered = matrix_vector(column_down.astype(jnp.float32), column_local)
    parent_local = rotate_by(
        jnp.broadcast_to(lowered[:, None, None, None], parents.shape), -phase_grid
    )
    far_parents = parent_offsets()
    parent_stack = jnp.stack(
        [
            parent_rim[
                :,
                2 + offset[0] : 2 + offset[0] + half_x,
                2 + offset[1] : 2 + offset[1] + half_y,
                2 + offset[2] : 2 + offset[2] + half_z,
            ]
            for offset in far_parents
        ]
    )
    parent_turns = offset_phases(waves, far_parents).reshape(len(far_parents), half_count, 1, 1, 1)
    parent_sum = jnp.sum(jax.vmap(rotate_by)(parent_stack, parent_turns), axis=0)
    parent_local = parent_local + jnp.einsum(
        "kj,jxyz->kxyz", parent_far.astype(jnp.float32), parent_sum, precision=highest
    )
    leaf_local = descend_children(parent_local, child_down.astype(jnp.float32))
    near_leaves = leaf_offsets()
    leaf_stack = jnp.stack(
        [
            leaf_rim[
                :,
                1 + offset[0] : 1 + offset[0] + size_x,
                1 + offset[1] : 1 + offset[1] + size_y,
                1 + offset[2] : 1 + offset[2] + size_z,
            ]
            for offset in near_leaves
        ]
    )
    leaf_stack = leaf_stack * (1.0 - near_flags.astype(jnp.float32))[:, None]
    leaf_turns = offset_phases(waves, near_leaves).reshape(len(near_leaves), half_count, 1, 1, 1)
    leaf_sum = jnp.sum(jax.vmap(rotate_by)(leaf_stack, leaf_turns), axis=0)
    leaf_local = leaf_local + jnp.einsum(
        "kj,jxyz->kxyz", leaf_far.astype(jnp.float32), leaf_sum, precision=highest
    )
    potential, field_parts = evaluate(charged, leaf_local, waves)
    return assemble(near_terms, potential, field_parts, charged[3], live_slots)


def solution(mesh):
    in_specs = (
        P(None, "gx", "gy", None, None),
        P("gx", "gy", None),
        P(None, "gx", "gy", None),
        P(),
        P(),
        P(),
        P(),
        P(),
        P(),
        P(),
        P(),
        P(),
        P(),
    )
    out_specs = P(None, "gx", "gy", None, None)
    return jax.shard_map(body, mesh=mesh, in_specs=in_specs, out_specs=out_specs, check_vma=False)
```

```python
import functools

import jax
import numpy as np
import jax.numpy as jnp
from jax import lax
from jax.experimental import pallas as pl
from jax.experimental.pallas import tpu as pltpu
from jax.sharding import PartitionSpec as P

soften = 0.04
coulomb = 0.1
highest = lax.Precision.HIGHEST


def from_partner(value, axis, bit):
    mask = 2**bit
    pairs = [(source, source ^ mask) for source in range(lax.axis_size(axis))]
    return lax.ppermute(value, axis, pairs)


def extended_2(block, sides, width):
    return extended_joint([(block, width)], sides)[0]


def extended_joint(parts, sides):
    blocks = [block for block, width in parts]
    for axis, dim in sides:
        count = lax.axis_size(axis)
        forward = [(i, i + 1) for i in range(count - 1)]
        forward.append((count - 1, 0))
        backward = [(target, source) for source, target in forward]
        lows = [lax.slice_in_dim(b, b.shape[dim] - w, None, axis=dim) for b, (_, w) in zip(blocks, parts)]
        highs = [lax.slice_in_dim(b, 0, w, axis=dim) for b, (_, w) in zip(blocks, parts)]
        sizes = [piece.size for piece in lows]
        low_all = lax.ppermute(jnp.concatenate([piece.reshape(-1) for piece in lows]), axis, forward)
        high_all = lax.ppermute(jnp.concatenate([piece.reshape(-1) for piece in highs]), axis, backward)
        grown = []
        place = 0
        for b, piece, size in zip(blocks, lows, sizes):
            low = low_all[place : place + size].reshape(piece.shape)
            high = high_all[place : place + size].reshape(piece.shape)
            place += size
            grown.append(jnp.concatenate([low, b, high], axis=dim))
        blocks = grown
    return blocks


def wave_table(coef_count, float_type):
    half_count = (coef_count - 1) // 2
    order_index = jnp.arange(1, half_count + 1, dtype=jnp.int32).astype(float_type)
    height = 1.0 - 2.0 * (order_index - 0.5) / half_count
    radius = jnp.sqrt(jnp.maximum(1.0 - height * height, 0.0))
    angle_turn = 2.399963 * order_index
    magnitude = 1.5 + jnp.mod(order_index, 3.0)
    return (
        jnp.stack([radius * jnp.cos(angle_turn), radius * jnp.sin(angle_turn), height])
        * magnitude[None]
    )


def waves_at(atom_data, waves):
    shape_lead = (waves.shape[1],) + (1,) * (atom_data.ndim - 1)
    phases = waves[0].reshape(shape_lead) * (atom_data[0] - 0.5)[None]
    phases = phases + waves[1].reshape(shape_lead) * (atom_data[1] - 0.5)[None]
    phases = phases + waves[2].reshape(shape_lead) * (atom_data[2] - 0.5)[None]
    return (jnp.cos(phases), jnp.sin(phases))


def rotate_by(field, phase):
    half_count = phase.shape[0]
    cosine = jnp.cos(phase)
    sine_part = jnp.sin(phase)
    cos_coef = field[1 : 1 + half_count]
    sin_coef = field[1 + half_count :]
    return jnp.concatenate(
        [
            field[0:1],
            cos_coef * cosine - sin_coef * sine_part,
            cos_coef * sine_part + sin_coef * cosine,
        ],
        axis=0,
    )


def offset_phases(waves, offsets):
    table = jnp.array(offsets, dtype=jnp.float32)
    return (
        table[:, 0:1] * waves[0][None]
        + table[:, 1:2] * waves[1][None]
        + table[:, 2:3] * waves[2][None]
    )


def block_phase(waves, size_x, size_y, size_z, float_type):
    place_x = jnp.arange(size_x, dtype=jnp.int32).astype(float_type)
    place_y = jnp.arange(size_y, dtype=jnp.int32).astype(float_type)
    place_z = jnp.arange(size_z, dtype=jnp.int32).astype(float_type)
    phase = waves[0][:, None, None, None] * place_x[None, :, None, None]
    phase = phase + waves[1][:, None, None, None] * place_y[None, None, :, None]
    return phase + waves[2][:, None, None, None] * place_z[None, None, None, :]


def leaf_moments(atom_data, waves):
    cosine, sine_part = waves_at(atom_data, waves)
    charge = atom_data[3]
    summed = jnp.sum(charge, axis=-1)[None]
    return jnp.concatenate(
        [
            summed,
            jnp.sum(cosine * charge[None], axis=-1),
            jnp.sum(sine_part * charge[None], axis=-1),
        ],
        axis=0,
    )


def evaluate(atom_data, local_exp, waves):
    cosine, sine_part = waves_at(atom_data, waves)
    half_count = waves.shape[1]
    cos_local = local_exp[1 : 1 + half_count][..., None]
    sin_local = local_exp[1 + half_count :][..., None]
    potential = local_exp[0][..., None] + jnp.sum(
        cos_local * cosine + sin_local * sine_part, axis=0
    )
    mixed_term = cos_local * sine_part - sin_local * cosine
    shape_lead = (half_count,) + (1,) * (mixed_term.ndim - 1)
    field_parts = [
        jnp.sum(waves[component].reshape(shape_lead) * mixed_term, axis=0) for component in range(3)
    ]
    return (potential, field_parts)


def near_row(target, source, flag_grid, shift_vec, keep_self):
    weight = source[3] * flag_grid[..., None]
    delta_x = target[0][..., :, None] - (source[0][..., None, :] + shift_vec[0])
    delta_y = target[1][..., :, None] - (source[1][..., None, :] + shift_vec[1])
    delta_z = target[2][..., :, None] - (source[2][..., None, :] + shift_vec[2])
    inverse = lax.rsqrt(delta_x * delta_x + delta_y * delta_y + delta_z * delta_z + soften)
    pair_term = weight[..., None, :] * keep_self * inverse
    cube_term = pair_term * inverse * inverse
    return jnp.stack(
        [
            jnp.sum(pair_term, axis=-1),
            jnp.sum(cube_term * delta_x, axis=-1),
            jnp.sum(cube_term * delta_y, axis=-1),
            jnp.sum(cube_term * delta_z, axis=-1),
        ]
    )


def full_flags(near_flags, float_type):
    flags_float = near_flags.astype(float_type)
    centre = jnp.ones((1,) + flags_float.shape[1:], float_type)
    return jnp.concatenate([flags_float[:13], centre, flags_float[13:]], axis=0)


def leaf_offsets():
    return [
        (shift_x, shift_y, shift_z)
        for shift_x in (-1, 0, 1)
        for shift_y in (-1, 0, 1)
        for shift_z in (-1, 0, 1)
        if (shift_x, shift_y, shift_z) != (0, 0, 0)
    ]


def parent_offsets():
    return [
        (shift_x, shift_y, shift_z)
        for shift_x in range(-2, 3)
        for shift_y in range(-2, 3)
        for shift_z in range(-2, 3)
        if max(abs(shift_x), abs(shift_y), abs(shift_z)) == 2
    ]


def climb_children(moments, matrices):
    coef_count, size_x, size_y, size_z = moments.shape
    parted = moments.reshape(coef_count, size_x // 2, 2, size_y // 2, 2, size_z // 2, 2)
    return jnp.einsum(
        "abckj,jxaybzc->kxyz",
        matrices.reshape(2, 2, 2, coef_count, coef_count),
        parted,
        precision=highest,
    )


def descend_children(parent_local, matrices):
    coef_count, size_x, size_y, size_z = parent_local.shape
    spread = jnp.einsum(
        "abckj,jxyz->kxaybzc",
        matrices.reshape(2, 2, 2, coef_count, coef_count),
        parent_local,
        precision=highest,
    )
    return spread.reshape(coef_count, 2 * size_x, 2 * size_y, 2 * size_z)


def matrix_vector(matrix, vector):
    return jnp.dot(matrix, vector, precision=highest)


def pick_side(matrices, own_side):
    return lax.dynamic_index_in_dim(matrices, own_side, 0, keepdims=False)


def pair_step(matrices, own_side, current, partner):
    return matrix_vector(pick_side(matrices, own_side), current) + matrix_vector(
        pick_side(matrices, 1 - own_side), partner
    )


def chain_tree(column, tree_up, tree_down, tree_side, lattice, hook):
    climbs = tree_up.astype(jnp.float32)
    lowers = tree_down.astype(jnp.float32)
    sideways = tree_side.astype(jnp.float32)
    current = column
    visited = []
    partner = None
    for level_bit in range(lax.axis_size("gx").bit_length() - 1):
        current = hook(current, partner)
        partner = from_partner(current, "gx", level_bit)
        own_side = lax.axis_index("gx") // 2**level_bit % 2
        current = pair_step(climbs[0], own_side, current, partner)
        visited.append((0, own_side, partner))
    for level_bit in range(lax.axis_size("gy").bit_length() - 1):
        current = hook(current, partner)
        partner = from_partner(current, "gy", level_bit)
        own_side = lax.axis_index("gy") // 2**level_bit % 2
        current = pair_step(climbs[1], own_side, current, partner)
        visited.append((1, own_side, partner))
    local_exp = matrix_vector(lattice.astype(jnp.float32), current)
    for axis_num, own_side, partner in reversed(visited):
        local_exp = matrix_vector(pick_side(lowers[axis_num], own_side), local_exp) + matrix_vector(
            pick_side(sideways[axis_num], own_side), partner
        )
    return local_exp


def flip_pair(column_grid, axis_num, level_bit):
    coef_count, size_x, size_y = column_grid.shape
    span_size = 2**level_bit
    if axis_num == 0:
        parted = column_grid.reshape(coef_count, size_x // (2 * span_size), 2, span_size, size_y)
        return parted[:, :, ::-1].reshape(column_grid.shape)
    parted = column_grid.reshape(coef_count, size_x, size_y // (2 * span_size), 2, span_size)
    return parted[:, :, :, ::-1].reshape(column_grid.shape)


def side_grid(axis_num, level_bit, size_x, size_y):
    positions = jnp.arange(size_x if axis_num == 0 else size_y, dtype=jnp.int32)
    own_side = positions // 2**level_bit % 2
    return own_side[:, None] if axis_num == 0 else own_side[None, :]


def choose_side(matrices, own_side, column_grid):
    first = jnp.einsum("kj,jxy->kxy", matrices[0], column_grid, precision=highest)
    second = jnp.einsum("kj,jxy->kxy", matrices[1], column_grid, precision=highest)
    return jnp.where(own_side[None] == 0, first, second)


def gathered_tree(column, tree_up, tree_down, tree_side, lattice):
    size_x, size_y = lax.axis_size("gx"), lax.axis_size("gy")
    gathered = lax.all_gather(column, ("gx", "gy")).reshape(size_x, size_y, -1)
    current = jnp.transpose(gathered, (2, 0, 1))
    levels = [(0, bit) for bit in range(size_x.bit_length() - 1)] + [
        (1, bit) for bit in range(size_y.bit_length() - 1)
    ]
    visited = []
    for axis_num, level_bit in levels:
        partner = flip_pair(current, axis_num, level_bit)
        own_side = side_grid(axis_num, level_bit, size_x, size_y)
        climbs = tree_up[axis_num].astype(jnp.float32)
        current = choose_side(climbs, own_side, current) + choose_side(climbs, 1 - own_side, partner)
        visited.append((axis_num, own_side, partner))
    local_exp = jnp.einsum("kj,jxy->kxy", lattice.astype(jnp.float32), current, precision=highest)
    for axis_num, own_side, partner in reversed(visited):
        local_exp = choose_side(tree_down[axis_num].astype(jnp.float32), own_side, local_exp) + choose_side(
            tree_side[axis_num].astype(jnp.float32), own_side, partner
        )
    own = lax.dynamic_slice(local_exp, (0, lax.axis_index("gx"), lax.axis_index("gy")), (local_exp.shape[0], 1, 1))
    return own.reshape(-1)


def assemble(near_terms, potential, field_parts, charge, live_slots):
    rows = [coulomb * (near_terms[0] + potential) * live_slots]
    for component in range(3):
        rows.append(coulomb * charge * (near_terms[1 + component] + field_parts[component]))
    return jnp.stack(rows)


NEAR_ROWS = 64
NEAR_PIECES = 8
NEAR_UNROLL = 2


def near_pairs(tx, ty, tz, srow, mask):
    weight = srow[3:4, :]
    delta_x = tx - srow[0:1, :]
    delta_y = ty - srow[1:2, :]
    delta_z = tz - srow[2:3, :]
    inverse = lax.rsqrt(delta_x * delta_x + delta_y * delta_y + delta_z * delta_z + soften)
    pair_term = weight * inverse
    if mask is not None:
        pair_term = jnp.where(mask, pair_term, 0.0)
    cube_term = pair_term * inverse * inverse
    return (pair_term, cube_term * delta_x, cube_term * delta_y, cube_term * delta_z)


def near_kernel(first_leaf, piece_leaves, leaf_count, listed_width, *refs):
    if len(refs) == 7:
        table_ref, target_ref, source_ref, shift_ref, previous_ref, out_ref, tile_ref = refs
        out_ref[...] = previous_ref[...]
    else:
        table_ref, target_ref, source_ref, shift_ref, out_ref, tile_ref = refs
        out_ref[...] = jnp.zeros(out_ref.shape, out_ref.dtype)
    place_start = 2 * leaf_count
    kind_start = place_start + leaf_count * listed_width
    big = NEAR_ROWS
    small = NEAR_ROWS // 2
    lanes = out_ref.shape[2]

    def leaf_body(local, carry):
        leaf = first_leaf + local
        count = table_ref[leaf]
        full_count = count // big
        rest = count - full_count * big
        listed = table_ref[leaf_count + leaf]
        base = leaf * listed_width
        tile_ref[...] = jnp.zeros(tile_ref.shape, tile_ref.dtype)

        def chunk_at(first, rows):
            lane = lax.broadcasted_iota(jnp.int32, (rows, lanes), 1)
            row = lax.broadcasted_iota(jnp.int32, (rows, lanes), 0)
            column = target_ref[local, pl.ds(first, rows), :]
            tx = jnp.broadcast_to(column[:, 0:1], (rows, lanes))
            ty = jnp.broadcast_to(column[:, 1:2], (rows, lanes))
            tz = jnp.broadcast_to(column[:, 2:3], (rows, lanes))
            acc = near_pairs(tx, ty, tz, source_ref[table_ref[place_start + base]], row + first != lane)

            def offset_body(step, acc):
                number = base + 1 + NEAR_UNROLL * step
                for extra in range(NEAR_UNROLL):
                    srow = source_ref[table_ref[place_start + number + extra]]
                    srow = srow + shift_ref[table_ref[kind_start + number + extra]]
                    terms = near_pairs(tx, ty, tz, srow, None)
                    acc = tuple(a + b for a, b in zip(acc, terms))
                return acc

            acc = lax.fori_loop(0, (listed - 1) // NEAR_UNROLL, offset_body, acc)
            sums = [jnp.sum(part, axis=1, keepdims=True) for part in acc]
            tile = jnp.where(
                lane == 0, sums[0], jnp.where(lane == 1, sums[1], jnp.where(lane == 2, sums[2], sums[3]))
            )
            tile_ref[pl.ds(first, rows), :] = jnp.where(lane < 4, tile, 0.0)

        def full_body(chunk, carry2):
            chunk_at(pl.multiple_of(chunk * big, big), big)
            return carry2

        lax.fori_loop(0, full_count, full_body, 0)
        last = pl.multiple_of(full_count * big, small)

        ladder = [small // 2, small, small + small // 4, small + small // 2, big - small // 4, big]
        for lower, upper in zip([0] + ladder[:-1], ladder):

            @pl.when((rest > lower) & (rest <= upper))
            def _(upper=upper):
                chunk_at(last, upper)

        out_ref[leaf] = jnp.transpose(tile_ref[...])[0 : out_ref.shape[1], :]
        return carry

    lax.fori_loop(0, piece_leaves, leaf_body, 0)


def near_local(charged, rimmed, counts, near_flags):
    size_x, size_y, size_z, slot_count = charged.shape[1:]
    leaf_count = size_x * size_y * size_z
    ext_y = size_y + 2
    target = jnp.transpose(charged, (1, 2, 3, 4, 0)).reshape(leaf_count, slot_count, 4)
    source = jnp.transpose(rimmed, (1, 2, 3, 0, 4)).reshape(-1, 4, slot_count)
    source = jnp.pad(source, ((0, 1), (0, 4), (0, 0)))
    empty_leaf = source.shape[0] - 1
    offsets = [(0, 0, 0)] + leaf_offsets()
    shift_rows = np.array([[float(v) for v in offset] + [0.0] * 5 for offset in offsets], np.float32)
    shift_table = jnp.asarray(np.ascontiguousarray(np.broadcast_to(shift_rows[:, :, None], (len(offsets), 8, slot_count))))
    leaf_x = jnp.arange(size_x, dtype=jnp.int32)[:, None, None]
    leaf_y = jnp.arange(size_y, dtype=jnp.int32)[None, :, None]
    leaf_z = jnp.arange(size_z, dtype=jnp.int32)[None, None, :]
    places = []
    for offset in offsets:
        place = ((leaf_x + 1 + offset[0]) * ext_y + leaf_y + 1 + offset[1]) * size_z + leaf_z + offset[2]
        places.append(jnp.broadcast_to(place, (size_x, size_y, size_z)))
    places = jnp.stack(places).reshape(len(offsets), leaf_count)
    layer = jnp.arange(size_z, dtype=jnp.int32)
    valid = jnp.stack([((layer + offset[2] >= 0) & (layer + offset[2] < size_z)) for offset in offsets[1:]])
    active = (near_flags != 0) & valid[:, None, None, :]
    active = jnp.concatenate([jnp.ones((1, leaf_count), bool), active.reshape(len(offsets) - 1, leaf_count)])
    listed = jnp.sum(active.astype(jnp.int32), axis=0)
    listed = listed + (NEAR_UNROLL - (listed - 1) % NEAR_UNROLL) % NEAR_UNROLL
    position = jnp.cumsum(active.astype(jnp.int32), axis=0) - 1
    width = 1 + -(-(len(offsets) - 1) // NEAR_UNROLL) * NEAR_UNROLL
    slots = jnp.arange(width, dtype=jnp.int32)
    chosen = active[None] & (position[None] == slots[:, None, None])
    kinds = jnp.arange(len(offsets), dtype=jnp.int32)
    kind_list = jnp.sum(jnp.where(chosen, kinds[None, :, None], 0), axis=1)
    place_list = jnp.sum(jnp.where(chosen, places[None], 0), axis=1)
    place_list = jnp.where(slots[:, None] < jnp.sum(active.astype(jnp.int32), axis=0)[None], place_list, empty_leaf)
    table = jnp.concatenate(
        [counts.reshape(-1), listed, jnp.transpose(place_list).reshape(-1), jnp.transpose(kind_list).reshape(-1)]
    ).astype(jnp.int32)
    piece = leaf_count // NEAR_PIECES if leaf_count % NEAR_PIECES == 0 else leaf_count
    pairs = piece * slot_count * slot_count * 10

    chained = []

    def run_piece(number, gate):
        first_leaf = number * piece
        own = target[first_leaf : first_leaf + piece]
        if gate is not None:
            own, unused = lax.optimization_barrier((own, gate))
        operands = [table, own, source, shift_table] + chained[-1:]
        result = pl.pallas_call(
            functools.partial(near_kernel, first_leaf, piece, leaf_count, width),
            out_shape=jax.ShapeDtypeStruct((leaf_count, 8, slot_count), jnp.float32),
            in_specs=[pl.BlockSpec(memory_space=pltpu.SMEM)] + [pl.BlockSpec(memory_space=pltpu.VMEM)] * (len(operands) - 1),
            out_specs=pl.BlockSpec(memory_space=pltpu.VMEM),
            scratch_shapes=[pltpu.VMEM((slot_count, 128), jnp.float32)],
            input_output_aliases={4: 0} if chained else {},
            cost_estimate=pl.CostEstimate(
                flops=20 * pairs, transcendentals=pairs, bytes_accessed=8 * piece * slot_count * 128
            ),
        )(*operands)
        chained.append(result)
        return result

    def finish_near(outs):
        near = jnp.transpose(chained[-1][:, :4, :], (1, 0, 2))
        return near.reshape(4, size_x, size_y, size_z, slot_count)

    return leaf_count // piece, run_piece, finish_near


def body(
    atom_data,
    counts,
    near_flags,
    child_up,
    child_down,
    leaf_far,
    parent_far,
    column_up,
    column_down,
    tree_up,
    tree_down,
    tree_side,
    lattice,
):
    coef_count = lattice.shape[0]
    slot_count = atom_data.shape[4]
    size_x, size_y, size_z = (atom_data.shape[1], atom_data.shape[2], atom_data.shape[3])
    live_slots = (
        jnp.arange(slot_count, dtype=jnp.int32)[None, None, None, :] < counts[..., None]
    ).astype(jnp.float32)
    charged = jnp.concatenate([atom_data[:3], (atom_data[3] * live_slots)[None]], axis=0)
    waves = wave_table(coef_count, jnp.float32)
    half_count = waves.shape[1]
    moments = leaf_moments(charged, waves)
    parents = climb_children(moments, child_up.astype(jnp.float32))
    rimmed, parent_rim, leaf_rim = extended_joint([(charged, 1), (parents, 2), (moments, 1)], (("gx", 1), ("gy", 2)))
    parent_rim = jnp.pad(parent_rim, ((0, 0), (0, 0), (0, 0), (2, 2)))
    half_x, half_y, half_z = (parents.shape[1], parents.shape[2], parents.shape[3])
    phase_grid = block_phase(waves, half_x, half_y, half_z, jnp.float32)
    turned = jnp.sum(rotate_by(parents, phase_grid), axis=(1, 2, 3))
    column = matrix_vector(column_up.astype(jnp.float32), turned)
    piece_count, run_piece, finish_near = near_local(charged, rimmed, counts, near_flags)
    pieces = []

    sent = []

    def hook(value, prior):
        number = len(pieces)
        if number < piece_count:
            if number > 0:
                value, unused = lax.optimization_barrier((value, pieces[-1]))
            pieces.append(run_piece(number, prior))
        sent.append(value)
        return value

    column_local = chain_tree(column, tree_up, tree_down, tree_side, lattice, hook)
    while len(pieces) < piece_count:
        pieces.append(run_piece(len(pieces), sent[-1]))
    near_terms = finish_near(pieces)
    leaf_rim = jnp.pad(leaf_rim, ((0, 0), (0, 0), (0, 0), (1, 1)))
    lowered = matrix_vector(column_down.astype(jnp.float32), column_local)
    parent_local = rotate_by(
        jnp.broadcast_to(lowered[:, None, None, None], parents.shape), -phase_grid
    )
    far_parents = parent_offsets()
    parent_stack = jnp.stack(
        [
            parent_rim[
                :,
                2 + offset[0] : 2 + offset[0] + half_x,
                2 + offset[1] : 2 + offset[1] + half_y,
                2 + offset[2] : 2 + offset[2] + half_z,
            ]
            for offset in far_parents
        ]
    )
    parent_turns = offset_phases(waves, far_parents).reshape(len(far_parents), half_count, 1, 1, 1)
    parent_sum = jnp.sum(jax.vmap(rotate_by)(parent_stack, parent_turns), axis=0)
    parent_local = parent_local + jnp.einsum(
        "kj,jxyz->kxyz", parent_far.astype(jnp.float32), parent_sum, precision=highest
    )
    leaf_local = descend_children(parent_local, child_down.astype(jnp.float32))
    near_leaves = leaf_offsets()
    leaf_stack = jnp.stack(
        [
            leaf_rim[
                :,
                1 + offset[0] : 1 + offset[0] + size_x,
                1 + offset[1] : 1 + offset[1] + size_y,
                1 + offset[2] : 1 + offset[2] + size_z,
            ]
            for offset in near_leaves
        ]
    )
    leaf_stack = leaf_stack * (1.0 - near_flags.astype(jnp.float32))[:, None]
    leaf_turns = offset_phases(waves, near_leaves).reshape(len(near_leaves), half_count, 1, 1, 1)
    leaf_sum = jnp.sum(jax.vmap(rotate_by)(leaf_stack, leaf_turns), axis=0)
    leaf_local = leaf_local + jnp.einsum(
        "kj,jxyz->kxyz", leaf_far.astype(jnp.float32), leaf_sum, precision=highest
    )
    potential, field_parts = evaluate(charged, leaf_local, waves)
    return assemble(near_terms, potential, field_parts, charged[3], live_slots)


def solution(mesh):
    in_specs = (
        P(None, "gx", "gy", None, None),
        P("gx", "gy", None),
        P(None, "gx", "gy", None),
        P(),
        P(),
        P(),
        P(),
        P(),
        P(),
        P(),
        P(),
        P(),
        P(),
    )
    out_specs = P(None, "gx", "gy", None, None)
    return jax.shard_map(body, mesh=mesh, in_specs=in_specs, out_specs=out_specs, check_vma=False)
```

```python
import functools

import jax
import numpy as np
import jax.numpy as jnp
from jax import lax
from jax.experimental import pallas as pl
from jax.experimental.pallas import tpu as pltpu
from jax.sharding import PartitionSpec as P

soften = 0.04
coulomb = 0.1
highest = lax.Precision.HIGHEST


def from_partner(value, axis, bit):
    mask = 2**bit
    pairs = [(source, source ^ mask) for source in range(lax.axis_size(axis))]
    return lax.ppermute(value, axis, pairs)


def extended_2(block, sides, width):
    return extended_joint([(block, width)], sides)[0]


def extended_joint(parts, sides):
    blocks = [block for block, width in parts]
    for axis, dim in sides:
        count = lax.axis_size(axis)
        forward = [(i, i + 1) for i in range(count - 1)]
        forward.append((count - 1, 0))
        backward = [(target, source) for source, target in forward]
        lows = [lax.slice_in_dim(b, b.shape[dim] - w, None, axis=dim) for b, (_, w) in zip(blocks, parts)]
        highs = [lax.slice_in_dim(b, 0, w, axis=dim) for b, (_, w) in zip(blocks, parts)]
        sizes = [piece.size for piece in lows]
        low_all = lax.ppermute(jnp.concatenate([piece.reshape(-1) for piece in lows]), axis, forward)
        high_all = lax.ppermute(jnp.concatenate([piece.reshape(-1) for piece in highs]), axis, backward)
        grown = []
        place = 0
        for b, piece, size in zip(blocks, lows, sizes):
            low = low_all[place : place + size].reshape(piece.shape)
            high = high_all[place : place + size].reshape(piece.shape)
            place += size
            grown.append(jnp.concatenate([low, b, high], axis=dim))
        blocks = grown
    return blocks


def wave_table(coef_count, float_type):
    half_count = (coef_count - 1) // 2
    order_index = jnp.arange(1, half_count + 1, dtype=jnp.int32).astype(float_type)
    height = 1.0 - 2.0 * (order_index - 0.5) / half_count
    radius = jnp.sqrt(jnp.maximum(1.0 - height * height, 0.0))
    angle_turn = 2.399963 * order_index
    magnitude = 1.5 + jnp.mod(order_index, 3.0)
    return (
        jnp.stack([radius * jnp.cos(angle_turn), radius * jnp.sin(angle_turn), height])
        * magnitude[None]
    )


def waves_at(atom_data, waves):
    shape_lead = (waves.shape[1],) + (1,) * (atom_data.ndim - 1)
    phases = waves[0].reshape(shape_lead) * (atom_data[0] - 0.5)[None]
    phases = phases + waves[1].reshape(shape_lead) * (atom_data[1] - 0.5)[None]
    phases = phases + waves[2].reshape(shape_lead) * (atom_data[2] - 0.5)[None]
    return (jnp.cos(phases), jnp.sin(phases))


def rotate_by(field, phase):
    half_count = phase.shape[0]
    cosine = jnp.cos(phase)
    sine_part = jnp.sin(phase)
    cos_coef = field[1 : 1 + half_count]
    sin_coef = field[1 + half_count :]
    return jnp.concatenate(
        [
            field[0:1],
            cos_coef * cosine - sin_coef * sine_part,
            cos_coef * sine_part + sin_coef * cosine,
        ],
        axis=0,
    )


def offset_phases(waves, offsets):
    table = jnp.array(offsets, dtype=jnp.float32)
    return (
        table[:, 0:1] * waves[0][None]
        + table[:, 1:2] * waves[1][None]
        + table[:, 2:3] * waves[2][None]
    )


def block_phase(waves, size_x, size_y, size_z, float_type):
    place_x = jnp.arange(size_x, dtype=jnp.int32).astype(float_type)
    place_y = jnp.arange(size_y, dtype=jnp.int32).astype(float_type)
    place_z = jnp.arange(size_z, dtype=jnp.int32).astype(float_type)
    phase = waves[0][:, None, None, None] * place_x[None, :, None, None]
    phase = phase + waves[1][:, None, None, None] * place_y[None, None, :, None]
    return phase + waves[2][:, None, None, None] * place_z[None, None, None, :]


def leaf_moments(atom_data, waves):
    cosine, sine_part = waves_at(atom_data, waves)
    charge = atom_data[3]
    summed = jnp.sum(charge, axis=-1)[None]
    return jnp.concatenate(
        [
            summed,
            jnp.sum(cosine * charge[None], axis=-1),
            jnp.sum(sine_part * charge[None], axis=-1),
        ],
        axis=0,
    )


def evaluate(atom_data, local_exp, waves):
    cosine, sine_part = waves_at(atom_data, waves)
    half_count = waves.shape[1]
    cos_local = local_exp[1 : 1 + half_count][..., None]
    sin_local = local_exp[1 + half_count :][..., None]
    potential = local_exp[0][..., None] + jnp.sum(
        cos_local * cosine + sin_local * sine_part, axis=0
    )
    mixed_term = cos_local * sine_part - sin_local * cosine
    shape_lead = (half_count,) + (1,) * (mixed_term.ndim - 1)
    field_parts = [
        jnp.sum(waves[component].reshape(shape_lead) * mixed_term, axis=0) for component in range(3)
    ]
    return (potential, field_parts)


def near_row(target, source, flag_grid, shift_vec, keep_self):
    weight = source[3] * flag_grid[..., None]
    delta_x = target[0][..., :, None] - (source[0][..., None, :] + shift_vec[0])
    delta_y = target[1][..., :, None] - (source[1][..., None, :] + shift_vec[1])
    delta_z = target[2][..., :, None] - (source[2][..., None, :] + shift_vec[2])
    inverse = lax.rsqrt(delta_x * delta_x + delta_y * delta_y + delta_z * delta_z + soften)
    pair_term = weight[..., None, :] * keep_self * inverse
    cube_term = pair_term * inverse * inverse
    return jnp.stack(
        [
            jnp.sum(pair_term, axis=-1),
            jnp.sum(cube_term * delta_x, axis=-1),
            jnp.sum(cube_term * delta_y, axis=-1),
            jnp.sum(cube_term * delta_z, axis=-1),
        ]
    )


def full_flags(near_flags, float_type):
    flags_float = near_flags.astype(float_type)
    centre = jnp.ones((1,) + flags_float.shape[1:], float_type)
    return jnp.concatenate([flags_float[:13], centre, flags_float[13:]], axis=0)


def leaf_offsets():
    return [
        (shift_x, shift_y, shift_z)
        for shift_x in (-1, 0, 1)
        for shift_y in (-1, 0, 1)
        for shift_z in (-1, 0, 1)
        if (shift_x, shift_y, shift_z) != (0, 0, 0)
    ]


def parent_offsets():
    return [
        (shift_x, shift_y, shift_z)
        for shift_x in range(-2, 3)
        for shift_y in range(-2, 3)
        for shift_z in range(-2, 3)
        if max(abs(shift_x), abs(shift_y), abs(shift_z)) == 2
    ]


def climb_children(moments, matrices):
    coef_count, size_x, size_y, size_z = moments.shape
    parted = moments.reshape(coef_count, size_x // 2, 2, size_y // 2, 2, size_z // 2, 2)
    return jnp.einsum(
        "abckj,jxaybzc->kxyz",
        matrices.reshape(2, 2, 2, coef_count, coef_count),
        parted,
        precision=highest,
    )


def descend_children(parent_local, matrices):
    coef_count, size_x, size_y, size_z = parent_local.shape
    spread = jnp.einsum(
        "abckj,jxyz->kxaybzc",
        matrices.reshape(2, 2, 2, coef_count, coef_count),
        parent_local,
        precision=highest,
    )
    return spread.reshape(coef_count, 2 * size_x, 2 * size_y, 2 * size_z)


def matrix_vector(matrix, vector):
    return jnp.dot(matrix, vector, precision=highest)


def pick_side(matrices, own_side):
    return lax.dynamic_index_in_dim(matrices, own_side, 0, keepdims=False)


def pair_step(matrices, own_side, current, partner):
    return matrix_vector(pick_side(matrices, own_side), current) + matrix_vector(
        pick_side(matrices, 1 - own_side), partner
    )


def chain_tree(column, tree_up, tree_down, tree_side, lattice, hook):
    climbs = tree_up.astype(jnp.float32)
    lowers = tree_down.astype(jnp.float32)
    sideways = tree_side.astype(jnp.float32)
    current = column
    visited = []
    partner = None
    for level_bit in range(lax.axis_size("gx").bit_length() - 1):
        current = hook(current, partner)
        partner = from_partner(current, "gx", level_bit)
        own_side = lax.axis_index("gx") // 2**level_bit % 2
        current = pair_step(climbs[0], own_side, current, partner)
        visited.append((0, own_side, partner))
    for level_bit in range(lax.axis_size("gy").bit_length() - 1):
        current = hook(current, partner)
        partner = from_partner(current, "gy", level_bit)
        own_side = lax.axis_index("gy") // 2**level_bit % 2
        current = pair_step(climbs[1], own_side, current, partner)
        visited.append((1, own_side, partner))
    local_exp = matrix_vector(lattice.astype(jnp.float32), current)
    for axis_num, own_side, partner in reversed(visited):
        local_exp = matrix_vector(pick_side(lowers[axis_num], own_side), local_exp) + matrix_vector(
            pick_side(sideways[axis_num], own_side), partner
        )
    return local_exp


def flip_pair(column_grid, axis_num, level_bit):
    coef_count, size_x, size_y = column_grid.shape
    span_size = 2**level_bit
    if axis_num == 0:
        parted = column_grid.reshape(coef_count, size_x // (2 * span_size), 2, span_size, size_y)
        return parted[:, :, ::-1].reshape(column_grid.shape)
    parted = column_grid.reshape(coef_count, size_x, size_y // (2 * span_size), 2, span_size)
    return parted[:, :, :, ::-1].reshape(column_grid.shape)


def side_grid(axis_num, level_bit, size_x, size_y):
    positions = jnp.arange(size_x if axis_num == 0 else size_y, dtype=jnp.int32)
    own_side = positions // 2**level_bit % 2
    return own_side[:, None] if axis_num == 0 else own_side[None, :]


def choose_side(matrices, own_side, column_grid):
    first = jnp.einsum("kj,jxy->kxy", matrices[0], column_grid, precision=highest)
    second = jnp.einsum("kj,jxy->kxy", matrices[1], column_grid, precision=highest)
    return jnp.where(own_side[None] == 0, first, second)


def gathered_tree(column, tree_up, tree_down, tree_side, lattice):
    size_x, size_y = lax.axis_size("gx"), lax.axis_size("gy")
    gathered = lax.all_gather(column, ("gx", "gy")).reshape(size_x, size_y, -1)
    current = jnp.transpose(gathered, (2, 0, 1))
    levels = [(0, bit) for bit in range(size_x.bit_length() - 1)] + [
        (1, bit) for bit in range(size_y.bit_length() - 1)
    ]
    visited = []
    for axis_num, level_bit in levels:
        partner = flip_pair(current, axis_num, level_bit)
        own_side = side_grid(axis_num, level_bit, size_x, size_y)
        climbs = tree_up[axis_num].astype(jnp.float32)
        current = choose_side(climbs, own_side, current) + choose_side(climbs, 1 - own_side, partner)
        visited.append((axis_num, own_side, partner))
    local_exp = jnp.einsum("kj,jxy->kxy", lattice.astype(jnp.float32), current, precision=highest)
    for axis_num, own_side, partner in reversed(visited):
        local_exp = choose_side(tree_down[axis_num].astype(jnp.float32), own_side, local_exp) + choose_side(
            tree_side[axis_num].astype(jnp.float32), own_side, partner
        )
    own = lax.dynamic_slice(local_exp, (0, lax.axis_index("gx"), lax.axis_index("gy")), (local_exp.shape[0], 1, 1))
    return own.reshape(-1)


def assemble(near_terms, potential, field_parts, charge, live_slots):
    rows = [coulomb * (near_terms[0] + potential) * live_slots]
    for component in range(3):
        rows.append(coulomb * charge * (near_terms[1 + component] + field_parts[component]))
    return jnp.stack(rows)


NEAR_ROWS = 64
NEAR_PIECES = 8
NEAR_UNROLL = 2


def near_pairs(tx, ty, tz, srow, mask):
    weight = srow[3:4, :]
    delta_x = tx - srow[0:1, :]
    delta_y = ty - srow[1:2, :]
    delta_z = tz - srow[2:3, :]
    inverse = lax.rsqrt(delta_x * delta_x + delta_y * delta_y + delta_z * delta_z + soften)
    pair_term = weight * inverse
    if mask is not None:
        pair_term = jnp.where(mask, pair_term, 0.0)
    cube_term = pair_term * inverse * inverse
    return (pair_term, cube_term * delta_x, cube_term * delta_y, cube_term * delta_z)


def near_kernel(first_leaf, piece_leaves, leaf_count, listed_width, *refs):
    if len(refs) == 7:
        table_ref, target_ref, source_ref, shift_ref, previous_ref, out_ref, tile_ref = refs
        out_ref[...] = previous_ref[...]
    else:
        table_ref, target_ref, source_ref, shift_ref, out_ref, tile_ref = refs
        out_ref[...] = jnp.zeros(out_ref.shape, out_ref.dtype)
    place_start = 2 * leaf_count
    kind_start = place_start + leaf_count * listed_width
    big = NEAR_ROWS
    small = NEAR_ROWS // 2
    lanes = out_ref.shape[2]

    def leaf_body(local, carry):
        leaf = first_leaf + local
        count = table_ref[leaf]
        full_count = count // big
        rest = count - full_count * big
        listed = table_ref[leaf_count + leaf]
        base = leaf * listed_width
        tile_ref[...] = jnp.zeros(tile_ref.shape, tile_ref.dtype)

        def chunk_at(first, rows):
            lane = lax.broadcasted_iota(jnp.int32, (rows, lanes), 1)
            row = lax.broadcasted_iota(jnp.int32, (rows, lanes), 0)
            column = target_ref[local, pl.ds(first, rows), :]
            tx = jnp.broadcast_to(column[:, 0:1], (rows, lanes))
            ty = jnp.broadcast_to(column[:, 1:2], (rows, lanes))
            tz = jnp.broadcast_to(column[:, 2:3], (rows, lanes))
            acc = near_pairs(tx, ty, tz, source_ref[table_ref[place_start + base]], row + first != lane)

            def offset_body(step, acc):
                number = base + 1 + NEAR_UNROLL * step
                for extra in range(NEAR_UNROLL):
                    srow = source_ref[table_ref[place_start + number + extra]]
                    srow = srow + shift_ref[table_ref[kind_start + number + extra]]
                    terms = near_pairs(tx, ty, tz, srow, None)
                    acc = tuple(a + b for a, b in zip(acc, terms))
                return acc

            acc = lax.fori_loop(0, (listed - 1) // NEAR_UNROLL, offset_body, acc)
            sums = [jnp.sum(part, axis=1, keepdims=True) for part in acc]
            tile = jnp.where(
                lane == 0, sums[0], jnp.where(lane == 1, sums[1], jnp.where(lane == 2, sums[2], sums[3]))
            )
            tile_ref[pl.ds(first, rows), :] = jnp.where(lane < 4, tile, 0.0)

        def full_body(chunk, carry2):
            chunk_at(pl.multiple_of(chunk * big, big), big)
            return carry2

        lax.fori_loop(0, full_count, full_body, 0)
        last = pl.multiple_of(full_count * big, small)

        ladder = [small, small + small // 4, small + small // 2, big - small // 4, big]
        for lower, upper in zip([0] + ladder[:-1], ladder):

            @pl.when((rest > lower) & (rest <= upper))
            def _(upper=upper):
                chunk_at(last, upper)

        out_ref[leaf] = jnp.transpose(tile_ref[...])[0 : out_ref.shape[1], :]
        return carry

    lax.fori_loop(0, piece_leaves, leaf_body, 0)


def near_local(charged, rimmed, counts, near_flags):
    size_x, size_y, size_z, slot_count = charged.shape[1:]
    leaf_count = size_x * size_y * size_z
    ext_y = size_y + 2
    target = jnp.transpose(charged, (1, 2, 3, 4, 0)).reshape(leaf_count, slot_count, 4)
    source = jnp.transpose(rimmed, (1, 2, 3, 0, 4)).reshape(-1, 4, slot_count)
    source = jnp.pad(source, ((0, 1), (0, 4), (0, 0)))
    empty_leaf = source.shape[0] - 1
    offsets = [(0, 0, 0)] + leaf_offsets()
    shift_rows = np.array([[float(v) for v in offset] + [0.0] * 5 for offset in offsets], np.float32)
    shift_table = jnp.asarray(np.ascontiguousarray(np.broadcast_to(shift_rows[:, :, None], (len(offsets), 8, slot_count))))
    leaf_x = jnp.arange(size_x, dtype=jnp.int32)[:, None, None]
    leaf_y = jnp.arange(size_y, dtype=jnp.int32)[None, :, None]
    leaf_z = jnp.arange(size_z, dtype=jnp.int32)[None, None, :]
    places = []
    for offset in offsets:
        place = ((leaf_x + 1 + offset[0]) * ext_y + leaf_y + 1 + offset[1]) * size_z + leaf_z + offset[2]
        places.append(jnp.broadcast_to(place, (size_x, size_y, size_z)))
    places = jnp.stack(places).reshape(len(offsets), leaf_count)
    layer = jnp.arange(size_z, dtype=jnp.int32)
    valid = jnp.stack([((layer + offset[2] >= 0) & (layer + offset[2] < size_z)) for offset in offsets[1:]])
    active = (near_flags != 0) & valid[:, None, None, :]
    active = jnp.concatenate([jnp.ones((1, leaf_count), bool), active.reshape(len(offsets) - 1, leaf_count)])
    listed = jnp.sum(active.astype(jnp.int32), axis=0)
    listed = listed + (NEAR_UNROLL - (listed - 1) % NEAR_UNROLL) % NEAR_UNROLL
    position = jnp.cumsum(active.astype(jnp.int32), axis=0) - 1
    width = 1 + -(-(len(offsets) - 1) // NEAR_UNROLL) * NEAR_UNROLL
    slots = jnp.arange(width, dtype=jnp.int32)
    chosen = active[None] & (position[None] == slots[:, None, None])
    kinds = jnp.arange(len(offsets), dtype=jnp.int32)
    kind_list = jnp.sum(jnp.where(chosen, kinds[None, :, None], 0), axis=1)
    place_list = jnp.sum(jnp.where(chosen, places[None], 0), axis=1)
    place_list = jnp.where(slots[:, None] < jnp.sum(active.astype(jnp.int32), axis=0)[None], place_list, empty_leaf)
    table = jnp.concatenate(
        [counts.reshape(-1), listed, jnp.transpose(place_list).reshape(-1), jnp.transpose(kind_list).reshape(-1)]
    ).astype(jnp.int32)
    piece = leaf_count // NEAR_PIECES if leaf_count % NEAR_PIECES == 0 else leaf_count
    pairs = piece * slot_count * slot_count * 10

    chained = []

    def run_piece(number, gate):
        first_leaf = number * piece
        own = target[first_leaf : first_leaf + piece]
        if gate is not None:
            own, unused = lax.optimization_barrier((own, gate))
        operands = [table, own, source, shift_table] + chained[-1:]
        result = pl.pallas_call(
            functools.partial(near_kernel, first_leaf, piece, leaf_count, width),
            out_shape=jax.ShapeDtypeStruct((leaf_count, 8, slot_count), jnp.float32),
            in_specs=[pl.BlockSpec(memory_space=pltpu.SMEM)] + [pl.BlockSpec(memory_space=pltpu.VMEM)] * (len(operands) - 1),
            out_specs=pl.BlockSpec(memory_space=pltpu.VMEM),
            scratch_shapes=[pltpu.VMEM((slot_count, 128), jnp.float32)],
            input_output_aliases={4: 0} if chained else {},
            cost_estimate=pl.CostEstimate(
                flops=20 * pairs, transcendentals=pairs, bytes_accessed=8 * piece * slot_count * 128
            ),
        )(*operands)
        chained.append(result)
        return result

    def finish_near(outs):
        near = jnp.transpose(chained[-1][:, :4, :], (1, 0, 2))
        return near.reshape(4, size_x, size_y, size_z, slot_count)

    return leaf_count // piece, run_piece, finish_near


def body(
    atom_data,
    counts,
    near_flags,
    child_up,
    child_down,
    leaf_far,
    parent_far,
    column_up,
    column_down,
    tree_up,
    tree_down,
    tree_side,
    lattice,
):
    coef_count = lattice.shape[0]
    slot_count = atom_data.shape[4]
    size_x, size_y, size_z = (atom_data.shape[1], atom_data.shape[2], atom_data.shape[3])
    live_slots = (
        jnp.arange(slot_count, dtype=jnp.int32)[None, None, None, :] < counts[..., None]
    ).astype(jnp.float32)
    charged = jnp.concatenate([atom_data[:3], (atom_data[3] * live_slots)[None]], axis=0)
    waves = wave_table(coef_count, jnp.float32)
    half_count = waves.shape[1]
    moments = leaf_moments(charged, waves)
    parents = climb_children(moments, child_up.astype(jnp.float32))
    rimmed, parent_rim, leaf_rim = extended_joint([(charged, 1), (parents, 2), (moments, 1)], (("gx", 1), ("gy", 2)))
    parent_rim = jnp.pad(parent_rim, ((0, 0), (0, 0), (0, 0), (2, 2)))
    half_x, half_y, half_z = (parents.shape[1], parents.shape[2], parents.shape[3])
    phase_grid = block_phase(waves, half_x, half_y, half_z, jnp.float32)
    turned = jnp.sum(rotate_by(parents, phase_grid), axis=(1, 2, 3))
    column = matrix_vector(column_up.astype(jnp.float32), turned)
    piece_count, run_piece, finish_near = near_local(charged, rimmed, counts, near_flags)
    pieces = []

    sent = []

    def hook(value, prior):
        number = len(pieces)
        if number < piece_count:
            if number > 0:
                value, unused = lax.optimization_barrier((value, pieces[-1]))
            pieces.append(run_piece(number, prior))
        sent.append(value)
        return value

    column_local = chain_tree(column, tree_up, tree_down, tree_side, lattice, hook)
    while len(pieces) < piece_count:
        pieces.append(run_piece(len(pieces), sent[-1]))
    near_terms = finish_near(pieces)
    leaf_rim = jnp.pad(leaf_rim, ((0, 0), (0, 0), (0, 0), (1, 1)))
    lowered = matrix_vector(column_down.astype(jnp.float32), column_local)
    parent_local = rotate_by(
        jnp.broadcast_to(lowered[:, None, None, None], parents.shape), -phase_grid
    )
    far_parents = parent_offsets()
    parent_stack = jnp.stack(
        [
            parent_rim[
                :,
                2 + offset[0] : 2 + offset[0] + half_x,
                2 + offset[1] : 2 + offset[1] + half_y,
                2 + offset[2] : 2 + offset[2] + half_z,
            ]
            for offset in far_parents
        ]
    )
    parent_turns = offset_phases(waves, far_parents).reshape(len(far_parents), half_count, 1, 1, 1)
    parent_sum = jnp.sum(jax.vmap(rotate_by)(parent_stack, parent_turns), axis=0)
    parent_local = parent_local + jnp.einsum(
        "kj,jxyz->kxyz", parent_far.astype(jnp.float32), parent_sum, precision=highest
    )
    leaf_local = descend_children(parent_local, child_down.astype(jnp.float32))
    near_leaves = leaf_offsets()
    leaf_stack = jnp.stack(
        [
            leaf_rim[
                :,
                1 + offset[0] : 1 + offset[0] + size_x,
                1 + offset[1] : 1 + offset[1] + size_y,
                1 + offset[2] : 1 + offset[2] + size_z,
            ]
            for offset in near_leaves
        ]
    )
    leaf_stack = leaf_stack * (1.0 - near_flags.astype(jnp.float32))[:, None]
    leaf_turns = offset_phases(waves, near_leaves).reshape(len(near_leaves), half_count, 1, 1, 1)
    leaf_sum = jnp.sum(jax.vmap(rotate_by)(leaf_stack, leaf_turns), axis=0)
    leaf_local = leaf_local + jnp.einsum(
        "kj,jxyz->kxyz", leaf_far.astype(jnp.float32), leaf_sum, precision=highest
    )
    potential, field_parts = evaluate(charged, leaf_local, waves)
    return assemble(near_terms, potential, field_parts, charged[3], live_slots)


def solution(mesh):
    in_specs = (
        P(None, "gx", "gy", None, None),
        P("gx", "gy", None),
        P(None, "gx", "gy", None),
        P(),
        P(),
        P(),
        P(),
        P(),
        P(),
        P(),
        P(),
        P(),
        P(),
    )
    out_specs = P(None, "gx", "gy", None, None)
    return jax.shard_map(body, mesh=mesh, in_specs=in_specs, out_specs=out_specs, check_vma=False)
```
